128 devices in a mesh: shot: 16 (over z, x_lo, core), brick: 8 (over y, x_hi).
Axes of the slice: x: 4 (x_hi: 2, x_lo: 2; x = x_hi * 2 + x_lo), y: 4, z: 4, core: 2. Of those that a mesh axis runs over, the one named last changes fastest.
Arguments:
- sources: float32 [16, 2, 2, 256, 64, 256], P('shot', None, None, None, 'brick'), may hold values from -24 to 24
- slowness: float32 [16, 256, 64, 256], P('shot', None, 'brick'), may hold values from 0.5 to 2
- group_size: int32 [16], replicated, may hold values from 2 to 8, as said below
- window_anchor: int32 [16], replicated, may hold values from 0 to 56
- tile_slot: int32 [64], replicated, may hold values from 0 to 63, each once
Outputs:
- gradient: float32 [8, 64, 65536], P('brick', 'shot')
The draws below stay inside these ranges and needn't reach their ends.
Inputs may be any that keep to these rules, and one draw needn't show every extreme that they name: `group_size`: some shot spans all 8 bricks and some shot only 2. Window s covers model tiles window_anchor[s] to window_anchor[s] + 7. `tile_slot`: each slot of 0 to 63 once.
All inputs are finite; a program needn't handle non-finite values.
Results may differ from the reference program's by a relative error of at most 0.0003.
Values sent between devices are 32-bit elements; how exact they have to be, the bound alone decides.
No kernel may reach another device: no remote copies, remote signals or barrier semaphores. Data moves between devices by JAX's collectives and lax.ppermute only.
A program may use at most 128 MiB of HBM per device.

```python
import math
import jax
import jax.numpy as jnp
from jax import lax

PLANES = 8
WIDE_Y = 256
WIDE_Z = 256
BLOCKS = 8
SWEEPS = 2
SHOTS = 16
BANDS = 8
DEPTH = 64
TILES = 64
TILE_CELLS = 65536


def draw_group_size(key, part):
    shot_order = jax.random.permutation(jax.random.fold_in(key, 11), SHOTS)
    bricks_used = jax.random.randint(jax.random.fold_in(key, 12), (SHOTS,), 2, BANDS + 1, dtype=jnp.int32)
    bricks_used = bricks_used.at[shot_order[0]].set(BANDS)
    return bricks_used.at[shot_order[1]].set(2)


def touch_ends(entries, key, smallest, high):
    shape = entries.shape
    spot = [jax.random.randint(jax.random.fold_in(key, axis), (), 0, shape[axis]) for axis in range(len(shape))]
    entries = entries.at[tuple(spot)].set(smallest)
    longest = shape.index(max(shape))
    spot[longest] = (spot[longest] + 1) % shape[longest]
    return entries.at[tuple(spot)].set(high)


def steps_of(key, dims, shards, smallest, high):
    gain, own = 1.0, jax.random.fold_in(key, 6)
    for dim, parts in shards:
        heights = jnp.exp(jax.random.uniform(jax.random.fold_in(own, dim), (parts,), jnp.float32, smallest / len(shards), high / len(shards)))
        gain = gain * jnp.repeat(heights, dims[dim] // parts).reshape([-1 if axis == dim else 1 for axis in range(len(dims))])
    return gain


def normal_values(stream_key, shape, deviation, most, split=(), held_as=jnp.bfloat16):
    drawn = deviation * jax.random.normal(stream_key, shape, jnp.float32)
    if split:
        drawn = drawn * steps_of(stream_key, shape, split, -0.22, 0.18)
    return jnp.clip(drawn, -most, most).astype(held_as)


def setup_inputs(seed: int = 0) -> dict:
    splits = jax.random.split(jax.random.key(seed), 6)
    return {
        "sources": normal_values(splits[0], (SHOTS, 2, 2, WIDE_Y, DEPTH, WIDE_Z), 4.0, 24.0, ((0, 16), (4, 8)), jnp.float32),
        "slowness": jnp.clip(jnp.exp(math.log(2.0) - 1.3862944 * jax.random.uniform(splits[1], (SHOTS, WIDE_Y, DEPTH, WIDE_Z), jnp.float32) ** steps_of(splits[1], (SHOTS, WIDE_Y, DEPTH, WIDE_Z), ((0, 16), (2, 8)), -0.2, 0.2)), 0.5, 2.0),
        "group_size": draw_group_size(jax.random.fold_in(splits[5], 71), 0),
        "window_anchor": touch_ends(jax.random.randint(splits[3], (SHOTS,), 0, TILES - BLOCKS + 1), jax.random.fold_in(splits[3], 1), 0, TILES - BLOCKS).astype(jnp.int32),
        "tile_slot": jax.random.permutation(splits[4], TILES).astype(jnp.int32),
    }


shift_beta = 0.5
relaxation = 0.8


def neighbour_sum(field):
    summed = jnp.zeros_like(field)
    for along_axis in (1, 2, 3):
        widths = [(0, 0)] * 4
        widths[along_axis] = (1, 1)
        padded = jnp.pad(field, widths)
        count = field.shape[along_axis]
        summed = summed + lax.slice_in_dim(padded, 0, count, axis=along_axis)
        summed = summed + lax.slice_in_dim(padded, 2, count + 2, axis=along_axis)
    return summed


def apply_inverse(values, inv_re, inv_im):
    fwd_re = values[0] * inv_re - values[1] * inv_im
    fwd_im = values[0] * inv_im + values[1] * inv_re
    adj_re = values[2] * inv_re - values[3] * inv_im
    adj_im = values[2] * inv_im + values[3] * inv_re
    return jnp.stack([fwd_re, fwd_im, adj_re, adj_im])


def sine_taper(count, extent):
    positions = jnp.arange(count, dtype=jnp.int32).astype(jnp.float32)
    return jnp.sin(jnp.pi * (positions + 0.5) / extent)


def window_gradient(source_window, slowness_window, group_bricks):
    wide_y, depth, wide_z = slowness_window.shape
    extent = group_bricks * PLANES
    depth_ids = jnp.arange(depth, dtype=jnp.int32)
    active = depth_ids < extent
    active_mask = active.astype(jnp.float32)[None, :, None]
    real_d = 6.0 - slowness_window
    imag_d = shift_beta * slowness_window
    denominator = real_d * real_d + imag_d * imag_d
    inv_re = real_d / denominator
    inv_im = imag_d / denominator
    forcing = source_window.reshape(4, wide_y, depth, wide_z)
    field = jnp.zeros_like(forcing)
    for sweep_index in range(SWEEPS):
        updated = apply_inverse(forcing + neighbour_sum(field), inv_re, inv_im)
        field = ((1.0 - relaxation) * field + relaxation * updated) * active_mask
    imaging = field[0] * field[2] - field[1] * field[3] - shift_beta * (field[0] * field[3] + field[1] * field[2])
    extent_float = extent.astype(jnp.float32)
    depth_float = depth_ids.astype(jnp.float32)
    taper_x = jnp.where(active, jnp.sin(jnp.pi * (depth_float + 0.5) / extent_float), 0.0)
    taper_y = sine_taper(wide_y, float(wide_y))
    taper_z = sine_taper(wide_z, float(wide_z))
    gradient = imaging * (taper_y[:, None, None] * taper_x[None, :, None] * taper_z[None, None, :])
    banded = gradient.reshape(wide_y, BANDS, PLANES, wide_z).transpose(1, 0, 2, 3)
    return banded.reshape(BANDS, BLOCKS, TILE_CELLS)


def reference(sources, slowness, group_size, window_anchor, tile_slot):
    def one_shot(totals, shot_items):
        source_window, slowness_window, group_bricks, anchor = shot_items
        blocks = window_gradient(source_window, slowness_window, group_bricks)
        tile_slots = tile_slot[anchor + jnp.arange(BLOCKS, dtype=jnp.int32)]
        totals = totals.at[:, tile_slots, :].add(blocks)
        return totals, None

    start = jnp.zeros((BANDS, TILES, TILE_CELLS), jnp.float32)
    totals, unused = lax.scan(one_shot, start, (sources, slowness, group_size, window_anchor))
    return totals
```

```python
import jax
import jax.numpy as jnp
from jax import lax
from jax.experimental import pallas as pl
from jax.experimental.pallas import tpu as pltpu
from jax.sharding import PartitionSpec as P

BLOCKS = 8


shift_beta = 0.5
relaxation = 0.8


def sine_taper(count, extent):
    positions = jnp.arange(count, dtype=jnp.int32).astype(jnp.float32)
    return jnp.sin(jnp.pi * (positions + 0.5) / extent)


def inverse_of(slow):
    real_d = 6.0 - slow
    imag_d = shift_beta * slow
    denominator = real_d * real_d + imag_d * imag_d
    return real_d / denominator, imag_d / denominator


def first_sweep(s0, s1, s2, s3, inv_re, inv_im, mask):
    return (
        relaxation * (s0 * inv_re - s1 * inv_im) * mask,
        relaxation * (s0 * inv_im + s1 * inv_re) * mask,
        relaxation * (s2 * inv_re - s3 * inv_im) * mask,
        relaxation * (s2 * inv_im + s3 * inv_re) * mask,
    )


def gradient_kernel(
    ty_ref, src_ref, src_lo_ref, src_hi_ref, sl_ref, sl_lo_ref, sl_hi_ref,
    lo_ref, hi_ref, mask_ref, tx_ref, tz_ref, out_ref, f1_s, inv_s,
):
    b = pl.program_id(0)
    nb = pl.num_programs(0)
    rows = src_ref.shape[1]
    mask = mask_ref[...]

    def sweep_one(r, carry):
        inv_re, inv_im = inverse_of(sl_ref[r])
        inv_s[0, r] = inv_re
        inv_s[1, r] = inv_im
        f = first_sweep(src_ref[0, r], src_ref[1, r], src_ref[2, r], src_ref[3, r], inv_re, inv_im, mask)
        for k in range(4):
            f1_s[k, r + 1] = f[k]
        return carry

    lax.fori_loop(0, rows, sweep_one, 0, unroll=2)

    lo_keep = jnp.where(b > 0, 1.0, 0.0).astype(jnp.float32)
    hi_keep = jnp.where(b < nb - 1, 1.0, 0.0).astype(jnp.float32)
    for slot, s_ref, l_ref, keep in ((0, src_lo_ref, sl_lo_ref, lo_keep), (rows + 1, src_hi_ref, sl_hi_ref, hi_keep)):
        inv_re, inv_im = inverse_of(l_ref[0])
        f = first_sweep(s_ref[0, 0], s_ref[1, 0], s_ref[2, 0], s_ref[3, 0], inv_re, inv_im, mask)
        for k in range(4):
            f1_s[k, slot] = f[k] * keep

    shape = mask.shape
    p_ids = lax.broadcasted_iota(jnp.int32, shape, 0)
    z_ids = lax.broadcasted_iota(jnp.int32, shape, 1)
    planes, width = shape
    tx = tx_ref[...]
    tz = tz_ref[...]

    def sweep_two(g, carry):
        base = pl.multiple_of(g * 8, 8)
        lo8 = [lo_ref[k, pl.ds(base, 8), :] for k in range(4)]
        hi8 = [hi_ref[k, pl.ds(base, 8), :] for k in range(4)]
        for i in range(8):
            r = base + i
            inv_re = inv_s[0, r]
            inv_im = inv_s[1, r]
            cur = []
            vals = []
            for k in range(4):
                c = f1_s[k, r + 1]
                acc = f1_s[k, r] + f1_s[k, r + 2]
                down = jnp.where(p_ids == 0, lo8[k][i:i + 1, :], pltpu.roll(c, 1, 0))
                acc = acc + down
                up = jnp.where(p_ids == planes - 1, hi8[k][i:i + 1, :], pltpu.roll(c, planes - 1, 0))
                acc = acc + up
                zm = jnp.where(z_ids == 0, 0.0, pltpu.roll(c, 1, 1))
                acc = acc + zm
                zp = jnp.where(z_ids == width - 1, 0.0, pltpu.roll(c, width - 1, 1))
                acc = acc + zp
                cur.append(c)
                vals.append(src_ref[k, r] + acc)
            upd = (
                vals[0] * inv_re - vals[1] * inv_im,
                vals[0] * inv_im + vals[1] * inv_re,
                vals[2] * inv_re - vals[3] * inv_im,
                vals[2] * inv_im + vals[3] * inv_re,
            )
            f2 = [((1.0 - relaxation) * cur[k] + relaxation * upd[k]) * mask for k in range(4)]
            imaging = f2[0] * f2[2] - f2[1] * f2[3] - shift_beta * (f2[0] * f2[3] + f2[1] * f2[2])
            taper = (ty_ref[b * rows + r] * tx) * tz
            out_ref[0, r] = imaging * taper
        return carry

    lax.fori_loop(0, rows // 8, sweep_two, 0)


def window_blocks(src4, slow, lo, hi, mask_b, tx_b, tz_b, ty):
    four, wide_y, planes, wide_z = src4.shape
    rows = wide_y // BLOCKS
    last = wide_y - 1

    def row_spec(pick):
        return pl.BlockSpec((four, 1, planes, wide_z), lambda b, t: (0, pick(b), 0, 0))

    def slow_row_spec(pick):
        return pl.BlockSpec((1, planes, wide_z), lambda b, t: (pick(b), 0, 0))

    below = lambda b: jnp.maximum(b * rows - 1, 0)
    above = lambda b: jnp.minimum(b * rows + rows, last)
    grid_spec = pltpu.PrefetchScalarGridSpec(
        num_scalar_prefetch=1,
        grid=(BLOCKS,),
        in_specs=[
            pl.BlockSpec((four, rows, planes, wide_z), lambda b, t: (0, b, 0, 0)),
            row_spec(below),
            row_spec(above),
            pl.BlockSpec((rows, planes, wide_z), lambda b, t: (b, 0, 0)),
            slow_row_spec(below),
            slow_row_spec(above),
            pl.BlockSpec((four, rows, wide_z), lambda b, t: (0, b, 0)),
            pl.BlockSpec((four, rows, wide_z), lambda b, t: (0, b, 0)),
            pl.BlockSpec((planes, wide_z), lambda b, t: (0, 0)),
            pl.BlockSpec((planes, wide_z), lambda b, t: (0, 0)),
            pl.BlockSpec((1, wide_z), lambda b, t: (0, 0)),
        ],
        out_specs=pl.BlockSpec((1, rows, planes, wide_z), lambda b, t: (b, 0, 0, 0)),
        scratch_shapes=[
            pltpu.VMEM((four, rows + 2, planes, wide_z), jnp.float32),
            pltpu.VMEM((2, rows, planes, wide_z), jnp.float32),
        ],
    )
    return pl.pallas_call(
        gradient_kernel,
        grid_spec=grid_spec,
        out_shape=jax.ShapeDtypeStruct((BLOCKS, rows, planes, wide_z), jnp.float32),
    )(ty, src4, src4, src4, slow, slow, slow, lo, hi, mask_b, tx_b, tz_b)


def per_device(sources, slowness, group_size, window_anchor, tile_slot):
    slowness_window = slowness[0]
    wide_y, planes, wide_z = slowness_window.shape
    brick_index = lax.axis_index("brick")
    shot_index = lax.axis_index("shot")
    brick_count = lax.axis_size("brick")
    extent = group_size[shot_index] * planes
    depth_ids = brick_index * planes + jnp.arange(planes, dtype=jnp.int32)
    active = depth_ids < extent
    mask_col = active.astype(jnp.float32)
    src4 = sources[0].reshape(4, wide_y, planes, wide_z)

    def boundary(plane):
        inv_re, inv_im = inverse_of(slowness_window[:, plane, :])
        s = src4[:, :, plane, :]
        f = first_sweep(s[0], s[1], s[2], s[3], inv_re, inv_im, mask_col[plane])
        return jnp.stack(f)

    up = [(i, i + 1) for i in range(brick_count - 1)]
    down = [(j, i) for i, j in up]
    lo = lax.ppermute(boundary(planes - 1), "brick", up)
    hi = lax.ppermute(boundary(0), "brick", down)

    extent_float = extent.astype(jnp.float32)
    depth_float = depth_ids.astype(jnp.float32)
    taper_x = jnp.where(active, jnp.sin(jnp.pi * (depth_float + 0.5) / extent_float), 0.0)
    taper_y = sine_taper(wide_y, float(wide_y))
    taper_z = sine_taper(wide_z, float(wide_z))
    mask_b = jnp.broadcast_to(mask_col[:, None], (planes, wide_z))
    tx_b = jnp.broadcast_to(taper_x[:, None], (planes, wide_z))
    tz_b = taper_z[None, :]
    blocks = window_blocks(src4, slowness_window, lo, hi, mask_b, tx_b, tz_b, taper_y)

    shot_count = lax.axis_size("shot")
    tile_dev = tile_slot.shape[0] // shot_count
    owned = shot_index * tile_dev + jnp.arange(tile_dev, dtype=jnp.int32)
    piece_slots = tile_slot[window_anchor[:, None] + jnp.arange(BLOCKS, dtype=jnp.int32)[None, :]]
    weights = (owned[:, None, None] == piece_slots[None, :, :]).astype(jnp.float32)
    summed = jnp.einsum(
        "qkb,kbyps->qyps",
        weights,
        lax.all_gather(blocks[None], "shot", axis=0, tiled=True),
        precision=lax.Precision.HIGHEST,
    )
    return summed.reshape(1, tile_dev, -1)


def solution(mesh):
    return jax.shard_map(
        per_device,
        mesh=mesh,
        in_specs=(
            P("shot", None, None, None, "brick", None),
            P("shot", None, "brick", None),
            P(),
            P(),
            P(),
        ),
        out_specs=P("brick", "shot", None),
        check_vma=False,
    )
```

```python
import jax
import jax.numpy as jnp
from jax import lax
from jax.experimental import pallas as pl
from jax.experimental.pallas import tpu as pltpu
from jax.sharding import PartitionSpec as P

BLOCKS = 8


shift_beta = 0.5
relaxation = 0.8


def sine_taper(count, extent):
    positions = jnp.arange(count, dtype=jnp.int32).astype(jnp.float32)
    return jnp.sin(jnp.pi * (positions + 0.5) / extent)


def inverse_of(slow):
    real_d = 6.0 - slow
    imag_d = shift_beta * slow
    denominator = real_d * real_d + imag_d * imag_d
    return real_d / denominator, imag_d / denominator


def first_sweep(s0, s1, s2, s3, inv_re, inv_im, mask):
    return (
        relaxation * (s0 * inv_re - s1 * inv_im) * mask,
        relaxation * (s0 * inv_im + s1 * inv_re) * mask,
        relaxation * (s2 * inv_re - s3 * inv_im) * mask,
        relaxation * (s2 * inv_im + s3 * inv_re) * mask,
    )


def gradient_kernel(
    ty_ref, src_ref, src_lo_ref, src_hi_ref, sl_ref, sl_lo_ref, sl_hi_ref,
    lo_ref, hi_ref, mask_ref, tx_ref, tz_ref, out_ref, f1_s, inv_s,
):
    b = pl.program_id(0)
    nb = pl.num_programs(0)
    rows = src_ref.shape[1]
    mask = mask_ref[...]

    def sweep_one(r, carry):
        inv_re, inv_im = inverse_of(sl_ref[r])
        inv_s[0, r] = inv_re
        inv_s[1, r] = inv_im
        f = first_sweep(src_ref[0, r], src_ref[1, r], src_ref[2, r], src_ref[3, r], inv_re, inv_im, mask)
        for k in range(4):
            f1_s[k, r + 1] = f[k]
        return carry

    lax.fori_loop(0, rows, sweep_one, 0, unroll=2)

    lo_keep = jnp.where(b > 0, 1.0, 0.0).astype(jnp.float32)
    hi_keep = jnp.where(b < nb - 1, 1.0, 0.0).astype(jnp.float32)
    for slot, s_ref, l_ref, keep in ((0, src_lo_ref, sl_lo_ref, lo_keep), (rows + 1, src_hi_ref, sl_hi_ref, hi_keep)):
        inv_re, inv_im = inverse_of(l_ref[0])
        f = first_sweep(s_ref[0, 0], s_ref[1, 0], s_ref[2, 0], s_ref[3, 0], inv_re, inv_im, mask)
        for k in range(4):
            f1_s[k, slot] = f[k] * keep

    shape = mask.shape
    p_ids = lax.broadcasted_iota(jnp.int32, shape, 0)
    z_ids = lax.broadcasted_iota(jnp.int32, shape, 1)
    planes, width = shape
    tx = tx_ref[...]
    tz = tz_ref[...]

    def sweep_two(g, carry):
        base = pl.multiple_of(g * 8, 8)
        lo8 = [lo_ref[k, pl.ds(base, 8), :] for k in range(4)]
        hi8 = [hi_ref[k, pl.ds(base, 8), :] for k in range(4)]
        for i in range(8):
            r = base + i
            inv_re = inv_s[0, r]
            inv_im = inv_s[1, r]
            cur = []
            vals = []
            for k in range(4):
                c = f1_s[k, r + 1]
                acc = f1_s[k, r] + f1_s[k, r + 2]
                down = jnp.where(p_ids == 0, lo8[k][i:i + 1, :], pltpu.roll(c, 1, 0))
                acc = acc + down
                up = jnp.where(p_ids == planes - 1, hi8[k][i:i + 1, :], pltpu.roll(c, planes - 1, 0))
                acc = acc + up
                zm = jnp.where(z_ids == 0, 0.0, pltpu.roll(c, 1, 1))
                acc = acc + zm
                zp = jnp.where(z_ids == width - 1, 0.0, pltpu.roll(c, width - 1, 1))
                acc = acc + zp
                cur.append(c)
                vals.append(src_ref[k, r] + acc)
            upd = (
                vals[0] * inv_re - vals[1] * inv_im,
                vals[0] * inv_im + vals[1] * inv_re,
                vals[2] * inv_re - vals[3] * inv_im,
                vals[2] * inv_im + vals[3] * inv_re,
            )
            f2 = [((1.0 - relaxation) * cur[k] + relaxation * upd[k]) * mask for k in range(4)]
            imaging = f2[0] * f2[2] - f2[1] * f2[3] - shift_beta * (f2[0] * f2[3] + f2[1] * f2[2])
            taper = (ty_ref[b * rows + r] * tx) * tz
            out_ref[0, r] = imaging * taper
        return carry

    lax.fori_loop(0, rows // 8, sweep_two, 0)


def window_blocks(src4, slow, lo, hi, mask_b, tx_b, tz_b, ty):
    four, wide_y, planes, wide_z = src4.shape
    rows = wide_y // BLOCKS
    last = wide_y - 1

    def row_spec(pick):
        return pl.BlockSpec((four, 1, planes, wide_z), lambda b, t: (0, pick(b), 0, 0))

    def slow_row_spec(pick):
        return pl.BlockSpec((1, planes, wide_z), lambda b, t: (pick(b), 0, 0))

    below = lambda b: jnp.maximum(b * rows - 1, 0)
    above = lambda b: jnp.minimum(b * rows + rows, last)
    grid_spec = pltpu.PrefetchScalarGridSpec(
        num_scalar_prefetch=1,
        grid=(BLOCKS,),
        in_specs=[
            pl.BlockSpec((four, rows, planes, wide_z), lambda b, t: (0, b, 0, 0)),
            row_spec(below),
            row_spec(above),
            pl.BlockSpec((rows, planes, wide_z), lambda b, t: (b, 0, 0)),
            slow_row_spec(below),
            slow_row_spec(above),
            pl.BlockSpec((four, rows, wide_z), lambda b, t: (0, b, 0)),
            pl.BlockSpec((four, rows, wide_z), lambda b, t: (0, b, 0)),
            pl.BlockSpec((planes, wide_z), lambda b, t: (0, 0)),
            pl.BlockSpec((planes, wide_z), lambda b, t: (0, 0)),
            pl.BlockSpec((1, wide_z), lambda b, t: (0, 0)),
        ],
        out_specs=pl.BlockSpec((1, rows, planes, wide_z), lambda b, t: (b, 0, 0, 0)),
        scratch_shapes=[
            pltpu.VMEM((four, rows + 2, planes, wide_z), jnp.float32),
            pltpu.VMEM((2, rows, planes, wide_z), jnp.float32),
        ],
    )
    return pl.pallas_call(
        gradient_kernel,
        grid_spec=grid_spec,
        out_shape=jax.ShapeDtypeStruct((BLOCKS, rows, planes, wide_z), jnp.float32),
    )(ty, src4, src4, src4, slow, slow, slow, lo, hi, mask_b, tx_b, tz_b)


def per_device(sources, slowness, group_size, window_anchor, tile_slot):
    slowness_window = slowness[0]
    wide_y, planes, wide_z = slowness_window.shape
    brick_index = lax.axis_index("brick")
    shot_index = lax.axis_index("shot")
    brick_count = lax.axis_size("brick")
    extent = group_size[shot_index] * planes
    depth_ids = brick_index * planes + jnp.arange(planes, dtype=jnp.int32)
    active = depth_ids < extent
    mask_col = active.astype(jnp.float32)
    src4 = sources[0].reshape(4, wide_y, planes, wide_z)

    def boundary(plane):
        inv_re, inv_im = inverse_of(slowness_window[:, plane, :])
        s = src4[:, :, plane, :]
        f = first_sweep(s[0], s[1], s[2], s[3], inv_re, inv_im, mask_col[plane])
        return jnp.stack(f)

    up = [(i, i + 1) for i in range(brick_count - 1)]
    down = [(j, i) for i, j in up]
    lo = lax.ppermute(boundary(planes - 1), "brick", up)
    hi = lax.ppermute(boundary(0), "brick", down)

    extent_float = extent.astype(jnp.float32)
    depth_float = depth_ids.astype(jnp.float32)
    taper_x = jnp.where(active, jnp.sin(jnp.pi * (depth_float + 0.5) / extent_float), 0.0)
    taper_y = sine_taper(wide_y, float(wide_y))
    taper_z = sine_taper(wide_z, float(wide_z))
    mask_b = jnp.broadcast_to(mask_col[:, None], (planes, wide_z))
    tx_b = jnp.broadcast_to(taper_x[:, None], (planes, wide_z))
    tz_b = taper_z[None, :]
    blocks = window_blocks(src4, slowness_window, lo, hi, mask_b, tx_b, tz_b, taper_y)

    shot_count = lax.axis_size("shot")
    tile_dev = tile_slot.shape[0] // shot_count
    owned = shot_index * tile_dev + jnp.arange(tile_dev, dtype=jnp.int32)
    piece_slots = tile_slot[window_anchor[:, None] + jnp.arange(BLOCKS, dtype=jnp.int32)[None, :]]
    match = owned[:, None, None] == piece_slots[None, :, :]
    gathered = lax.all_gather(blocks[None], "shot", axis=0, tiled=True)
    return gather_sum(gathered, match).reshape(1, tile_dev, -1)


def select_kernel(es_ref, eb_ref, eq_ref, n_ref, g_hbm, out_ref, buf, sem):
    n = n_ref[0]
    out_ref[...] = jnp.zeros_like(out_ref)

    def copy(e, slot):
        return pltpu.make_async_copy(g_hbm.at[es_ref[e], eb_ref[e]], buf.at[slot], sem.at[slot])

    @pl.when(n > 0)
    def _():
        copy(0, 0).start()

    def body(e, carry):
        slot = e % 2

        @pl.when(e + 1 < n)
        def _():
            copy(e + 1, 1 - slot).start()

        copy(e, slot).wait()
        q = eq_ref[e]
        out_ref[q] = out_ref[q] + buf[slot]
        return carry

    lax.fori_loop(0, n, body, 0)


def gather_sum(gathered, match):
    owners, shots, blocks = match.shape
    cell_shape = gathered.shape[2:]
    valid = jnp.any(match, axis=2).reshape(-1)
    which_block = jnp.sum(jnp.where(match, jnp.arange(blocks, dtype=jnp.int32), 0), axis=2).reshape(-1)
    shot_of = jnp.broadcast_to(jnp.arange(shots, dtype=jnp.int32)[None, :], (owners, shots)).reshape(-1)
    owner_of = jnp.broadcast_to(jnp.arange(owners, dtype=jnp.int32)[:, None], (owners, shots)).reshape(-1)
    count = owners * shots
    position = jnp.where(valid, jnp.cumsum(valid.astype(jnp.int32)) - 1, count)
    empty = jnp.zeros((count,), jnp.int32)
    es = empty.at[position].set(shot_of, mode="drop")
    eb = empty.at[position].set(which_block, mode="drop")
    eq = empty.at[position].set(owner_of, mode="drop")
    n = jnp.sum(valid.astype(jnp.int32)).reshape(1)
    return pl.pallas_call(
        select_kernel,
        grid_spec=pltpu.PrefetchScalarGridSpec(
            num_scalar_prefetch=4,
            grid=(1,),
            in_specs=[pl.BlockSpec(memory_space=pl.ANY)],
            out_specs=pl.BlockSpec((owners,) + cell_shape, lambda i, *_: (0,) * (1 + len(cell_shape))),
            scratch_shapes=[
                pltpu.VMEM((2,) + cell_shape, jnp.float32),
                pltpu.SemaphoreType.DMA((2,)),
            ],
        ),
        out_shape=jax.ShapeDtypeStruct((owners,) + cell_shape, jnp.float32),
    )(es, eb, eq, n, gathered)


def solution(mesh):
    return jax.shard_map(
        per_device,
        mesh=mesh,
        in_specs=(
            P("shot", None, None, None, "brick", None),
            P("shot", None, "brick", None),
            P(),
            P(),
            P(),
        ),
        out_specs=P("brick", "shot", None),
        check_vma=False,
    )
```

```python
import jax
import jax.numpy as jnp
from jax import lax
from jax.experimental import pallas as pl
from jax.experimental.pallas import tpu as pltpu
from jax.sharding import PartitionSpec as P

BLOCKS = 8


shift_beta = 0.5
relaxation = 0.8


def sine_taper(count, extent):
    positions = jnp.arange(count, dtype=jnp.int32).astype(jnp.float32)
    return jnp.sin(jnp.pi * (positions + 0.5) / extent)


def inverse_of(slow):
    real_d = 6.0 - slow
    imag_d = shift_beta * slow
    denominator = real_d * real_d + imag_d * imag_d
    return real_d / denominator, imag_d / denominator


def first_sweep(s0, s1, s2, s3, inv_re, inv_im, mask):
    return (
        relaxation * (s0 * inv_re - s1 * inv_im) * mask,
        relaxation * (s0 * inv_im + s1 * inv_re) * mask,
        relaxation * (s2 * inv_re - s3 * inv_im) * mask,
        relaxation * (s2 * inv_im + s3 * inv_re) * mask,
    )


def gradient_kernel(
    ty_ref, src_ref, src_lo_ref, src_hi_ref, sl_ref, sl_lo_ref, sl_hi_ref,
    lo_ref, hi_ref, mask_ref, tx_ref, tz_ref, out_ref, f1_s, inv_s,
):
    b = pl.program_id(0)
    nb = pl.num_programs(0)
    rows = src_ref.shape[1]
    mask = mask_ref[...]

    def sweep_one(r, carry):
        inv_re, inv_im = inverse_of(sl_ref[r])
        inv_s[0, r] = inv_re
        inv_s[1, r] = inv_im
        f = first_sweep(src_ref[0, r], src_ref[1, r], src_ref[2, r], src_ref[3, r], inv_re, inv_im, mask)
        for k in range(4):
            f1_s[k, r + 1] = f[k]
        return carry

    lax.fori_loop(0, rows, sweep_one, 0, unroll=2)

    lo_keep = jnp.where(b > 0, 1.0, 0.0).astype(jnp.float32)
    hi_keep = jnp.where(b < nb - 1, 1.0, 0.0).astype(jnp.float32)
    for slot, s_ref, l_ref, keep in ((0, src_lo_ref, sl_lo_ref, lo_keep), (rows + 1, src_hi_ref, sl_hi_ref, hi_keep)):
        inv_re, inv_im = inverse_of(l_ref[0])
        f = first_sweep(s_ref[0, 0], s_ref[1, 0], s_ref[2, 0], s_ref[3, 0], inv_re, inv_im, mask)
        for k in range(4):
            f1_s[k, slot] = f[k] * keep

    shape = mask.shape
    p_ids = lax.broadcasted_iota(jnp.int32, shape, 0)
    z_ids = lax.broadcasted_iota(jnp.int32, shape, 1)
    planes, width = shape
    tx = tx_ref[...]
    tz = tz_ref[...]

    def sweep_two(g, carry):
        base = pl.multiple_of(g * 8, 8)
        lo8 = [lo_ref[k, pl.ds(base, 8), :] for k in range(4)]
        hi8 = [hi_ref[k, pl.ds(base, 8), :] for k in range(4)]
        for i in range(8):
            r = base + i
            inv_re = inv_s[0, r]
            inv_im = inv_s[1, r]
            cur = []
            vals = []
            for k in range(4):
                c = f1_s[k, r + 1]
                acc = f1_s[k, r] + f1_s[k, r + 2]
                down = jnp.where(p_ids == 0, lo8[k][i:i + 1, :], pltpu.roll(c, 1, 0))
                acc = acc + down
                up = jnp.where(p_ids == planes - 1, hi8[k][i:i + 1, :], pltpu.roll(c, planes - 1, 0))
                acc = acc + up
                zm = jnp.where(z_ids == 0, 0.0, pltpu.roll(c, 1, 1))
                acc = acc + zm
                zp = jnp.where(z_ids == width - 1, 0.0, pltpu.roll(c, width - 1, 1))
                acc = acc + zp
                cur.append(c)
                vals.append(src_ref[k, r] + acc)
            upd = (
                vals[0] * inv_re - vals[1] * inv_im,
                vals[0] * inv_im + vals[1] * inv_re,
                vals[2] * inv_re - vals[3] * inv_im,
                vals[2] * inv_im + vals[3] * inv_re,
            )
            f2 = [((1.0 - relaxation) * cur[k] + relaxation * upd[k]) * mask for k in range(4)]
            imaging = f2[0] * f2[2] - f2[1] * f2[3] - shift_beta * (f2[0] * f2[3] + f2[1] * f2[2])
            taper = (ty_ref[b * rows + r] * tx) * tz
            out_ref[0, r] = imaging * taper
        return carry

    lax.fori_loop(0, rows // 8, sweep_two, 0)


def window_blocks(src4, slow, lo, hi, mask_b, tx_b, tz_b, ty):
    four, wide_y, planes, wide_z = src4.shape
    rows = wide_y // BLOCKS
    last = wide_y - 1

    def row_spec(pick):
        return pl.BlockSpec((four, 1, planes, wide_z), lambda b, t: (0, pick(b), 0, 0))

    def slow_row_spec(pick):
        return pl.BlockSpec((1, planes, wide_z), lambda b, t: (pick(b), 0, 0))

    below = lambda b: jnp.maximum(b * rows - 1, 0)
    above = lambda b: jnp.minimum(b * rows + rows, last)
    grid_spec = pltpu.PrefetchScalarGridSpec(
        num_scalar_prefetch=1,
        grid=(BLOCKS,),
        in_specs=[
            pl.BlockSpec((four, rows, planes, wide_z), lambda b, t: (0, b, 0, 0)),
            row_spec(below),
            row_spec(above),
            pl.BlockSpec((rows, planes, wide_z), lambda b, t: (b, 0, 0)),
            slow_row_spec(below),
            slow_row_spec(above),
            pl.BlockSpec((four, rows, wide_z), lambda b, t: (0, b, 0)),
            pl.BlockSpec((four, rows, wide_z), lambda b, t: (0, b, 0)),
            pl.BlockSpec((planes, wide_z), lambda b, t: (0, 0)),
            pl.BlockSpec((planes, wide_z), lambda b, t: (0, 0)),
            pl.BlockSpec((1, wide_z), lambda b, t: (0, 0)),
        ],
        out_specs=pl.BlockSpec((1, rows, planes, wide_z), lambda b, t: (b, 0, 0, 0)),
        scratch_shapes=[
            pltpu.VMEM((four, rows + 2, planes, wide_z), jnp.float32),
            pltpu.VMEM((2, rows, planes, wide_z), jnp.float32),
        ],
    )
    return pl.pallas_call(
        gradient_kernel,
        grid_spec=grid_spec,
        out_shape=jax.ShapeDtypeStruct((BLOCKS, rows, planes, wide_z), jnp.float32),
    )(ty, src4, src4, src4, slow, slow, slow, lo, hi, mask_b, tx_b, tz_b)


def per_device(sources, slowness, group_size, window_anchor, tile_slot):
    slowness_window = slowness[0]
    wide_y, planes, wide_z = slowness_window.shape
    brick_index = lax.axis_index("brick")
    core_index = lax.axis_index("core")
    shot_index = lax.axis_index("pair") * 2 + core_index
    brick_count = lax.axis_size("brick")
    extent = group_size[shot_index] * planes
    depth_ids = brick_index * planes + jnp.arange(planes, dtype=jnp.int32)
    active = depth_ids < extent
    mask_col = active.astype(jnp.float32)
    src4 = sources[0].reshape(4, wide_y, planes, wide_z)

    def boundary(plane):
        inv_re, inv_im = inverse_of(slowness_window[:, plane, :])
        s = src4[:, :, plane, :]
        f = first_sweep(s[0], s[1], s[2], s[3], inv_re, inv_im, mask_col[plane])
        return jnp.stack(f)

    up = [(i, i + 1) for i in range(brick_count - 1)]
    down = [(j, i) for i, j in up]
    lo = lax.ppermute(boundary(planes - 1), "brick", up)
    hi = lax.ppermute(boundary(0), "brick", down)

    extent_float = extent.astype(jnp.float32)
    depth_float = depth_ids.astype(jnp.float32)
    taper_x = jnp.where(active, jnp.sin(jnp.pi * (depth_float + 0.5) / extent_float), 0.0)
    taper_y = sine_taper(wide_y, float(wide_y))
    taper_z = sine_taper(wide_z, float(wide_z))
    mask_b = jnp.broadcast_to(mask_col[:, None], (planes, wide_z))
    tx_b = jnp.broadcast_to(taper_x[:, None], (planes, wide_z))
    tz_b = taper_z[None, :]
    blocks = window_blocks(src4, slowness_window, lo, hi, mask_b, tx_b, tz_b, taper_y)

    shot_count = lax.axis_size("pair") * 2
    tile_dev = tile_slot.shape[0] // shot_count
    sibling = shot_index + 1 - 2 * core_index
    owners = jnp.concatenate([shot_index * tile_dev + jnp.arange(tile_dev, dtype=jnp.int32),
                              sibling * tile_dev + jnp.arange(tile_dev, dtype=jnp.int32)])
    same_core = lax.axis_size("pair")
    shot_ids = jnp.arange(same_core, dtype=jnp.int32) * 2 + core_index
    piece_slots = tile_slot[window_anchor[shot_ids][:, None] + jnp.arange(BLOCKS, dtype=jnp.int32)[None, :]]
    match = owners[:, None, None] == piece_slots[None, :, :]
    gathered = lax.all_gather(blocks[None], "pair", axis=0, tiled=True)
    partial = gather_sum(gathered, match)
    theirs = lax.ppermute(partial[tile_dev:], "core", [(0, 1), (1, 0)])
    return (partial[:tile_dev] + theirs).reshape(1, tile_dev, -1)


def select_kernel(es_ref, eb_ref, eq_ref, n_ref, g_hbm, out_ref, buf, sem):
    n = n_ref[0]
    out_ref[...] = jnp.zeros_like(out_ref)

    def copy(e, slot):
        return pltpu.make_async_copy(g_hbm.at[es_ref[e], eb_ref[e]], buf.at[slot], sem.at[slot])

    @pl.when(n > 0)
    def _():
        copy(0, 0).start()

    def body(e, carry):
        slot = e % 2

        @pl.when(e + 1 < n)
        def _():
            copy(e + 1, 1 - slot).start()

        copy(e, slot).wait()
        q = eq_ref[e]
        out_ref[q] = out_ref[q] + buf[slot]
        return carry

    lax.fori_loop(0, n, body, 0)


def gather_sum(gathered, match):
    owners, shots, blocks = match.shape
    cell_shape = gathered.shape[2:]
    valid = jnp.any(match, axis=2).reshape(-1)
    which_block = jnp.sum(jnp.where(match, jnp.arange(blocks, dtype=jnp.int32), 0), axis=2).reshape(-1)
    shot_of = jnp.broadcast_to(jnp.arange(shots, dtype=jnp.int32)[None, :], (owners, shots)).reshape(-1)
    owner_of = jnp.broadcast_to(jnp.arange(owners, dtype=jnp.int32)[:, None], (owners, shots)).reshape(-1)
    count = owners * shots
    position = jnp.where(valid, jnp.cumsum(valid.astype(jnp.int32)) - 1, count)
    empty = jnp.zeros((count,), jnp.int32)
    es = empty.at[position].set(shot_of, mode="drop")
    eb = empty.at[position].set(which_block, mode="drop")
    eq = empty.at[position].set(owner_of, mode="drop")
    n = jnp.sum(valid.astype(jnp.int32)).reshape(1)
    return pl.pallas_call(
        select_kernel,
        grid_spec=pltpu.PrefetchScalarGridSpec(
            num_scalar_prefetch=4,
            grid=(1,),
            in_specs=[pl.BlockSpec(memory_space=pl.ANY)],
            out_specs=pl.BlockSpec((owners,) + cell_shape, lambda i, *_: (0,) * (1 + len(cell_shape))),
            scratch_shapes=[
                pltpu.VMEM((2,) + cell_shape, jnp.float32),
                pltpu.SemaphoreType.DMA((2,)),
            ],
        ),
        out_shape=jax.ShapeDtypeStruct((owners,) + cell_shape, jnp.float32),
    )(es, eb, eq, n, gathered)


def solution(mesh):
    devices = mesh.devices
    shots, bricks = devices.shape
    split = jax.sharding.Mesh(devices.reshape(shots // 2, 2, bricks), ("pair", "core", "brick"))
    shot = ("pair", "core")
    return jax.shard_map(
        per_device,
        mesh=split,
        in_specs=(
            P(shot, None, None, None, "brick", None),
            P(shot, None, "brick", None),
            P(),
            P(),
            P(),
        ),
        out_specs=P("brick", shot, None),
        check_vma=False,
    )
```

```python
import functools

import jax
import jax.numpy as jnp
from jax import lax
from jax.experimental import pallas as pl
from jax.experimental.pallas import tpu as pltpu
from jax.sharding import PartitionSpec as P

BLOCKS = 8


shift_beta = 0.5
relaxation = 0.8


def sine_taper(count, extent):
    positions = jnp.arange(count, dtype=jnp.int32).astype(jnp.float32)
    return jnp.sin(jnp.pi * (positions + 0.5) / extent)


def inverse_of(slow):
    real_d = 6.0 - slow
    imag_d = shift_beta * slow
    denominator = real_d * real_d + imag_d * imag_d
    return real_d / denominator, imag_d / denominator


def first_sweep(s0, s1, s2, s3, inv_re, inv_im, mask):
    return (
        relaxation * (s0 * inv_re - s1 * inv_im) * mask,
        relaxation * (s0 * inv_im + s1 * inv_re) * mask,
        relaxation * (s2 * inv_re - s3 * inv_im) * mask,
        relaxation * (s2 * inv_im + s3 * inv_re) * mask,
    )


def gradient_kernel(
    first, last_block, ty_ref, src_ref, src_lo_ref, src_hi_ref, sl_ref, sl_lo_ref, sl_hi_ref,
    lo_ref, hi_ref, mask_ref, tx_ref, tz_ref, out_ref, f1_s, inv_s,
):
    b = pl.program_id(0) + first
    rows = src_ref.shape[1]
    mask = mask_ref[...]

    def sweep_one(r, carry):
        inv_re, inv_im = inverse_of(sl_ref[r])
        inv_s[0, r] = inv_re
        inv_s[1, r] = inv_im
        f = first_sweep(src_ref[0, r], src_ref[1, r], src_ref[2, r], src_ref[3, r], inv_re, inv_im, mask)
        for k in range(4):
            f1_s[k, r + 1] = f[k]
        return carry

    lax.fori_loop(0, rows, sweep_one, 0, unroll=2)

    lo_keep = jnp.where(b > 0, 1.0, 0.0).astype(jnp.float32)
    hi_keep = jnp.where(b < last_block, 1.0, 0.0).astype(jnp.float32)
    for slot, s_ref, l_ref, keep in ((0, src_lo_ref, sl_lo_ref, lo_keep), (rows + 1, src_hi_ref, sl_hi_ref, hi_keep)):
        inv_re, inv_im = inverse_of(l_ref[0])
        f = first_sweep(s_ref[0, 0], s_ref[1, 0], s_ref[2, 0], s_ref[3, 0], inv_re, inv_im, mask)
        for k in range(4):
            f1_s[k, slot] = f[k] * keep

    shape = mask.shape
    p_ids = lax.broadcasted_iota(jnp.int32, shape, 0)
    z_ids = lax.broadcasted_iota(jnp.int32, shape, 1)
    planes, width = shape
    tx = tx_ref[...]
    tz = tz_ref[...]

    def sweep_two(g, carry):
        base = pl.multiple_of(g * 8, 8)
        lo8 = [lo_ref[k, pl.ds(base, 8), :] for k in range(4)]
        hi8 = [hi_ref[k, pl.ds(base, 8), :] for k in range(4)]
        for i in range(8):
            r = base + i
            inv_re = inv_s[0, r]
            inv_im = inv_s[1, r]
            cur = []
            vals = []
            for k in range(4):
                c = f1_s[k, r + 1]
                acc = f1_s[k, r] + f1_s[k, r + 2]
                down = jnp.where(p_ids == 0, lo8[k][i:i + 1, :], pltpu.roll(c, 1, 0))
                acc = acc + down
                up = jnp.where(p_ids == planes - 1, hi8[k][i:i + 1, :], pltpu.roll(c, planes - 1, 0))
                acc = acc + up
                zm = jnp.where(z_ids == 0, 0.0, pltpu.roll(c, 1, 1))
                acc = acc + zm
                zp = jnp.where(z_ids == width - 1, 0.0, pltpu.roll(c, width - 1, 1))
                acc = acc + zp
                cur.append(c)
                vals.append(src_ref[k, r] + acc)
            upd = (
                vals[0] * inv_re - vals[1] * inv_im,
                vals[0] * inv_im + vals[1] * inv_re,
                vals[2] * inv_re - vals[3] * inv_im,
                vals[2] * inv_im + vals[3] * inv_re,
            )
            f2 = [((1.0 - relaxation) * cur[k] + relaxation * upd[k]) * mask for k in range(4)]
            imaging = f2[0] * f2[2] - f2[1] * f2[3] - shift_beta * (f2[0] * f2[3] + f2[1] * f2[2])
            taper = (ty_ref[b * rows + r] * tx) * tz
            out_ref[0, r] = imaging * taper
        return carry

    lax.fori_loop(0, rows // 8, sweep_two, 0)


def boundary_kernel(src_ref, sl_ref, mask_ref, lo_ref, hi_ref):
    rows = src_ref.shape[1]
    mask = mask_ref[...]
    planes = mask.shape[0]
    for r in range(rows):
        inv_re, inv_im = inverse_of(sl_ref[r])
        f = first_sweep(src_ref[0, r], src_ref[1, r], src_ref[2, r], src_ref[3, r], inv_re, inv_im, mask)
        for k in range(4):
            lo_ref[k, r:r + 1, :] = f[k][planes - 1:planes, :]
            hi_ref[k, r:r + 1, :] = f[k][0:1, :]


def boundary_planes(src4, slow, mask_b):
    four, wide_y, planes, wide_z = src4.shape
    rows = wide_y // BLOCKS
    face = jax.ShapeDtypeStruct((four, wide_y, wide_z), jnp.float32)
    face_spec = pl.BlockSpec((four, rows, wide_z), lambda b: (0, b, 0))
    return pl.pallas_call(
        boundary_kernel,
        grid=(BLOCKS,),
        in_specs=[
            pl.BlockSpec((four, rows, planes, wide_z), lambda b: (0, b, 0, 0)),
            pl.BlockSpec((rows, planes, wide_z), lambda b: (b, 0, 0)),
            pl.BlockSpec((planes, wide_z), lambda b: (0, 0)),
        ],
        out_specs=[face_spec, face_spec],
        out_shape=[face, face],
    )(src4, slow, mask_b)


def window_blocks(src4, slow, lo, hi, mask_b, tx_b, tz_b, ty, first, count):
    four, wide_y, planes, wide_z = src4.shape
    rows = wide_y // BLOCKS
    last = wide_y - 1

    def row_spec(pick):
        return pl.BlockSpec((four, 1, planes, wide_z), lambda b, t: (0, pick(b + first), 0, 0))

    def slow_row_spec(pick):
        return pl.BlockSpec((1, planes, wide_z), lambda b, t: (pick(b + first), 0, 0))

    below = lambda b: jnp.maximum(b * rows - 1, 0)
    above = lambda b: jnp.minimum(b * rows + rows, last)
    grid_spec = pltpu.PrefetchScalarGridSpec(
        num_scalar_prefetch=1,
        grid=(count,),
        in_specs=[
            pl.BlockSpec((four, rows, planes, wide_z), lambda b, t: (0, b + first, 0, 0)),
            row_spec(below),
            row_spec(above),
            pl.BlockSpec((rows, planes, wide_z), lambda b, t: (b + first, 0, 0)),
            slow_row_spec(below),
            slow_row_spec(above),
            pl.BlockSpec((four, rows, wide_z), lambda b, t: (0, b, 0)),
            pl.BlockSpec((four, rows, wide_z), lambda b, t: (0, b, 0)),
            pl.BlockSpec((planes, wide_z), lambda b, t: (0, 0)),
            pl.BlockSpec((planes, wide_z), lambda b, t: (0, 0)),
            pl.BlockSpec((1, wide_z), lambda b, t: (0, 0)),
        ],
        out_specs=pl.BlockSpec((1, rows, planes, wide_z), lambda b, t: (b, 0, 0, 0)),
        scratch_shapes=[
            pltpu.VMEM((four, rows + 2, planes, wide_z), jnp.float32),
            pltpu.VMEM((2, rows, planes, wide_z), jnp.float32),
        ],
    )
    return pl.pallas_call(
        functools.partial(gradient_kernel, first, BLOCKS - 1),
        grid_spec=grid_spec,
        out_shape=jax.ShapeDtypeStruct((count, rows, planes, wide_z), jnp.float32),
    )(ty, src4, src4, src4, slow, slow, slow, lo, hi, mask_b, tx_b, tz_b)


def per_device(sources, slowness, group_size, window_anchor, tile_slot):
    slowness_window = slowness[0]
    wide_y, planes, wide_z = slowness_window.shape
    brick_index = lax.axis_index("brick")
    shot_index = lax.axis_index("shot")
    brick_count = lax.axis_size("brick")
    extent = group_size[shot_index] * planes
    depth_ids = brick_index * planes + jnp.arange(planes, dtype=jnp.int32)
    active = depth_ids < extent
    mask_col = active.astype(jnp.float32)
    src4 = sources[0].reshape(4, wide_y, planes, wide_z)

    mask_b = jnp.broadcast_to(mask_col[:, None], (planes, wide_z))
    lo_send, hi_send = boundary_planes(src4, slowness_window, mask_b)
    up = [(i, i + 1) for i in range(brick_count - 1)]
    down = [(j, i) for i, j in up]
    halves = 2
    span = wide_y // halves
    per_half = BLOCKS // halves

    extent_float = extent.astype(jnp.float32)
    depth_float = depth_ids.astype(jnp.float32)
    taper_x = jnp.where(active, jnp.sin(jnp.pi * (depth_float + 0.5) / extent_float), 0.0)
    taper_y = sine_taper(wide_y, float(wide_y))
    taper_z = sine_taper(wide_z, float(wide_z))
    tx_b = jnp.broadcast_to(taper_x[:, None], (planes, wide_z))
    tz_b = taper_z[None, :]

    shot_count = lax.axis_size("shot")
    tile_dev = tile_slot.shape[0] // shot_count
    owned = shot_index * tile_dev + jnp.arange(tile_dev, dtype=jnp.int32)
    piece_slots = tile_slot[window_anchor[:, None] + jnp.arange(BLOCKS, dtype=jnp.int32)[None, :]]
    match = owned[:, None, None] == piece_slots[None, :, :]

    total = jnp.zeros((tile_dev, span // per_half, planes, wide_z), jnp.float32)
    for h in range(halves):
        rows_h = slice(h * span, (h + 1) * span)
        lo = lax.ppermute(lo_send[:, rows_h], "brick", up)
        hi = lax.ppermute(hi_send[:, rows_h], "brick", down)
        blocks = window_blocks(src4, slowness_window, lo, hi, mask_b, tx_b, tz_b, taper_y, h * per_half, per_half)
        gathered = lax.all_gather(blocks[None], "shot", axis=0, tiled=True)
        total = gather_sum(gathered, match[:, :, h * per_half:(h + 1) * per_half], total)
    return total.reshape(1, tile_dev, -1)


def select_kernel(es_ref, eb_ref, eq_ref, n_ref, init_ref, g_hbm, out_ref, buf, sem):
    n = n_ref[0]
    out_ref[...] = init_ref[...]

    def copy(e, slot):
        return pltpu.make_async_copy(g_hbm.at[es_ref[e], eb_ref[e]], buf.at[slot], sem.at[slot])

    @pl.when(n > 0)
    def _():
        copy(0, 0).start()

    def body(e, carry):
        slot = e % 2

        @pl.when(e + 1 < n)
        def _():
            copy(e + 1, 1 - slot).start()

        copy(e, slot).wait()
        q = eq_ref[e]
        out_ref[q] = out_ref[q] + buf[slot]
        return carry

    lax.fori_loop(0, n, body, 0)


def gather_sum(gathered, match, init):
    owners, shots, blocks = match.shape
    cell_shape = gathered.shape[2:]
    valid = jnp.any(match, axis=2).reshape(-1)
    which_block = jnp.sum(jnp.where(match, jnp.arange(blocks, dtype=jnp.int32), 0), axis=2).reshape(-1)
    shot_of = jnp.broadcast_to(jnp.arange(shots, dtype=jnp.int32)[None, :], (owners, shots)).reshape(-1)
    owner_of = jnp.broadcast_to(jnp.arange(owners, dtype=jnp.int32)[:, None], (owners, shots)).reshape(-1)
    count = owners * shots
    position = jnp.where(valid, jnp.cumsum(valid.astype(jnp.int32)) - 1, count)
    empty = jnp.zeros((count,), jnp.int32)
    es = empty.at[position].set(shot_of, mode="drop")
    eb = empty.at[position].set(which_block, mode="drop")
    eq = empty.at[position].set(owner_of, mode="drop")
    n = jnp.sum(valid.astype(jnp.int32)).reshape(1)
    return pl.pallas_call(
        select_kernel,
        grid_spec=pltpu.PrefetchScalarGridSpec(
            num_scalar_prefetch=4,
            grid=(1,),
            in_specs=[
                pl.BlockSpec((owners,) + cell_shape, lambda i, *_: (0,) * (1 + len(cell_shape))),
                pl.BlockSpec(memory_space=pl.ANY),
            ],
            out_specs=pl.BlockSpec((owners,) + cell_shape, lambda i, *_: (0,) * (1 + len(cell_shape))),
            scratch_shapes=[
                pltpu.VMEM((2,) + cell_shape, jnp.float32),
                pltpu.SemaphoreType.DMA((2,)),
            ],
        ),
        out_shape=jax.ShapeDtypeStruct((owners,) + cell_shape, jnp.float32),
    )(es, eb, eq, n, init, gathered)


def solution(mesh):
    return jax.shard_map(
        per_device,
        mesh=mesh,
        in_specs=(
            P("shot", None, None, None, "brick", None),
            P("shot", None, "brick", None),
            P(),
            P(),
            P(),
        ),
        out_specs=P("brick", "shot", None),
        check_vma=False,
    )
```

```python
import jax
import jax.numpy as jnp
from jax import lax
from jax.experimental import pallas as pl
from jax.experimental.pallas import tpu as pltpu
from jax.sharding import PartitionSpec as P

BLOCKS = 8


shift_beta = 0.5
relaxation = 0.8


def sine_taper(count, extent):
    positions = jnp.arange(count, dtype=jnp.int32).astype(jnp.float32)
    return jnp.sin(jnp.pi * (positions + 0.5) / extent)


def inverse_of(slow):
    real_d = 6.0 - slow
    imag_d = shift_beta * slow
    denominator = real_d * real_d + imag_d * imag_d
    return real_d / denominator, imag_d / denominator


def first_sweep(s0, s1, s2, s3, inv_re, inv_im, mask):
    return (
        relaxation * (s0 * inv_re - s1 * inv_im) * mask,
        relaxation * (s0 * inv_im + s1 * inv_re) * mask,
        relaxation * (s2 * inv_re - s3 * inv_im) * mask,
        relaxation * (s2 * inv_im + s3 * inv_re) * mask,
    )


def gather_plane(rows8, plane, sub_ids):
    tile = jnp.broadcast_to(rows8[0][plane:plane + 1, :], rows8[0].shape)
    for i in range(1, len(rows8)):
        tile = jnp.where(sub_ids == i, jnp.broadcast_to(rows8[i][plane:plane + 1, :], tile.shape), tile)
    return tile


def gradient_kernel(ty_ref, src_ref, src_lo_ref, src_hi_ref, sl_ref, sl_lo_ref, sl_hi_ref, mask_ref, tx_ref, tz_ref,
                    out_ref, aux_ref, f1_s, inv_s):
    b = pl.program_id(0)
    nb = pl.num_programs(0)
    rows = src_ref.shape[1]
    mask = mask_ref[...]

    def sweep_one(r, carry):
        inv_re, inv_im = inverse_of(sl_ref[r])
        inv_s[0, r] = inv_re
        inv_s[1, r] = inv_im
        f = first_sweep(src_ref[0, r], src_ref[1, r], src_ref[2, r], src_ref[3, r], inv_re, inv_im, mask)
        for k in range(4):
            f1_s[k, r + 1] = f[k]
        return carry

    lax.fori_loop(0, rows, sweep_one, 0, unroll=2)

    lo_keep = jnp.where(b > 0, 1.0, 0.0).astype(jnp.float32)
    hi_keep = jnp.where(b < nb - 1, 1.0, 0.0).astype(jnp.float32)
    for slot, s_ref, l_ref, keep in ((0, src_lo_ref, sl_lo_ref, lo_keep), (rows + 1, src_hi_ref, sl_hi_ref, hi_keep)):
        inv_re, inv_im = inverse_of(l_ref[0])
        f = first_sweep(s_ref[0, 0], s_ref[1, 0], s_ref[2, 0], s_ref[3, 0], inv_re, inv_im, mask)
        for k in range(4):
            f1_s[k, slot] = f[k] * keep

    shape = mask.shape
    p_ids = lax.broadcasted_iota(jnp.int32, shape, 0)
    z_ids = lax.broadcasted_iota(jnp.int32, shape, 1)
    planes, width = shape
    tx = tx_ref[...]
    tz = tz_ref[...]

    def sweep_two(g, carry):
        base = pl.multiple_of(g * 8, 8)
        kept = [[] for _ in range(6)]
        for i in range(8):
            r = base + i
            inv_re = inv_s[0, r]
            inv_im = inv_s[1, r]
            cur = []
            vals = []
            for k in range(4):
                c = f1_s[k, r + 1]
                acc = f1_s[k, r] + f1_s[k, r + 2]
                down = jnp.where(p_ids == 0, 0.0, pltpu.roll(c, 1, 0))
                acc = acc + down
                up = jnp.where(p_ids == planes - 1, 0.0, pltpu.roll(c, planes - 1, 0))
                acc = acc + up
                zm = jnp.where(z_ids == 0, 0.0, pltpu.roll(c, 1, 1))
                acc = acc + zm
                zp = jnp.where(z_ids == width - 1, 0.0, pltpu.roll(c, width - 1, 1))
                acc = acc + zp
                cur.append(c)
                vals.append(src_ref[k, r] + acc)
            upd = (
                vals[0] * inv_re - vals[1] * inv_im,
                vals[0] * inv_im + vals[1] * inv_re,
                vals[2] * inv_re - vals[3] * inv_im,
                vals[2] * inv_im + vals[3] * inv_re,
            )
            f2 = [((1.0 - relaxation) * cur[k] + relaxation * upd[k]) * mask for k in range(4)]
            imaging = f2[0] * f2[2] - f2[1] * f2[3] - shift_beta * (f2[0] * f2[3] + f2[1] * f2[2])
            taper = (ty_ref[b * rows + r] * tx) * tz
            out_ref[0, r] = imaging * taper
            for k, v in enumerate(f2 + [inv_re, inv_im]):
                kept[k].append(v)
        for k in range(6):
            for j, plane in enumerate((0, planes - 1)):
                aux_ref[k, j, pl.ds(base, 8), :] = gather_plane(kept[k], plane, p_ids)
        return carry

    lax.fori_loop(0, rows // 8, sweep_two, 0)


def window_blocks(src4, slow, mask_b, tx_b, tz_b, ty):
    four, wide_y, planes, wide_z = src4.shape
    rows = wide_y // BLOCKS
    last = wide_y - 1

    def row_spec(pick):
        return pl.BlockSpec((four, 1, planes, wide_z), lambda b, t: (0, pick(b), 0, 0))

    def slow_row_spec(pick):
        return pl.BlockSpec((1, planes, wide_z), lambda b, t: (pick(b), 0, 0))

    below = lambda b: jnp.maximum(b * rows - 1, 0)
    above = lambda b: jnp.minimum(b * rows + rows, last)
    grid_spec = pltpu.PrefetchScalarGridSpec(
        num_scalar_prefetch=1,
        grid=(BLOCKS,),
        in_specs=[
            pl.BlockSpec((four, rows, planes, wide_z), lambda b, t: (0, b, 0, 0)),
            row_spec(below),
            row_spec(above),
            pl.BlockSpec((rows, planes, wide_z), lambda b, t: (b, 0, 0)),
            slow_row_spec(below),
            slow_row_spec(above),
            pl.BlockSpec((planes, wide_z), lambda b, t: (0, 0)),
            pl.BlockSpec((planes, wide_z), lambda b, t: (0, 0)),
            pl.BlockSpec((1, wide_z), lambda b, t: (0, 0)),
        ],
        out_specs=[
            pl.BlockSpec((1, rows, planes, wide_z), lambda b, t: (b, 0, 0, 0)),
            pl.BlockSpec((6, 2, rows, wide_z), lambda b, t: (0, 0, b, 0)),
        ],
        scratch_shapes=[
            pltpu.VMEM((four, rows + 2, planes, wide_z), jnp.float32),
            pltpu.VMEM((2, rows, planes, wide_z), jnp.float32),
        ],
    )
    return pl.pallas_call(
        gradient_kernel,
        grid_spec=grid_spec,
        out_shape=[
            jax.ShapeDtypeStruct((BLOCKS, rows, planes, wide_z), jnp.float32),
            jax.ShapeDtypeStruct((6, 2, wide_y, wide_z), jnp.float32),
        ],
    )(ty, src4, src4, src4, slow, slow, slow, mask_b, tx_b, tz_b)


def halo_kernel(grad_ref, aux_ref, lo_ref, hi_ref, ty_ref, mask_ref, tx_ref, tz_ref, out_ref):
    rows = grad_ref.shape[1]
    planes, width = mask_ref.shape
    p_ids = lax.broadcasted_iota(jnp.int32, (planes, width), 0)
    tz = tz_ref[...]
    for g in range(rows // 8):
        span = pl.ds(g * 8, 8)
        ty = ty_ref[span, :]
        fixed = []
        for j, plane, h_ref in ((0, 0, lo_ref), (1, planes - 1, hi_ref)):
            inv_re = aux_ref[4, j, span, :]
            inv_im = aux_ref[5, j, span, :]
            h = [h_ref[k, span, :] for k in range(4)]
            m = mask_ref[plane:plane + 1, :]
            d = (
                h[0] * inv_re - h[1] * inv_im,
                h[0] * inv_im + h[1] * inv_re,
                h[2] * inv_re - h[3] * inv_im,
                h[2] * inv_im + h[3] * inv_re,
            )
            f2 = [aux_ref[k, j, span, :] + relaxation * d[k] * m for k in range(4)]
            imaging = f2[0] * f2[2] - f2[1] * f2[3] - shift_beta * (f2[0] * f2[3] + f2[1] * f2[2])
            fixed.append(imaging * ((ty * tx_ref[plane:plane + 1, :]) * tz))
        for i in range(8):
            r = g * 8 + i
            slab = grad_ref[0, r]
            slab = jnp.where(p_ids == 0, jnp.broadcast_to(fixed[0][i:i + 1, :], slab.shape), slab)
            slab = jnp.where(p_ids == planes - 1, jnp.broadcast_to(fixed[1][i:i + 1, :], slab.shape), slab)
            out_ref[0, r] = slab


def apply_halo(grad, aux, lo, hi, ty_b, mask_b, tx_b, tz_b):
    count, rows, planes, wide_z = grad.shape
    four = lo.shape[0]
    full = lambda b: (0, 0)
    return pl.pallas_call(
        halo_kernel,
        grid=(count,),
        in_specs=[
            pl.BlockSpec((1, rows, planes, wide_z), lambda b: (b, 0, 0, 0)),
            pl.BlockSpec((6, 2, rows, wide_z), lambda b: (0, 0, b, 0)),
            pl.BlockSpec((four, rows, wide_z), lambda b: (0, b, 0)),
            pl.BlockSpec((four, rows, wide_z), lambda b: (0, b, 0)),
            pl.BlockSpec((rows, wide_z), lambda b: (b, 0)),
            pl.BlockSpec((planes, wide_z), full),
            pl.BlockSpec((planes, wide_z), full),
            pl.BlockSpec((1, wide_z), full),
        ],
        out_specs=pl.BlockSpec((1, rows, planes, wide_z), lambda b: (b, 0, 0, 0)),
        out_shape=jax.ShapeDtypeStruct(grad.shape, jnp.float32),
        input_output_aliases={0: 0},
    )(grad, aux, lo, hi, ty_b, mask_b, tx_b, tz_b)


def per_device(sources, slowness, group_size, window_anchor, tile_slot):
    slowness_window = slowness[0]
    wide_y, planes, wide_z = slowness_window.shape
    brick_index = lax.axis_index("brick")
    shot_index = lax.axis_index("shot")
    brick_count = lax.axis_size("brick")
    extent = group_size[shot_index] * planes
    depth_ids = brick_index * planes + jnp.arange(planes, dtype=jnp.int32)
    active = depth_ids < extent
    mask_col = active.astype(jnp.float32)
    src4 = sources[0].reshape(4, wide_y, planes, wide_z)

    def boundary(plane):
        inv_re, inv_im = inverse_of(slowness_window[:, plane, :])
        s = src4[:, :, plane, :]
        f = first_sweep(s[0], s[1], s[2], s[3], inv_re, inv_im, mask_col[plane])
        return jnp.stack(f)

    up = [(i, i + 1) for i in range(brick_count - 1)]
    down = [(j, i) for i, j in up]
    lo = lax.ppermute(boundary(planes - 1), "brick", up)
    hi = lax.ppermute(boundary(0), "brick", down)

    extent_float = extent.astype(jnp.float32)
    depth_float = depth_ids.astype(jnp.float32)
    taper_x = jnp.where(active, jnp.sin(jnp.pi * (depth_float + 0.5) / extent_float), 0.0)
    taper_y = sine_taper(wide_y, float(wide_y))
    taper_z = sine_taper(wide_z, float(wide_z))
    mask_b = jnp.broadcast_to(mask_col[:, None], (planes, wide_z))
    tx_b = jnp.broadcast_to(taper_x[:, None], (planes, wide_z))
    tz_b = taper_z[None, :]
    ty_b = jnp.broadcast_to(taper_y[:, None], (wide_y, wide_z))
    interior, aux = window_blocks(src4, slowness_window, mask_b, tx_b, tz_b, taper_y)
    blocks = apply_halo(interior, aux, lo, hi, ty_b, mask_b, tx_b, tz_b)

    shot_count = lax.axis_size("shot")
    tile_dev = tile_slot.shape[0] // shot_count
    owned = shot_index * tile_dev + jnp.arange(tile_dev, dtype=jnp.int32)
    piece_slots = tile_slot[window_anchor[:, None] + jnp.arange(BLOCKS, dtype=jnp.int32)[None, :]]
    match = owned[:, None, None] == piece_slots[None, :, :]
    gathered = lax.all_gather(blocks[None], "shot", axis=0, tiled=True)
    return gather_sum(gathered, match).reshape(1, tile_dev, -1)


def select_kernel(es_ref, eb_ref, eq_ref, n_ref, g_hbm, out_ref, buf, sem):
    n = n_ref[0]
    out_ref[...] = jnp.zeros_like(out_ref)

    def copy(e, slot):
        return pltpu.make_async_copy(g_hbm.at[es_ref[e], eb_ref[e]], buf.at[slot], sem.at[slot])

    @pl.when(n > 0)
    def _():
        copy(0, 0).start()

    def body(e, carry):
        slot = e % 2

        @pl.when(e + 1 < n)
        def _():
            copy(e + 1, 1 - slot).start()

        copy(e, slot).wait()
        q = eq_ref[e]
        out_ref[q] = out_ref[q] + buf[slot]
        return carry

    lax.fori_loop(0, n, body, 0)


def gather_sum(gathered, match):
    owners, shots, blocks = match.shape
    cell_shape = gathered.shape[2:]
    valid = jnp.any(match, axis=2).reshape(-1)
    which_block = jnp.sum(jnp.where(match, jnp.arange(blocks, dtype=jnp.int32), 0), axis=2).reshape(-1)
    shot_of = jnp.broadcast_to(jnp.arange(shots, dtype=jnp.int32)[None, :], (owners, shots)).reshape(-1)
    owner_of = jnp.broadcast_to(jnp.arange(owners, dtype=jnp.int32)[:, None], (owners, shots)).reshape(-1)
    count = owners * shots
    position = jnp.where(valid, jnp.cumsum(valid.astype(jnp.int32)) - 1, count)
    empty = jnp.zeros((count,), jnp.int32)
    es = empty.at[position].set(shot_of, mode="drop")
    eb = empty.at[position].set(which_block, mode="drop")
    eq = empty.at[position].set(owner_of, mode="drop")
    n = jnp.sum(valid.astype(jnp.int32)).reshape(1)
    return pl.pallas_call(
        select_kernel,
        grid_spec=pltpu.PrefetchScalarGridSpec(
            num_scalar_prefetch=4,
            grid=(1,),
            in_specs=[pl.BlockSpec(memory_space=pl.ANY)],
            out_specs=pl.BlockSpec((owners,) + cell_shape, lambda i, *_: (0,) * (1 + len(cell_shape))),
            scratch_shapes=[
                pltpu.VMEM((2,) + cell_shape, jnp.float32),
                pltpu.SemaphoreType.DMA((2,)),
            ],
        ),
        out_shape=jax.ShapeDtypeStruct((owners,) + cell_shape, jnp.float32),
    )(es, eb, eq, n, gathered)


def solution(mesh):
    return jax.shard_map(
        per_device,
        mesh=mesh,
        in_specs=(
            P("shot", None, None, None, "brick", None),
            P("shot", None, "brick", None),
            P(),
            P(),
            P(),
        ),
        out_specs=P("brick", "shot", None),
        check_vma=False,
    )
```

```python
import jax
import jax.numpy as jnp
from jax import lax
from jax.experimental import pallas as pl
from jax.experimental.pallas import tpu as pltpu
from jax.sharding import PartitionSpec as P

BLOCKS = 8


shift_beta = 0.5
relaxation = 0.8


def sine_taper(count, extent):
    positions = jnp.arange(count, dtype=jnp.int32).astype(jnp.float32)
    return jnp.sin(jnp.pi * (positions + 0.5) / extent)


def inverse_of(slow):
    real_d = 6.0 - slow
    imag_d = shift_beta * slow
    denominator = real_d * real_d + imag_d * imag_d
    return real_d / denominator, imag_d / denominator


def first_sweep(s0, s1, s2, s3, inv_re, inv_im, mask):
    return (
        relaxation * (s0 * inv_re - s1 * inv_im) * mask,
        relaxation * (s0 * inv_im + s1 * inv_re) * mask,
        relaxation * (s2 * inv_re - s3 * inv_im) * mask,
        relaxation * (s2 * inv_im + s3 * inv_re) * mask,
    )


def gather_plane(rows8, plane, sub_ids):
    tile = jnp.broadcast_to(rows8[0][plane:plane + 1, :], rows8[0].shape)
    for i in range(1, len(rows8)):
        tile = jnp.where(sub_ids == i, jnp.broadcast_to(rows8[i][plane:plane + 1, :], tile.shape), tile)
    return tile


def gradient_kernel(ty_ref, src_ref, src_lo_ref, src_hi_ref, sl_ref, sl_lo_ref, sl_hi_ref, mask_ref, tx_ref, tz_ref,
                    out_ref, aux_ref, f1_s, inv_s):
    b = pl.program_id(0)
    nb = pl.num_programs(0)
    rows = src_ref.shape[1]
    mask = mask_ref[...]

    def sweep_one(r, carry):
        inv_re, inv_im = inverse_of(sl_ref[r])
        inv_s[0, r] = inv_re
        inv_s[1, r] = inv_im
        f = first_sweep(src_ref[0, r], src_ref[1, r], src_ref[2, r], src_ref[3, r], inv_re, inv_im, mask)
        for k in range(4):
            f1_s[k, r + 1] = f[k]
        return carry

    lax.fori_loop(0, rows, sweep_one, 0, unroll=2)

    lo_keep = jnp.where(b > 0, 1.0, 0.0).astype(jnp.float32)
    hi_keep = jnp.where(b < nb - 1, 1.0, 0.0).astype(jnp.float32)
    for slot, s_ref, l_ref, keep in ((0, src_lo_ref, sl_lo_ref, lo_keep), (rows + 1, src_hi_ref, sl_hi_ref, hi_keep)):
        inv_re, inv_im = inverse_of(l_ref[0])
        f = first_sweep(s_ref[0, 0], s_ref[1, 0], s_ref[2, 0], s_ref[3, 0], inv_re, inv_im, mask)
        for k in range(4):
            f1_s[k, slot] = f[k] * keep

    shape = mask.shape
    p_ids = lax.broadcasted_iota(jnp.int32, shape, 0)
    z_ids = lax.broadcasted_iota(jnp.int32, shape, 1)
    planes, width = shape
    tx = tx_ref[...]
    tz = tz_ref[...]

    def sweep_two(g, carry):
        base = pl.multiple_of(g * 8, 8)
        kept = [[] for _ in range(6)]
        for i in range(8):
            r = base + i
            inv_re = inv_s[0, r]
            inv_im = inv_s[1, r]
            cur = []
            vals = []
            for k in range(4):
                c = f1_s[k, r + 1]
                acc = f1_s[k, r] + f1_s[k, r + 2]
                down = jnp.where(p_ids == 0, 0.0, pltpu.roll(c, 1, 0))
                acc = acc + down
                up = jnp.where(p_ids == planes - 1, 0.0, pltpu.roll(c, planes - 1, 0))
                acc = acc + up
                zm = jnp.where(z_ids == 0, 0.0, pltpu.roll(c, 1, 1))
                acc = acc + zm
                zp = jnp.where(z_ids == width - 1, 0.0, pltpu.roll(c, width - 1, 1))
                acc = acc + zp
                cur.append(c)
                vals.append(src_ref[k, r] + acc)
            upd = (
                vals[0] * inv_re - vals[1] * inv_im,
                vals[0] * inv_im + vals[1] * inv_re,
                vals[2] * inv_re - vals[3] * inv_im,
                vals[2] * inv_im + vals[3] * inv_re,
            )
            f2 = [((1.0 - relaxation) * cur[k] + relaxation * upd[k]) * mask for k in range(4)]
            imaging = f2[0] * f2[2] - f2[1] * f2[3] - shift_beta * (f2[0] * f2[3] + f2[1] * f2[2])
            taper = (ty_ref[b * rows + r] * tx) * tz
            out_ref[0, r] = imaging * taper
            for k, v in enumerate(f2 + [inv_re, inv_im]):
                kept[k].append(v)
        for k in range(6):
            for j, plane in enumerate((0, planes - 1)):
                aux_ref[k, j, pl.ds(base, 8), :] = gather_plane(kept[k], plane, p_ids)
        return carry

    lax.fori_loop(0, rows // 8, sweep_two, 0)


def window_blocks(src4, slow, mask_b, tx_b, tz_b, ty):
    four, wide_y, planes, wide_z = src4.shape
    rows = wide_y // BLOCKS
    last = wide_y - 1

    def row_spec(pick):
        return pl.BlockSpec((four, 1, planes, wide_z), lambda b, t: (0, pick(b), 0, 0))

    def slow_row_spec(pick):
        return pl.BlockSpec((1, planes, wide_z), lambda b, t: (pick(b), 0, 0))

    below = lambda b: jnp.maximum(b * rows - 1, 0)
    above = lambda b: jnp.minimum(b * rows + rows, last)
    grid_spec = pltpu.PrefetchScalarGridSpec(
        num_scalar_prefetch=1,
        grid=(BLOCKS,),
        in_specs=[
            pl.BlockSpec((four, rows, planes, wide_z), lambda b, t: (0, b, 0, 0)),
            row_spec(below),
            row_spec(above),
            pl.BlockSpec((rows, planes, wide_z), lambda b, t: (b, 0, 0)),
            slow_row_spec(below),
            slow_row_spec(above),
            pl.BlockSpec((planes, wide_z), lambda b, t: (0, 0)),
            pl.BlockSpec((planes, wide_z), lambda b, t: (0, 0)),
            pl.BlockSpec((1, wide_z), lambda b, t: (0, 0)),
        ],
        out_specs=[
            pl.BlockSpec((1, rows, planes, wide_z), lambda b, t: (b, 0, 0, 0)),
            pl.BlockSpec((6, 2, rows, wide_z), lambda b, t: (0, 0, b, 0)),
        ],
        scratch_shapes=[
            pltpu.VMEM((four, rows + 2, planes, wide_z), jnp.float32),
            pltpu.VMEM((2, rows, planes, wide_z), jnp.float32),
        ],
    )
    return pl.pallas_call(
        gradient_kernel,
        grid_spec=grid_spec,
        out_shape=[
            jax.ShapeDtypeStruct((BLOCKS, rows, planes, wide_z), jnp.float32),
            jax.ShapeDtypeStruct((6, 2, wide_y, wide_z), jnp.float32),
        ],
    )(ty, src4, src4, src4, slow, slow, slow, mask_b, tx_b, tz_b)


def halo_kernel(grad_ref, aux_ref, lo_ref, hi_ref, ty_ref, mask_ref, tx_ref, tz_ref, out_ref):
    rows = grad_ref.shape[1]
    planes, width = mask_ref.shape
    p_ids = lax.broadcasted_iota(jnp.int32, (planes, width), 0)
    tz = tz_ref[...]
    for g in range(rows // 8):
        span = pl.ds(g * 8, 8)
        ty = ty_ref[span, :]
        fixed = []
        for j, plane, h_ref in ((0, 0, lo_ref), (1, planes - 1, hi_ref)):
            inv_re = aux_ref[4, j, span, :]
            inv_im = aux_ref[5, j, span, :]
            h = [h_ref[k, span, :] for k in range(4)]
            m = mask_ref[plane:plane + 1, :]
            d = (
                h[0] * inv_re - h[1] * inv_im,
                h[0] * inv_im + h[1] * inv_re,
                h[2] * inv_re - h[3] * inv_im,
                h[2] * inv_im + h[3] * inv_re,
            )
            f2 = [aux_ref[k, j, span, :] + relaxation * d[k] * m for k in range(4)]
            imaging = f2[0] * f2[2] - f2[1] * f2[3] - shift_beta * (f2[0] * f2[3] + f2[1] * f2[2])
            fixed.append(imaging * ((ty * tx_ref[plane:plane + 1, :]) * tz))
        for i in range(8):
            r = g * 8 + i
            slab = grad_ref[0, r]
            slab = jnp.where(p_ids == 0, jnp.broadcast_to(fixed[0][i:i + 1, :], slab.shape), slab)
            slab = jnp.where(p_ids == planes - 1, jnp.broadcast_to(fixed[1][i:i + 1, :], slab.shape), slab)
            out_ref[0, r] = slab


def apply_halo(grad, aux, lo, hi, ty_b, mask_b, tx_b, tz_b):
    count, rows, planes, wide_z = grad.shape
    four = lo.shape[0]
    full = lambda b: (0, 0)
    return pl.pallas_call(
        halo_kernel,
        grid=(count,),
        in_specs=[
            pl.BlockSpec((1, rows, planes, wide_z), lambda b: (b, 0, 0, 0)),
            pl.BlockSpec((6, 2, rows, wide_z), lambda b: (0, 0, b, 0)),
            pl.BlockSpec((four, rows, wide_z), lambda b: (0, b, 0)),
            pl.BlockSpec((four, rows, wide_z), lambda b: (0, b, 0)),
            pl.BlockSpec((rows, wide_z), lambda b: (b, 0)),
            pl.BlockSpec((planes, wide_z), full),
            pl.BlockSpec((planes, wide_z), full),
            pl.BlockSpec((1, wide_z), full),
        ],
        out_specs=pl.BlockSpec((1, rows, planes, wide_z), lambda b: (b, 0, 0, 0)),
        out_shape=jax.ShapeDtypeStruct(grad.shape, jnp.float32),
        input_output_aliases={0: 0},
    )(grad, aux, lo, hi, ty_b, mask_b, tx_b, tz_b)


def per_device(sources, slowness, group_size, window_anchor, tile_slot):
    slowness_window = slowness[0]
    wide_y, planes, wide_z = slowness_window.shape
    brick_index = lax.axis_index("brick")
    shot_index = lax.axis_index("shot")
    brick_count = lax.axis_size("brick")
    extent = group_size[shot_index] * planes
    depth_ids = brick_index * planes + jnp.arange(planes, dtype=jnp.int32)
    active = depth_ids < extent
    mask_col = active.astype(jnp.float32)
    src4 = sources[0].reshape(4, wide_y, planes, wide_z)

    def boundary(plane):
        pick = (jnp.arange(planes) == plane).astype(jnp.float32)[:, None]
        inv_re, inv_im = inverse_of(jnp.sum(slowness_window * pick, axis=1))
        s = jnp.sum(src4 * pick, axis=2)
        f = first_sweep(s[0], s[1], s[2], s[3], inv_re, inv_im, mask_col[plane])
        return jnp.stack(f)

    up = [(i, i + 1) for i in range(brick_count - 1)]
    down = [(j, i) for i, j in up]
    lo = lax.ppermute(boundary(planes - 1), "brick", up)
    hi = lax.ppermute(boundary(0), "brick", down)

    extent_float = extent.astype(jnp.float32)
    depth_float = depth_ids.astype(jnp.float32)
    taper_x = jnp.where(active, jnp.sin(jnp.pi * (depth_float + 0.5) / extent_float), 0.0)
    taper_y = sine_taper(wide_y, float(wide_y))
    taper_z = sine_taper(wide_z, float(wide_z))
    mask_b = jnp.broadcast_to(mask_col[:, None], (planes, wide_z))
    tx_b = jnp.broadcast_to(taper_x[:, None], (planes, wide_z))
    tz_b = taper_z[None, :]
    ty_b = jnp.broadcast_to(taper_y[:, None], (wide_y, wide_z))
    interior, aux = window_blocks(src4, slowness_window, mask_b, tx_b, tz_b, taper_y)
    blocks = apply_halo(interior, aux, lo, hi, ty_b, mask_b, tx_b, tz_b)

    shot_count = lax.axis_size("shot")
    tile_dev = tile_slot.shape[0] // shot_count
    owned = shot_index * tile_dev + jnp.arange(tile_dev, dtype=jnp.int32)
    piece_slots = tile_slot[window_anchor[:, None] + jnp.arange(BLOCKS, dtype=jnp.int32)[None, :]]
    match = owned[:, None, None] == piece_slots[None, :, :]
    gathered = lax.all_gather(blocks[None], "shot", axis=0, tiled=True)
    return gather_sum(gathered, match).reshape(1, tile_dev, -1)


def select_kernel(es_ref, eb_ref, eq_ref, n_ref, g_hbm, out_ref, buf, sem):
    n = n_ref[0]
    out_ref[...] = jnp.zeros_like(out_ref)

    def copy(e, slot):
        return pltpu.make_async_copy(g_hbm.at[es_ref[e], eb_ref[e]], buf.at[slot], sem.at[slot])

    @pl.when(n > 0)
    def _():
        copy(0, 0).start()

    def body(e, carry):
        slot = e % 2

        @pl.when(e + 1 < n)
        def _():
            copy(e + 1, 1 - slot).start()

        copy(e, slot).wait()
        q = eq_ref[e]
        out_ref[q] = out_ref[q] + buf[slot]
        return carry

    lax.fori_loop(0, n, body, 0)


def gather_sum(gathered, match):
    owners, shots, blocks = match.shape
    cell_shape = gathered.shape[2:]
    valid = jnp.any(match, axis=2).reshape(-1)
    which_block = jnp.sum(jnp.where(match, jnp.arange(blocks, dtype=jnp.int32), 0), axis=2).reshape(-1)
    shot_of = jnp.broadcast_to(jnp.arange(shots, dtype=jnp.int32)[None, :], (owners, shots)).reshape(-1)
    owner_of = jnp.broadcast_to(jnp.arange(owners, dtype=jnp.int32)[:, None], (owners, shots)).reshape(-1)
    count = owners * shots
    position = jnp.where(valid, jnp.cumsum(valid.astype(jnp.int32)) - 1, count)
    empty = jnp.zeros((count,), jnp.int32)
    es = empty.at[position].set(shot_of, mode="drop")
    eb = empty.at[position].set(which_block, mode="drop")
    eq = empty.at[position].set(owner_of, mode="drop")
    n = jnp.sum(valid.astype(jnp.int32)).reshape(1)
    return pl.pallas_call(
        select_kernel,
        grid_spec=pltpu.PrefetchScalarGridSpec(
            num_scalar_prefetch=4,
            grid=(1,),
            in_specs=[pl.BlockSpec(memory_space=pl.ANY)],
            out_specs=pl.BlockSpec((owners,) + cell_shape, lambda i, *_: (0,) * (1 + len(cell_shape))),
            scratch_shapes=[
                pltpu.VMEM((2,) + cell_shape, jnp.float32),
                pltpu.SemaphoreType.DMA((2,)),
            ],
        ),
        out_shape=jax.ShapeDtypeStruct((owners,) + cell_shape, jnp.float32),
    )(es, eb, eq, n, gathered)


def solution(mesh):
    return jax.shard_map(
        per_device,
        mesh=mesh,
        in_specs=(
            P("shot", None, None, None, "brick", None),
            P("shot", None, "brick", None),
            P(),
            P(),
            P(),
        ),
        out_specs=P("brick", "shot", None),
        check_vma=False,
    )
```

```python
import jax
import jax.numpy as jnp
from jax import lax
from jax.experimental import pallas as pl
from jax.experimental.pallas import tpu as pltpu
from jax.sharding import PartitionSpec as P

BLOCKS = 8


shift_beta = 0.5
relaxation = 0.8


def sine_taper(count, extent):
    positions = jnp.arange(count, dtype=jnp.int32).astype(jnp.float32)
    return jnp.sin(jnp.pi * (positions + 0.5) / extent)


def inverse_of(slow):
    real_d = 6.0 - slow
    imag_d = shift_beta * slow
    denominator = real_d * real_d + imag_d * imag_d
    return real_d / denominator, imag_d / denominator


def first_sweep(s0, s1, s2, s3, inv_re, inv_im, mask):
    return (
        relaxation * (s0 * inv_re - s1 * inv_im) * mask,
        relaxation * (s0 * inv_im + s1 * inv_re) * mask,
        relaxation * (s2 * inv_re - s3 * inv_im) * mask,
        relaxation * (s2 * inv_im + s3 * inv_re) * mask,
    )


def gather_plane(rows8, plane, sub_ids):
    tile = jnp.broadcast_to(rows8[0][plane:plane + 1, :], rows8[0].shape)
    for i in range(1, len(rows8)):
        tile = jnp.where(sub_ids == i, jnp.broadcast_to(rows8[i][plane:plane + 1, :], tile.shape), tile)
    return tile


def gradient_kernel(ty_ref, src_ref, src_lo_ref, src_hi_ref, sl_ref, sl_lo_ref, sl_hi_ref, consts_ref,
                    out_ref, aux_ref, f1_s, inv_s):
    b = pl.program_id(0)
    nb = pl.num_programs(0)
    rows = src_ref.shape[1]
    mask = consts_ref[0]

    def sweep_one(r, carry):
        inv_re, inv_im = inverse_of(sl_ref[r])
        inv_s[0, r] = inv_re
        inv_s[1, r] = inv_im
        f = first_sweep(src_ref[0, r], src_ref[1, r], src_ref[2, r], src_ref[3, r], inv_re, inv_im, mask)
        for k in range(4):
            f1_s[k, r + 1] = f[k]
        return carry

    lax.fori_loop(0, rows, sweep_one, 0, unroll=2)

    lo_keep = jnp.where(b > 0, 1.0, 0.0).astype(jnp.float32)
    hi_keep = jnp.where(b < nb - 1, 1.0, 0.0).astype(jnp.float32)
    for slot, s_ref, l_ref, keep in ((0, src_lo_ref, sl_lo_ref, lo_keep), (rows + 1, src_hi_ref, sl_hi_ref, hi_keep)):
        inv_re, inv_im = inverse_of(l_ref[0])
        f = first_sweep(s_ref[0, 0], s_ref[1, 0], s_ref[2, 0], s_ref[3, 0], inv_re, inv_im, mask)
        for k in range(4):
            f1_s[k, slot] = f[k] * keep

    shape = mask.shape
    p_ids = lax.broadcasted_iota(jnp.int32, shape, 0)
    z_ids = lax.broadcasted_iota(jnp.int32, shape, 1)
    planes, width = shape
    tx = consts_ref[1]
    tz = consts_ref[2]

    def sweep_two(g, carry):
        base = pl.multiple_of(g * 8, 8)
        kept = [[] for _ in range(6)]
        for i in range(8):
            r = base + i
            inv_re = inv_s[0, r]
            inv_im = inv_s[1, r]
            cur = []
            vals = []
            for k in range(4):
                c = f1_s[k, r + 1]
                acc = f1_s[k, r] + f1_s[k, r + 2]
                down = jnp.where(p_ids == 0, 0.0, pltpu.roll(c, 1, 0))
                acc = acc + down
                up = jnp.where(p_ids == planes - 1, 0.0, pltpu.roll(c, planes - 1, 0))
                acc = acc + up
                zm = jnp.where(z_ids == 0, 0.0, pltpu.roll(c, 1, 1))
                acc = acc + zm
                zp = jnp.where(z_ids == width - 1, 0.0, pltpu.roll(c, width - 1, 1))
                acc = acc + zp
                cur.append(c)
                vals.append(src_ref[k, r] + acc)
            upd = (
                vals[0] * inv_re - vals[1] * inv_im,
                vals[0] * inv_im + vals[1] * inv_re,
                vals[2] * inv_re - vals[3] * inv_im,
                vals[2] * inv_im + vals[3] * inv_re,
            )
            f2 = [((1.0 - relaxation) * cur[k] + relaxation * upd[k]) * mask for k in range(4)]
            imaging = f2[0] * f2[2] - f2[1] * f2[3] - shift_beta * (f2[0] * f2[3] + f2[1] * f2[2])
            taper = (ty_ref[b * rows + r] * tx) * tz
            out_ref[0, r] = imaging * taper
            for k, v in enumerate(f2 + [inv_re, inv_im]):
                kept[k].append(v)
        for k in range(6):
            for j, plane in enumerate((0, planes - 1)):
                aux_ref[k, j, pl.ds(base, 8), :] = gather_plane(kept[k], plane, p_ids)
        return carry

    lax.fori_loop(0, rows // 8, sweep_two, 0)


def boundary_kernel(src_ref, sl_ref, consts_ref, lo_ref, hi_ref):
    rows = src_ref.shape[1]
    mask = consts_ref[0]
    planes = mask.shape[0]
    sub_ids = lax.broadcasted_iota(jnp.int32, mask.shape, 0)
    for g in range(rows // 8):
        group = range(g * 8, g * 8 + 8)
        slabs = [[src_ref[k, r] for r in group] for k in range(4)] + [[sl_ref[r] for r in group]]
        for plane, out in ((planes - 1, lo_ref), (0, hi_ref)):
            t = [gather_plane(s, plane, sub_ids) for s in slabs]
            inv_re, inv_im = inverse_of(t[4])
            m = mask[plane:plane + 1, :]
            f = first_sweep(t[0], t[1], t[2], t[3], inv_re, inv_im, m)
            for k in range(4):
                out[k, g * 8:g * 8 + 8, :] = f[k]


def boundary_planes(src4, slow, consts):
    four, wide_y, planes, wide_z = src4.shape
    rows = wide_y // BLOCKS
    face = jax.ShapeDtypeStruct((four, wide_y, wide_z), jnp.float32)
    face_spec = pl.BlockSpec((four, rows, wide_z), lambda b: (0, b, 0))
    return pl.pallas_call(
        boundary_kernel,
        grid=(BLOCKS,),
        in_specs=[
            pl.BlockSpec((four, rows, planes, wide_z), lambda b: (0, b, 0, 0)),
            pl.BlockSpec((rows, planes, wide_z), lambda b: (b, 0, 0)),
            pl.BlockSpec(consts.shape, lambda b: (0, 0, 0)),
        ],
        out_specs=[face_spec, face_spec],
        out_shape=[face, face],
    )(src4, slow, consts)


def window_blocks(src4, slow, consts, ty):
    four, wide_y, planes, wide_z = src4.shape
    rows = wide_y // BLOCKS
    last = wide_y - 1

    def row_spec(pick):
        return pl.BlockSpec((four, 1, planes, wide_z), lambda b, t: (0, pick(b), 0, 0))

    def slow_row_spec(pick):
        return pl.BlockSpec((1, planes, wide_z), lambda b, t: (pick(b), 0, 0))

    below = lambda b: jnp.maximum(b * rows - 1, 0)
    above = lambda b: jnp.minimum(b * rows + rows, last)
    grid_spec = pltpu.PrefetchScalarGridSpec(
        num_scalar_prefetch=1,
        grid=(BLOCKS,),
        in_specs=[
            pl.BlockSpec((four, rows, planes, wide_z), lambda b, t: (0, b, 0, 0)),
            row_spec(below),
            row_spec(above),
            pl.BlockSpec((rows, planes, wide_z), lambda b, t: (b, 0, 0)),
            slow_row_spec(below),
            slow_row_spec(above),
            pl.BlockSpec(consts.shape, lambda b, t: (0, 0, 0)),
        ],
        out_specs=[
            pl.BlockSpec((1, rows, planes, wide_z), lambda b, t: (b, 0, 0, 0)),
            pl.BlockSpec((6, 2, rows, wide_z), lambda b, t: (0, 0, b, 0)),
        ],
        scratch_shapes=[
            pltpu.VMEM((four, rows + 2, planes, wide_z), jnp.float32),
            pltpu.VMEM((2, rows, planes, wide_z), jnp.float32),
        ],
    )
    return pl.pallas_call(
        gradient_kernel,
        grid_spec=grid_spec,
        out_shape=[
            jax.ShapeDtypeStruct((BLOCKS, rows, planes, wide_z), jnp.float32),
            jax.ShapeDtypeStruct((6, 2, wide_y, wide_z), jnp.float32),
        ],
    )(ty, src4, src4, src4, slow, slow, slow, consts)


def halo_kernel(grad_ref, aux_ref, lo_ref, hi_ref, ty_ref, consts_ref, out_ref):
    rows = grad_ref.shape[1]
    planes, width = consts_ref.shape[1:]
    p_ids = lax.broadcasted_iota(jnp.int32, (planes, width), 0)
    mask_all = consts_ref[0]
    tx_all = consts_ref[1]
    tz = consts_ref[2][0:1, :]
    for g in range(rows // 8):
        span = pl.ds(g * 8, 8)
        ty = ty_ref[span, :]
        fixed = []
        for j, plane, h_ref in ((0, 0, lo_ref), (1, planes - 1, hi_ref)):
            inv_re = aux_ref[4, j, span, :]
            inv_im = aux_ref[5, j, span, :]
            h = [h_ref[k, span, :] for k in range(4)]
            m = mask_all[plane:plane + 1, :]
            d = (
                h[0] * inv_re - h[1] * inv_im,
                h[0] * inv_im + h[1] * inv_re,
                h[2] * inv_re - h[3] * inv_im,
                h[2] * inv_im + h[3] * inv_re,
            )
            f2 = [aux_ref[k, j, span, :] + relaxation * d[k] * m for k in range(4)]
            imaging = f2[0] * f2[2] - f2[1] * f2[3] - shift_beta * (f2[0] * f2[3] + f2[1] * f2[2])
            fixed.append(imaging * ((ty * tx_all[plane:plane + 1, :]) * tz))
        for i in range(8):
            r = g * 8 + i
            slab = grad_ref[0, r]
            slab = jnp.where(p_ids == 0, jnp.broadcast_to(fixed[0][i:i + 1, :], slab.shape), slab)
            slab = jnp.where(p_ids == planes - 1, jnp.broadcast_to(fixed[1][i:i + 1, :], slab.shape), slab)
            out_ref[0, r] = slab


def apply_halo(grad, aux, lo, hi, ty_col, consts):
    count, rows, planes, wide_z = grad.shape
    four = lo.shape[0]
    return pl.pallas_call(
        halo_kernel,
        grid=(count,),
        in_specs=[
            pl.BlockSpec((1, rows, planes, wide_z), lambda b: (b, 0, 0, 0)),
            pl.BlockSpec((6, 2, rows, wide_z), lambda b: (0, 0, b, 0)),
            pl.BlockSpec((four, rows, wide_z), lambda b: (0, b, 0)),
            pl.BlockSpec((four, rows, wide_z), lambda b: (0, b, 0)),
            pl.BlockSpec((rows, 1), lambda b: (b, 0)),
            pl.BlockSpec(consts.shape, lambda b: (0, 0, 0)),
        ],
        out_specs=pl.BlockSpec((1, rows, planes, wide_z), lambda b: (b, 0, 0, 0)),
        out_shape=jax.ShapeDtypeStruct(grad.shape, jnp.float32),
        input_output_aliases={0: 0},
    )(grad, aux, lo, hi, ty_col, consts)


def per_device(sources, slowness, group_size, window_anchor, tile_slot):
    slowness_window = slowness[0]
    wide_y, planes, wide_z = slowness_window.shape
    brick_index = lax.axis_index("brick")
    shot_index = lax.axis_index("shot")
    brick_count = lax.axis_size("brick")
    extent = group_size[shot_index] * planes
    depth_ids = brick_index * planes + jnp.arange(planes, dtype=jnp.int32)
    active = depth_ids < extent
    mask_col = active.astype(jnp.float32)
    src4 = sources[0].reshape(4, wide_y, planes, wide_z)

    extent_float = extent.astype(jnp.float32)
    depth_float = depth_ids.astype(jnp.float32)
    taper_x = jnp.where(active, jnp.sin(jnp.pi * (depth_float + 0.5) / extent_float), 0.0)
    taper_y = sine_taper(wide_y, float(wide_y))
    taper_z = sine_taper(wide_z, float(wide_z))
    consts = jnp.stack([
        jnp.broadcast_to(mask_col[:, None], (planes, wide_z)),
        jnp.broadcast_to(taper_x[:, None], (planes, wide_z)),
        jnp.broadcast_to(taper_z[None, :], (planes, wide_z)),
    ])
    lo_send, hi_send = boundary_planes(src4, slowness_window, consts)
    up = [(i, i + 1) for i in range(brick_count - 1)]
    down = [(j, i) for i, j in up]
    lo = lax.ppermute(lo_send, "brick", up)
    hi = lax.ppermute(hi_send, "brick", down)
    interior, aux = window_blocks(src4, slowness_window, consts, taper_y)
    blocks = apply_halo(interior, aux, lo, hi, taper_y[:, None], consts)

    shot_count = lax.axis_size("shot")
    tile_dev = tile_slot.shape[0] // shot_count
    owned = shot_index * tile_dev + jnp.arange(tile_dev, dtype=jnp.int32)
    piece_slots = tile_slot[window_anchor[:, None] + jnp.arange(BLOCKS, dtype=jnp.int32)[None, :]]
    match = owned[:, None, None] == piece_slots[None, :, :]
    gathered = lax.all_gather(blocks[None], "shot", axis=0, tiled=True)
    return gather_sum(gathered, match).reshape(1, tile_dev, -1)


def select_kernel(es_ref, eb_ref, eq_ref, n_ref, g_hbm, out_ref, buf, sem):
    n = n_ref[0]
    out_ref[...] = jnp.zeros_like(out_ref)

    def copy(e, slot):
        return pltpu.make_async_copy(g_hbm.at[es_ref[e], eb_ref[e]], buf.at[slot], sem.at[slot])

    @pl.when(n > 0)
    def _():
        copy(0, 0).start()

    def body(e, carry):
        slot = e % 2

        @pl.when(e + 1 < n)
        def _():
            copy(e + 1, 1 - slot).start()

        copy(e, slot).wait()
        q = eq_ref[e]
        out_ref[q] = out_ref[q] + buf[slot]
        return carry

    lax.fori_loop(0, n, body, 0)


def gather_sum(gathered, match):
    owners, shots, blocks = match.shape
    cell_shape = gathered.shape[2:]
    valid = jnp.any(match, axis=2).reshape(-1)
    which_block = jnp.sum(jnp.where(match, jnp.arange(blocks, dtype=jnp.int32), 0), axis=2).reshape(-1)
    shot_of = jnp.broadcast_to(jnp.arange(shots, dtype=jnp.int32)[None, :], (owners, shots)).reshape(-1)
    owner_of = jnp.broadcast_to(jnp.arange(owners, dtype=jnp.int32)[:, None], (owners, shots)).reshape(-1)
    count = owners * shots
    position = jnp.where(valid, jnp.cumsum(valid.astype(jnp.int32)) - 1, count)
    empty = jnp.zeros((count,), jnp.int32)
    es = empty.at[position].set(shot_of, mode="drop")
    eb = empty.at[position].set(which_block, mode="drop")
    eq = empty.at[position].set(owner_of, mode="drop")
    n = jnp.sum(valid.astype(jnp.int32)).reshape(1)
    return pl.pallas_call(
        select_kernel,
        grid_spec=pltpu.PrefetchScalarGridSpec(
            num_scalar_prefetch=4,
            grid=(1,),
            in_specs=[pl.BlockSpec(memory_space=pl.ANY)],
            out_specs=pl.BlockSpec((owners,) + cell_shape, lambda i, *_: (0,) * (1 + len(cell_shape))),
            scratch_shapes=[
                pltpu.VMEM((2,) + cell_shape, jnp.float32),
                pltpu.SemaphoreType.DMA((2,)),
            ],
        ),
        out_shape=jax.ShapeDtypeStruct((owners,) + cell_shape, jnp.float32),
    )(es, eb, eq, n, gathered)


def solution(mesh):
    return jax.shard_map(
        per_device,
        mesh=mesh,
        in_specs=(
            P("shot", None, None, None, "brick", None),
            P("shot", None, "brick", None),
            P(),
            P(),
            P(),
        ),
        out_specs=P("brick", "shot", None),
        check_vma=False,
    )
```

```python
import jax
import jax.numpy as jnp
from jax import lax
from jax.experimental import pallas as pl
from jax.experimental.pallas import tpu as pltpu
from jax.sharding import PartitionSpec as P

BLOCKS = 8


shift_beta = 0.5
relaxation = 0.8


def sine_taper(count, extent):
    positions = jnp.arange(count, dtype=jnp.int32).astype(jnp.float32)
    return jnp.sin(jnp.pi * (positions + 0.5) / extent)


def inverse_of(slow):
    real_d = 6.0 - slow
    imag_d = shift_beta * slow
    denominator = real_d * real_d + imag_d * imag_d
    return real_d / denominator, imag_d / denominator


def first_sweep(s0, s1, s2, s3, inv_re, inv_im, mask):
    return (
        relaxation * (s0 * inv_re - s1 * inv_im) * mask,
        relaxation * (s0 * inv_im + s1 * inv_re) * mask,
        relaxation * (s2 * inv_re - s3 * inv_im) * mask,
        relaxation * (s2 * inv_im + s3 * inv_re) * mask,
    )


def gather_plane(rows8, plane, sub_ids):
    tile = jnp.broadcast_to(rows8[0][plane:plane + 1, :], rows8[0].shape)
    for i in range(1, len(rows8)):
        tile = jnp.where(sub_ids == i, jnp.broadcast_to(rows8[i][plane:plane + 1, :], tile.shape), tile)
    return tile


def gradient_kernel(ty_ref, src_ref, src_lo_ref, src_hi_ref, sl_ref, sl_lo_ref, sl_hi_ref, mask_ref, tx_ref, tz_ref,
                    out_ref, aux_ref, f1_s, inv_s):
    b = pl.program_id(0)
    nb = pl.num_programs(0)
    rows = src_ref.shape[1]
    mask = mask_ref[...]

    def sweep_one(r, carry):
        inv_re, inv_im = inverse_of(sl_ref[r])
        inv_s[0, r] = inv_re
        inv_s[1, r] = inv_im
        f = first_sweep(src_ref[0, r], src_ref[1, r], src_ref[2, r], src_ref[3, r], inv_re, inv_im, mask)
        for k in range(4):
            f1_s[k, r + 1] = f[k]
        return carry

    lax.fori_loop(0, rows, sweep_one, 0, unroll=2)

    lo_keep = jnp.where(b > 0, 1.0, 0.0).astype(jnp.float32)
    hi_keep = jnp.where(b < nb - 1, 1.0, 0.0).astype(jnp.float32)
    for slot, s_ref, l_ref, keep in ((0, src_lo_ref, sl_lo_ref, lo_keep), (rows + 1, src_hi_ref, sl_hi_ref, hi_keep)):
        inv_re, inv_im = inverse_of(l_ref[0])
        f = first_sweep(s_ref[0, 0], s_ref[1, 0], s_ref[2, 0], s_ref[3, 0], inv_re, inv_im, mask)
        for k in range(4):
            f1_s[k, slot] = f[k] * keep

    shape = mask.shape
    p_ids = lax.broadcasted_iota(jnp.int32, shape, 0)
    z_ids = lax.broadcasted_iota(jnp.int32, shape, 1)
    planes, width = shape
    tx = tx_ref[...]
    tz = tz_ref[...]

    def sweep_two(g, carry):
        base = pl.multiple_of(g * 8, 8)
        kept = [[] for _ in range(6)]
        grads = []
        for i in range(8):
            r = base + i
            inv_re = inv_s[0, r]
            inv_im = inv_s[1, r]
            cur = []
            vals = []
            for k in range(4):
                c = f1_s[k, r + 1]
                acc = f1_s[k, r] + f1_s[k, r + 2]
                down = jnp.where(p_ids == 0, 0.0, pltpu.roll(c, 1, 0))
                acc = acc + down
                up = jnp.where(p_ids == planes - 1, 0.0, pltpu.roll(c, planes - 1, 0))
                acc = acc + up
                zm = jnp.where(z_ids == 0, 0.0, pltpu.roll(c, 1, 1))
                acc = acc + zm
                zp = jnp.where(z_ids == width - 1, 0.0, pltpu.roll(c, width - 1, 1))
                acc = acc + zp
                cur.append(c)
                vals.append(src_ref[k, r] + acc)
            upd = (
                vals[0] * inv_re - vals[1] * inv_im,
                vals[0] * inv_im + vals[1] * inv_re,
                vals[2] * inv_re - vals[3] * inv_im,
                vals[2] * inv_im + vals[3] * inv_re,
            )
            f2 = [((1.0 - relaxation) * cur[k] + relaxation * upd[k]) * mask for k in range(4)]
            imaging = f2[0] * f2[2] - f2[1] * f2[3] - shift_beta * (f2[0] * f2[3] + f2[1] * f2[2])
            taper = (ty_ref[b * rows + r] * tx) * tz
            grads.append(imaging * taper)
            for k, v in enumerate(f2 + [inv_re, inv_im]):
                kept[k].append(v)
        for k in range(6):
            for j, plane in enumerate((0, planes - 1)):
                aux_ref[k, j, pl.ds(base, 8), :] = gather_plane(kept[k], plane, p_ids)
        for plane in range(1, planes - 1):
            out_ref[0, plane - 1, pl.ds(base, 8), :] = gather_plane(grads, plane, p_ids)
        return carry

    lax.fori_loop(0, rows // 8, sweep_two, 0)


def window_blocks(src4, slow, mask_b, tx_b, tz_b, ty):
    four, wide_y, planes, wide_z = src4.shape
    rows = wide_y // BLOCKS
    last = wide_y - 1

    def row_spec(pick):
        return pl.BlockSpec((four, 1, planes, wide_z), lambda b, t: (0, pick(b), 0, 0))

    def slow_row_spec(pick):
        return pl.BlockSpec((1, planes, wide_z), lambda b, t: (pick(b), 0, 0))

    below = lambda b: jnp.maximum(b * rows - 1, 0)
    above = lambda b: jnp.minimum(b * rows + rows, last)
    grid_spec = pltpu.PrefetchScalarGridSpec(
        num_scalar_prefetch=1,
        grid=(BLOCKS,),
        in_specs=[
            pl.BlockSpec((four, rows, planes, wide_z), lambda b, t: (0, b, 0, 0)),
            row_spec(below),
            row_spec(above),
            pl.BlockSpec((rows, planes, wide_z), lambda b, t: (b, 0, 0)),
            slow_row_spec(below),
            slow_row_spec(above),
            pl.BlockSpec((planes, wide_z), lambda b, t: (0, 0)),
            pl.BlockSpec((planes, wide_z), lambda b, t: (0, 0)),
            pl.BlockSpec((1, wide_z), lambda b, t: (0, 0)),
        ],
        out_specs=[
            pl.BlockSpec((1, planes - 2, rows, wide_z), lambda b, t: (b, 0, 0, 0)),
            pl.BlockSpec((6, 2, rows, wide_z), lambda b, t: (0, 0, b, 0)),
        ],
        scratch_shapes=[
            pltpu.VMEM((four, rows + 2, planes, wide_z), jnp.float32),
            pltpu.VMEM((2, rows, planes, wide_z), jnp.float32),
        ],
    )
    return pl.pallas_call(
        gradient_kernel,
        grid_spec=grid_spec,
        out_shape=[
            jax.ShapeDtypeStruct((BLOCKS, planes - 2, rows, wide_z), jnp.float32),
            jax.ShapeDtypeStruct((6, 2, wide_y, wide_z), jnp.float32),
        ],
    )(ty, src4, src4, src4, slow, slow, slow, mask_b, tx_b, tz_b)


def halo_kernel(aux_ref, lo_ref, hi_ref, ty_ref, mask_ref, tx_ref, tz_ref, out_ref):
    rows = aux_ref.shape[2]
    planes = mask_ref.shape[0]
    tz = tz_ref[...]
    for g in range(rows // 8):
        span = pl.ds(g * 8, 8)
        ty = ty_ref[span, :]
        for j, plane, h_ref in ((0, 0, lo_ref), (1, planes - 1, hi_ref)):
            inv_re = aux_ref[4, j, span, :]
            inv_im = aux_ref[5, j, span, :]
            h = [h_ref[k, span, :] for k in range(4)]
            m = mask_ref[plane:plane + 1, :]
            d = (
                h[0] * inv_re - h[1] * inv_im,
                h[0] * inv_im + h[1] * inv_re,
                h[2] * inv_re - h[3] * inv_im,
                h[2] * inv_im + h[3] * inv_re,
            )
            f2 = [aux_ref[k, j, span, :] + relaxation * d[k] * m for k in range(4)]
            imaging = f2[0] * f2[2] - f2[1] * f2[3] - shift_beta * (f2[0] * f2[3] + f2[1] * f2[2])
            out_ref[0, j, span, :] = imaging * ((ty * tx_ref[plane:plane + 1, :]) * tz)


def edge_planes(aux, lo, hi, ty_col, mask_b, tx_b, tz_b):
    wide_y, wide_z = lo.shape[1:]
    rows = wide_y // BLOCKS
    four = lo.shape[0]
    planes = mask_b.shape[0]
    full = lambda b: (0, 0)
    return pl.pallas_call(
        halo_kernel,
        grid=(BLOCKS,),
        in_specs=[
            pl.BlockSpec((6, 2, rows, wide_z), lambda b: (0, 0, b, 0)),
            pl.BlockSpec((four, rows, wide_z), lambda b: (0, b, 0)),
            pl.BlockSpec((four, rows, wide_z), lambda b: (0, b, 0)),
            pl.BlockSpec((rows, 1), lambda b: (b, 0)),
            pl.BlockSpec((planes, wide_z), full),
            pl.BlockSpec((planes, wide_z), full),
            pl.BlockSpec((1, wide_z), full),
        ],
        out_specs=pl.BlockSpec((1, 2, rows, wide_z), lambda b: (b, 0, 0, 0)),
        out_shape=jax.ShapeDtypeStruct((BLOCKS, 2, rows, wide_z), jnp.float32),
    )(aux, lo, hi, ty_col, mask_b, tx_b, tz_b)


def per_device(sources, slowness, group_size, window_anchor, tile_slot):
    slowness_window = slowness[0]
    wide_y, planes, wide_z = slowness_window.shape
    brick_index = lax.axis_index("brick")
    shot_index = lax.axis_index("shot")
    brick_count = lax.axis_size("brick")
    extent = group_size[shot_index] * planes
    depth_ids = brick_index * planes + jnp.arange(planes, dtype=jnp.int32)
    active = depth_ids < extent
    mask_col = active.astype(jnp.float32)
    src4 = sources[0].reshape(4, wide_y, planes, wide_z)

    def boundary(plane):
        inv_re, inv_im = inverse_of(slowness_window[:, plane, :])
        s = src4[:, :, plane, :]
        f = first_sweep(s[0], s[1], s[2], s[3], inv_re, inv_im, mask_col[plane])
        return jnp.stack(f)

    up = [(i, i + 1) for i in range(brick_count - 1)]
    down = [(j, i) for i, j in up]
    lo = lax.ppermute(boundary(planes - 1), "brick", up)
    hi = lax.ppermute(boundary(0), "brick", down)

    extent_float = extent.astype(jnp.float32)
    depth_float = depth_ids.astype(jnp.float32)
    taper_x = jnp.where(active, jnp.sin(jnp.pi * (depth_float + 0.5) / extent_float), 0.0)
    taper_y = sine_taper(wide_y, float(wide_y))
    taper_z = sine_taper(wide_z, float(wide_z))
    mask_b = jnp.broadcast_to(mask_col[:, None], (planes, wide_z))
    tx_b = jnp.broadcast_to(taper_x[:, None], (planes, wide_z))
    tz_b = taper_z[None, :]
    interior, aux = window_blocks(src4, slowness_window, mask_b, tx_b, tz_b, taper_y)
    mid = lax.all_gather(interior[None], "shot", axis=0, tiled=True)
    mid, lo, hi = lax.optimization_barrier((mid, lo, hi))
    edges = edge_planes(aux, lo, hi, taper_y[:, None], mask_b, tx_b, tz_b)

    shot_count = lax.axis_size("shot")
    tile_dev = tile_slot.shape[0] // shot_count
    owned = shot_index * tile_dev + jnp.arange(tile_dev, dtype=jnp.int32)
    piece_slots = tile_slot[window_anchor[:, None] + jnp.arange(BLOCKS, dtype=jnp.int32)[None, :]]
    match = owned[:, None, None] == piece_slots[None, :, :]
    rim = lax.all_gather(edges[None], "shot", axis=0, tiled=True)
    summed = gather_sum(mid, rim, match)
    return jnp.transpose(summed, (0, 2, 1, 3)).reshape(1, tile_dev, -1)


def select_kernel(es_ref, eb_ref, eq_ref, n_ref, mid_hbm, rim_hbm, out_ref, buf, sem):
    n = n_ref[0]
    last = buf.shape[1] - 1
    out_ref[...] = jnp.zeros_like(out_ref)

    def copies(e, slot):
        s = es_ref[e]
        b = eb_ref[e]
        return (
            pltpu.make_async_copy(mid_hbm.at[s, b], buf.at[slot, pl.ds(1, last - 1)], sem.at[slot, 0]),
            pltpu.make_async_copy(rim_hbm.at[s, b, 0], buf.at[slot, 0], sem.at[slot, 1]),
            pltpu.make_async_copy(rim_hbm.at[s, b, 1], buf.at[slot, last], sem.at[slot, 2]),
        )

    @pl.when(n > 0)
    def _():
        for c in copies(0, 0):
            c.start()

    def body(e, carry):
        slot = e % 2

        @pl.when(e + 1 < n)
        def _():
            for c in copies(e + 1, 1 - slot):
                c.start()

        for c in copies(e, slot):
            c.wait()
        q = eq_ref[e]
        out_ref[q] = out_ref[q] + buf[slot]
        return carry

    lax.fori_loop(0, n, body, 0)


def gather_sum(mid, rim, match):
    owners, shots, blocks = match.shape
    cell_shape = (mid.shape[2] + rim.shape[2],) + mid.shape[3:]
    valid = jnp.any(match, axis=2).reshape(-1)
    which_block = jnp.sum(jnp.where(match, jnp.arange(blocks, dtype=jnp.int32), 0), axis=2).reshape(-1)
    shot_of = jnp.broadcast_to(jnp.arange(shots, dtype=jnp.int32)[None, :], (owners, shots)).reshape(-1)
    owner_of = jnp.broadcast_to(jnp.arange(owners, dtype=jnp.int32)[:, None], (owners, shots)).reshape(-1)
    count = owners * shots
    position = jnp.where(valid, jnp.cumsum(valid.astype(jnp.int32)) - 1, count)
    empty = jnp.zeros((count,), jnp.int32)
    es = empty.at[position].set(shot_of, mode="drop")
    eb = empty.at[position].set(which_block, mode="drop")
    eq = empty.at[position].set(owner_of, mode="drop")
    n = jnp.sum(valid.astype(jnp.int32)).reshape(1)
    return pl.pallas_call(
        select_kernel,
        grid_spec=pltpu.PrefetchScalarGridSpec(
            num_scalar_prefetch=4,
            grid=(1,),
            in_specs=[pl.BlockSpec(memory_space=pl.ANY), pl.BlockSpec(memory_space=pl.ANY)],
            out_specs=pl.BlockSpec((owners,) + cell_shape, lambda i, *_: (0,) * (1 + len(cell_shape))),
            scratch_shapes=[
                pltpu.VMEM((2,) + cell_shape, jnp.float32),
                pltpu.SemaphoreType.DMA((2, 3)),
            ],
        ),
        out_shape=jax.ShapeDtypeStruct((owners,) + cell_shape, jnp.float32),
    )(es, eb, eq, n, mid, rim)


def solution(mesh):
    return jax.shard_map(
        per_device,
        mesh=mesh,
        in_specs=(
            P("shot", None, None, None, "brick", None),
            P("shot", None, "brick", None),
            P(),
            P(),
            P(),
        ),
        out_specs=P("brick", "shot", None),
        check_vma=False,
    )
```

```python
import jax
import jax.numpy as jnp
from jax import lax
from jax.experimental import pallas as pl
from jax.experimental.pallas import tpu as pltpu
from jax.sharding import PartitionSpec as P

BLOCKS = 8


shift_beta = 0.5
relaxation = 0.8


def sine_taper(count, extent):
    positions = jnp.arange(count, dtype=jnp.int32).astype(jnp.float32)
    return jnp.sin(jnp.pi * (positions + 0.5) / extent)


def inverse_of(slow):
    real_d = 6.0 - slow
    imag_d = shift_beta * slow
    denominator = real_d * real_d + imag_d * imag_d
    return real_d / denominator, imag_d / denominator


def first_sweep(s0, s1, s2, s3, inv_re, inv_im, mask):
    return (
        relaxation * (s0 * inv_re - s1 * inv_im) * mask,
        relaxation * (s0 * inv_im + s1 * inv_re) * mask,
        relaxation * (s2 * inv_re - s3 * inv_im) * mask,
        relaxation * (s2 * inv_im + s3 * inv_re) * mask,
    )


def gather_plane(rows8, plane, sub_ids):
    tile = jnp.broadcast_to(rows8[0][plane:plane + 1, :], rows8[0].shape)
    for i in range(1, len(rows8)):
        tile = jnp.where(sub_ids == i, jnp.broadcast_to(rows8[i][plane:plane + 1, :], tile.shape), tile)
    return tile


def gradient_kernel(ty_ref, src_ref, src_lo_ref, src_hi_ref, sl_ref, sl_lo_ref, sl_hi_ref, mask_ref, tx_ref, tz_ref,
                    out_ref, aux_ref, f1_s, inv_s):
    b = pl.program_id(0)
    nb = pl.num_programs(0)
    rows = src_ref.shape[1]
    mask = mask_ref[...]

    def sweep_one(r, carry):
        inv_re, inv_im = inverse_of(sl_ref[r])
        inv_s[0, r] = inv_re
        inv_s[1, r] = inv_im
        f = first_sweep(src_ref[0, r], src_ref[1, r], src_ref[2, r], src_ref[3, r], inv_re, inv_im, mask)
        for k in range(4):
            f1_s[k, r + 1] = f[k]
        return carry

    lax.fori_loop(0, rows, sweep_one, 0, unroll=2)

    lo_keep = jnp.where(b > 0, 1.0, 0.0).astype(jnp.float32)
    hi_keep = jnp.where(b < nb - 1, 1.0, 0.0).astype(jnp.float32)
    for slot, s_ref, l_ref, keep in ((0, src_lo_ref, sl_lo_ref, lo_keep), (rows + 1, src_hi_ref, sl_hi_ref, hi_keep)):
        inv_re, inv_im = inverse_of(l_ref[0])
        f = first_sweep(s_ref[0, 0], s_ref[1, 0], s_ref[2, 0], s_ref[3, 0], inv_re, inv_im, mask)
        for k in range(4):
            f1_s[k, slot] = f[k] * keep

    shape = mask.shape
    p_ids = lax.broadcasted_iota(jnp.int32, shape, 0)
    z_ids = lax.broadcasted_iota(jnp.int32, shape, 1)
    planes, width = shape
    tx = tx_ref[...]
    tz = tz_ref[...]

    def sweep_two(g, carry):
        base = pl.multiple_of(g * 8, 8)
        kept = [[] for _ in range(6)]
        for i in range(8):
            r = base + i
            inv_re = inv_s[0, r]
            inv_im = inv_s[1, r]
            cur = []
            vals = []
            for k in range(4):
                c = f1_s[k, r + 1]
                acc = f1_s[k, r] + f1_s[k, r + 2]
                down = jnp.where(p_ids == 0, 0.0, pltpu.roll(c, 1, 0))
                acc = acc + down
                up = jnp.where(p_ids == planes - 1, 0.0, pltpu.roll(c, planes - 1, 0))
                acc = acc + up
                zm = jnp.where(z_ids == 0, 0.0, pltpu.roll(c, 1, 1))
                acc = acc + zm
                zp = jnp.where(z_ids == width - 1, 0.0, pltpu.roll(c, width - 1, 1))
                acc = acc + zp
                cur.append(c)
                vals.append(src_ref[k, r] + acc)
            upd = (
                vals[0] * inv_re - vals[1] * inv_im,
                vals[0] * inv_im + vals[1] * inv_re,
                vals[2] * inv_re - vals[3] * inv_im,
                vals[2] * inv_im + vals[3] * inv_re,
            )
            f2 = [((1.0 - relaxation) * cur[k] + relaxation * upd[k]) * mask for k in range(4)]
            imaging = f2[0] * f2[2] - f2[1] * f2[3] - shift_beta * (f2[0] * f2[3] + f2[1] * f2[2])
            taper = (ty_ref[b * rows + r] * tx) * tz
            out_ref[0, r] = imaging * taper
            for k, v in enumerate(f2 + [inv_re, inv_im]):
                kept[k].append(v)
        for k in range(6):
            for j, plane in enumerate((0, planes - 1)):
                aux_ref[k, j, pl.ds(base, 8), :] = gather_plane(kept[k], plane, p_ids)
        return carry

    lax.fori_loop(0, rows // 8, sweep_two, 0)


def boundary_kernel(mask_ref, src_hbm, sl_hbm, lo_ref, hi_ref, src_buf, sl_buf, sem):
    four = src_hbm.shape[0]
    planes = src_hbm.shape[2]
    copies = []
    for j, plane in enumerate((planes - 1, 0)):
        for k in range(four):
            copies.append(pltpu.make_async_copy(src_hbm.at[k, :, plane, :], src_buf.at[j, k], sem.at[j, k]))
        copies.append(pltpu.make_async_copy(sl_hbm.at[:, plane, :], sl_buf.at[j], sem.at[j, four]))
    for c in copies:
        c.start()
    for c in copies:
        c.wait()
    for j, (plane, out) in enumerate(((planes - 1, lo_ref), (0, hi_ref))):
        m = mask_ref[plane]
        inv_re, inv_im = inverse_of(sl_buf[j])
        f = first_sweep(src_buf[j, 0], src_buf[j, 1], src_buf[j, 2], src_buf[j, 3], inv_re, inv_im, m)
        for k in range(four):
            out[k] = f[k]


def boundary_planes(src4, slow, mask_col):
    four, wide_y, planes, wide_z = src4.shape
    face = jax.ShapeDtypeStruct((four, wide_y, wide_z), jnp.float32)
    vmem = pl.BlockSpec(memory_space=pltpu.VMEM)
    return pl.pallas_call(
        boundary_kernel,
        in_specs=[
            pl.BlockSpec(memory_space=pltpu.SMEM),
            pl.BlockSpec(memory_space=pl.ANY),
            pl.BlockSpec(memory_space=pl.ANY),
        ],
        out_specs=[vmem, vmem],
        out_shape=[face, face],
        scratch_shapes=[
            pltpu.VMEM((2, four, wide_y, wide_z), jnp.float32),
            pltpu.VMEM((2, wide_y, wide_z), jnp.float32),
            pltpu.SemaphoreType.DMA((2, four + 1)),
        ],
    )(mask_col, src4, slow)


def window_blocks(src4, slow, mask_b, tx_b, tz_b, ty):
    four, wide_y, planes, wide_z = src4.shape
    rows = wide_y // BLOCKS
    last = wide_y - 1

    def row_spec(pick):
        return pl.BlockSpec((four, 1, planes, wide_z), lambda b, t: (0, pick(b), 0, 0))

    def slow_row_spec(pick):
        return pl.BlockSpec((1, planes, wide_z), lambda b, t: (pick(b), 0, 0))

    below = lambda b: jnp.maximum(b * rows - 1, 0)
    above = lambda b: jnp.minimum(b * rows + rows, last)
    grid_spec = pltpu.PrefetchScalarGridSpec(
        num_scalar_prefetch=1,
        grid=(BLOCKS,),
        in_specs=[
            pl.BlockSpec((four, rows, planes, wide_z), lambda b, t: (0, b, 0, 0)),
            row_spec(below),
            row_spec(above),
            pl.BlockSpec((rows, planes, wide_z), lambda b, t: (b, 0, 0)),
            slow_row_spec(below),
            slow_row_spec(above),
            pl.BlockSpec((planes, wide_z), lambda b, t: (0, 0)),
            pl.BlockSpec((planes, wide_z), lambda b, t: (0, 0)),
            pl.BlockSpec((1, wide_z), lambda b, t: (0, 0)),
        ],
        out_specs=[
            pl.BlockSpec((1, rows, planes, wide_z), lambda b, t: (b, 0, 0, 0)),
            pl.BlockSpec((6, 2, rows, wide_z), lambda b, t: (0, 0, b, 0)),
        ],
        scratch_shapes=[
            pltpu.VMEM((four, rows + 2, planes, wide_z), jnp.float32),
            pltpu.VMEM((2, rows, planes, wide_z), jnp.float32),
        ],
    )
    return pl.pallas_call(
        gradient_kernel,
        grid_spec=grid_spec,
        out_shape=[
            jax.ShapeDtypeStruct((BLOCKS, rows, planes, wide_z), jnp.float32),
            jax.ShapeDtypeStruct((6, 2, wide_y, wide_z), jnp.float32),
        ],
    )(ty, src4, src4, src4, slow, slow, slow, mask_b, tx_b, tz_b)


def halo_kernel(grad_ref, aux_ref, lo_ref, hi_ref, ty_ref, mask_ref, tx_ref, tz_ref, out_ref):
    rows = grad_ref.shape[1]
    planes, width = mask_ref.shape
    p_ids = lax.broadcasted_iota(jnp.int32, (planes, width), 0)
    tz = tz_ref[...]
    for g in range(rows // 8):
        span = pl.ds(g * 8, 8)
        ty = ty_ref[span, :]
        fixed = []
        for j, plane, h_ref in ((0, 0, lo_ref), (1, planes - 1, hi_ref)):
            inv_re = aux_ref[4, j, span, :]
            inv_im = aux_ref[5, j, span, :]
            h = [h_ref[k, span, :] for k in range(4)]
            m = mask_ref[plane:plane + 1, :]
            d = (
                h[0] * inv_re - h[1] * inv_im,
                h[0] * inv_im + h[1] * inv_re,
                h[2] * inv_re - h[3] * inv_im,
                h[2] * inv_im + h[3] * inv_re,
            )
            f2 = [aux_ref[k, j, span, :] + relaxation * d[k] * m for k in range(4)]
            imaging = f2[0] * f2[2] - f2[1] * f2[3] - shift_beta * (f2[0] * f2[3] + f2[1] * f2[2])
            fixed.append(imaging * ((ty * tx_ref[plane:plane + 1, :]) * tz))
        for i in range(8):
            r = g * 8 + i
            slab = grad_ref[0, r]
            slab = jnp.where(p_ids == 0, jnp.broadcast_to(fixed[0][i:i + 1, :], slab.shape), slab)
            slab = jnp.where(p_ids == planes - 1, jnp.broadcast_to(fixed[1][i:i + 1, :], slab.shape), slab)
            out_ref[0, r] = slab


def apply_halo(grad, aux, lo, hi, ty_b, mask_b, tx_b, tz_b):
    count, rows, planes, wide_z = grad.shape
    four = lo.shape[0]
    full = lambda b: (0, 0)
    return pl.pallas_call(
        halo_kernel,
        grid=(count,),
        in_specs=[
            pl.BlockSpec((1, rows, planes, wide_z), lambda b: (b, 0, 0, 0)),
            pl.BlockSpec((6, 2, rows, wide_z), lambda b: (0, 0, b, 0)),
            pl.BlockSpec((four, rows, wide_z), lambda b: (0, b, 0)),
            pl.BlockSpec((four, rows, wide_z), lambda b: (0, b, 0)),
            pl.BlockSpec((rows, wide_z), lambda b: (b, 0)),
            pl.BlockSpec((planes, wide_z), full),
            pl.BlockSpec((planes, wide_z), full),
            pl.BlockSpec((1, wide_z), full),
        ],
        out_specs=pl.BlockSpec((1, rows, planes, wide_z), lambda b: (b, 0, 0, 0)),
        out_shape=jax.ShapeDtypeStruct(grad.shape, jnp.float32),
        input_output_aliases={0: 0},
    )(grad, aux, lo, hi, ty_b, mask_b, tx_b, tz_b)


def per_device(sources, slowness, group_size, window_anchor, tile_slot):
    slowness_window = slowness[0]
    wide_y, planes, wide_z = slowness_window.shape
    brick_index = lax.axis_index("brick")
    shot_index = lax.axis_index("shot")
    brick_count = lax.axis_size("brick")
    extent = group_size[shot_index] * planes
    depth_ids = brick_index * planes + jnp.arange(planes, dtype=jnp.int32)
    active = depth_ids < extent
    mask_col = active.astype(jnp.float32)
    src4 = sources[0].reshape(4, wide_y, planes, wide_z)

    lo_send, hi_send = boundary_planes(src4, slowness_window, mask_col)
    up = [(i, i + 1) for i in range(brick_count - 1)]
    down = [(j, i) for i, j in up]
    lo = lax.ppermute(lo_send, "brick", up)
    hi = lax.ppermute(hi_send, "brick", down)

    extent_float = extent.astype(jnp.float32)
    depth_float = depth_ids.astype(jnp.float32)
    taper_x = jnp.where(active, jnp.sin(jnp.pi * (depth_float + 0.5) / extent_float), 0.0)
    taper_y = sine_taper(wide_y, float(wide_y))
    taper_z = sine_taper(wide_z, float(wide_z))
    mask_b = jnp.broadcast_to(mask_col[:, None], (planes, wide_z))
    tx_b = jnp.broadcast_to(taper_x[:, None], (planes, wide_z))
    tz_b = taper_z[None, :]
    ty_b = jnp.broadcast_to(taper_y[:, None], (wide_y, wide_z))
    interior, aux = window_blocks(src4, slowness_window, mask_b, tx_b, tz_b, taper_y)
    blocks = apply_halo(interior, aux, lo, hi, ty_b, mask_b, tx_b, tz_b)

    shot_count = lax.axis_size("shot")
    tile_dev = tile_slot.shape[0] // shot_count
    owned = shot_index * tile_dev + jnp.arange(tile_dev, dtype=jnp.int32)
    piece_slots = tile_slot[window_anchor[:, None] + jnp.arange(BLOCKS, dtype=jnp.int32)[None, :]]
    match = owned[:, None, None] == piece_slots[None, :, :]
    gathered = lax.all_gather(blocks[None], "shot", axis=0, tiled=True)
    return gather_sum(gathered, match).reshape(1, tile_dev, -1)


def select_kernel(es_ref, eb_ref, eq_ref, n_ref, g_hbm, out_ref, buf, sem):
    n = n_ref[0]
    out_ref[...] = jnp.zeros_like(out_ref)

    def copy(e, slot):
        return pltpu.make_async_copy(g_hbm.at[es_ref[e], eb_ref[e]], buf.at[slot], sem.at[slot])

    @pl.when(n > 0)
    def _():
        copy(0, 0).start()

    def body(e, carry):
        slot = e % 2

        @pl.when(e + 1 < n)
        def _():
            copy(e + 1, 1 - slot).start()

        copy(e, slot).wait()
        q = eq_ref[e]
        out_ref[q] = out_ref[q] + buf[slot]
        return carry

    lax.fori_loop(0, n, body, 0)


def gather_sum(gathered, match):
    owners, shots, blocks = match.shape
    cell_shape = gathered.shape[2:]
    valid = jnp.any(match, axis=2).reshape(-1)
    which_block = jnp.sum(jnp.where(match, jnp.arange(blocks, dtype=jnp.int32), 0), axis=2).reshape(-1)
    shot_of = jnp.broadcast_to(jnp.arange(shots, dtype=jnp.int32)[None, :], (owners, shots)).reshape(-1)
    owner_of = jnp.broadcast_to(jnp.arange(owners, dtype=jnp.int32)[:, None], (owners, shots)).reshape(-1)
    count = owners * shots
    position = jnp.where(valid, jnp.cumsum(valid.astype(jnp.int32)) - 1, count)
    empty = jnp.zeros((count,), jnp.int32)
    es = empty.at[position].set(shot_of, mode="drop")
    eb = empty.at[position].set(which_block, mode="drop")
    eq = empty.at[position].set(owner_of, mode="drop")
    n = jnp.sum(valid.astype(jnp.int32)).reshape(1)
    return pl.pallas_call(
        select_kernel,
        grid_spec=pltpu.PrefetchScalarGridSpec(
            num_scalar_prefetch=4,
            grid=(1,),
            in_specs=[pl.BlockSpec(memory_space=pl.ANY)],
            out_specs=pl.BlockSpec((owners,) + cell_shape, lambda i, *_: (0,) * (1 + len(cell_shape))),
            scratch_shapes=[
                pltpu.VMEM((2,) + cell_shape, jnp.float32),
                pltpu.SemaphoreType.DMA((2,)),
            ],
        ),
        out_shape=jax.ShapeDtypeStruct((owners,) + cell_shape, jnp.float32),
    )(es, eb, eq, n, gathered)


def solution(mesh):
    return jax.shard_map(
        per_device,
        mesh=mesh,
        in_specs=(
            P("shot", None, None, None, "brick", None),
            P("shot", None, "brick", None),
            P(),
            P(),
            P(),
        ),
        out_specs=P("brick", "shot", None),
        check_vma=False,
    )
```

```python
import jax
import jax.numpy as jnp
from jax import lax
from jax.experimental import pallas as pl
from jax.experimental.pallas import tpu as pltpu
from jax.sharding import PartitionSpec as P

BLOCKS = 8


shift_beta = 0.5
relaxation = 0.8


def sine_taper(count, extent):
    positions = jnp.arange(count, dtype=jnp.int32).astype(jnp.float32)
    return jnp.sin(jnp.pi * (positions + 0.5) / extent)


def inverse_of(slow):
    real_d = 6.0 - slow
    imag_d = shift_beta * slow
    denominator = real_d * real_d + imag_d * imag_d
    return real_d / denominator, imag_d / denominator


def first_sweep(s0, s1, s2, s3, inv_re, inv_im, mask):
    return (
        relaxation * (s0 * inv_re - s1 * inv_im) * mask,
        relaxation * (s0 * inv_im + s1 * inv_re) * mask,
        relaxation * (s2 * inv_re - s3 * inv_im) * mask,
        relaxation * (s2 * inv_im + s3 * inv_re) * mask,
    )


def gather_plane(rows8, plane, sub_ids):
    tile = jnp.broadcast_to(rows8[0][plane:plane + 1, :], rows8[0].shape)
    for i in range(1, len(rows8)):
        tile = jnp.where(sub_ids == i, jnp.broadcast_to(rows8[i][plane:plane + 1, :], tile.shape), tile)
    return tile


def gradient_kernel(ty_ref, src_ref, src_lo_ref, src_hi_ref, sl_ref, sl_lo_ref, sl_hi_ref, mask_ref, tx_ref, tz_ref,
                    out_ref, aux_ref, f1_s, inv_s):
    b = pl.program_id(0)
    nb = pl.num_programs(0)
    rows = src_ref.shape[1]
    mask = mask_ref[...]

    def sweep_one(r, carry):
        inv_re, inv_im = inverse_of(sl_ref[r])
        inv_s[0, r] = inv_re
        inv_s[1, r] = inv_im
        f = first_sweep(src_ref[0, r], src_ref[1, r], src_ref[2, r], src_ref[3, r], inv_re, inv_im, mask)
        for k in range(4):
            f1_s[k, r + 1] = f[k]
        return carry

    lax.fori_loop(0, rows, sweep_one, 0, unroll=2)

    lo_keep = jnp.where(b > 0, 1.0, 0.0).astype(jnp.float32)
    hi_keep = jnp.where(b < nb - 1, 1.0, 0.0).astype(jnp.float32)
    for slot, s_ref, l_ref, keep in ((0, src_lo_ref, sl_lo_ref, lo_keep), (rows + 1, src_hi_ref, sl_hi_ref, hi_keep)):
        inv_re, inv_im = inverse_of(l_ref[0])
        f = first_sweep(s_ref[0, 0], s_ref[1, 0], s_ref[2, 0], s_ref[3, 0], inv_re, inv_im, mask)
        for k in range(4):
            f1_s[k, slot] = f[k] * keep

    shape = mask.shape
    p_ids = lax.broadcasted_iota(jnp.int32, shape, 0)
    z_ids = lax.broadcasted_iota(jnp.int32, shape, 1)
    planes, width = shape
    tx = tx_ref[...]
    tz = tz_ref[...]

    def sweep_two(g, carry):
        base = pl.multiple_of(g * 8, 8)
        kept = [[] for _ in range(6)]
        for i in range(8):
            r = base + i
            inv_re = inv_s[0, r]
            inv_im = inv_s[1, r]
            cur = []
            vals = []
            for k in range(4):
                c = f1_s[k, r + 1]
                acc = f1_s[k, r] + f1_s[k, r + 2]
                down = jnp.where(p_ids == 0, 0.0, pltpu.roll(c, 1, 0))
                acc = acc + down
                up = jnp.where(p_ids == planes - 1, 0.0, pltpu.roll(c, planes - 1, 0))
                acc = acc + up
                zm = jnp.where(z_ids == 0, 0.0, pltpu.roll(c, 1, 1))
                acc = acc + zm
                zp = jnp.where(z_ids == width - 1, 0.0, pltpu.roll(c, width - 1, 1))
                acc = acc + zp
                cur.append(c)
                vals.append(src_ref[k, r] + acc)
            upd = (
                vals[0] * inv_re - vals[1] * inv_im,
                vals[0] * inv_im + vals[1] * inv_re,
                vals[2] * inv_re - vals[3] * inv_im,
                vals[2] * inv_im + vals[3] * inv_re,
            )
            f2 = [((1.0 - relaxation) * cur[k] + relaxation * upd[k]) * mask for k in range(4)]
            imaging = f2[0] * f2[2] - f2[1] * f2[3] - shift_beta * (f2[0] * f2[3] + f2[1] * f2[2])
            taper = (ty_ref[b * rows + r] * tx) * tz
            out_ref[0, r] = imaging * taper
            for k, v in enumerate(f2 + [inv_re, inv_im]):
                kept[k].append(v)
        for k in range(6):
            for j, plane in enumerate((0, planes - 1)):
                aux_ref[k, j, pl.ds(base, 8), :] = gather_plane(kept[k], plane, p_ids)
        return carry

    lax.fori_loop(0, rows // 8, sweep_two, 0)


def boundary_kernel(mask_ref, src_hbm, sl_hbm, lo_ref, hi_ref, src_buf, sl_buf, sem):
    four = src_hbm.shape[0]
    planes = src_hbm.shape[2]
    copies = []
    for j, plane in enumerate((planes - 1, 0)):
        for k in range(four):
            copies.append(pltpu.make_async_copy(src_hbm.at[k, :, plane, :], src_buf.at[j, k], sem.at[j, k]))
        copies.append(pltpu.make_async_copy(sl_hbm.at[:, plane, :], sl_buf.at[j], sem.at[j, four]))
    for c in copies:
        c.start()
    for c in copies:
        c.wait()
    for j, (plane, out) in enumerate(((planes - 1, lo_ref), (0, hi_ref))):
        m = mask_ref[plane]
        inv_re, inv_im = inverse_of(sl_buf[j])
        f = first_sweep(src_buf[j, 0], src_buf[j, 1], src_buf[j, 2], src_buf[j, 3], inv_re, inv_im, m)
        for k in range(four):
            out[k] = f[k]


def boundary_planes(src4, slow, mask_col):
    four, wide_y, planes, wide_z = src4.shape
    face = jax.ShapeDtypeStruct((four, wide_y, wide_z), jnp.float32)
    vmem = pl.BlockSpec(memory_space=pltpu.VMEM)
    return pl.pallas_call(
        boundary_kernel,
        in_specs=[
            pl.BlockSpec(memory_space=pltpu.SMEM),
            pl.BlockSpec(memory_space=pl.ANY),
            pl.BlockSpec(memory_space=pl.ANY),
        ],
        out_specs=[vmem, vmem],
        out_shape=[face, face],
        scratch_shapes=[
            pltpu.VMEM((2, four, wide_y, wide_z), jnp.float32),
            pltpu.VMEM((2, wide_y, wide_z), jnp.float32),
            pltpu.SemaphoreType.DMA((2, four + 1)),
        ],
    )(mask_col, src4, slow)


def window_blocks(src4, slow, mask_b, tx_b, tz_b, ty):
    four, wide_y, planes, wide_z = src4.shape
    rows = wide_y // BLOCKS
    last = wide_y - 1

    def row_spec(pick):
        return pl.BlockSpec((four, 1, planes, wide_z), lambda b, t: (0, pick(b), 0, 0))

    def slow_row_spec(pick):
        return pl.BlockSpec((1, planes, wide_z), lambda b, t: (pick(b), 0, 0))

    below = lambda b: jnp.maximum(b * rows - 1, 0)
    above = lambda b: jnp.minimum(b * rows + rows, last)
    grid_spec = pltpu.PrefetchScalarGridSpec(
        num_scalar_prefetch=1,
        grid=(BLOCKS,),
        in_specs=[
            pl.BlockSpec((four, rows, planes, wide_z), lambda b, t: (0, b, 0, 0)),
            row_spec(below),
            row_spec(above),
            pl.BlockSpec((rows, planes, wide_z), lambda b, t: (b, 0, 0)),
            slow_row_spec(below),
            slow_row_spec(above),
            pl.BlockSpec((planes, wide_z), lambda b, t: (0, 0)),
            pl.BlockSpec((planes, wide_z), lambda b, t: (0, 0)),
            pl.BlockSpec((1, wide_z), lambda b, t: (0, 0)),
        ],
        out_specs=[
            pl.BlockSpec((1, rows, planes, wide_z), lambda b, t: (b, 0, 0, 0)),
            pl.BlockSpec((6, 2, rows, wide_z), lambda b, t: (0, 0, b, 0)),
        ],
        scratch_shapes=[
            pltpu.VMEM((four, rows + 2, planes, wide_z), jnp.float32),
            pltpu.VMEM((2, rows, planes, wide_z), jnp.float32),
        ],
    )
    return pl.pallas_call(
        gradient_kernel,
        grid_spec=grid_spec,
        out_shape=[
            jax.ShapeDtypeStruct((BLOCKS, rows, planes, wide_z), jnp.float32),
            jax.ShapeDtypeStruct((6, 2, wide_y, wide_z), jnp.float32),
        ],
    )(ty, src4, src4, src4, slow, slow, slow, mask_b, tx_b, tz_b)


def halo_kernel(aux_ref, lo_ref, hi_ref, ty_ref, mask_ref, tx_ref, tz_ref, grad_hbm, out_hbm, fixed, sem):
    wide_y = aux_ref.shape[2]
    planes = mask_ref.shape[0]
    count, rows = out_hbm.shape[:2]
    tz = tz_ref[...]
    for g in range(wide_y // 8):
        span = pl.ds(g * 8, 8)
        ty = ty_ref[span, :]
        for j, plane, h_ref in ((0, 0, lo_ref), (1, planes - 1, hi_ref)):
            inv_re = aux_ref[4, j, span, :]
            inv_im = aux_ref[5, j, span, :]
            h = [h_ref[k, span, :] for k in range(4)]
            m = mask_ref[plane:plane + 1, :]
            d = (
                h[0] * inv_re - h[1] * inv_im,
                h[0] * inv_im + h[1] * inv_re,
                h[2] * inv_re - h[3] * inv_im,
                h[2] * inv_im + h[3] * inv_re,
            )
            f2 = [aux_ref[k, j, span, :] + relaxation * d[k] * m for k in range(4)]
            imaging = f2[0] * f2[2] - f2[1] * f2[3] - shift_beta * (f2[0] * f2[3] + f2[1] * f2[2])
            fixed[j, span, :] = imaging * ((ty * tx_ref[plane:plane + 1, :]) * tz)
    copies = []
    for j, plane in enumerate((0, planes - 1)):
        for b in range(count):
            copies.append(pltpu.make_async_copy(
                fixed.at[j, pl.ds(b * rows, rows)], out_hbm.at[b, :, plane, :], sem.at[j, b]))
    for c in copies:
        c.start()
    for c in copies:
        c.wait()


def apply_halo(grad, aux, lo, hi, ty_col, mask_b, tx_b, tz_b):
    count, rows, planes, wide_z = grad.shape
    vmem = pl.BlockSpec(memory_space=pltpu.VMEM)
    return pl.pallas_call(
        halo_kernel,
        in_specs=[vmem] * 7 + [pl.BlockSpec(memory_space=pl.ANY)],
        out_specs=pl.BlockSpec(memory_space=pl.ANY),
        out_shape=jax.ShapeDtypeStruct(grad.shape, jnp.float32),
        scratch_shapes=[
            pltpu.VMEM((2, count * rows, wide_z), jnp.float32),
            pltpu.SemaphoreType.DMA((2, count)),
        ],
        input_output_aliases={7: 0},
    )(aux, lo, hi, ty_col, mask_b, tx_b, tz_b, grad)


def per_device(sources, slowness, group_size, window_anchor, tile_slot):
    slowness_window = slowness[0]
    wide_y, planes, wide_z = slowness_window.shape
    brick_index = lax.axis_index("brick")
    shot_index = lax.axis_index("shot")
    brick_count = lax.axis_size("brick")
    extent = group_size[shot_index] * planes
    depth_ids = brick_index * planes + jnp.arange(planes, dtype=jnp.int32)
    active = depth_ids < extent
    mask_col = active.astype(jnp.float32)
    src4 = sources[0].reshape(4, wide_y, planes, wide_z)

    lo_send, hi_send = boundary_planes(src4, slowness_window, mask_col)
    up = [(i, i + 1) for i in range(brick_count - 1)]
    down = [(j, i) for i, j in up]
    lo = lax.ppermute(lo_send, "brick", up)
    hi = lax.ppermute(hi_send, "brick", down)

    extent_float = extent.astype(jnp.float32)
    depth_float = depth_ids.astype(jnp.float32)
    taper_x = jnp.where(active, jnp.sin(jnp.pi * (depth_float + 0.5) / extent_float), 0.0)
    taper_y = sine_taper(wide_y, float(wide_y))
    taper_z = sine_taper(wide_z, float(wide_z))
    mask_b = jnp.broadcast_to(mask_col[:, None], (planes, wide_z))
    tx_b = jnp.broadcast_to(taper_x[:, None], (planes, wide_z))
    tz_b = taper_z[None, :]
    interior, aux = window_blocks(src4, slowness_window, mask_b, tx_b, tz_b, taper_y)
    blocks = apply_halo(interior, aux, lo, hi, taper_y[:, None], mask_b, tx_b, tz_b)

    shot_count = lax.axis_size("shot")
    tile_dev = tile_slot.shape[0] // shot_count
    owned = shot_index * tile_dev + jnp.arange(tile_dev, dtype=jnp.int32)
    piece_slots = tile_slot[window_anchor[:, None] + jnp.arange(BLOCKS, dtype=jnp.int32)[None, :]]
    match = owned[:, None, None] == piece_slots[None, :, :]
    gathered = lax.all_gather(blocks[None], "shot", axis=0, tiled=True)
    return gather_sum(gathered, match).reshape(1, tile_dev, -1)


def select_kernel(es_ref, eb_ref, eq_ref, n_ref, g_hbm, out_ref, buf, sem):
    n = n_ref[0]
    depth = buf.shape[0]
    out_ref[...] = jnp.zeros_like(out_ref)

    def copy(e, slot):
        return pltpu.make_async_copy(g_hbm.at[es_ref[e], eb_ref[e]], buf.at[slot], sem.at[slot])

    for e in range(depth):
        @pl.when(e < n)
        def _():
            copy(e, e).start()

    def body(e, carry):
        slot = e % depth
        copy(e, slot).wait()
        q = eq_ref[e]
        out_ref[q] = out_ref[q] + buf[slot]

        @pl.when(e + depth < n)
        def _():
            copy(e + depth, slot).start()

        return carry

    lax.fori_loop(0, n, body, 0)


def gather_sum(gathered, match):
    owners, shots, blocks = match.shape
    cell_shape = gathered.shape[2:]
    valid = jnp.any(match, axis=2).reshape(-1)
    which_block = jnp.sum(jnp.where(match, jnp.arange(blocks, dtype=jnp.int32), 0), axis=2).reshape(-1)
    shot_of = jnp.broadcast_to(jnp.arange(shots, dtype=jnp.int32)[None, :], (owners, shots)).reshape(-1)
    owner_of = jnp.broadcast_to(jnp.arange(owners, dtype=jnp.int32)[:, None], (owners, shots)).reshape(-1)
    count = owners * shots
    position = jnp.where(valid, jnp.cumsum(valid.astype(jnp.int32)) - 1, count)
    empty = jnp.zeros((count,), jnp.int32)
    es = empty.at[position].set(shot_of, mode="drop")
    eb = empty.at[position].set(which_block, mode="drop")
    eq = empty.at[position].set(owner_of, mode="drop")
    n = jnp.sum(valid.astype(jnp.int32)).reshape(1)
    return pl.pallas_call(
        select_kernel,
        grid_spec=pltpu.PrefetchScalarGridSpec(
            num_scalar_prefetch=4,
            grid=(1,),
            in_specs=[pl.BlockSpec(memory_space=pl.ANY)],
            out_specs=pl.BlockSpec((owners,) + cell_shape, lambda i, *_: (0,) * (1 + len(cell_shape))),
            scratch_shapes=[
                pltpu.VMEM((8,) + cell_shape, jnp.float32),
                pltpu.SemaphoreType.DMA((8,)),
            ],
        ),
        out_shape=jax.ShapeDtypeStruct((owners,) + cell_shape, jnp.float32),
    )(es, eb, eq, n, gathered)


def solution(mesh):
    return jax.shard_map(
        per_device,
        mesh=mesh,
        in_specs=(
            P("shot", None, None, None, "brick", None),
            P("shot", None, "brick", None),
            P(),
            P(),
            P(),
        ),
        out_specs=P("brick", "shot", None),
        check_vma=False,
    )
```

```python
import jax
import jax.numpy as jnp
from jax import lax
from jax.experimental import pallas as pl
from jax.experimental.pallas import tpu as pltpu
from jax.sharding import PartitionSpec as P

BLOCKS = 8


shift_beta = 0.5
relaxation = 0.8


def sine_taper(count, extent):
    positions = jnp.arange(count, dtype=jnp.int32).astype(jnp.float32)
    return jnp.sin(jnp.pi * (positions + 0.5) / extent)


def inverse_of(slow):
    real_d = 6.0 - slow
    imag_d = shift_beta * slow
    denominator = real_d * real_d + imag_d * imag_d
    return real_d / denominator, imag_d / denominator


def first_sweep(s0, s1, s2, s3, inv_re, inv_im, mask):
    return (
        relaxation * (s0 * inv_re - s1 * inv_im) * mask,
        relaxation * (s0 * inv_im + s1 * inv_re) * mask,
        relaxation * (s2 * inv_re - s3 * inv_im) * mask,
        relaxation * (s2 * inv_im + s3 * inv_re) * mask,
    )


def gather_plane(rows8, plane, sub_ids):
    tile = jnp.broadcast_to(rows8[0][plane:plane + 1, :], rows8[0].shape)
    for i in range(1, len(rows8)):
        tile = jnp.where(sub_ids == i, jnp.broadcast_to(rows8[i][plane:plane + 1, :], tile.shape), tile)
    return tile


def gradient_kernel(ty_ref, src_ref, src_lo_ref, src_hi_ref, sl_ref, sl_lo_ref, sl_hi_ref, mask_ref, tx_ref, tz_ref,
                    out_ref, aux_ref, f1_s, inv_s):
    b = pl.program_id(0)
    nb = pl.num_programs(0)
    rows = src_ref.shape[1]
    mask = mask_ref[...]

    def sweep_one(r, carry):
        inv_re, inv_im = inverse_of(sl_ref[r])
        inv_s[0, r] = inv_re
        inv_s[1, r] = inv_im
        f = first_sweep(src_ref[0, r], src_ref[1, r], src_ref[2, r], src_ref[3, r], inv_re, inv_im, mask)
        for k in range(4):
            f1_s[k, r + 1] = f[k]
        return carry

    lax.fori_loop(0, rows, sweep_one, 0, unroll=2)

    lo_keep = jnp.where(b > 0, 1.0, 0.0).astype(jnp.float32)
    hi_keep = jnp.where(b < nb - 1, 1.0, 0.0).astype(jnp.float32)
    for slot, s_ref, l_ref, keep in ((0, src_lo_ref, sl_lo_ref, lo_keep), (rows + 1, src_hi_ref, sl_hi_ref, hi_keep)):
        inv_re, inv_im = inverse_of(l_ref[0])
        f = first_sweep(s_ref[0, 0], s_ref[1, 0], s_ref[2, 0], s_ref[3, 0], inv_re, inv_im, mask)
        for k in range(4):
            f1_s[k, slot] = f[k] * keep

    shape = mask.shape
    p_ids = lax.broadcasted_iota(jnp.int32, shape, 0)
    z_ids = lax.broadcasted_iota(jnp.int32, shape, 1)
    planes, width = shape
    tx = tx_ref[...]
    tz = tz_ref[...]

    def sweep_two(g, carry):
        base = pl.multiple_of(g * 8, 8)
        kept = [[] for _ in range(6)]
        for i in range(8):
            r = base + i
            inv_re = inv_s[0, r]
            inv_im = inv_s[1, r]
            cur = []
            vals = []
            for k in range(4):
                c = f1_s[k, r + 1]
                acc = f1_s[k, r] + f1_s[k, r + 2]
                down = jnp.where(p_ids == 0, 0.0, pltpu.roll(c, 1, 0))
                acc = acc + down
                up = jnp.where(p_ids == planes - 1, 0.0, pltpu.roll(c, planes - 1, 0))
                acc = acc + up
                zm = jnp.where(z_ids == 0, 0.0, pltpu.roll(c, 1, 1))
                acc = acc + zm
                zp = jnp.where(z_ids == width - 1, 0.0, pltpu.roll(c, width - 1, 1))
                acc = acc + zp
                cur.append(c)
                vals.append(src_ref[k, r] + acc)
            upd = (
                vals[0] * inv_re - vals[1] * inv_im,
                vals[0] * inv_im + vals[1] * inv_re,
                vals[2] * inv_re - vals[3] * inv_im,
                vals[2] * inv_im + vals[3] * inv_re,
            )
            f2 = [((1.0 - relaxation) * cur[k] + relaxation * upd[k]) * mask for k in range(4)]
            imaging = f2[0] * f2[2] - f2[1] * f2[3] - shift_beta * (f2[0] * f2[3] + f2[1] * f2[2])
            taper = (ty_ref[b * rows + r] * tx) * tz
            out_ref[0, r] = imaging * taper
            for k, v in enumerate(f2 + [inv_re, inv_im]):
                kept[k].append(v)
        for k in range(6):
            for j, plane in enumerate((0, planes - 1)):
                aux_ref[k, j, pl.ds(base, 8), :] = gather_plane(kept[k], plane, p_ids)
        return carry

    lax.fori_loop(0, rows // 8, sweep_two, 0)


def boundary_kernel(mask_ref, src_hbm, sl_hbm, lo_ref, hi_ref, src_buf, sl_buf, sem):
    four = src_hbm.shape[0]
    planes = src_hbm.shape[2]
    copies = []
    for j, plane in enumerate((planes - 1, 0)):
        for k in range(four):
            copies.append(pltpu.make_async_copy(src_hbm.at[k, :, plane, :], src_buf.at[j, k], sem.at[j, k]))
        copies.append(pltpu.make_async_copy(sl_hbm.at[:, plane, :], sl_buf.at[j], sem.at[j, four]))
    for c in copies:
        c.start()
    for c in copies:
        c.wait()
    for j, (plane, out) in enumerate(((planes - 1, lo_ref), (0, hi_ref))):
        m = mask_ref[plane]
        inv_re, inv_im = inverse_of(sl_buf[j])
        f = first_sweep(src_buf[j, 0], src_buf[j, 1], src_buf[j, 2], src_buf[j, 3], inv_re, inv_im, m)
        for k in range(four):
            out[k] = f[k]


def boundary_planes(src4, slow, mask_col):
    four, wide_y, planes, wide_z = src4.shape
    face = jax.ShapeDtypeStruct((four, wide_y, wide_z), jnp.float32)
    vmem = pl.BlockSpec(memory_space=pltpu.VMEM)
    return pl.pallas_call(
        boundary_kernel,
        in_specs=[
            pl.BlockSpec(memory_space=pltpu.SMEM),
            pl.BlockSpec(memory_space=pl.ANY),
            pl.BlockSpec(memory_space=pl.ANY),
        ],
        out_specs=[vmem, vmem],
        out_shape=[face, face],
        scratch_shapes=[
            pltpu.VMEM((2, four, wide_y, wide_z), jnp.float32),
            pltpu.VMEM((2, wide_y, wide_z), jnp.float32),
            pltpu.SemaphoreType.DMA((2, four + 1)),
        ],
    )(mask_col, src4, slow)


def window_blocks(src4, slow, mask_b, tx_b, tz_b, ty):
    four, wide_y, planes, wide_z = src4.shape
    rows = wide_y // BLOCKS
    last = wide_y - 1

    def row_spec(pick):
        return pl.BlockSpec((four, 1, planes, wide_z), lambda b, t: (0, pick(b), 0, 0))

    def slow_row_spec(pick):
        return pl.BlockSpec((1, planes, wide_z), lambda b, t: (pick(b), 0, 0))

    below = lambda b: jnp.maximum(b * rows - 1, 0)
    above = lambda b: jnp.minimum(b * rows + rows, last)
    grid_spec = pltpu.PrefetchScalarGridSpec(
        num_scalar_prefetch=1,
        grid=(BLOCKS,),
        in_specs=[
            pl.BlockSpec((four, rows, planes, wide_z), lambda b, t: (0, b, 0, 0)),
            row_spec(below),
            row_spec(above),
            pl.BlockSpec((rows, planes, wide_z), lambda b, t: (b, 0, 0)),
            slow_row_spec(below),
            slow_row_spec(above),
            pl.BlockSpec((planes, wide_z), lambda b, t: (0, 0)),
            pl.BlockSpec((planes, wide_z), lambda b, t: (0, 0)),
            pl.BlockSpec((1, wide_z), lambda b, t: (0, 0)),
        ],
        out_specs=[
            pl.BlockSpec((1, rows, planes, wide_z), lambda b, t: (b, 0, 0, 0)),
            pl.BlockSpec((6, 2, rows, wide_z), lambda b, t: (0, 0, b, 0)),
        ],
        scratch_shapes=[
            pltpu.VMEM((four, rows + 2, planes, wide_z), jnp.float32),
            pltpu.VMEM((2, rows, planes, wide_z), jnp.float32),
        ],
    )
    return pl.pallas_call(
        gradient_kernel,
        grid_spec=grid_spec,
        out_shape=[
            jax.ShapeDtypeStruct((BLOCKS, rows, planes, wide_z), jnp.float32),
            jax.ShapeDtypeStruct((6, 2, wide_y, wide_z), jnp.float32),
        ],
    )(ty, src4, src4, src4, slow, slow, slow, mask_b, tx_b, tz_b)


def halo_kernel(aux_ref, lo_ref, hi_ref, ty_ref, mask_ref, tx_ref, tz_ref, grad_hbm, out_hbm, fixed, sem):
    wide_y = aux_ref.shape[2]
    planes = mask_ref.shape[0]
    count, rows = out_hbm.shape[:2]
    tz = tz_ref[...]
    for g in range(wide_y // 8):
        span = pl.ds(g * 8, 8)
        ty = ty_ref[span, :]
        for j, plane, h_ref in ((0, 0, lo_ref), (1, planes - 1, hi_ref)):
            inv_re = aux_ref[4, j, span, :]
            inv_im = aux_ref[5, j, span, :]
            h = [h_ref[k, span, :] for k in range(4)]
            m = mask_ref[plane:plane + 1, :]
            d = (
                h[0] * inv_re - h[1] * inv_im,
                h[0] * inv_im + h[1] * inv_re,
                h[2] * inv_re - h[3] * inv_im,
                h[2] * inv_im + h[3] * inv_re,
            )
            f2 = [aux_ref[k, j, span, :] + relaxation * d[k] * m for k in range(4)]
            imaging = f2[0] * f2[2] - f2[1] * f2[3] - shift_beta * (f2[0] * f2[3] + f2[1] * f2[2])
            fixed[j, span, :] = imaging * ((ty * tx_ref[plane:plane + 1, :]) * tz)
    copies = []
    for j, plane in enumerate((0, planes - 1)):
        for b in range(count):
            copies.append(pltpu.make_async_copy(
                fixed.at[j, pl.ds(b * rows, rows)], out_hbm.at[b, :, plane, :], sem.at[j, b]))
    for c in copies:
        c.start()
    for c in copies:
        c.wait()


def apply_halo(grad, aux, lo, hi, ty_col, mask_b, tx_b, tz_b):
    count, rows, planes, wide_z = grad.shape
    vmem = pl.BlockSpec(memory_space=pltpu.VMEM)
    return pl.pallas_call(
        halo_kernel,
        in_specs=[vmem] * 7 + [pl.BlockSpec(memory_space=pl.ANY)],
        out_specs=pl.BlockSpec(memory_space=pl.ANY),
        out_shape=jax.ShapeDtypeStruct(grad.shape, jnp.float32),
        scratch_shapes=[
            pltpu.VMEM((2, count * rows, wide_z), jnp.float32),
            pltpu.SemaphoreType.DMA((2, count)),
        ],
        input_output_aliases={7: 0},
    )(aux, lo, hi, ty_col, mask_b, tx_b, tz_b, grad)


def per_device(sources, slowness, group_size, window_anchor, tile_slot):
    slowness_window = slowness[0]
    wide_y, planes, wide_z = slowness_window.shape
    brick_index = lax.axis_index("brick")
    z_index = lax.axis_index("z")
    x_index = lax.axis_index("xl")
    core_index = lax.axis_index("core")
    x_count = lax.axis_size("xl")
    core_count = lax.axis_size("core")
    shot_index = (z_index * x_count + x_index) * core_count + core_index
    brick_count = lax.axis_size("brick")
    extent = group_size[shot_index] * planes
    depth_ids = brick_index * planes + jnp.arange(planes, dtype=jnp.int32)
    active = depth_ids < extent
    mask_col = active.astype(jnp.float32)
    src4 = sources[0].reshape(4, wide_y, planes, wide_z)

    lo_send, hi_send = boundary_planes(src4, slowness_window, mask_col)
    up = [(i, i + 1) for i in range(brick_count - 1)]
    down = [(j, i) for i, j in up]
    lo = lax.ppermute(lo_send, "brick", up)
    hi = lax.ppermute(hi_send, "brick", down)

    extent_float = extent.astype(jnp.float32)
    depth_float = depth_ids.astype(jnp.float32)
    taper_x = jnp.where(active, jnp.sin(jnp.pi * (depth_float + 0.5) / extent_float), 0.0)
    taper_y = sine_taper(wide_y, float(wide_y))
    taper_z = sine_taper(wide_z, float(wide_z))
    mask_b = jnp.broadcast_to(mask_col[:, None], (planes, wide_z))
    tx_b = jnp.broadcast_to(taper_x[:, None], (planes, wide_z))
    tz_b = taper_z[None, :]
    interior, aux = window_blocks(src4, slowness_window, mask_b, tx_b, tz_b, taper_y)
    blocks = apply_halo(interior, aux, lo, hi, taper_y[:, None], mask_b, tx_b, tz_b)

    shot_count = lax.axis_size("z") * x_count * core_count
    tile_dev = tile_slot.shape[0] // shot_count
    partner = (z_index * x_count + (x_count - 1 - x_index)) * core_count + core_index
    slots = jnp.arange(tile_dev, dtype=jnp.int32)
    owners = jnp.concatenate([shot_index * tile_dev + slots, partner * tile_dev + slots])
    zs = jnp.arange(lax.axis_size("z"), dtype=jnp.int32)
    cs = jnp.arange(core_count, dtype=jnp.int32)
    held = ((zs[:, None] * x_count + x_index) * core_count + cs[None, :]).reshape(-1)
    piece_slots = tile_slot[window_anchor[held][:, None] + jnp.arange(BLOCKS, dtype=jnp.int32)[None, :]]
    match = owners[:, None, None] == piece_slots[None, :, :]
    gathered = lax.all_gather(blocks[None], ("z", "core"), axis=0, tiled=True)
    partial = gather_sum(gathered, match)
    theirs = lax.ppermute(partial[tile_dev:], "xl", [(0, 1), (1, 0)])
    return (partial[:tile_dev] + theirs).reshape(1, tile_dev, -1)


def select_kernel(es_ref, eb_ref, eq_ref, n_ref, g_hbm, out_ref, buf, sem):
    n = n_ref[0]
    depth = buf.shape[0]
    out_ref[...] = jnp.zeros_like(out_ref)

    def copy(e, slot):
        return pltpu.make_async_copy(g_hbm.at[es_ref[e], eb_ref[e]], buf.at[slot], sem.at[slot])

    for e in range(depth):
        @pl.when(e < n)
        def _():
            copy(e, e).start()

    def body(e, carry):
        slot = e % depth
        copy(e, slot).wait()
        q = eq_ref[e]
        out_ref[q] = out_ref[q] + buf[slot]

        @pl.when(e + depth < n)
        def _():
            copy(e + depth, slot).start()

        return carry

    lax.fori_loop(0, n, body, 0)


def gather_sum(gathered, match):
    owners, shots, blocks = match.shape
    cell_shape = gathered.shape[2:]
    valid = jnp.any(match, axis=2).reshape(-1)
    which_block = jnp.sum(jnp.where(match, jnp.arange(blocks, dtype=jnp.int32), 0), axis=2).reshape(-1)
    shot_of = jnp.broadcast_to(jnp.arange(shots, dtype=jnp.int32)[None, :], (owners, shots)).reshape(-1)
    owner_of = jnp.broadcast_to(jnp.arange(owners, dtype=jnp.int32)[:, None], (owners, shots)).reshape(-1)
    count = owners * shots
    position = jnp.where(valid, jnp.cumsum(valid.astype(jnp.int32)) - 1, count)
    empty = jnp.zeros((count,), jnp.int32)
    es = empty.at[position].set(shot_of, mode="drop")
    eb = empty.at[position].set(which_block, mode="drop")
    eq = empty.at[position].set(owner_of, mode="drop")
    n = jnp.sum(valid.astype(jnp.int32)).reshape(1)
    return pl.pallas_call(
        select_kernel,
        grid_spec=pltpu.PrefetchScalarGridSpec(
            num_scalar_prefetch=4,
            grid=(1,),
            in_specs=[pl.BlockSpec(memory_space=pl.ANY)],
            out_specs=pl.BlockSpec((owners,) + cell_shape, lambda i, *_: (0,) * (1 + len(cell_shape))),
            scratch_shapes=[
                pltpu.VMEM((8,) + cell_shape, jnp.float32),
                pltpu.SemaphoreType.DMA((8,)),
            ],
        ),
        out_shape=jax.ShapeDtypeStruct((owners,) + cell_shape, jnp.float32),
    )(es, eb, eq, n, gathered)


def solution(mesh):
    devices = mesh.devices
    shots, bricks = devices.shape
    split = jax.sharding.Mesh(devices.reshape(shots // 4, 2, 2, bricks), ("z", "xl", "core", "brick"))
    shot = ("z", "xl", "core")
    return jax.shard_map(
        per_device,
        mesh=split,
        in_specs=(
            P(shot, None, None, None, "brick", None),
            P(shot, None, "brick", None),
            P(),
            P(),
            P(),
        ),
        out_specs=P("brick", shot, None),
        check_vma=False,
    )
```

```python
import jax
import jax.numpy as jnp
from jax import lax
from jax.experimental import pallas as pl
from jax.experimental.pallas import tpu as pltpu
from jax.sharding import PartitionSpec as P

BLOCKS = 8


shift_beta = 0.5
relaxation = 0.8


def sine_taper(count, extent):
    positions = jnp.arange(count, dtype=jnp.int32).astype(jnp.float32)
    return jnp.sin(jnp.pi * (positions + 0.5) / extent)


def inverse_of(slow):
    real_d = 6.0 - slow
    imag_d = shift_beta * slow
    denominator = real_d * real_d + imag_d * imag_d
    return real_d / denominator, imag_d / denominator


def first_sweep(s0, s1, s2, s3, inv_re, inv_im, mask):
    return (
        relaxation * (s0 * inv_re - s1 * inv_im) * mask,
        relaxation * (s0 * inv_im + s1 * inv_re) * mask,
        relaxation * (s2 * inv_re - s3 * inv_im) * mask,
        relaxation * (s2 * inv_im + s3 * inv_re) * mask,
    )


def gather_plane(rows8, plane, sub_ids):
    tile = jnp.broadcast_to(rows8[0][plane:plane + 1, :], rows8[0].shape)
    for i in range(1, len(rows8)):
        tile = jnp.where(sub_ids == i, jnp.broadcast_to(rows8[i][plane:plane + 1, :], tile.shape), tile)
    return tile


def boundary_kernel(mask_ref, src_hbm, sl_hbm, lo_ref, hi_ref, src_buf, sl_buf, sem):
    four = src_hbm.shape[0]
    planes = src_hbm.shape[2]
    copies = []
    for j, plane in enumerate((planes - 1, 0)):
        for k in range(four):
            copies.append(pltpu.make_async_copy(src_hbm.at[k, :, plane, :], src_buf.at[j, k], sem.at[j, k]))
        copies.append(pltpu.make_async_copy(sl_hbm.at[:, plane, :], sl_buf.at[j], sem.at[j, four]))
    for c in copies:
        c.start()
    for c in copies:
        c.wait()
    for j, (plane, out) in enumerate(((planes - 1, lo_ref), (0, hi_ref))):
        m = mask_ref[plane]
        inv_re, inv_im = inverse_of(sl_buf[j])
        f = first_sweep(src_buf[j, 0], src_buf[j, 1], src_buf[j, 2], src_buf[j, 3], inv_re, inv_im, m)
        for k in range(four):
            out[k] = f[k]


def boundary_planes(src4, slow, mask_col):
    four, wide_y, planes, wide_z = src4.shape
    face = jax.ShapeDtypeStruct((four, wide_y, wide_z), jnp.float32)
    vmem = pl.BlockSpec(memory_space=pltpu.VMEM)
    return pl.pallas_call(
        boundary_kernel,
        in_specs=[
            pl.BlockSpec(memory_space=pltpu.SMEM),
            pl.BlockSpec(memory_space=pl.ANY),
            pl.BlockSpec(memory_space=pl.ANY),
        ],
        out_specs=[vmem, vmem],
        out_shape=[face, face],
        scratch_shapes=[
            pltpu.VMEM((2, four, wide_y, wide_z), jnp.float32),
            pltpu.VMEM((2, wide_y, wide_z), jnp.float32),
            pltpu.SemaphoreType.DMA((2, four + 1)),
        ],
    )(mask_col, src4, slow)


def gradient_kernel(ty_ref, src_ref, src_lo_ref, src_hi_ref, sl_ref, sl_lo_ref, sl_hi_ref, mask_ref, tx_ref, tz_ref,
                    out_ref, aux_ref, f1_s, inv_s):
    b = pl.program_id(0)
    nb = pl.num_programs(0)
    rows = src_ref.shape[1]
    mask = mask_ref[...]

    def sweep_one(r, carry):
        inv_re, inv_im = inverse_of(sl_ref[r])
        inv_s[0, r] = inv_re
        inv_s[1, r] = inv_im
        f = first_sweep(src_ref[0, r], src_ref[1, r], src_ref[2, r], src_ref[3, r], inv_re, inv_im, mask)
        for k in range(4):
            f1_s[k, r + 1] = f[k]
        return carry

    lax.fori_loop(0, rows, sweep_one, 0, unroll=2)

    lo_keep = jnp.where(b > 0, 1.0, 0.0).astype(jnp.float32)
    hi_keep = jnp.where(b < nb - 1, 1.0, 0.0).astype(jnp.float32)
    for slot, s_ref, l_ref, keep in ((0, src_lo_ref, sl_lo_ref, lo_keep), (rows + 1, src_hi_ref, sl_hi_ref, hi_keep)):
        inv_re, inv_im = inverse_of(l_ref[0])
        f = first_sweep(s_ref[0, 0], s_ref[1, 0], s_ref[2, 0], s_ref[3, 0], inv_re, inv_im, mask)
        for k in range(4):
            f1_s[k, slot] = f[k] * keep

    shape = mask.shape
    p_ids = lax.broadcasted_iota(jnp.int32, shape, 0)
    z_ids = lax.broadcasted_iota(jnp.int32, shape, 1)
    planes, width = shape
    tx = tx_ref[...]
    tz = tz_ref[...]

    def sweep_two(g, carry):
        base = pl.multiple_of(g * 8, 8)
        kept = [[] for _ in range(6)]
        grads = []
        for i in range(8):
            r = base + i
            inv_re = inv_s[0, r]
            inv_im = inv_s[1, r]
            cur = []
            vals = []
            for k in range(4):
                c = f1_s[k, r + 1]
                acc = f1_s[k, r] + f1_s[k, r + 2]
                down = jnp.where(p_ids == 0, 0.0, pltpu.roll(c, 1, 0))
                acc = acc + down
                up = jnp.where(p_ids == planes - 1, 0.0, pltpu.roll(c, planes - 1, 0))
                acc = acc + up
                zm = jnp.where(z_ids == 0, 0.0, pltpu.roll(c, 1, 1))
                acc = acc + zm
                zp = jnp.where(z_ids == width - 1, 0.0, pltpu.roll(c, width - 1, 1))
                acc = acc + zp
                cur.append(c)
                vals.append(src_ref[k, r] + acc)
            upd = (
                vals[0] * inv_re - vals[1] * inv_im,
                vals[0] * inv_im + vals[1] * inv_re,
                vals[2] * inv_re - vals[3] * inv_im,
                vals[2] * inv_im + vals[3] * inv_re,
            )
            f2 = [((1.0 - relaxation) * cur[k] + relaxation * upd[k]) * mask for k in range(4)]
            imaging = f2[0] * f2[2] - f2[1] * f2[3] - shift_beta * (f2[0] * f2[3] + f2[1] * f2[2])
            taper = (ty_ref[b * rows + r] * tx) * tz
            grads.append(imaging * taper)
            for k, v in enumerate(f2 + [inv_re, inv_im]):
                kept[k].append(v)
        for k in range(6):
            for j, plane in enumerate((0, planes - 1)):
                aux_ref[k, j, pl.ds(base, 8), :] = gather_plane(kept[k], plane, p_ids)
        for plane in range(1, planes - 1):
            out_ref[0, plane - 1, pl.ds(base, 8), :] = gather_plane(grads, plane, p_ids)
        return carry

    lax.fori_loop(0, rows // 8, sweep_two, 0)


def window_blocks(src4, slow, mask_b, tx_b, tz_b, ty):
    four, wide_y, planes, wide_z = src4.shape
    rows = wide_y // BLOCKS
    last = wide_y - 1

    def row_spec(pick):
        return pl.BlockSpec((four, 1, planes, wide_z), lambda b, t: (0, pick(b), 0, 0))

    def slow_row_spec(pick):
        return pl.BlockSpec((1, planes, wide_z), lambda b, t: (pick(b), 0, 0))

    below = lambda b: jnp.maximum(b * rows - 1, 0)
    above = lambda b: jnp.minimum(b * rows + rows, last)
    grid_spec = pltpu.PrefetchScalarGridSpec(
        num_scalar_prefetch=1,
        grid=(BLOCKS,),
        in_specs=[
            pl.BlockSpec((four, rows, planes, wide_z), lambda b, t: (0, b, 0, 0)),
            row_spec(below),
            row_spec(above),
            pl.BlockSpec((rows, planes, wide_z), lambda b, t: (b, 0, 0)),
            slow_row_spec(below),
            slow_row_spec(above),
            pl.BlockSpec((planes, wide_z), lambda b, t: (0, 0)),
            pl.BlockSpec((planes, wide_z), lambda b, t: (0, 0)),
            pl.BlockSpec((1, wide_z), lambda b, t: (0, 0)),
        ],
        out_specs=[
            pl.BlockSpec((1, planes - 2, rows, wide_z), lambda b, t: (b, 0, 0, 0)),
            pl.BlockSpec((6, 2, rows, wide_z), lambda b, t: (0, 0, b, 0)),
        ],
        scratch_shapes=[
            pltpu.VMEM((four, rows + 2, planes, wide_z), jnp.float32),
            pltpu.VMEM((2, rows, planes, wide_z), jnp.float32),
        ],
    )
    return pl.pallas_call(
        gradient_kernel,
        grid_spec=grid_spec,
        out_shape=[
            jax.ShapeDtypeStruct((BLOCKS, planes - 2, rows, wide_z), jnp.float32),
            jax.ShapeDtypeStruct((6, 2, wide_y, wide_z), jnp.float32),
        ],
    )(ty, src4, src4, src4, slow, slow, slow, mask_b, tx_b, tz_b)


def halo_kernel(aux_ref, lo_ref, hi_ref, ty_ref, mask_ref, tx_ref, tz_ref, out_ref):
    rows = aux_ref.shape[2]
    planes = mask_ref.shape[0]
    tz = tz_ref[...]
    for g in range(rows // 8):
        span = pl.ds(g * 8, 8)
        ty = ty_ref[span, :]
        for j, plane, h_ref in ((0, 0, lo_ref), (1, planes - 1, hi_ref)):
            inv_re = aux_ref[4, j, span, :]
            inv_im = aux_ref[5, j, span, :]
            h = [h_ref[k, span, :] for k in range(4)]
            m = mask_ref[plane:plane + 1, :]
            d = (
                h[0] * inv_re - h[1] * inv_im,
                h[0] * inv_im + h[1] * inv_re,
                h[2] * inv_re - h[3] * inv_im,
                h[2] * inv_im + h[3] * inv_re,
            )
            f2 = [aux_ref[k, j, span, :] + relaxation * d[k] * m for k in range(4)]
            imaging = f2[0] * f2[2] - f2[1] * f2[3] - shift_beta * (f2[0] * f2[3] + f2[1] * f2[2])
            out_ref[0, j, span, :] = imaging * ((ty * tx_ref[plane:plane + 1, :]) * tz)


def edge_planes(aux, lo, hi, ty_col, mask_b, tx_b, tz_b):
    wide_y, wide_z = lo.shape[1:]
    rows = wide_y // BLOCKS
    four = lo.shape[0]
    planes = mask_b.shape[0]
    full = lambda b: (0, 0)
    return pl.pallas_call(
        halo_kernel,
        grid=(BLOCKS,),
        in_specs=[
            pl.BlockSpec((6, 2, rows, wide_z), lambda b: (0, 0, b, 0)),
            pl.BlockSpec((four, rows, wide_z), lambda b: (0, b, 0)),
            pl.BlockSpec((four, rows, wide_z), lambda b: (0, b, 0)),
            pl.BlockSpec((rows, 1), lambda b: (b, 0)),
            pl.BlockSpec((planes, wide_z), full),
            pl.BlockSpec((planes, wide_z), full),
            pl.BlockSpec((1, wide_z), full),
        ],
        out_specs=pl.BlockSpec((1, 2, rows, wide_z), lambda b: (b, 0, 0, 0)),
        out_shape=jax.ShapeDtypeStruct((BLOCKS, 2, rows, wide_z), jnp.float32),
    )(aux, lo, hi, ty_col, mask_b, tx_b, tz_b)


def per_device(sources, slowness, group_size, window_anchor, tile_slot):
    slowness_window = slowness[0]
    wide_y, planes, wide_z = slowness_window.shape
    brick_index = lax.axis_index("brick")
    z_index = lax.axis_index("z")
    x_index = lax.axis_index("xl")
    core_index = lax.axis_index("core")
    x_count = lax.axis_size("xl")
    core_count = lax.axis_size("core")
    shot_index = (z_index * x_count + x_index) * core_count + core_index
    brick_count = lax.axis_size("brick")
    extent = group_size[shot_index] * planes
    depth_ids = brick_index * planes + jnp.arange(planes, dtype=jnp.int32)
    active = depth_ids < extent
    mask_col = active.astype(jnp.float32)
    src4 = sources[0].reshape(4, wide_y, planes, wide_z)

    lo_send, hi_send = boundary_planes(src4, slowness_window, mask_col)
    up = [(i, i + 1) for i in range(brick_count - 1)]
    down = [(j, i) for i, j in up]
    lo = lax.ppermute(lo_send, "brick", up)
    hi = lax.ppermute(hi_send, "brick", down)

    extent_float = extent.astype(jnp.float32)
    depth_float = depth_ids.astype(jnp.float32)
    taper_x = jnp.where(active, jnp.sin(jnp.pi * (depth_float + 0.5) / extent_float), 0.0)
    taper_y = sine_taper(wide_y, float(wide_y))
    taper_z = sine_taper(wide_z, float(wide_z))
    mask_b = jnp.broadcast_to(mask_col[:, None], (planes, wide_z))
    tx_b = jnp.broadcast_to(taper_x[:, None], (planes, wide_z))
    tz_b = taper_z[None, :]
    interior, aux = window_blocks(src4, slowness_window, mask_b, tx_b, tz_b, taper_y)
    mid = lax.all_gather(interior[None], ("z", "core"), axis=0, tiled=True)
    mid, lo, hi = lax.optimization_barrier((mid, lo, hi))
    edges = edge_planes(aux, lo, hi, taper_y[:, None], mask_b, tx_b, tz_b)

    shot_count = lax.axis_size("z") * x_count * core_count
    tile_dev = tile_slot.shape[0] // shot_count
    partner = (z_index * x_count + (x_count - 1 - x_index)) * core_count + core_index
    slots = jnp.arange(tile_dev, dtype=jnp.int32)
    owners = jnp.concatenate([shot_index * tile_dev + slots, partner * tile_dev + slots])
    zs = jnp.arange(lax.axis_size("z"), dtype=jnp.int32)
    cs = jnp.arange(core_count, dtype=jnp.int32)
    held = ((zs[:, None] * x_count + x_index) * core_count + cs[None, :]).reshape(-1)
    piece_slots = tile_slot[window_anchor[held][:, None] + jnp.arange(BLOCKS, dtype=jnp.int32)[None, :]]
    match = owners[:, None, None] == piece_slots[None, :, :]
    rim = lax.all_gather(edges[None], ("z", "core"), axis=0, tiled=True)
    partial = gather_sum(mid, rim, match)
    theirs = lax.ppermute(partial[tile_dev:], "xl", [(0, 1), (1, 0)])
    summed = partial[:tile_dev] + theirs
    return jnp.transpose(summed, (0, 2, 1, 3)).reshape(1, tile_dev, -1)


def select_kernel(es_ref, eb_ref, eq_ref, n_ref, mid_hbm, rim_hbm, out_ref, buf, sem):
    n = n_ref[0]
    depth = buf.shape[0]
    last = buf.shape[1] - 1
    out_ref[...] = jnp.zeros_like(out_ref)

    def copies(e, slot):
        s = es_ref[e]
        b = eb_ref[e]
        return (
            pltpu.make_async_copy(mid_hbm.at[s, b], buf.at[slot, pl.ds(1, last - 1)], sem.at[slot, 0]),
            pltpu.make_async_copy(rim_hbm.at[s, b, 0], buf.at[slot, 0], sem.at[slot, 1]),
            pltpu.make_async_copy(rim_hbm.at[s, b, 1], buf.at[slot, last], sem.at[slot, 2]),
        )

    for e in range(depth):
        @pl.when(e < n)
        def _():
            for c in copies(e, e):
                c.start()

    def body(e, carry):
        slot = e % depth
        for c in copies(e, slot):
            c.wait()
        q = eq_ref[e]
        out_ref[q] = out_ref[q] + buf[slot]

        @pl.when(e + depth < n)
        def _():
            for c in copies(e + depth, slot):
                c.start()

        return carry

    lax.fori_loop(0, n, body, 0)


def gather_sum(mid, rim, match):
    owners, shots, blocks = match.shape
    cell_shape = (mid.shape[2] + rim.shape[2],) + mid.shape[3:]
    valid = jnp.any(match, axis=2).reshape(-1)
    which_block = jnp.sum(jnp.where(match, jnp.arange(blocks, dtype=jnp.int32), 0), axis=2).reshape(-1)
    shot_of = jnp.broadcast_to(jnp.arange(shots, dtype=jnp.int32)[None, :], (owners, shots)).reshape(-1)
    owner_of = jnp.broadcast_to(jnp.arange(owners, dtype=jnp.int32)[:, None], (owners, shots)).reshape(-1)
    count = owners * shots
    position = jnp.where(valid, jnp.cumsum(valid.astype(jnp.int32)) - 1, count)
    empty = jnp.zeros((count,), jnp.int32)
    es = empty.at[position].set(shot_of, mode="drop")
    eb = empty.at[position].set(which_block, mode="drop")
    eq = empty.at[position].set(owner_of, mode="drop")
    n = jnp.sum(valid.astype(jnp.int32)).reshape(1)
    return pl.pallas_call(
        select_kernel,
        grid_spec=pltpu.PrefetchScalarGridSpec(
            num_scalar_prefetch=4,
            grid=(1,),
            in_specs=[pl.BlockSpec(memory_space=pl.ANY), pl.BlockSpec(memory_space=pl.ANY)],
            out_specs=pl.BlockSpec((owners,) + cell_shape, lambda i, *_: (0,) * (1 + len(cell_shape))),
            scratch_shapes=[
                pltpu.VMEM((4,) + cell_shape, jnp.float32),
                pltpu.SemaphoreType.DMA((4, 3)),
            ],
        ),
        out_shape=jax.ShapeDtypeStruct((owners,) + cell_shape, jnp.float32),
    )(es, eb, eq, n, mid, rim)


def solution(mesh):
    devices = mesh.devices
    shots, bricks = devices.shape
    split = jax.sharding.Mesh(devices.reshape(shots // 4, 2, 2, bricks), ("z", "xl", "core", "brick"))
    shot = ("z", "xl", "core")
    return jax.shard_map(
        per_device,
        mesh=split,
        in_specs=(
            P(shot, None, None, None, "brick", None),
            P(shot, None, "brick", None),
            P(),
            P(),
            P(),
        ),
        out_specs=P("brick", shot, None),
        check_vma=False,
    )
```

```python
import jax
import jax.numpy as jnp
from jax import lax
from jax.experimental import pallas as pl
from jax.experimental.pallas import tpu as pltpu
from jax.sharding import PartitionSpec as P

BLOCKS = 8


shift_beta = 0.5
relaxation = 0.8


def sine_taper(count, extent):
    positions = jnp.arange(count, dtype=jnp.int32).astype(jnp.float32)
    return jnp.sin(jnp.pi * (positions + 0.5) / extent)


def inverse_of(slow):
    real_d = 6.0 - slow
    imag_d = shift_beta * slow
    denominator = real_d * real_d + imag_d * imag_d
    return real_d / denominator, imag_d / denominator


def first_sweep(s0, s1, s2, s3, inv_re, inv_im, mask):
    return (
        relaxation * (s0 * inv_re - s1 * inv_im) * mask,
        relaxation * (s0 * inv_im + s1 * inv_re) * mask,
        relaxation * (s2 * inv_re - s3 * inv_im) * mask,
        relaxation * (s2 * inv_im + s3 * inv_re) * mask,
    )


def gather_plane(rows8, plane, sub_ids):
    tile = jnp.broadcast_to(rows8[0][plane:plane + 1, :], rows8[0].shape)
    for i in range(1, len(rows8)):
        tile = jnp.where(sub_ids == i, jnp.broadcast_to(rows8[i][plane:plane + 1, :], tile.shape), tile)
    return tile


def boundary_kernel(mask_ref, src_hbm, sl_hbm, lo_ref, hi_ref, src_buf, sl_buf, sem):
    four = src_hbm.shape[0]
    planes = src_hbm.shape[2]
    copies = []
    for j, plane in enumerate((planes - 1, 0)):
        for k in range(four):
            copies.append(pltpu.make_async_copy(src_hbm.at[k, :, plane, :], src_buf.at[j, k], sem.at[j, k]))
        copies.append(pltpu.make_async_copy(sl_hbm.at[:, plane, :], sl_buf.at[j], sem.at[j, four]))
    for c in copies:
        c.start()
    for c in copies:
        c.wait()
    for j, (plane, out) in enumerate(((planes - 1, lo_ref), (0, hi_ref))):
        m = mask_ref[plane]
        inv_re, inv_im = inverse_of(sl_buf[j])
        f = first_sweep(src_buf[j, 0], src_buf[j, 1], src_buf[j, 2], src_buf[j, 3], inv_re, inv_im, m)
        for k in range(four):
            out[k] = f[k]


def boundary_planes(src4, slow, mask_col):
    four, wide_y, planes, wide_z = src4.shape
    face = jax.ShapeDtypeStruct((four, wide_y, wide_z), jnp.float32)
    vmem = pl.BlockSpec(memory_space=pltpu.VMEM)
    return pl.pallas_call(
        boundary_kernel,
        in_specs=[
            pl.BlockSpec(memory_space=pltpu.SMEM),
            pl.BlockSpec(memory_space=pl.ANY),
            pl.BlockSpec(memory_space=pl.ANY),
        ],
        out_specs=[vmem, vmem],
        out_shape=[face, face],
        scratch_shapes=[
            pltpu.VMEM((2, four, wide_y, wide_z), jnp.float32),
            pltpu.VMEM((2, wide_y, wide_z), jnp.float32),
            pltpu.SemaphoreType.DMA((2, four + 1)),
        ],
    )(mask_col, src4, slow)


def gradient_kernel(ty_ref, src_ref, src_lo_ref, src_hi_ref, sl_ref, sl_lo_ref, sl_hi_ref, mask_ref, tx_ref, tz_ref,
                    out_ref, aux_ref, f1_s, inv_s):
    b = pl.program_id(0)
    nb = pl.num_programs(0)
    rows = src_ref.shape[1]
    mask = mask_ref[...]

    def sweep_one(r, carry):
        inv_re, inv_im = inverse_of(sl_ref[r])
        inv_s[0, r] = inv_re
        inv_s[1, r] = inv_im
        f = first_sweep(src_ref[0, r], src_ref[1, r], src_ref[2, r], src_ref[3, r], inv_re, inv_im, mask)
        for k in range(4):
            f1_s[k, r + 1] = f[k]
        return carry

    lax.fori_loop(0, rows, sweep_one, 0, unroll=2)

    lo_keep = jnp.where(b > 0, 1.0, 0.0).astype(jnp.float32)
    hi_keep = jnp.where(b < nb - 1, 1.0, 0.0).astype(jnp.float32)
    for slot, s_ref, l_ref, keep in ((0, src_lo_ref, sl_lo_ref, lo_keep), (rows + 1, src_hi_ref, sl_hi_ref, hi_keep)):
        inv_re, inv_im = inverse_of(l_ref[0])
        f = first_sweep(s_ref[0, 0], s_ref[1, 0], s_ref[2, 0], s_ref[3, 0], inv_re, inv_im, mask)
        for k in range(4):
            f1_s[k, slot] = f[k] * keep

    shape = mask.shape
    p_ids = lax.broadcasted_iota(jnp.int32, shape, 0)
    z_ids = lax.broadcasted_iota(jnp.int32, shape, 1)
    planes, width = shape
    tx = tx_ref[...]
    tz = tz_ref[...]

    def sweep_two(g, carry):
        base = pl.multiple_of(g * 8, 8)
        kept = [[] for _ in range(6)]
        grads = []
        for i in range(8):
            r = base + i
            inv_re = inv_s[0, r]
            inv_im = inv_s[1, r]
            cur = []
            vals = []
            for k in range(4):
                c = f1_s[k, r + 1]
                acc = f1_s[k, r] + f1_s[k, r + 2]
                down = jnp.where(p_ids == 0, 0.0, pltpu.roll(c, 1, 0))
                acc = acc + down
                up = jnp.where(p_ids == planes - 1, 0.0, pltpu.roll(c, planes - 1, 0))
                acc = acc + up
                zm = jnp.where(z_ids == 0, 0.0, pltpu.roll(c, 1, 1))
                acc = acc + zm
                zp = jnp.where(z_ids == width - 1, 0.0, pltpu.roll(c, width - 1, 1))
                acc = acc + zp
                cur.append(c)
                vals.append(src_ref[k, r] + acc)
            upd = (
                vals[0] * inv_re - vals[1] * inv_im,
                vals[0] * inv_im + vals[1] * inv_re,
                vals[2] * inv_re - vals[3] * inv_im,
                vals[2] * inv_im + vals[3] * inv_re,
            )
            f2 = [((1.0 - relaxation) * cur[k] + relaxation * upd[k]) * mask for k in range(4)]
            imaging = f2[0] * f2[2] - f2[1] * f2[3] - shift_beta * (f2[0] * f2[3] + f2[1] * f2[2])
            taper = (ty_ref[b * rows + r] * tx) * tz
            grads.append(imaging * taper)
            for k, v in enumerate(f2 + [inv_re, inv_im]):
                kept[k].append(v)
        for k in range(6):
            for j, plane in enumerate((0, planes - 1)):
                aux_ref[k, j, pl.ds(base, 8), :] = gather_plane(kept[k], plane, p_ids)
        for plane in range(1, planes - 1):
            out_ref[0, plane - 1, pl.ds(base, 8), :] = gather_plane(grads, plane, p_ids)
        return carry

    lax.fori_loop(0, rows // 8, sweep_two, 0)


def window_blocks(src4, slow, mask_b, tx_b, tz_b, ty):
    four, wide_y, planes, wide_z = src4.shape
    rows = wide_y // BLOCKS
    last = wide_y - 1

    def row_spec(pick):
        return pl.BlockSpec((four, 1, planes, wide_z), lambda b, t: (0, pick(b), 0, 0))

    def slow_row_spec(pick):
        return pl.BlockSpec((1, planes, wide_z), lambda b, t: (pick(b), 0, 0))

    below = lambda b: jnp.maximum(b * rows - 1, 0)
    above = lambda b: jnp.minimum(b * rows + rows, last)
    grid_spec = pltpu.PrefetchScalarGridSpec(
        num_scalar_prefetch=1,
        grid=(BLOCKS,),
        in_specs=[
            pl.BlockSpec((four, rows, planes, wide_z), lambda b, t: (0, b, 0, 0)),
            row_spec(below),
            row_spec(above),
            pl.BlockSpec((rows, planes, wide_z), lambda b, t: (b, 0, 0)),
            slow_row_spec(below),
            slow_row_spec(above),
            pl.BlockSpec((planes, wide_z), lambda b, t: (0, 0)),
            pl.BlockSpec((planes, wide_z), lambda b, t: (0, 0)),
            pl.BlockSpec((1, wide_z), lambda b, t: (0, 0)),
        ],
        out_specs=[
            pl.BlockSpec((1, planes - 2, rows, wide_z), lambda b, t: (b, 0, 0, 0)),
            pl.BlockSpec((6, 2, rows, wide_z), lambda b, t: (0, 0, b, 0)),
        ],
        scratch_shapes=[
            pltpu.VMEM((four, rows + 2, planes, wide_z), jnp.float32),
            pltpu.VMEM((2, rows, planes, wide_z), jnp.float32),
        ],
    )
    return pl.pallas_call(
        gradient_kernel,
        grid_spec=grid_spec,
        out_shape=[
            jax.ShapeDtypeStruct((BLOCKS, planes - 2, rows, wide_z), jnp.float32),
            jax.ShapeDtypeStruct((6, 2, wide_y, wide_z), jnp.float32),
        ],
    )(ty, src4, src4, src4, slow, slow, slow, mask_b, tx_b, tz_b)


def halo_kernel(aux_ref, lo_ref, hi_ref, ty_ref, mask_ref, tx_ref, tz_ref, out_ref):
    rows = aux_ref.shape[2]
    planes = mask_ref.shape[0]
    tz = tz_ref[...]
    for g in range(rows // 8):
        span = pl.ds(g * 8, 8)
        ty = ty_ref[span, :]
        for j, plane, h_ref in ((0, 0, lo_ref), (1, planes - 1, hi_ref)):
            inv_re = aux_ref[4, j, span, :]
            inv_im = aux_ref[5, j, span, :]
            h = [h_ref[k, span, :] for k in range(4)]
            m = mask_ref[plane:plane + 1, :]
            d = (
                h[0] * inv_re - h[1] * inv_im,
                h[0] * inv_im + h[1] * inv_re,
                h[2] * inv_re - h[3] * inv_im,
                h[2] * inv_im + h[3] * inv_re,
            )
            f2 = [aux_ref[k, j, span, :] + relaxation * d[k] * m for k in range(4)]
            imaging = f2[0] * f2[2] - f2[1] * f2[3] - shift_beta * (f2[0] * f2[3] + f2[1] * f2[2])
            per_block = out_ref.shape[2]
            out_ref[(g * 8) // per_block, j, pl.ds((g * 8) % per_block, 8), :] = imaging * ((ty * tx_ref[plane:plane + 1, :]) * tz)


def edge_planes(aux, lo, hi, ty_col, mask_b, tx_b, tz_b):
    wide_y, wide_z = lo.shape[1:]
    rows = wide_y // 2
    four = lo.shape[0]
    planes = mask_b.shape[0]
    full = lambda b: (0, 0)
    return pl.pallas_call(
        halo_kernel,
        grid=(2,),
        in_specs=[
            pl.BlockSpec((6, 2, rows, wide_z), lambda b: (0, 0, b, 0)),
            pl.BlockSpec((four, rows, wide_z), lambda b: (0, b, 0)),
            pl.BlockSpec((four, rows, wide_z), lambda b: (0, b, 0)),
            pl.BlockSpec((rows, 1), lambda b: (b, 0)),
            pl.BlockSpec((planes, wide_z), full),
            pl.BlockSpec((planes, wide_z), full),
            pl.BlockSpec((1, wide_z), full),
        ],
        out_specs=pl.BlockSpec((BLOCKS // 2, 2, wide_y // BLOCKS, wide_z), lambda b: (b, 0, 0, 0)),
        out_shape=jax.ShapeDtypeStruct((BLOCKS, 2, wide_y // BLOCKS, wide_z), jnp.float32),
    )(aux, lo, hi, ty_col, mask_b, tx_b, tz_b)


def per_device(sources, slowness, group_size, window_anchor, tile_slot):
    slowness_window = slowness[0]
    wide_y, planes, wide_z = slowness_window.shape
    brick_index = lax.axis_index("brick")
    z_index = lax.axis_index("z")
    x_index = lax.axis_index("xl")
    core_index = lax.axis_index("core")
    x_count = lax.axis_size("xl")
    core_count = lax.axis_size("core")
    shot_index = (z_index * x_count + x_index) * core_count + core_index
    brick_count = lax.axis_size("brick")
    extent = group_size[shot_index] * planes
    depth_ids = brick_index * planes + jnp.arange(planes, dtype=jnp.int32)
    active = depth_ids < extent
    mask_col = active.astype(jnp.float32)
    src4 = sources[0].reshape(4, wide_y, planes, wide_z)

    lo_send, hi_send = boundary_planes(src4, slowness_window, mask_col)
    up = [(i, i + 1) for i in range(brick_count - 1)]
    down = [(j, i) for i, j in up]
    lo = lax.ppermute(lo_send, "brick", up)
    hi = lax.ppermute(hi_send, "brick", down)

    extent_float = extent.astype(jnp.float32)
    depth_float = depth_ids.astype(jnp.float32)
    taper_x = jnp.where(active, jnp.sin(jnp.pi * (depth_float + 0.5) / extent_float), 0.0)
    taper_y = sine_taper(wide_y, float(wide_y))
    taper_z = sine_taper(wide_z, float(wide_z))
    mask_b = jnp.broadcast_to(mask_col[:, None], (planes, wide_z))
    tx_b = jnp.broadcast_to(taper_x[:, None], (planes, wide_z))
    tz_b = taper_z[None, :]
    interior, aux = window_blocks(src4, slowness_window, mask_b, tx_b, tz_b, taper_y)
    shot_count = lax.axis_size("z") * x_count * core_count
    tile_dev = tile_slot.shape[0] // shot_count
    partner = (z_index * x_count + (x_count - 1 - x_index)) * core_count + core_index
    slots = jnp.arange(tile_dev, dtype=jnp.int32)
    owners = jnp.concatenate([shot_index * tile_dev + slots, partner * tile_dev + slots])
    zs = jnp.arange(lax.axis_size("z"), dtype=jnp.int32)
    cs = jnp.arange(core_count, dtype=jnp.int32)
    held = ((zs[:, None] * x_count + x_index) * core_count + cs[None, :]).reshape(-1)
    piece_slots = tile_slot[window_anchor[held][:, None] + jnp.arange(BLOCKS, dtype=jnp.int32)[None, :]]
    match = owners[:, None, None] == piece_slots[None, :, :]
    tables = contribution_tables(match)
    swap = [(0, 1), (1, 0)]
    mid = lax.all_gather(interior[None], ("z", "core"), axis=0, tiled=True)
    mid, lo, hi = lax.optimization_barrier((mid, lo, hi))
    part_mid = gather_sum(mid, tables)
    theirs_mid = lax.ppermute(part_mid[tile_dev:], "xl", swap)
    edges = edge_planes(aux, lo, hi, taper_y[:, None], mask_b, tx_b, tz_b)
    rim = lax.all_gather(edges[None], ("z", "core"), axis=0, tiled=True)
    part_rim = gather_sum(rim, tables)
    theirs_rim = lax.ppermute(part_rim[tile_dev:], "xl", swap)
    mid_sum = part_mid[:tile_dev] + theirs_mid
    rim_sum = part_rim[:tile_dev] + theirs_rim
    summed = jnp.concatenate([rim_sum[:, :1], mid_sum, rim_sum[:, 1:]], axis=1)
    return jnp.transpose(summed, (0, 2, 1, 3)).reshape(1, tile_dev, -1)


def select_kernel(es_ref, eb_ref, eq_ref, n_ref, g_hbm, out_ref, buf, sem):
    n = n_ref[0]
    depth = buf.shape[0]
    out_ref[...] = jnp.zeros_like(out_ref)

    def copy(e, slot):
        return pltpu.make_async_copy(g_hbm.at[es_ref[e], eb_ref[e]], buf.at[slot], sem.at[slot])

    for e in range(depth):
        @pl.when(e < n)
        def _():
            copy(e, e).start()

    def body(e, carry):
        slot = e % depth
        copy(e, slot).wait()
        q = eq_ref[e]
        out_ref[q] = out_ref[q] + buf[slot]

        @pl.when(e + depth < n)
        def _():
            copy(e + depth, slot).start()

        return carry

    lax.fori_loop(0, n, body, 0)


def contribution_tables(match):
    owners, shots, blocks = match.shape
    valid = jnp.any(match, axis=2).reshape(-1)
    which_block = jnp.sum(jnp.where(match, jnp.arange(blocks, dtype=jnp.int32), 0), axis=2).reshape(-1)
    shot_of = jnp.broadcast_to(jnp.arange(shots, dtype=jnp.int32)[None, :], (owners, shots)).reshape(-1)
    owner_of = jnp.broadcast_to(jnp.arange(owners, dtype=jnp.int32)[:, None], (owners, shots)).reshape(-1)
    count = owners * shots
    position = jnp.where(valid, jnp.cumsum(valid.astype(jnp.int32)) - 1, count)
    empty = jnp.zeros((count,), jnp.int32)
    es = empty.at[position].set(shot_of, mode="drop")
    eb = empty.at[position].set(which_block, mode="drop")
    eq = empty.at[position].set(owner_of, mode="drop")
    n = jnp.sum(valid.astype(jnp.int32)).reshape(1)
    return owners, (es, eb, eq, n)


def gather_sum(gathered, tables):
    owners, (es, eb, eq, n) = tables
    cell_shape = gathered.shape[2:]
    return pl.pallas_call(
        select_kernel,
        grid_spec=pltpu.PrefetchScalarGridSpec(
            num_scalar_prefetch=4,
            grid=(1,),
            in_specs=[pl.BlockSpec(memory_space=pl.ANY)],
            out_specs=pl.BlockSpec((owners,) + cell_shape, lambda i, *_: (0,) * (1 + len(cell_shape))),
            scratch_shapes=[
                pltpu.VMEM((8,) + cell_shape, jnp.float32),
                pltpu.SemaphoreType.DMA((8,)),
            ],
        ),
        out_shape=jax.ShapeDtypeStruct((owners,) + cell_shape, jnp.float32),
    )(es, eb, eq, n, gathered)


def solution(mesh):
    devices = mesh.devices
    shots, bricks = devices.shape
    split = jax.sharding.Mesh(devices.reshape(shots // 4, 2, 2, bricks), ("z", "xl", "core", "brick"))
    shot = ("z", "xl", "core")
    return jax.shard_map(
        per_device,
        mesh=split,
        in_specs=(
            P(shot, None, None, None, "brick", None),
            P(shot, None, "brick", None),
            P(),
            P(),
            P(),
        ),
        out_specs=P("brick", shot, None),
        check_vma=False,
    )
```

```python
import jax
import jax.numpy as jnp
from jax import lax
from jax.experimental import pallas as pl
from jax.experimental.pallas import tpu as pltpu
from jax.sharding import PartitionSpec as P

BLOCKS = 8


shift_beta = 0.5
relaxation = 0.8


def sine_taper(count, extent):
    positions = jnp.arange(count, dtype=jnp.int32).astype(jnp.float32)
    return jnp.sin(jnp.pi * (positions + 0.5) / extent)


def inverse_of(slow):
    real_d = 6.0 - slow
    imag_d = shift_beta * slow
    denominator = real_d * real_d + imag_d * imag_d
    scale = 1.0 / denominator
    return real_d * scale, imag_d * scale


def first_sweep(s0, s1, s2, s3, inv_re, inv_im, mask):
    return (
        relaxation * (s0 * inv_re - s1 * inv_im) * mask,
        relaxation * (s0 * inv_im + s1 * inv_re) * mask,
        relaxation * (s2 * inv_re - s3 * inv_im) * mask,
        relaxation * (s2 * inv_im + s3 * inv_re) * mask,
    )


def gather_plane(rows8, plane, sub_ids):
    tile = jnp.broadcast_to(rows8[0][plane:plane + 1, :], rows8[0].shape)
    for i in range(1, len(rows8)):
        tile = jnp.where(sub_ids == i, jnp.broadcast_to(rows8[i][plane:plane + 1, :], tile.shape), tile)
    return tile


def boundary_kernel(mask_ref, src_hbm, sl_hbm, lo_ref, hi_ref, src_buf, sl_buf, sem):
    four = src_hbm.shape[0]
    planes = src_hbm.shape[2]
    copies = []
    for j, plane in enumerate((planes - 1, 0)):
        for k in range(four):
            copies.append(pltpu.make_async_copy(src_hbm.at[k, :, plane, :], src_buf.at[j, k], sem.at[j, k]))
        copies.append(pltpu.make_async_copy(sl_hbm.at[:, plane, :], sl_buf.at[j], sem.at[j, four]))
    for c in copies:
        c.start()
    for c in copies:
        c.wait()
    for j, (plane, out) in enumerate(((planes - 1, lo_ref), (0, hi_ref))):
        m = mask_ref[plane]
        inv_re, inv_im = inverse_of(sl_buf[j])
        f = first_sweep(src_buf[j, 0], src_buf[j, 1], src_buf[j, 2], src_buf[j, 3], inv_re, inv_im, m)
        for k in range(four):
            out[k] = f[k]


def boundary_planes(src4, slow, mask_col):
    four, wide_y, planes, wide_z = src4.shape
    face = jax.ShapeDtypeStruct((four, wide_y, wide_z), jnp.float32)
    vmem = pl.BlockSpec(memory_space=pltpu.VMEM)
    return pl.pallas_call(
        boundary_kernel,
        in_specs=[
            pl.BlockSpec(memory_space=pltpu.SMEM),
            pl.BlockSpec(memory_space=pl.ANY),
            pl.BlockSpec(memory_space=pl.ANY),
        ],
        out_specs=[vmem, vmem],
        out_shape=[face, face],
        scratch_shapes=[
            pltpu.VMEM((2, four, wide_y, wide_z), jnp.float32),
            pltpu.VMEM((2, wide_y, wide_z), jnp.float32),
            pltpu.SemaphoreType.DMA((2, four + 1)),
        ],
    )(mask_col, src4, slow)


def gradient_kernel(ty_ref, src_ref, src_lo_ref, src_hi_ref, sl_ref, sl_lo_ref, sl_hi_ref, mask_ref, tx_ref, tz_ref,
                    out_ref, aux_ref, f1_s, inv_s):
    b = pl.program_id(0)
    nb = pl.num_programs(0)
    rows = src_ref.shape[1]
    mask = mask_ref[...]

    def sweep_one(r, carry):
        inv_re, inv_im = inverse_of(sl_ref[r])
        inv_s[0, r] = inv_re
        inv_s[1, r] = inv_im
        f = first_sweep(src_ref[0, r], src_ref[1, r], src_ref[2, r], src_ref[3, r], inv_re, inv_im, mask)
        for k in range(4):
            f1_s[k, r + 1] = f[k]
        return carry

    lax.fori_loop(0, rows, sweep_one, 0, unroll=2)

    lo_keep = jnp.where(b > 0, 1.0, 0.0).astype(jnp.float32)
    hi_keep = jnp.where(b < nb - 1, 1.0, 0.0).astype(jnp.float32)
    for slot, s_ref, l_ref, keep in ((0, src_lo_ref, sl_lo_ref, lo_keep), (rows + 1, src_hi_ref, sl_hi_ref, hi_keep)):
        inv_re, inv_im = inverse_of(l_ref[0])
        f = first_sweep(s_ref[0, 0], s_ref[1, 0], s_ref[2, 0], s_ref[3, 0], inv_re, inv_im, mask)
        for k in range(4):
            f1_s[k, slot] = f[k] * keep

    shape = mask.shape
    p_ids = lax.broadcasted_iota(jnp.int32, shape, 0)
    z_ids = lax.broadcasted_iota(jnp.int32, shape, 1)
    planes, width = shape
    tx = tx_ref[...]
    tz = tz_ref[...]

    def sweep_two(g, carry):
        base = pl.multiple_of(g * 8, 8)
        kept = [[] for _ in range(6)]
        grads = []
        for i in range(8):
            r = base + i
            inv_re = inv_s[0, r]
            inv_im = inv_s[1, r]
            cur = []
            vals = []
            for k in range(4):
                c = f1_s[k, r + 1]
                acc = f1_s[k, r] + f1_s[k, r + 2]
                down = jnp.where(p_ids == 0, 0.0, pltpu.roll(c, 1, 0))
                acc = acc + down
                up = jnp.where(p_ids == planes - 1, 0.0, pltpu.roll(c, planes - 1, 0))
                acc = acc + up
                zm = jnp.where(z_ids == 0, 0.0, pltpu.roll(c, 1, 1))
                acc = acc + zm
                zp = jnp.where(z_ids == width - 1, 0.0, pltpu.roll(c, width - 1, 1))
                acc = acc + zp
                cur.append(c)
                vals.append(src_ref[k, r] + acc)
            upd = (
                vals[0] * inv_re - vals[1] * inv_im,
                vals[0] * inv_im + vals[1] * inv_re,
                vals[2] * inv_re - vals[3] * inv_im,
                vals[2] * inv_im + vals[3] * inv_re,
            )
            f2 = [((1.0 - relaxation) * cur[k] + relaxation * upd[k]) * mask for k in range(4)]
            imaging = f2[0] * f2[2] - f2[1] * f2[3] - shift_beta * (f2[0] * f2[3] + f2[1] * f2[2])
            taper = (ty_ref[b * rows + r] * tx) * tz
            grads.append(imaging * taper)
            for k, v in enumerate(f2 + [inv_re, inv_im]):
                kept[k].append(v)
        for k in range(6):
            for j, plane in enumerate((0, planes - 1)):
                aux_ref[k, j, pl.ds(base, 8), :] = gather_plane(kept[k], plane, p_ids)
        for plane in range(1, planes - 1):
            out_ref[0, plane - 1, pl.ds(base, 8), :] = gather_plane(grads, plane, p_ids)
        return carry

    lax.fori_loop(0, rows // 8, sweep_two, 0)


def window_blocks(src4, slow, mask_b, tx_b, tz_b, ty):
    four, wide_y, planes, wide_z = src4.shape
    rows = wide_y // BLOCKS
    last = wide_y - 1

    def row_spec(pick):
        return pl.BlockSpec((four, 1, planes, wide_z), lambda b, t: (0, pick(b), 0, 0))

    def slow_row_spec(pick):
        return pl.BlockSpec((1, planes, wide_z), lambda b, t: (pick(b), 0, 0))

    below = lambda b: jnp.maximum(b * rows - 1, 0)
    above = lambda b: jnp.minimum(b * rows + rows, last)
    grid_spec = pltpu.PrefetchScalarGridSpec(
        num_scalar_prefetch=1,
        grid=(BLOCKS,),
        in_specs=[
            pl.BlockSpec((four, rows, planes, wide_z), lambda b, t: (0, b, 0, 0)),
            row_spec(below),
            row_spec(above),
            pl.BlockSpec((rows, planes, wide_z), lambda b, t: (b, 0, 0)),
            slow_row_spec(below),
            slow_row_spec(above),
            pl.BlockSpec((planes, wide_z), lambda b, t: (0, 0)),
            pl.BlockSpec((planes, wide_z), lambda b, t: (0, 0)),
            pl.BlockSpec((1, wide_z), lambda b, t: (0, 0)),
        ],
        out_specs=[
            pl.BlockSpec((1, planes - 2, rows, wide_z), lambda b, t: (b, 0, 0, 0)),
            pl.BlockSpec((6, 2, rows, wide_z), lambda b, t: (0, 0, b, 0)),
        ],
        scratch_shapes=[
            pltpu.VMEM((four, rows + 2, planes, wide_z), jnp.float32),
            pltpu.VMEM((2, rows, planes, wide_z), jnp.float32),
        ],
    )
    return pl.pallas_call(
        gradient_kernel,
        grid_spec=grid_spec,
        out_shape=[
            jax.ShapeDtypeStruct((BLOCKS, planes - 2, rows, wide_z), jnp.float32),
            jax.ShapeDtypeStruct((6, 2, wide_y, wide_z), jnp.float32),
        ],
    )(ty, src4, src4, src4, slow, slow, slow, mask_b, tx_b, tz_b)


def halo_kernel(aux_ref, lo_ref, hi_ref, ty_ref, mask_ref, tx_ref, tz_ref, out_ref):
    rows = aux_ref.shape[2]
    planes = mask_ref.shape[0]
    tz = tz_ref[...]
    for g in range(rows // 8):
        span = pl.ds(g * 8, 8)
        ty = ty_ref[span, :]
        for j, plane, h_ref in ((0, 0, lo_ref), (1, planes - 1, hi_ref)):
            inv_re = aux_ref[4, j, span, :]
            inv_im = aux_ref[5, j, span, :]
            h = [h_ref[k, span, :] for k in range(4)]
            m = mask_ref[plane:plane + 1, :]
            d = (
                h[0] * inv_re - h[1] * inv_im,
                h[0] * inv_im + h[1] * inv_re,
                h[2] * inv_re - h[3] * inv_im,
                h[2] * inv_im + h[3] * inv_re,
            )
            f2 = [aux_ref[k, j, span, :] + relaxation * d[k] * m for k in range(4)]
            imaging = f2[0] * f2[2] - f2[1] * f2[3] - shift_beta * (f2[0] * f2[3] + f2[1] * f2[2])
            per_block = out_ref.shape[2]
            out_ref[(g * 8) // per_block, j, pl.ds((g * 8) % per_block, 8), :] = imaging * ((ty * tx_ref[plane:plane + 1, :]) * tz)


def edge_planes(aux, lo, hi, ty_col, mask_b, tx_b, tz_b):
    wide_y, wide_z = lo.shape[1:]
    rows = wide_y // 2
    four = lo.shape[0]
    planes = mask_b.shape[0]
    full = lambda b: (0, 0)
    return pl.pallas_call(
        halo_kernel,
        grid=(2,),
        in_specs=[
            pl.BlockSpec((6, 2, rows, wide_z), lambda b: (0, 0, b, 0)),
            pl.BlockSpec((four, rows, wide_z), lambda b: (0, b, 0)),
            pl.BlockSpec((four, rows, wide_z), lambda b: (0, b, 0)),
            pl.BlockSpec((rows, 1), lambda b: (b, 0)),
            pl.BlockSpec((planes, wide_z), full),
            pl.BlockSpec((planes, wide_z), full),
            pl.BlockSpec((1, wide_z), full),
        ],
        out_specs=pl.BlockSpec((BLOCKS // 2, 2, wide_y // BLOCKS, wide_z), lambda b: (b, 0, 0, 0)),
        out_shape=jax.ShapeDtypeStruct((BLOCKS, 2, wide_y // BLOCKS, wide_z), jnp.float32),
    )(aux, lo, hi, ty_col, mask_b, tx_b, tz_b)


def per_device(sources, slowness, group_size, window_anchor, tile_slot):
    slowness_window = slowness[0]
    wide_y, planes, wide_z = slowness_window.shape
    brick_index = lax.axis_index("brick")
    z_index = lax.axis_index("z")
    x_index = lax.axis_index("xl")
    core_index = lax.axis_index("core")
    x_count = lax.axis_size("xl")
    core_count = lax.axis_size("core")
    shot_index = (z_index * x_count + x_index) * core_count + core_index
    brick_count = lax.axis_size("brick")
    extent = group_size[shot_index] * planes
    depth_ids = brick_index * planes + jnp.arange(planes, dtype=jnp.int32)
    active = depth_ids < extent
    mask_col = active.astype(jnp.float32)
    src4 = sources[0].reshape(4, wide_y, planes, wide_z)

    lo_send, hi_send = boundary_planes(src4, slowness_window, mask_col)
    up = [(i, i + 1) for i in range(brick_count - 1)]
    down = [(j, i) for i, j in up]
    lo = lax.ppermute(lo_send, "brick", up)
    hi = lax.ppermute(hi_send, "brick", down)

    extent_float = extent.astype(jnp.float32)
    depth_float = depth_ids.astype(jnp.float32)
    taper_x = jnp.where(active, jnp.sin(jnp.pi * (depth_float + 0.5) / extent_float), 0.0)
    taper_y = sine_taper(wide_y, float(wide_y))
    taper_z = sine_taper(wide_z, float(wide_z))
    mask_b = jnp.broadcast_to(mask_col[:, None], (planes, wide_z))
    tx_b = jnp.broadcast_to(taper_x[:, None], (planes, wide_z))
    tz_b = taper_z[None, :]
    interior, aux = window_blocks(src4, slowness_window, mask_b, tx_b, tz_b, taper_y)
    shot_count = lax.axis_size("z") * x_count * core_count
    tile_dev = tile_slot.shape[0] // shot_count
    partner = (z_index * x_count + (x_count - 1 - x_index)) * core_count + core_index
    slots = jnp.arange(tile_dev, dtype=jnp.int32)
    owners = jnp.concatenate([shot_index * tile_dev + slots, partner * tile_dev + slots])
    zs = jnp.arange(lax.axis_size("z"), dtype=jnp.int32)
    cs = jnp.arange(core_count, dtype=jnp.int32)
    held = ((zs[:, None] * x_count + x_index) * core_count + cs[None, :]).reshape(-1)
    piece_slots = tile_slot[window_anchor[held][:, None] + jnp.arange(BLOCKS, dtype=jnp.int32)[None, :]]
    match = owners[:, None, None] == piece_slots[None, :, :]
    tables = contribution_tables(match)
    swap = [(0, 1), (1, 0)]
    mid = lax.all_gather(interior[None], ("z", "core"), axis=0, tiled=True)
    mid, lo, hi = lax.optimization_barrier((mid, lo, hi))
    own_mid, other_mid = gather_sum(mid, tables)
    theirs_mid = lax.ppermute(other_mid, "xl", swap)
    edges = edge_planes(aux, lo, hi, taper_y[:, None], mask_b, tx_b, tz_b)
    rim = lax.all_gather(edges[None], ("z", "core"), axis=0, tiled=True)
    own_rim, other_rim = gather_sum(rim, tables)
    theirs_rim = lax.ppermute(other_rim, "xl", swap)
    mid_sum = own_mid + theirs_mid
    rim_sum = own_rim + theirs_rim
    summed = jnp.concatenate([rim_sum[:, :1], mid_sum, rim_sum[:, 1:]], axis=1)
    return jnp.transpose(summed, (0, 2, 1, 3)).reshape(1, tile_dev, -1)


def select_kernel(es_ref, eb_ref, eq_ref, n_ref, g_hbm, own_ref, other_ref, buf, sem):
    n = n_ref[0]
    depth = buf.shape[0]
    half = own_ref.shape[0]
    own_ref[...] = jnp.zeros_like(own_ref)
    other_ref[...] = jnp.zeros_like(other_ref)

    def copy(e, slot):
        return pltpu.make_async_copy(g_hbm.at[es_ref[e], eb_ref[e]], buf.at[slot], sem.at[slot])

    for e in range(depth):
        @pl.when(e < n)
        def _():
            copy(e, e).start()

    def body(e, carry):
        slot = e % depth
        copy(e, slot).wait()
        q = eq_ref[e]

        @pl.when(q < half)
        def _():
            mine = jnp.minimum(q, half - 1)
            own_ref[mine] = own_ref[mine] + buf[slot]

        @pl.when(q >= half)
        def _():
            theirs = jnp.maximum(q - half, 0)
            other_ref[theirs] = other_ref[theirs] + buf[slot]

        @pl.when(e + depth < n)
        def _():
            copy(e + depth, slot).start()

        return carry

    lax.fori_loop(0, n, body, 0)


def contribution_tables(match):
    owners, shots, blocks = match.shape
    valid = jnp.any(match, axis=2).reshape(-1)
    which_block = jnp.sum(jnp.where(match, jnp.arange(blocks, dtype=jnp.int32), 0), axis=2).reshape(-1)
    shot_of = jnp.broadcast_to(jnp.arange(shots, dtype=jnp.int32)[None, :], (owners, shots)).reshape(-1)
    owner_of = jnp.broadcast_to(jnp.arange(owners, dtype=jnp.int32)[:, None], (owners, shots)).reshape(-1)
    count = owners * shots
    position = jnp.where(valid, jnp.cumsum(valid.astype(jnp.int32)) - 1, count)
    empty = jnp.zeros((count,), jnp.int32)
    es = empty.at[position].set(shot_of, mode="drop")
    eb = empty.at[position].set(which_block, mode="drop")
    eq = empty.at[position].set(owner_of, mode="drop")
    n = jnp.sum(valid.astype(jnp.int32)).reshape(1)
    return owners, (es, eb, eq, n)


def gather_sum(gathered, tables):
    owners, (es, eb, eq, n) = tables
    cell_shape = gathered.shape[2:]
    return pl.pallas_call(
        select_kernel,
        grid_spec=pltpu.PrefetchScalarGridSpec(
            num_scalar_prefetch=4,
            grid=(1,),
            in_specs=[pl.BlockSpec(memory_space=pl.ANY)],
            out_specs=[pl.BlockSpec((owners // 2,) + cell_shape, lambda i, *_: (0,) * (1 + len(cell_shape)))] * 2,
            scratch_shapes=[
                pltpu.VMEM((8,) + cell_shape, jnp.float32),
                pltpu.SemaphoreType.DMA((8,)),
            ],
        ),
        out_shape=[jax.ShapeDtypeStruct((owners // 2,) + cell_shape, jnp.float32)] * 2,
    )(es, eb, eq, n, gathered)


def solution(mesh):
    devices = mesh.devices
    shots, bricks = devices.shape
    split = jax.sharding.Mesh(devices.reshape(shots // 4, 2, 2, bricks), ("z", "xl", "core", "brick"))
    shot = ("z", "xl", "core")
    return jax.shard_map(
        per_device,
        mesh=split,
        in_specs=(
            P(shot, None, None, None, "brick", None),
            P(shot, None, "brick", None),
            P(),
            P(),
            P(),
        ),
        out_specs=P("brick", shot, None),
        check_vma=False,
    )
```

```python
import jax
import jax.numpy as jnp
from jax import lax
from jax.experimental import pallas as pl
from jax.experimental.pallas import tpu as pltpu
from jax.sharding import PartitionSpec as P

BLOCKS = 8


shift_beta = 0.5
relaxation = 0.8


def sine_taper(count, extent):
    positions = jnp.arange(count, dtype=jnp.int32).astype(jnp.float32)
    return jnp.sin(jnp.pi * (positions + 0.5) / extent)


def inverse_of(slow):
    real_d = 6.0 - slow
    imag_d = shift_beta * slow
    denominator = real_d * real_d + imag_d * imag_d
    scale = 1.0 / denominator
    return real_d * scale, imag_d * scale


def first_sweep(s0, s1, s2, s3, inv_re, inv_im, mask):
    return (
        relaxation * (s0 * inv_re - s1 * inv_im) * mask,
        relaxation * (s0 * inv_im + s1 * inv_re) * mask,
        relaxation * (s2 * inv_re - s3 * inv_im) * mask,
        relaxation * (s2 * inv_im + s3 * inv_re) * mask,
    )


def gather_plane(rows8, plane, sub_ids):
    tile = jnp.broadcast_to(rows8[0][plane:plane + 1, :], rows8[0].shape)
    for i in range(1, len(rows8)):
        tile = jnp.where(sub_ids == i, jnp.broadcast_to(rows8[i][plane:plane + 1, :], tile.shape), tile)
    return tile


def boundary_kernel(mask_ref, src_hbm, sl_hbm, lo_ref, hi_ref, src_buf, sl_buf, sem):
    four = src_hbm.shape[0]
    planes = src_hbm.shape[2]
    copies = []
    for j, plane in enumerate((planes - 1, 0)):
        for k in range(four):
            copies.append(pltpu.make_async_copy(src_hbm.at[k, :, plane, :], src_buf.at[j, k], sem.at[j, k]))
        copies.append(pltpu.make_async_copy(sl_hbm.at[:, plane, :], sl_buf.at[j], sem.at[j, four]))
    for c in copies:
        c.start()
    for c in copies:
        c.wait()
    for j, (plane, out) in enumerate(((planes - 1, lo_ref), (0, hi_ref))):
        m = mask_ref[plane]
        inv_re, inv_im = inverse_of(sl_buf[j])
        f = first_sweep(src_buf[j, 0], src_buf[j, 1], src_buf[j, 2], src_buf[j, 3], inv_re, inv_im, m)
        for k in range(four):
            out[k] = f[k]


def boundary_planes(src4, slow, mask_col):
    four, wide_y, planes, wide_z = src4.shape
    face = jax.ShapeDtypeStruct((four, wide_y, wide_z), jnp.float32)
    vmem = pl.BlockSpec(memory_space=pltpu.VMEM)
    return pl.pallas_call(
        boundary_kernel,
        in_specs=[
            pl.BlockSpec(memory_space=pltpu.SMEM),
            pl.BlockSpec(memory_space=pl.ANY),
            pl.BlockSpec(memory_space=pl.ANY),
        ],
        out_specs=[vmem, vmem],
        out_shape=[face, face],
        scratch_shapes=[
            pltpu.VMEM((2, four, wide_y, wide_z), jnp.float32),
            pltpu.VMEM((2, wide_y, wide_z), jnp.float32),
            pltpu.SemaphoreType.DMA((2, four + 1)),
        ],
    )(mask_col, src4, slow)


def gradient_kernel(ty_ref, src_ref, src_lo_ref, src_hi_ref, sl_ref, sl_lo_ref, sl_hi_ref, mask_ref, tx_ref, tz_ref,
                    out_ref, aux_ref, f1_s, inv_s):
    b = pl.program_id(0)
    nb = pl.num_programs(0)
    rows = src_ref.shape[1]
    mask = mask_ref[...]

    def sweep_one(r, carry):
        inv_re, inv_im = inverse_of(sl_ref[r])
        inv_s[0, r] = inv_re
        inv_s[1, r] = inv_im
        f = first_sweep(src_ref[0, r], src_ref[1, r], src_ref[2, r], src_ref[3, r], inv_re, inv_im, mask)
        for k in range(4):
            f1_s[k, r + 1] = f[k]
        return carry

    lax.fori_loop(0, rows, sweep_one, 0, unroll=2)

    lo_keep = jnp.where(b > 0, 1.0, 0.0).astype(jnp.float32)
    hi_keep = jnp.where(b < nb - 1, 1.0, 0.0).astype(jnp.float32)
    for slot, s_ref, l_ref, keep in ((0, src_lo_ref, sl_lo_ref, lo_keep), (rows + 1, src_hi_ref, sl_hi_ref, hi_keep)):
        inv_re, inv_im = inverse_of(l_ref[0])
        f = first_sweep(s_ref[0, 0], s_ref[1, 0], s_ref[2, 0], s_ref[3, 0], inv_re, inv_im, mask)
        for k in range(4):
            f1_s[k, slot] = f[k] * keep

    shape = mask.shape
    p_ids = lax.broadcasted_iota(jnp.int32, shape, 0)
    z_ids = lax.broadcasted_iota(jnp.int32, shape, 1)
    planes, width = shape
    tx = tx_ref[...]
    tz = tz_ref[...]

    def sweep_two(g, carry):
        base = pl.multiple_of(g * 8, 8)
        kept = [[] for _ in range(6)]
        grads = []
        for i in range(8):
            r = base + i
            inv_re = inv_s[0, r]
            inv_im = inv_s[1, r]
            cur = []
            vals = []
            for k in range(4):
                c = f1_s[k, r + 1]
                acc = f1_s[k, r] + f1_s[k, r + 2]
                down = jnp.where(p_ids == 0, 0.0, pltpu.roll(c, 1, 0))
                acc = acc + down
                up = jnp.where(p_ids == planes - 1, 0.0, pltpu.roll(c, planes - 1, 0))
                acc = acc + up
                zm = jnp.where(z_ids == 0, 0.0, pltpu.roll(c, 1, 1))
                acc = acc + zm
                zp = jnp.where(z_ids == width - 1, 0.0, pltpu.roll(c, width - 1, 1))
                acc = acc + zp
                cur.append(c)
                vals.append(src_ref[k, r] + acc)
            upd = (
                vals[0] * inv_re - vals[1] * inv_im,
                vals[0] * inv_im + vals[1] * inv_re,
                vals[2] * inv_re - vals[3] * inv_im,
                vals[2] * inv_im + vals[3] * inv_re,
            )
            f2 = [((1.0 - relaxation) * cur[k] + relaxation * upd[k]) * mask for k in range(4)]
            imaging = f2[0] * f2[2] - f2[1] * f2[3] - shift_beta * (f2[0] * f2[3] + f2[1] * f2[2])
            taper = (ty_ref[b * rows + r] * tx) * tz
            grads.append(imaging * taper)
            for k, v in enumerate(f2 + [inv_re, inv_im]):
                kept[k].append(v)
        for k in range(6):
            for j, plane in enumerate((0, planes - 1)):
                aux_ref[k, j, pl.ds(base, 8), :] = gather_plane(kept[k], plane, p_ids)
        for plane in range(1, planes - 1):
            out_ref[0, plane - 1, pl.ds(base, 8), :] = gather_plane(grads, plane, p_ids)
        return carry

    lax.fori_loop(0, rows // 8, sweep_two, 0)


def window_blocks(src4, slow, consts, ty):
    four, wide_y, planes, wide_z = src4.shape
    rows = wide_y // BLOCKS
    last = wide_y - 1

    def row_spec(pick):
        return pl.BlockSpec((four, 1, planes, wide_z), lambda b, t: (0, pick(b), 0, 0))

    def slow_row_spec(pick):
        return pl.BlockSpec((1, planes, wide_z), lambda b, t: (pick(b), 0, 0))

    below = lambda b: jnp.maximum(b * rows - 1, 0)
    above = lambda b: jnp.minimum(b * rows + rows, last)
    grid_spec = pltpu.PrefetchScalarGridSpec(
        num_scalar_prefetch=1,
        grid=(BLOCKS,),
        in_specs=[
            pl.BlockSpec((four, rows, planes, wide_z), lambda b, t: (0, b, 0, 0)),
            row_spec(below),
            row_spec(above),
            pl.BlockSpec((rows, planes, wide_z), lambda b, t: (b, 0, 0)),
            slow_row_spec(below),
            slow_row_spec(above),
            pl.BlockSpec((None, planes, wide_z), lambda b, t: (0, 0, 0)),
            pl.BlockSpec((None, planes, wide_z), lambda b, t: (1, 0, 0)),
            pl.BlockSpec((None, planes, wide_z), lambda b, t: (2, 0, 0)),
        ],
        out_specs=[
            pl.BlockSpec((1, planes - 2, rows, wide_z), lambda b, t: (b, 0, 0, 0)),
            pl.BlockSpec((6, 2, rows, wide_z), lambda b, t: (0, 0, b, 0)),
        ],
        scratch_shapes=[
            pltpu.VMEM((four, rows + 2, planes, wide_z), jnp.float32),
            pltpu.VMEM((2, rows, planes, wide_z), jnp.float32),
        ],
    )
    return pl.pallas_call(
        gradient_kernel,
        grid_spec=grid_spec,
        out_shape=[
            jax.ShapeDtypeStruct((BLOCKS, planes - 2, rows, wide_z), jnp.float32),
            jax.ShapeDtypeStruct((6, 2, wide_y, wide_z), jnp.float32),
        ],
    )(ty, src4, src4, src4, slow, slow, slow, consts, consts, consts)


def halo_kernel(aux_ref, lo_ref, hi_ref, ty_ref, mask_ref, tx_ref, tz_ref, out_ref):
    rows = aux_ref.shape[2]
    planes = mask_ref.shape[0]
    tz = tz_ref[...]
    for g in range(rows // 8):
        span = pl.ds(g * 8, 8)
        ty = ty_ref[span, :]
        for j, plane, h_ref in ((0, 0, lo_ref), (1, planes - 1, hi_ref)):
            inv_re = aux_ref[4, j, span, :]
            inv_im = aux_ref[5, j, span, :]
            h = [h_ref[k, span, :] for k in range(4)]
            m = mask_ref[plane:plane + 1, :]
            d = (
                h[0] * inv_re - h[1] * inv_im,
                h[0] * inv_im + h[1] * inv_re,
                h[2] * inv_re - h[3] * inv_im,
                h[2] * inv_im + h[3] * inv_re,
            )
            f2 = [aux_ref[k, j, span, :] + relaxation * d[k] * m for k in range(4)]
            imaging = f2[0] * f2[2] - f2[1] * f2[3] - shift_beta * (f2[0] * f2[3] + f2[1] * f2[2])
            per_block = out_ref.shape[2]
            out_ref[(g * 8) // per_block, j, pl.ds((g * 8) % per_block, 8), :] = imaging * ((ty * tx_ref[plane:plane + 1, :]) * tz)


def edge_planes(aux, lo, hi, ty_col, consts):
    wide_y, wide_z = lo.shape[1:]
    rows = wide_y // 2
    four = lo.shape[0]
    planes = consts.shape[1]
    return pl.pallas_call(
        halo_kernel,
        grid=(2,),
        in_specs=[
            pl.BlockSpec((6, 2, rows, wide_z), lambda b: (0, 0, b, 0)),
            pl.BlockSpec((four, rows, wide_z), lambda b: (0, b, 0)),
            pl.BlockSpec((four, rows, wide_z), lambda b: (0, b, 0)),
            pl.BlockSpec((rows, 1), lambda b: (b, 0)),
            pl.BlockSpec((None, planes, wide_z), lambda b: (0, 0, 0)),
            pl.BlockSpec((None, planes, wide_z), lambda b: (1, 0, 0)),
            pl.BlockSpec((None, planes, wide_z), lambda b: (2, 0, 0)),
        ],
        out_specs=pl.BlockSpec((BLOCKS // 2, 2, wide_y // BLOCKS, wide_z), lambda b: (b, 0, 0, 0)),
        out_shape=jax.ShapeDtypeStruct((BLOCKS, 2, wide_y // BLOCKS, wide_z), jnp.float32),
    )(aux, lo, hi, ty_col, consts, consts, consts)


def per_device(sources, slowness, group_size, window_anchor, tile_slot):
    slowness_window = slowness[0]
    wide_y, planes, wide_z = slowness_window.shape
    brick_index = lax.axis_index("brick")
    z_index = lax.axis_index("z")
    x_index = lax.axis_index("xl")
    core_index = lax.axis_index("core")
    x_count = lax.axis_size("xl")
    core_count = lax.axis_size("core")
    shot_index = (z_index * x_count + x_index) * core_count + core_index
    brick_count = lax.axis_size("brick")
    shot_count_all = group_size.shape[0]
    extent = jnp.sum(jnp.where(jnp.arange(shot_count_all) == shot_index, group_size, 0)) * planes
    depth_ids = brick_index * planes + jnp.arange(planes, dtype=jnp.int32)
    active = depth_ids < extent
    mask_col = active.astype(jnp.float32)
    src4 = sources[0].reshape(4, wide_y, planes, wide_z)

    lo_send, hi_send = boundary_planes(src4, slowness_window, mask_col)
    up = [(i, i + 1) for i in range(brick_count - 1)]
    down = [(j, i) for i, j in up]
    lo = lax.ppermute(lo_send, "brick", up)
    hi = lax.ppermute(hi_send, "brick", down)

    extent_float = extent.astype(jnp.float32)
    depth_float = depth_ids.astype(jnp.float32)
    taper_x = jnp.where(active, jnp.sin(jnp.pi * (depth_float + 0.5) / extent_float), 0.0)
    taper_y = sine_taper(wide_y, float(wide_y))
    taper_z = sine_taper(wide_z, float(wide_z))
    consts = jnp.stack([
        jnp.broadcast_to(mask_col[:, None], (planes, wide_z)),
        jnp.broadcast_to(taper_x[:, None], (planes, wide_z)),
        jnp.broadcast_to(taper_z[None, :], (planes, wide_z)),
    ])
    interior, aux = window_blocks(src4, slowness_window, consts, taper_y)
    shot_count = lax.axis_size("z") * x_count * core_count
    tile_dev = tile_slot.shape[0] // shot_count
    partner = (z_index * x_count + (x_count - 1 - x_index)) * core_count + core_index
    slots = jnp.arange(tile_dev, dtype=jnp.int32)
    owners = jnp.concatenate([shot_index * tile_dev + slots, partner * tile_dev + slots])
    zs = jnp.arange(lax.axis_size("z"), dtype=jnp.int32)
    cs = jnp.arange(core_count, dtype=jnp.int32)
    held = ((zs[:, None] * x_count + x_index) * core_count + cs[None, :]).reshape(-1)
    piece_slots = tile_slot[window_anchor[held][:, None] + jnp.arange(BLOCKS, dtype=jnp.int32)[None, :]]
    match = owners[:, None, None] == piece_slots[None, :, :]
    tables = contribution_tables(match)
    swap = [(0, 1), (1, 0)]
    mid = lax.all_gather(interior[None], ("z", "core"), axis=0, tiled=True)
    mid, lo, hi = lax.optimization_barrier((mid, lo, hi))
    own_mid, other_mid = gather_sum(mid, tables)
    theirs_mid = lax.ppermute(other_mid, "xl", swap)
    edges = edge_planes(aux, lo, hi, taper_y[:, None], consts)
    rim = lax.all_gather(edges[None], ("z", "core"), axis=0, tiled=True)
    own_rim, other_rim = gather_sum(rim, tables)
    theirs_rim = lax.ppermute(other_rim, "xl", swap)
    mid_sum = own_mid + theirs_mid
    rim_sum = own_rim + theirs_rim
    summed = jnp.concatenate([rim_sum[:, :1], mid_sum, rim_sum[:, 1:]], axis=1)
    return jnp.transpose(summed, (0, 2, 1, 3)).reshape(1, tile_dev, -1)


def select_kernel(es_ref, eb_ref, eq_ref, n_ref, g_hbm, own_ref, other_ref, buf, sem):
    n = n_ref[0]
    depth = buf.shape[0]
    half = own_ref.shape[0]
    own_ref[...] = jnp.zeros_like(own_ref)
    other_ref[...] = jnp.zeros_like(other_ref)

    def copy(e, slot):
        return pltpu.make_async_copy(g_hbm.at[es_ref[e], eb_ref[e]], buf.at[slot], sem.at[slot])

    for e in range(depth):
        @pl.when(e < n)
        def _():
            copy(e, e).start()

    def body(e, carry):
        slot = e % depth
        copy(e, slot).wait()
        q = eq_ref[e]

        @pl.when(q < half)
        def _():
            mine = jnp.minimum(q, half - 1)
            own_ref[mine] = own_ref[mine] + buf[slot]

        @pl.when(q >= half)
        def _():
            theirs = jnp.maximum(q - half, 0)
            other_ref[theirs] = other_ref[theirs] + buf[slot]

        @pl.when(e + depth < n)
        def _():
            copy(e + depth, slot).start()

        return carry

    lax.fori_loop(0, n, body, 0)


def contribution_tables(match):
    owners, shots, blocks = match.shape
    valid = jnp.any(match, axis=2).reshape(-1)
    which_block = jnp.sum(jnp.where(match, jnp.arange(blocks, dtype=jnp.int32), 0), axis=2).reshape(-1)
    shot_of = jnp.broadcast_to(jnp.arange(shots, dtype=jnp.int32)[None, :], (owners, shots)).reshape(-1)
    owner_of = jnp.broadcast_to(jnp.arange(owners, dtype=jnp.int32)[:, None], (owners, shots)).reshape(-1)
    count = owners * shots
    position = jnp.where(valid, jnp.cumsum(valid.astype(jnp.int32)) - 1, count)
    empty = jnp.zeros((count,), jnp.int32)
    es = empty.at[position].set(shot_of, mode="drop")
    eb = empty.at[position].set(which_block, mode="drop")
    eq = empty.at[position].set(owner_of, mode="drop")
    n = jnp.sum(valid.astype(jnp.int32)).reshape(1)
    return owners, (es, eb, eq, n)


def gather_sum(gathered, tables):
    owners, (es, eb, eq, n) = tables
    cell_shape = gathered.shape[2:]
    return pl.pallas_call(
        select_kernel,
        grid_spec=pltpu.PrefetchScalarGridSpec(
            num_scalar_prefetch=4,
            grid=(1,),
            in_specs=[pl.BlockSpec(memory_space=pl.ANY)],
            out_specs=[pl.BlockSpec((owners // 2,) + cell_shape, lambda i, *_: (0,) * (1 + len(cell_shape)))] * 2,
            scratch_shapes=[
                pltpu.VMEM((8,) + cell_shape, jnp.float32),
                pltpu.SemaphoreType.DMA((8,)),
            ],
        ),
        out_shape=[jax.ShapeDtypeStruct((owners // 2,) + cell_shape, jnp.float32)] * 2,
    )(es, eb, eq, n, gathered)


def solution(mesh):
    devices = mesh.devices
    shots, bricks = devices.shape
    split = jax.sharding.Mesh(devices.reshape(shots // 4, 2, 2, bricks), ("z", "xl", "core", "brick"))
    shot = ("z", "xl", "core")
    return jax.shard_map(
        per_device,
        mesh=split,
        in_specs=(
            P(shot, None, None, None, "brick", None),
            P(shot, None, "brick", None),
            P(),
            P(),
            P(),
        ),
        out_specs=P("brick", shot, None),
        check_vma=False,
    )
```

```python
import jax
import jax.numpy as jnp
from jax import lax
from jax.experimental import pallas as pl
from jax.experimental.pallas import tpu as pltpu
from jax.sharding import PartitionSpec as P

BLOCKS = 8


shift_beta = 0.5
relaxation = 0.8


def sine_taper(count, extent):
    positions = jnp.arange(count, dtype=jnp.int32).astype(jnp.float32)
    return jnp.sin(jnp.pi * (positions + 0.5) / extent)


def inverse_of(slow):
    real_d = 6.0 - slow
    imag_d = shift_beta * slow
    denominator = real_d * real_d + imag_d * imag_d
    scale = 1.0 / denominator
    return real_d * scale, imag_d * scale


def first_sweep(s0, s1, s2, s3, inv_re, inv_im, mask=None):
    f = (
        relaxation * (s0 * inv_re - s1 * inv_im),
        relaxation * (s0 * inv_im + s1 * inv_re),
        relaxation * (s2 * inv_re - s3 * inv_im),
        relaxation * (s2 * inv_im + s3 * inv_re),
    )
    if mask is None:
        return f
    return tuple(v * mask for v in f)


def gather_plane(rows8, plane, sub_ids):
    tile = jnp.broadcast_to(rows8[0][plane:plane + 1, :], rows8[0].shape)
    for i in range(1, len(rows8)):
        tile = jnp.where(sub_ids == i, jnp.broadcast_to(rows8[i][plane:plane + 1, :], tile.shape), tile)
    return tile


def boundary_kernel(mask_ref, src_hbm, sl_hbm, lo_ref, hi_ref, src_buf, sl_buf, sem):
    four = src_hbm.shape[0]
    planes = src_hbm.shape[2]
    copies = []
    for j, plane in enumerate((planes - 1, 0)):
        for k in range(four):
            copies.append(pltpu.make_async_copy(src_hbm.at[k, :, plane, :], src_buf.at[j, k], sem.at[j, k]))
        copies.append(pltpu.make_async_copy(sl_hbm.at[:, plane, :], sl_buf.at[j], sem.at[j, four]))
    for c in copies:
        c.start()
    for c in copies:
        c.wait()
    for j, (plane, out) in enumerate(((planes - 1, lo_ref), (0, hi_ref))):
        m = mask_ref[plane]
        inv_re, inv_im = inverse_of(sl_buf[j])
        f = first_sweep(src_buf[j, 0], src_buf[j, 1], src_buf[j, 2], src_buf[j, 3], inv_re, inv_im, m)
        for k in range(four):
            out[k] = f[k]


def boundary_planes(src4, slow, mask_col):
    four, wide_y, planes, wide_z = src4.shape
    face = jax.ShapeDtypeStruct((four, wide_y, wide_z), jnp.float32)
    vmem = pl.BlockSpec(memory_space=pltpu.VMEM)
    return pl.pallas_call(
        boundary_kernel,
        in_specs=[
            pl.BlockSpec(memory_space=pltpu.SMEM),
            pl.BlockSpec(memory_space=pl.ANY),
            pl.BlockSpec(memory_space=pl.ANY),
        ],
        out_specs=[vmem, vmem],
        out_shape=[face, face],
        scratch_shapes=[
            pltpu.VMEM((2, four, wide_y, wide_z), jnp.float32),
            pltpu.VMEM((2, wide_y, wide_z), jnp.float32),
            pltpu.SemaphoreType.DMA((2, four + 1)),
        ],
    )(mask_col, src4, slow)


def gradient_kernel(ty_ref, act_ref, src_ref, src_lo_ref, src_hi_ref, sl_ref, sl_lo_ref, sl_hi_ref, mask_ref, tx_ref,
                    tz_ref, out_ref, aux_ref, f1_s, inv_s):
    active = act_ref[0] > 0

    @pl.when(jnp.logical_not(active))
    def _():
        out_ref[...] = jnp.zeros_like(out_ref)
        aux_ref[...] = jnp.zeros_like(aux_ref)

    @pl.when(active)
    def _():
        active_window(ty_ref, src_ref, src_lo_ref, src_hi_ref, sl_ref, sl_lo_ref, sl_hi_ref, mask_ref, tx_ref, tz_ref,
                      out_ref, aux_ref, f1_s, inv_s)


def active_window(ty_ref, src_ref, src_lo_ref, src_hi_ref, sl_ref, sl_lo_ref, sl_hi_ref, mask_ref, tx_ref, tz_ref,
                  out_ref, aux_ref, f1_s, inv_s):
    b = pl.program_id(0)
    nb = pl.num_programs(0)
    rows = src_ref.shape[1]
    mask = None

    def sweep_one(r, carry):
        inv_re, inv_im = inverse_of(sl_ref[r])
        inv_s[0, r] = inv_re
        inv_s[1, r] = inv_im
        f = first_sweep(src_ref[0, r], src_ref[1, r], src_ref[2, r], src_ref[3, r], inv_re, inv_im, mask)
        for k in range(4):
            f1_s[k, r + 1] = f[k]
        return carry

    lax.fori_loop(0, rows, sweep_one, 0, unroll=2)

    lo_keep = jnp.where(b > 0, 1.0, 0.0).astype(jnp.float32)
    hi_keep = jnp.where(b < nb - 1, 1.0, 0.0).astype(jnp.float32)
    for slot, s_ref, l_ref, keep in ((0, src_lo_ref, sl_lo_ref, lo_keep), (rows + 1, src_hi_ref, sl_hi_ref, hi_keep)):
        inv_re, inv_im = inverse_of(l_ref[0])
        f = first_sweep(s_ref[0, 0], s_ref[1, 0], s_ref[2, 0], s_ref[3, 0], inv_re, inv_im, mask)
        for k in range(4):
            f1_s[k, slot] = f[k] * keep

    shape = mask_ref.shape
    p_ids = lax.broadcasted_iota(jnp.int32, shape, 0)
    z_ids = lax.broadcasted_iota(jnp.int32, shape, 1)
    planes, width = shape
    tx = tx_ref[...]
    tz = tz_ref[...]

    def sweep_two(g, carry):
        base = pl.multiple_of(g * 8, 8)
        kept = [[] for _ in range(6)]
        grads = []
        for i in range(8):
            r = base + i
            inv_re = inv_s[0, r]
            inv_im = inv_s[1, r]
            cur = []
            vals = []
            for k in range(4):
                c = f1_s[k, r + 1]
                acc = f1_s[k, r] + f1_s[k, r + 2]
                down = jnp.where(p_ids == 0, 0.0, pltpu.roll(c, 1, 0))
                acc = acc + down
                up = jnp.where(p_ids == planes - 1, 0.0, pltpu.roll(c, planes - 1, 0))
                acc = acc + up
                zm = jnp.where(z_ids == 0, 0.0, pltpu.roll(c, 1, 1))
                acc = acc + zm
                zp = jnp.where(z_ids == width - 1, 0.0, pltpu.roll(c, width - 1, 1))
                acc = acc + zp
                cur.append(c)
                vals.append(src_ref[k, r] + acc)
            upd = (
                vals[0] * inv_re - vals[1] * inv_im,
                vals[0] * inv_im + vals[1] * inv_re,
                vals[2] * inv_re - vals[3] * inv_im,
                vals[2] * inv_im + vals[3] * inv_re,
            )
            f2 = [(1.0 - relaxation) * cur[k] + relaxation * upd[k] for k in range(4)]
            imaging = f2[0] * f2[2] - f2[1] * f2[3] - shift_beta * (f2[0] * f2[3] + f2[1] * f2[2])
            taper = (ty_ref[b * rows + r] * tx) * tz
            grads.append(imaging * taper)
            for k, v in enumerate(f2 + [inv_re, inv_im]):
                kept[k].append(v)
        for k in range(6):
            for j, plane in enumerate((0, planes - 1)):
                aux_ref[k, j, pl.ds(base, 8), :] = gather_plane(kept[k], plane, p_ids)
        for plane in range(1, planes - 1):
            out_ref[0, plane - 1, pl.ds(base, 8), :] = gather_plane(grads, plane, p_ids)
        return carry

    lax.fori_loop(0, rows // 8, sweep_two, 0)


def window_blocks(src4, slow, consts, ty, act):
    four, wide_y, planes, wide_z = src4.shape
    rows = wide_y // BLOCKS
    last = wide_y - 1

    def row_spec(pick):
        return pl.BlockSpec((four, 1, planes, wide_z), lambda b, t, a: (0, pick(b), 0, 0))

    def slow_row_spec(pick):
        return pl.BlockSpec((1, planes, wide_z), lambda b, t, a: (pick(b), 0, 0))

    below = lambda b: jnp.maximum(b * rows - 1, 0)
    above = lambda b: jnp.minimum(b * rows + rows, last)
    grid_spec = pltpu.PrefetchScalarGridSpec(
        num_scalar_prefetch=2,
        grid=(BLOCKS,),
        in_specs=[
            pl.BlockSpec((four, rows, planes, wide_z), lambda b, t, a: (0, b, 0, 0)),
            row_spec(below),
            row_spec(above),
            pl.BlockSpec((rows, planes, wide_z), lambda b, t, a: (b, 0, 0)),
            slow_row_spec(below),
            slow_row_spec(above),
            pl.BlockSpec((None, planes, wide_z), lambda b, t, a: (0, 0, 0)),
            pl.BlockSpec((None, planes, wide_z), lambda b, t, a: (1, 0, 0)),
            pl.BlockSpec((None, planes, wide_z), lambda b, t, a: (2, 0, 0)),
        ],
        out_specs=[
            pl.BlockSpec((1, planes - 2, rows, wide_z), lambda b, t, a: (b, 0, 0, 0)),
            pl.BlockSpec((6, 2, rows, wide_z), lambda b, t, a: (0, 0, b, 0)),
        ],
        scratch_shapes=[
            pltpu.VMEM((four, rows + 2, planes, wide_z), jnp.float32),
            pltpu.VMEM((2, rows, planes, wide_z), jnp.float32),
        ],
    )
    return pl.pallas_call(
        gradient_kernel,
        grid_spec=grid_spec,
        out_shape=[
            jax.ShapeDtypeStruct((BLOCKS, planes - 2, rows, wide_z), jnp.float32),
            jax.ShapeDtypeStruct((6, 2, wide_y, wide_z), jnp.float32),
        ],
    )(ty, act, src4, src4, src4, slow, slow, slow, consts, consts, consts)


def halo_kernel(aux_ref, lo_ref, hi_ref, ty_ref, mask_ref, tx_ref, tz_ref, out_ref):
    rows = aux_ref.shape[2]
    planes = mask_ref.shape[0]
    tz = tz_ref[...]
    for g in range(rows // 8):
        span = pl.ds(g * 8, 8)
        ty = ty_ref[span, :]
        for j, plane, h_ref in ((0, 0, lo_ref), (1, planes - 1, hi_ref)):
            inv_re = aux_ref[4, j, span, :]
            inv_im = aux_ref[5, j, span, :]
            h = [h_ref[k, span, :] for k in range(4)]
            m = mask_ref[plane:plane + 1, :]
            d = (
                h[0] * inv_re - h[1] * inv_im,
                h[0] * inv_im + h[1] * inv_re,
                h[2] * inv_re - h[3] * inv_im,
                h[2] * inv_im + h[3] * inv_re,
            )
            f2 = [aux_ref[k, j, span, :] + relaxation * d[k] * m for k in range(4)]
            imaging = f2[0] * f2[2] - f2[1] * f2[3] - shift_beta * (f2[0] * f2[3] + f2[1] * f2[2])
            per_block = out_ref.shape[2]
            out_ref[(g * 8) // per_block, j, pl.ds((g * 8) % per_block, 8), :] = imaging * ((ty * tx_ref[plane:plane + 1, :]) * tz)


def edge_planes(aux, lo, hi, ty_col, consts):
    wide_y, wide_z = lo.shape[1:]
    rows = wide_y // 2
    four = lo.shape[0]
    planes = consts.shape[1]
    return pl.pallas_call(
        halo_kernel,
        grid=(2,),
        in_specs=[
            pl.BlockSpec((6, 2, rows, wide_z), lambda b: (0, 0, b, 0)),
            pl.BlockSpec((four, rows, wide_z), lambda b: (0, b, 0)),
            pl.BlockSpec((four, rows, wide_z), lambda b: (0, b, 0)),
            pl.BlockSpec((rows, 1), lambda b: (b, 0)),
            pl.BlockSpec((None, planes, wide_z), lambda b: (0, 0, 0)),
            pl.BlockSpec((None, planes, wide_z), lambda b: (1, 0, 0)),
            pl.BlockSpec((None, planes, wide_z), lambda b: (2, 0, 0)),
        ],
        out_specs=pl.BlockSpec((BLOCKS // 2, 2, wide_y // BLOCKS, wide_z), lambda b: (b, 0, 0, 0)),
        out_shape=jax.ShapeDtypeStruct((BLOCKS, 2, wide_y // BLOCKS, wide_z), jnp.float32),
    )(aux, lo, hi, ty_col, consts, consts, consts)


def per_device(sources, slowness, group_size, window_anchor, tile_slot):
    slowness_window = slowness[0]
    wide_y, planes, wide_z = slowness_window.shape
    brick_index = lax.axis_index("brick")
    z_index = lax.axis_index("z")
    x_index = lax.axis_index("xl")
    core_index = lax.axis_index("core")
    x_count = lax.axis_size("xl")
    core_count = lax.axis_size("core")
    shot_index = (z_index * x_count + x_index) * core_count + core_index
    brick_count = lax.axis_size("brick")
    shot_count_all = group_size.shape[0]
    extent = jnp.sum(jnp.where(jnp.arange(shot_count_all) == shot_index, group_size, 0)) * planes
    depth_ids = brick_index * planes + jnp.arange(planes, dtype=jnp.int32)
    active = depth_ids < extent
    mask_col = active.astype(jnp.float32)
    src4 = sources[0].reshape(4, wide_y, planes, wide_z)

    lo_send, hi_send = boundary_planes(src4, slowness_window, mask_col)
    up = [(i, i + 1) for i in range(brick_count - 1)]
    down = [(j, i) for i, j in up]
    lo = lax.ppermute(lo_send, "brick", up)
    hi = lax.ppermute(hi_send, "brick", down)

    extent_float = extent.astype(jnp.float32)
    depth_float = depth_ids.astype(jnp.float32)
    taper_x = jnp.where(active, jnp.sin(jnp.pi * (depth_float + 0.5) / extent_float), 0.0)
    taper_y = sine_taper(wide_y, float(wide_y))
    taper_z = sine_taper(wide_z, float(wide_z))
    consts = jnp.stack([
        jnp.broadcast_to(mask_col[:, None], (planes, wide_z)),
        jnp.broadcast_to(taper_x[:, None], (planes, wide_z)),
        jnp.broadcast_to(taper_z[None, :], (planes, wide_z)),
    ])
    whole_brick = (extent > brick_index * planes).astype(jnp.int32).reshape(1)
    interior, aux = window_blocks(src4, slowness_window, consts, taper_y, whole_brick)
    shot_count = lax.axis_size("z") * x_count * core_count
    tile_dev = tile_slot.shape[0] // shot_count
    partner = (z_index * x_count + (x_count - 1 - x_index)) * core_count + core_index
    slots = jnp.arange(tile_dev, dtype=jnp.int32)
    owners = jnp.concatenate([shot_index * tile_dev + slots, partner * tile_dev + slots])
    zs = jnp.arange(lax.axis_size("z"), dtype=jnp.int32)
    cs = jnp.arange(core_count, dtype=jnp.int32)
    held = ((zs[:, None] * x_count + x_index) * core_count + cs[None, :]).reshape(-1)
    piece_slots = tile_slot[window_anchor[held][:, None] + jnp.arange(BLOCKS, dtype=jnp.int32)[None, :]]
    match = owners[:, None, None] == piece_slots[None, :, :]
    tables = contribution_tables(match)
    swap = [(0, 1), (1, 0)]
    mid = lax.all_gather(interior[None], ("z", "core"), axis=0, tiled=True)
    mid, lo, hi = lax.optimization_barrier((mid, lo, hi))
    own_mid, other_mid = gather_sum(mid, tables)
    theirs_mid = lax.ppermute(other_mid, "xl", swap)
    edges = edge_planes(aux, lo, hi, taper_y[:, None], consts)
    rim = lax.all_gather(edges[None], ("z", "core"), axis=0, tiled=True)
    own_rim, other_rim = gather_sum(rim, tables)
    theirs_rim = lax.ppermute(other_rim, "xl", swap)
    mid_sum = own_mid + theirs_mid
    rim_sum = own_rim + theirs_rim
    summed = jnp.concatenate([rim_sum[:, :1], mid_sum, rim_sum[:, 1:]], axis=1)
    return jnp.transpose(summed, (0, 2, 1, 3)).reshape(1, tile_dev, -1)


def select_kernel(es_ref, eb_ref, eq_ref, n_ref, g_hbm, own_ref, other_ref, buf, sem):
    n = n_ref[0]
    depth = buf.shape[0]
    half = own_ref.shape[0]
    own_ref[...] = jnp.zeros_like(own_ref)
    other_ref[...] = jnp.zeros_like(other_ref)

    def copy(e, slot):
        return pltpu.make_async_copy(g_hbm.at[es_ref[e], eb_ref[e]], buf.at[slot], sem.at[slot])

    for e in range(depth):
        @pl.when(e < n)
        def _():
            copy(e, e).start()

    def body(e, carry):
        slot = e % depth
        copy(e, slot).wait()
        q = eq_ref[e]

        @pl.when(q < half)
        def _():
            mine = jnp.minimum(q, half - 1)
            own_ref[mine] = own_ref[mine] + buf[slot]

        @pl.when(q >= half)
        def _():
            theirs = jnp.maximum(q - half, 0)
            other_ref[theirs] = other_ref[theirs] + buf[slot]

        @pl.when(e + depth < n)
        def _():
            copy(e + depth, slot).start()

        return carry

    lax.fori_loop(0, n, body, 0)


def contribution_tables(match):
    owners, shots, blocks = match.shape
    valid = jnp.any(match, axis=2).reshape(-1)
    which_block = jnp.sum(jnp.where(match, jnp.arange(blocks, dtype=jnp.int32), 0), axis=2).reshape(-1)
    shot_of = jnp.broadcast_to(jnp.arange(shots, dtype=jnp.int32)[None, :], (owners, shots)).reshape(-1)
    owner_of = jnp.broadcast_to(jnp.arange(owners, dtype=jnp.int32)[:, None], (owners, shots)).reshape(-1)
    count = owners * shots
    position = jnp.where(valid, jnp.cumsum(valid.astype(jnp.int32)) - 1, count)
    empty = jnp.zeros((count,), jnp.int32)
    es = empty.at[position].set(shot_of, mode="drop")
    eb = empty.at[position].set(which_block, mode="drop")
    eq = empty.at[position].set(owner_of, mode="drop")
    n = jnp.sum(valid.astype(jnp.int32)).reshape(1)
    return owners, (es, eb, eq, n)


def gather_sum(gathered, tables):
    owners, (es, eb, eq, n) = tables
    cell_shape = gathered.shape[2:]
    return pl.pallas_call(
        select_kernel,
        grid_spec=pltpu.PrefetchScalarGridSpec(
            num_scalar_prefetch=4,
            grid=(1,),
            in_specs=[pl.BlockSpec(memory_space=pl.ANY)],
            out_specs=[pl.BlockSpec((owners // 2,) + cell_shape, lambda i, *_: (0,) * (1 + len(cell_shape)))] * 2,
            scratch_shapes=[
                pltpu.VMEM((8,) + cell_shape, jnp.float32),
                pltpu.SemaphoreType.DMA((8,)),
            ],
        ),
        out_shape=[jax.ShapeDtypeStruct((owners // 2,) + cell_shape, jnp.float32)] * 2,
    )(es, eb, eq, n, gathered)


def solution(mesh):
    devices = mesh.devices
    shots, bricks = devices.shape
    split = jax.sharding.Mesh(devices.reshape(shots // 4, 2, 2, bricks), ("z", "xl", "core", "brick"))
    shot = ("z", "xl", "core")
    return jax.shard_map(
        per_device,
        mesh=split,
        in_specs=(
            P(shot, None, None, None, "brick", None),
            P(shot, None, "brick", None),
            P(),
            P(),
            P(),
        ),
        out_specs=P("brick", shot, None),
        check_vma=False,
    )
```

```python
import jax
import jax.numpy as jnp
from jax import lax
from jax.experimental import pallas as pl
from jax.experimental.pallas import tpu as pltpu
from jax.sharding import PartitionSpec as P

BLOCKS = 8


shift_beta = 0.5
relaxation = 0.8


def sine_taper(count, extent):
    positions = jnp.arange(count, dtype=jnp.int32).astype(jnp.float32)
    return jnp.sin(jnp.pi * (positions + 0.5) / extent)


def inverse_of(slow):
    real_d = 6.0 - slow
    imag_d = shift_beta * slow
    denominator = real_d * real_d + imag_d * imag_d
    scale = 1.0 / denominator
    return real_d * scale, imag_d * scale


def first_sweep(s0, s1, s2, s3, inv_re, inv_im, mask=None):
    f = (
        relaxation * (s0 * inv_re - s1 * inv_im),
        relaxation * (s0 * inv_im + s1 * inv_re),
        relaxation * (s2 * inv_re - s3 * inv_im),
        relaxation * (s2 * inv_im + s3 * inv_re),
    )
    if mask is None:
        return f
    return tuple(v * mask for v in f)


def gather_plane(rows8, plane, sub_ids):
    tile = jnp.broadcast_to(rows8[0][plane:plane + 1, :], rows8[0].shape)
    for i in range(1, len(rows8)):
        tile = jnp.where(sub_ids == i, jnp.broadcast_to(rows8[i][plane:plane + 1, :], tile.shape), tile)
    return tile


def boundary_kernel(mask_ref, src_hbm, sl_hbm, lo_ref, hi_ref, src_buf, sl_buf, sem):
    four = src_hbm.shape[0]
    planes = src_hbm.shape[2]
    copies = []
    for j, plane in enumerate((planes - 1, 0)):
        for k in range(four):
            copies.append(pltpu.make_async_copy(src_hbm.at[k, :, plane, :], src_buf.at[j, k], sem.at[j, k]))
        copies.append(pltpu.make_async_copy(sl_hbm.at[:, plane, :], sl_buf.at[j], sem.at[j, four]))
    for c in copies:
        c.start()
    for c in copies:
        c.wait()
    for j, (plane, out) in enumerate(((planes - 1, lo_ref), (0, hi_ref))):
        m = mask_ref[plane]
        inv_re, inv_im = inverse_of(sl_buf[j])
        f = first_sweep(src_buf[j, 0], src_buf[j, 1], src_buf[j, 2], src_buf[j, 3], inv_re, inv_im, m)
        for k in range(four):
            out[k] = f[k]


def boundary_planes(src4, slow, mask_col):
    four, wide_y, planes, wide_z = src4.shape
    face = jax.ShapeDtypeStruct((four, wide_y, wide_z), jnp.float32)
    vmem = pl.BlockSpec(memory_space=pltpu.VMEM)
    return pl.pallas_call(
        boundary_kernel,
        in_specs=[
            pl.BlockSpec(memory_space=pltpu.SMEM),
            pl.BlockSpec(memory_space=pl.ANY),
            pl.BlockSpec(memory_space=pl.ANY),
        ],
        out_specs=[vmem, vmem],
        out_shape=[face, face],
        scratch_shapes=[
            pltpu.VMEM((2, four, wide_y, wide_z), jnp.float32),
            pltpu.VMEM((2, wide_y, wide_z), jnp.float32),
            pltpu.SemaphoreType.DMA((2, four + 1)),
        ],
    )(mask_col, src4, slow)


def gradient_kernel(ty_ref, act_ref, src_ref, src_lo_ref, src_hi_ref, sl_ref, sl_lo_ref, sl_hi_ref, mask_ref, tx_ref,
                    tz_ref, out_ref, aux_ref, f1_s, inv_s, tp_s):
    active = act_ref[0] > 0

    @pl.when(jnp.logical_not(active))
    def _():
        out_ref[...] = jnp.zeros_like(out_ref)
        aux_ref[...] = jnp.zeros_like(aux_ref)

    @pl.when(active)
    def _():
        active_window(ty_ref, src_ref, src_lo_ref, src_hi_ref, sl_ref, sl_lo_ref, sl_hi_ref, mask_ref, tx_ref, tz_ref,
                      out_ref, aux_ref, f1_s, inv_s, tp_s)


def active_window(ty_ref, src_ref, src_lo_ref, src_hi_ref, sl_ref, sl_lo_ref, sl_hi_ref, mask_ref, tx_ref, tz_ref,
                  out_ref, aux_ref, f1_s, inv_s, tp_s):
    b = pl.program_id(0)
    nb = pl.num_programs(0)
    rows = src_ref.shape[1]
    mask = None

    def sweep_one(r, carry):
        inv_re, inv_im = inverse_of(sl_ref[r])
        inv_s[0, r] = inv_re
        inv_s[1, r] = inv_im
        f = first_sweep(src_ref[0, r], src_ref[1, r], src_ref[2, r], src_ref[3, r], inv_re, inv_im, mask)
        for k in range(4):
            f1_s[k, r + 1] = f[k]
        return carry

    lax.fori_loop(0, rows, sweep_one, 0, unroll=2)

    lo_keep = jnp.where(b > 0, 1.0, 0.0).astype(jnp.float32)
    hi_keep = jnp.where(b < nb - 1, 1.0, 0.0).astype(jnp.float32)
    for slot, s_ref, l_ref, keep in ((0, src_lo_ref, sl_lo_ref, lo_keep), (rows + 1, src_hi_ref, sl_hi_ref, hi_keep)):
        inv_re, inv_im = inverse_of(l_ref[0])
        f = first_sweep(s_ref[0, 0], s_ref[1, 0], s_ref[2, 0], s_ref[3, 0], inv_re, inv_im, mask)
        for k in range(4):
            f1_s[k, slot] = f[k] * keep

    shape = mask_ref.shape
    p_ids = lax.broadcasted_iota(jnp.int32, shape, 0)
    z_ids = lax.broadcasted_iota(jnp.int32, shape, 1)
    planes, width = shape
    tx = tx_ref[...]
    tz = tz_ref[...]

    def sweep_two(g, carry):
        base = pl.multiple_of(g * 8, 8)
        for i in range(8):
            r = base + i
            inv_re = inv_s[0, r]
            inv_im = inv_s[1, r]
            cur = []
            vals = []
            for k in range(4):
                c = f1_s[k, r + 1]
                acc = f1_s[k, r] + f1_s[k, r + 2]
                down = jnp.where(p_ids == 0, 0.0, pltpu.roll(c, 1, 0))
                acc = acc + down
                up = jnp.where(p_ids == planes - 1, 0.0, pltpu.roll(c, planes - 1, 0))
                acc = acc + up
                zm = jnp.where(z_ids == 0, 0.0, pltpu.roll(c, 1, 1))
                acc = acc + zm
                zp = jnp.where(z_ids == width - 1, 0.0, pltpu.roll(c, width - 1, 1))
                acc = acc + zp
                cur.append(c)
                vals.append(src_ref[k, r] + acc)
            upd = (
                vals[0] * inv_re - vals[1] * inv_im,
                vals[0] * inv_im + vals[1] * inv_re,
                vals[2] * inv_re - vals[3] * inv_im,
                vals[2] * inv_im + vals[3] * inv_re,
            )
            f2 = [(1.0 - relaxation) * cur[k] + relaxation * upd[k] for k in range(4)]
            imaging = f2[0] * f2[2] - f2[1] * f2[3] - shift_beta * (f2[0] * f2[3] + f2[1] * f2[2])
            taper = (ty_ref[b * rows + r] * tx) * tz
            for k, v in enumerate(f2 + [inv_re, inv_im, imaging * taper]):
                for h in range(2):
                    tp_s[k, h, i * planes:(i + 1) * planes, :] = v[:, h * 128:(h + 1) * 128]

        def plane_tile(k, plane):
            halves = [tp_s[k, h, pl.ds(plane, 8, stride=planes), :] for h in range(2)]
            return jnp.concatenate(halves, axis=1)

        for k in range(6):
            for j, plane in enumerate((0, planes - 1)):
                aux_ref[k, j, pl.ds(base, 8), :] = plane_tile(k, plane)
        for plane in range(1, planes - 1):
            out_ref[0, plane - 1, pl.ds(base, 8), :] = plane_tile(6, plane)
        return carry

    lax.fori_loop(0, rows // 8, sweep_two, 0)


def window_blocks(src4, slow, consts, ty, act):
    four, wide_y, planes, wide_z = src4.shape
    rows = wide_y // BLOCKS
    last = wide_y - 1

    def row_spec(pick):
        return pl.BlockSpec((four, 1, planes, wide_z), lambda b, t, a: (0, pick(b), 0, 0))

    def slow_row_spec(pick):
        return pl.BlockSpec((1, planes, wide_z), lambda b, t, a: (pick(b), 0, 0))

    below = lambda b: jnp.maximum(b * rows - 1, 0)
    above = lambda b: jnp.minimum(b * rows + rows, last)
    grid_spec = pltpu.PrefetchScalarGridSpec(
        num_scalar_prefetch=2,
        grid=(BLOCKS,),
        in_specs=[
            pl.BlockSpec((four, rows, planes, wide_z), lambda b, t, a: (0, b, 0, 0)),
            row_spec(below),
            row_spec(above),
            pl.BlockSpec((rows, planes, wide_z), lambda b, t, a: (b, 0, 0)),
            slow_row_spec(below),
            slow_row_spec(above),
            pl.BlockSpec((None, planes, wide_z), lambda b, t, a: (0, 0, 0)),
            pl.BlockSpec((None, planes, wide_z), lambda b, t, a: (1, 0, 0)),
            pl.BlockSpec((None, planes, wide_z), lambda b, t, a: (2, 0, 0)),
        ],
        out_specs=[
            pl.BlockSpec((1, planes - 2, rows, wide_z), lambda b, t, a: (b, 0, 0, 0)),
            pl.BlockSpec((6, 2, rows, wide_z), lambda b, t, a: (0, 0, b, 0)),
        ],
        scratch_shapes=[
            pltpu.VMEM((four, rows + 2, planes, wide_z), jnp.float32),
            pltpu.VMEM((2, rows, planes, wide_z), jnp.float32),
            pltpu.VMEM((7, 2, 8 * planes, wide_z // 2), jnp.float32),
        ],
    )
    return pl.pallas_call(
        gradient_kernel,
        grid_spec=grid_spec,
        out_shape=[
            jax.ShapeDtypeStruct((BLOCKS, planes - 2, rows, wide_z), jnp.float32),
            jax.ShapeDtypeStruct((6, 2, wide_y, wide_z), jnp.float32),
        ],
    )(ty, act, src4, src4, src4, slow, slow, slow, consts, consts, consts)


def halo_kernel(aux_ref, lo_ref, hi_ref, ty_ref, mask_ref, tx_ref, tz_ref, out_ref):
    rows = aux_ref.shape[2]
    planes = mask_ref.shape[0]
    tz = tz_ref[...]
    for g in range(rows // 8):
        span = pl.ds(g * 8, 8)
        ty = ty_ref[span, :]
        for j, plane, h_ref in ((0, 0, lo_ref), (1, planes - 1, hi_ref)):
            inv_re = aux_ref[4, j, span, :]
            inv_im = aux_ref[5, j, span, :]
            h = [h_ref[k, span, :] for k in range(4)]
            m = mask_ref[plane:plane + 1, :]
            d = (
                h[0] * inv_re - h[1] * inv_im,
                h[0] * inv_im + h[1] * inv_re,
                h[2] * inv_re - h[3] * inv_im,
                h[2] * inv_im + h[3] * inv_re,
            )
            f2 = [aux_ref[k, j, span, :] + relaxation * d[k] * m for k in range(4)]
            imaging = f2[0] * f2[2] - f2[1] * f2[3] - shift_beta * (f2[0] * f2[3] + f2[1] * f2[2])
            per_block = out_ref.shape[2]
            out_ref[(g * 8) // per_block, j, pl.ds((g * 8) % per_block, 8), :] = imaging * ((ty * tx_ref[plane:plane + 1, :]) * tz)


def edge_planes(aux, lo, hi, ty_col, consts):
    wide_y, wide_z = lo.shape[1:]
    rows = wide_y // 2
    four = lo.shape[0]
    planes = consts.shape[1]
    return pl.pallas_call(
        halo_kernel,
        grid=(2,),
        in_specs=[
            pl.BlockSpec((6, 2, rows, wide_z), lambda b: (0, 0, b, 0)),
            pl.BlockSpec((four, rows, wide_z), lambda b: (0, b, 0)),
            pl.BlockSpec((four, rows, wide_z), lambda b: (0, b, 0)),
            pl.BlockSpec((rows, 1), lambda b: (b, 0)),
            pl.BlockSpec((None, planes, wide_z), lambda b: (0, 0, 0)),
            pl.BlockSpec((None, planes, wide_z), lambda b: (1, 0, 0)),
            pl.BlockSpec((None, planes, wide_z), lambda b: (2, 0, 0)),
        ],
        out_specs=pl.BlockSpec((BLOCKS // 2, 2, wide_y // BLOCKS, wide_z), lambda b: (b, 0, 0, 0)),
        out_shape=jax.ShapeDtypeStruct((BLOCKS, 2, wide_y // BLOCKS, wide_z), jnp.float32),
    )(aux, lo, hi, ty_col, consts, consts, consts)


def per_device(sources, slowness, group_size, window_anchor, tile_slot):
    slowness_window = slowness[0]
    wide_y, planes, wide_z = slowness_window.shape
    brick_index = lax.axis_index("brick")
    z_index = lax.axis_index("z")
    x_index = lax.axis_index("xl")
    core_index = lax.axis_index("core")
    x_count = lax.axis_size("xl")
    core_count = lax.axis_size("core")
    shot_index = (z_index * x_count + x_index) * core_count + core_index
    brick_count = lax.axis_size("brick")
    shot_count_all = group_size.shape[0]
    extent = jnp.sum(jnp.where(jnp.arange(shot_count_all) == shot_index, group_size, 0)) * planes
    depth_ids = brick_index * planes + jnp.arange(planes, dtype=jnp.int32)
    active = depth_ids < extent
    mask_col = active.astype(jnp.float32)
    src4 = sources[0].reshape(4, wide_y, planes, wide_z)

    lo_send, hi_send = boundary_planes(src4, slowness_window, mask_col)
    up = [(i, i + 1) for i in range(brick_count - 1)]
    down = [(j, i) for i, j in up]
    lo = lax.ppermute(lo_send, "brick", up)
    hi = lax.ppermute(hi_send, "brick", down)

    extent_float = extent.astype(jnp.float32)
    depth_float = depth_ids.astype(jnp.float32)
    taper_x = jnp.where(active, jnp.sin(jnp.pi * (depth_float + 0.5) / extent_float), 0.0)
    taper_y = sine_taper(wide_y, float(wide_y))
    taper_z = sine_taper(wide_z, float(wide_z))
    consts = jnp.stack([
        jnp.broadcast_to(mask_col[:, None], (planes, wide_z)),
        jnp.broadcast_to(taper_x[:, None], (planes, wide_z)),
        jnp.broadcast_to(taper_z[None, :], (planes, wide_z)),
    ])
    whole_brick = (extent > brick_index * planes).astype(jnp.int32).reshape(1)
    interior, aux = window_blocks(src4, slowness_window, consts, taper_y, whole_brick)
    shot_count = lax.axis_size("z") * x_count * core_count
    tile_dev = tile_slot.shape[0] // shot_count
    partner = (z_index * x_count + (x_count - 1 - x_index)) * core_count + core_index
    slots = jnp.arange(tile_dev, dtype=jnp.int32)
    owners = jnp.concatenate([shot_index * tile_dev + slots, partner * tile_dev + slots])
    zs = jnp.arange(lax.axis_size("z"), dtype=jnp.int32)
    cs = jnp.arange(core_count, dtype=jnp.int32)
    held = ((zs[:, None] * x_count + x_index) * core_count + cs[None, :]).reshape(-1)
    piece_slots = tile_slot[window_anchor[held][:, None] + jnp.arange(BLOCKS, dtype=jnp.int32)[None, :]]
    match = owners[:, None, None] == piece_slots[None, :, :]
    tables = contribution_tables(match)
    swap = [(0, 1), (1, 0)]
    mid = lax.all_gather(interior[None], ("z", "core"), axis=0, tiled=True)
    mid, lo, hi = lax.optimization_barrier((mid, lo, hi))
    own_mid, other_mid = gather_sum(mid, tables)
    theirs_mid = lax.ppermute(other_mid, "xl", swap)
    edges = edge_planes(aux, lo, hi, taper_y[:, None], consts)
    rim = lax.all_gather(edges[None], ("z", "core"), axis=0, tiled=True)
    own_rim, other_rim = gather_sum(rim, tables)
    theirs_rim = lax.ppermute(other_rim, "xl", swap)
    mid_sum = own_mid + theirs_mid
    rim_sum = own_rim + theirs_rim
    summed = jnp.concatenate([rim_sum[:, :1], mid_sum, rim_sum[:, 1:]], axis=1)
    return jnp.transpose(summed, (0, 2, 1, 3)).reshape(1, tile_dev, -1)


def select_kernel(es_ref, eb_ref, eq_ref, n_ref, g_hbm, own_ref, other_ref, buf, sem):
    n = n_ref[0]
    depth = buf.shape[0]
    half = own_ref.shape[0]
    own_ref[...] = jnp.zeros_like(own_ref)
    other_ref[...] = jnp.zeros_like(other_ref)

    def copy(e, slot):
        return pltpu.make_async_copy(g_hbm.at[es_ref[e], eb_ref[e]], buf.at[slot], sem.at[slot])

    for e in range(depth):
        @pl.when(e < n)
        def _():
            copy(e, e).start()

    def body(e, carry):
        slot = e % depth
        copy(e, slot).wait()
        q = eq_ref[e]

        @pl.when(q < half)
        def _():
            mine = jnp.minimum(q, half - 1)
            own_ref[mine] = own_ref[mine] + buf[slot]

        @pl.when(q >= half)
        def _():
            theirs = jnp.maximum(q - half, 0)
            other_ref[theirs] = other_ref[theirs] + buf[slot]

        @pl.when(e + depth < n)
        def _():
            copy(e + depth, slot).start()

        return carry

    lax.fori_loop(0, n, body, 0)


def contribution_tables(match):
    owners, shots, blocks = match.shape
    valid = jnp.any(match, axis=2).reshape(-1)
    which_block = jnp.sum(jnp.where(match, jnp.arange(blocks, dtype=jnp.int32), 0), axis=2).reshape(-1)
    shot_of = jnp.broadcast_to(jnp.arange(shots, dtype=jnp.int32)[None, :], (owners, shots)).reshape(-1)
    owner_of = jnp.broadcast_to(jnp.arange(owners, dtype=jnp.int32)[:, None], (owners, shots)).reshape(-1)
    count = owners * shots
    position = jnp.where(valid, jnp.cumsum(valid.astype(jnp.int32)) - 1, count)
    empty = jnp.zeros((count,), jnp.int32)
    es = empty.at[position].set(shot_of, mode="drop")
    eb = empty.at[position].set(which_block, mode="drop")
    eq = empty.at[position].set(owner_of, mode="drop")
    n = jnp.sum(valid.astype(jnp.int32)).reshape(1)
    return owners, (es, eb, eq, n)


def gather_sum(gathered, tables):
    owners, (es, eb, eq, n) = tables
    cell_shape = gathered.shape[2:]
    return pl.pallas_call(
        select_kernel,
        grid_spec=pltpu.PrefetchScalarGridSpec(
            num_scalar_prefetch=4,
            grid=(1,),
            in_specs=[pl.BlockSpec(memory_space=pl.ANY)],
            out_specs=[pl.BlockSpec((owners // 2,) + cell_shape, lambda i, *_: (0,) * (1 + len(cell_shape)))] * 2,
            scratch_shapes=[
                pltpu.VMEM((8,) + cell_shape, jnp.float32),
                pltpu.SemaphoreType.DMA((8,)),
            ],
        ),
        out_shape=[jax.ShapeDtypeStruct((owners // 2,) + cell_shape, jnp.float32)] * 2,
    )(es, eb, eq, n, gathered)


def solution(mesh):
    devices = mesh.devices
    shots, bricks = devices.shape
    split = jax.sharding.Mesh(devices.reshape(shots // 4, 2, 2, bricks), ("z", "xl", "core", "brick"))
    shot = ("z", "xl", "core")
    return jax.shard_map(
        per_device,
        mesh=split,
        in_specs=(
            P(shot, None, None, None, "brick", None),
            P(shot, None, "brick", None),
            P(),
            P(),
            P(),
        ),
        out_specs=P("brick", shot, None),
        check_vma=False,
    )
```

```python
import jax
import jax.numpy as jnp
from jax import lax
from jax.experimental import pallas as pl
from jax.experimental.pallas import tpu as pltpu
from jax.sharding import PartitionSpec as P

BLOCKS = 8


shift_beta = 0.5
relaxation = 0.8


def sine_taper(count, extent):
    positions = jnp.arange(count, dtype=jnp.int32).astype(jnp.float32)
    return jnp.sin(jnp.pi * (positions + 0.5) / extent)


def inverse_of(slow):
    real_d = 6.0 - slow
    imag_d = shift_beta * slow
    denominator = real_d * real_d + imag_d * imag_d
    scale = 1.0 / denominator
    return real_d * scale, imag_d * scale


def first_sweep(s0, s1, s2, s3, inv_re, inv_im, mask=None):
    f = (
        relaxation * (s0 * inv_re - s1 * inv_im),
        relaxation * (s0 * inv_im + s1 * inv_re),
        relaxation * (s2 * inv_re - s3 * inv_im),
        relaxation * (s2 * inv_im + s3 * inv_re),
    )
    if mask is None:
        return f
    return tuple(v * mask for v in f)


def gather_plane(rows8, plane, sub_ids):
    tile = jnp.broadcast_to(rows8[0][plane:plane + 1, :], rows8[0].shape)
    for i in range(1, len(rows8)):
        tile = jnp.where(sub_ids == i, jnp.broadcast_to(rows8[i][plane:plane + 1, :], tile.shape), tile)
    return tile


def boundary_kernel(mask_ref, src_hbm, sl_hbm, lo_ref, hi_ref, src_buf, sl_buf, sem):
    four = src_hbm.shape[0]
    planes = src_hbm.shape[2]
    copies = []
    for j, plane in enumerate((planes - 1, 0)):
        for k in range(four):
            copies.append(pltpu.make_async_copy(src_hbm.at[k, :, plane, :], src_buf.at[j, k], sem.at[j, k]))
        copies.append(pltpu.make_async_copy(sl_hbm.at[:, plane, :], sl_buf.at[j], sem.at[j, four]))
    for c in copies:
        c.start()
    for c in copies:
        c.wait()
    for j, (plane, out) in enumerate(((planes - 1, lo_ref), (0, hi_ref))):
        m = mask_ref[plane]
        inv_re, inv_im = inverse_of(sl_buf[j])
        f = first_sweep(src_buf[j, 0], src_buf[j, 1], src_buf[j, 2], src_buf[j, 3], inv_re, inv_im, m)
        for k in range(four):
            out[k] = f[k]


def boundary_planes(src4, slow, mask_col):
    four, wide_y, planes, wide_z = src4.shape
    face = jax.ShapeDtypeStruct((four, wide_y, wide_z), jnp.float32)
    vmem = pl.BlockSpec(memory_space=pltpu.VMEM)
    return pl.pallas_call(
        boundary_kernel,
        in_specs=[
            pl.BlockSpec(memory_space=pltpu.SMEM),
            pl.BlockSpec(memory_space=pl.ANY),
            pl.BlockSpec(memory_space=pl.ANY),
        ],
        out_specs=[vmem, vmem],
        out_shape=[face, face],
        scratch_shapes=[
            pltpu.VMEM((2, four, wide_y, wide_z), jnp.float32),
            pltpu.VMEM((2, wide_y, wide_z), jnp.float32),
            pltpu.SemaphoreType.DMA((2, four + 1)),
        ],
    )(mask_col, src4, slow)


def gradient_kernel(ty_ref, act_ref, src_ref, src_lo_ref, src_hi_ref, sl_ref, sl_lo_ref, sl_hi_ref, mask_ref, tx_ref,
                    tz_ref, out_ref, aux_ref, f1_s, inv_s, tp_s):
    active = act_ref[0] > 0

    @pl.when(jnp.logical_not(active))
    def _():
        out_ref[...] = jnp.zeros_like(out_ref)
        aux_ref[...] = jnp.zeros_like(aux_ref)

    @pl.when(active)
    def _():
        active_window(ty_ref, src_ref, src_lo_ref, src_hi_ref, sl_ref, sl_lo_ref, sl_hi_ref, mask_ref, tx_ref, tz_ref,
                      out_ref, aux_ref, f1_s, inv_s, tp_s)


def active_window(ty_ref, src_ref, src_lo_ref, src_hi_ref, sl_ref, sl_lo_ref, sl_hi_ref, mask_ref, tx_ref, tz_ref,
                  out_ref, aux_ref, f1_s, inv_s, tp_s):
    b = pl.program_id(0)
    nb = pl.num_programs(0)
    rows = src_ref.shape[1]
    mask = None

    def sweep_one(r, carry):
        inv_re, inv_im = inverse_of(sl_ref[r])
        inv_s[0, r] = inv_re
        inv_s[1, r] = inv_im
        f = first_sweep(src_ref[0, r], src_ref[1, r], src_ref[2, r], src_ref[3, r], inv_re, inv_im, mask)
        for k in range(4):
            f1_s[k, r + 1] = f[k]
        return carry

    lax.fori_loop(0, rows, sweep_one, 0, unroll=2)

    lo_keep = jnp.where(b > 0, 1.0, 0.0).astype(jnp.float32)
    hi_keep = jnp.where(b < nb - 1, 1.0, 0.0).astype(jnp.float32)
    for slot, s_ref, l_ref, keep in ((0, src_lo_ref, sl_lo_ref, lo_keep), (rows + 1, src_hi_ref, sl_hi_ref, hi_keep)):
        inv_re, inv_im = inverse_of(l_ref[0])
        f = first_sweep(s_ref[0, 0], s_ref[1, 0], s_ref[2, 0], s_ref[3, 0], inv_re, inv_im, mask)
        for k in range(4):
            f1_s[k, slot] = f[k] * keep

    shape = mask_ref.shape
    p_ids = lax.broadcasted_iota(jnp.int32, shape, 0)
    z_ids = lax.broadcasted_iota(jnp.int32, shape, 1)
    planes, width = shape
    tx = tx_ref[...]
    tz = tz_ref[...]

    def sweep_two(g, carry):
        base = pl.multiple_of(g * 8, 8)
        for i in range(8):
            r = base + i
            inv_re = inv_s[0, r]
            inv_im = inv_s[1, r]
            cur = []
            vals = []
            for k in range(4):
                c = f1_s[k, r + 1]
                acc = f1_s[k, r] + f1_s[k, r + 2]
                down = jnp.where(p_ids == 0, 0.0, pltpu.roll(c, 1, 0))
                acc = acc + down
                up = jnp.where(p_ids == planes - 1, 0.0, pltpu.roll(c, planes - 1, 0))
                acc = acc + up
                zm = jnp.where(z_ids == 0, 0.0, pltpu.roll(c, 1, 1))
                acc = acc + zm
                zp = jnp.where(z_ids == width - 1, 0.0, pltpu.roll(c, width - 1, 1))
                acc = acc + zp
                cur.append(c)
                vals.append(src_ref[k, r] + acc)
            upd = (
                vals[0] * inv_re - vals[1] * inv_im,
                vals[0] * inv_im + vals[1] * inv_re,
                vals[2] * inv_re - vals[3] * inv_im,
                vals[2] * inv_im + vals[3] * inv_re,
            )
            f2 = [(1.0 - relaxation) * cur[k] + relaxation * upd[k] for k in range(4)]
            imaging = f2[0] * f2[2] - f2[1] * f2[3] - shift_beta * (f2[0] * f2[3] + f2[1] * f2[2])
            taper = (ty_ref[b * rows + r] * tx) * tz
            for k, v in enumerate(f2 + [inv_re, inv_im, imaging * taper]):
                for h in range(2):
                    tp_s[k, h, i * planes:(i + 1) * planes, :] = v[:, h * 128:(h + 1) * 128]

        def plane_tile(k, plane):
            halves = [tp_s[k, h, pl.ds(plane, 8, stride=planes), :] for h in range(2)]
            return jnp.concatenate(halves, axis=1)

        for k in range(6):
            for j, plane in enumerate((0, planes - 1)):
                aux_ref[k, j, pl.ds(base, 8), :] = plane_tile(k, plane)
        for plane in range(1, planes - 1):
            out_ref[0, plane - 1, pl.ds(base, 8), :] = plane_tile(6, plane)
        return carry

    lax.fori_loop(0, rows // 8, sweep_two, 0)


def window_blocks(src4, slow, consts, ty, act):
    four, wide_y, planes, wide_z = src4.shape
    rows = wide_y // BLOCKS
    last = wide_y - 1

    def row_spec(pick):
        return pl.BlockSpec((four, 1, planes, wide_z), lambda b, t, a: (0, pick(b), 0, 0))

    def slow_row_spec(pick):
        return pl.BlockSpec((1, planes, wide_z), lambda b, t, a: (pick(b), 0, 0))

    below = lambda b: jnp.maximum(b * rows - 1, 0)
    above = lambda b: jnp.minimum(b * rows + rows, last)
    grid_spec = pltpu.PrefetchScalarGridSpec(
        num_scalar_prefetch=2,
        grid=(BLOCKS,),
        in_specs=[
            pl.BlockSpec((four, rows, planes, wide_z), lambda b, t, a: (0, b, 0, 0)),
            row_spec(below),
            row_spec(above),
            pl.BlockSpec((rows, planes, wide_z), lambda b, t, a: (b, 0, 0)),
            slow_row_spec(below),
            slow_row_spec(above),
            pl.BlockSpec((None, planes, wide_z), lambda b, t, a: (0, 0, 0)),
            pl.BlockSpec((None, planes, wide_z), lambda b, t, a: (1, 0, 0)),
            pl.BlockSpec((None, planes, wide_z), lambda b, t, a: (2, 0, 0)),
        ],
        out_specs=[
            pl.BlockSpec((1, planes - 2, rows, wide_z), lambda b, t, a: (b, 0, 0, 0)),
            pl.BlockSpec((6, 2, rows, wide_z), lambda b, t, a: (0, 0, b, 0)),
        ],
        scratch_shapes=[
            pltpu.VMEM((four, rows + 2, planes, wide_z), jnp.float32),
            pltpu.VMEM((2, rows, planes, wide_z), jnp.float32),
            pltpu.VMEM((7, 2, 8 * planes, wide_z // 2), jnp.float32),
        ],
    )
    return pl.pallas_call(
        gradient_kernel,
        grid_spec=grid_spec,
        out_shape=[
            jax.ShapeDtypeStruct((BLOCKS, planes - 2, rows, wide_z), jnp.float32),
            jax.ShapeDtypeStruct((6, 2, wide_y, wide_z), jnp.float32),
        ],
    )(ty, act, src4, src4, src4, slow, slow, slow, consts, consts, consts)


def halo_kernel(aux_ref, lo_ref, hi_ref, ty_ref, mask_ref, tx_ref, tz_ref, out_ref):
    rows = aux_ref.shape[2]
    planes = mask_ref.shape[0]
    tz = tz_ref[...]
    for g in range(rows // 8):
        span = pl.ds(g * 8, 8)
        ty = ty_ref[span, :]
        for j, plane, h_ref in ((0, 0, lo_ref), (1, planes - 1, hi_ref)):
            inv_re = aux_ref[4, j, span, :]
            inv_im = aux_ref[5, j, span, :]
            h = [h_ref[k, span, :] for k in range(4)]
            m = mask_ref[plane:plane + 1, :]
            d = (
                h[0] * inv_re - h[1] * inv_im,
                h[0] * inv_im + h[1] * inv_re,
                h[2] * inv_re - h[3] * inv_im,
                h[2] * inv_im + h[3] * inv_re,
            )
            f2 = [aux_ref[k, j, span, :] + relaxation * d[k] * m for k in range(4)]
            imaging = f2[0] * f2[2] - f2[1] * f2[3] - shift_beta * (f2[0] * f2[3] + f2[1] * f2[2])
            per_block = out_ref.shape[2]
            out_ref[(g * 8) // per_block, j, pl.ds((g * 8) % per_block, 8), :] = imaging * ((ty * tx_ref[plane:plane + 1, :]) * tz)


def edge_planes(aux, lo, hi, ty_col, consts):
    wide_y, wide_z = lo.shape[1:]
    rows = wide_y
    four = lo.shape[0]
    planes = consts.shape[1]
    return pl.pallas_call(
        halo_kernel,
        grid=(1,),
        in_specs=[
            pl.BlockSpec((6, 2, rows, wide_z), lambda b: (0, 0, b, 0)),
            pl.BlockSpec((four, rows, wide_z), lambda b: (0, b, 0)),
            pl.BlockSpec((four, rows, wide_z), lambda b: (0, b, 0)),
            pl.BlockSpec((rows, 1), lambda b: (b, 0)),
            pl.BlockSpec((None, planes, wide_z), lambda b: (0, 0, 0)),
            pl.BlockSpec((None, planes, wide_z), lambda b: (1, 0, 0)),
            pl.BlockSpec((None, planes, wide_z), lambda b: (2, 0, 0)),
        ],
        out_specs=pl.BlockSpec((BLOCKS, 2, wide_y // BLOCKS, wide_z), lambda b: (b, 0, 0, 0)),
        out_shape=jax.ShapeDtypeStruct((BLOCKS, 2, wide_y // BLOCKS, wide_z), jnp.float32),
    )(aux, lo, hi, ty_col, consts, consts, consts)


def per_device(sources, slowness, group_size, window_anchor, tile_slot):
    slowness_window = slowness[0]
    wide_y, planes, wide_z = slowness_window.shape
    brick_index = lax.axis_index("brick")
    z_index = lax.axis_index("z")
    x_index = lax.axis_index("xl")
    core_index = lax.axis_index("core")
    x_count = lax.axis_size("xl")
    core_count = lax.axis_size("core")
    shot_index = (z_index * x_count + x_index) * core_count + core_index
    brick_count = lax.axis_size("brick")
    shot_count_all = group_size.shape[0]
    extent = jnp.sum(jnp.where(jnp.arange(shot_count_all) == shot_index, group_size, 0)) * planes
    depth_ids = brick_index * planes + jnp.arange(planes, dtype=jnp.int32)
    active = depth_ids < extent
    mask_col = active.astype(jnp.float32)
    src4 = sources[0].reshape(4, wide_y, planes, wide_z)

    lo_send, hi_send = boundary_planes(src4, slowness_window, mask_col)
    up = [(i, i + 1) for i in range(brick_count - 1)]
    down = [(j, i) for i, j in up]
    lo = lax.ppermute(lo_send, "brick", up)
    hi = lax.ppermute(hi_send, "brick", down)

    extent_float = extent.astype(jnp.float32)
    depth_float = depth_ids.astype(jnp.float32)
    taper_x = jnp.where(active, jnp.sin(jnp.pi * (depth_float + 0.5) / extent_float), 0.0)
    taper_y = sine_taper(wide_y, float(wide_y))
    taper_z = sine_taper(wide_z, float(wide_z))
    consts = jnp.stack([
        jnp.broadcast_to(mask_col[:, None], (planes, wide_z)),
        jnp.broadcast_to(taper_x[:, None], (planes, wide_z)),
        jnp.broadcast_to(taper_z[None, :], (planes, wide_z)),
    ])
    whole_brick = (extent > brick_index * planes).astype(jnp.int32).reshape(1)
    interior, aux = window_blocks(src4, slowness_window, consts, taper_y, whole_brick)
    shot_count = lax.axis_size("z") * x_count * core_count
    tile_dev = tile_slot.shape[0] // shot_count
    partner = (z_index * x_count + (x_count - 1 - x_index)) * core_count + core_index
    slots = jnp.arange(tile_dev, dtype=jnp.int32)
    owners = jnp.concatenate([shot_index * tile_dev + slots, partner * tile_dev + slots])
    zs = jnp.arange(lax.axis_size("z"), dtype=jnp.int32)
    cs = jnp.arange(core_count, dtype=jnp.int32)
    held = ((zs[:, None] * x_count + x_index) * core_count + cs[None, :]).reshape(-1)
    piece_slots = tile_slot[window_anchor[held][:, None] + jnp.arange(BLOCKS, dtype=jnp.int32)[None, :]]
    match = owners[:, None, None] == piece_slots[None, :, :]
    tables = contribution_tables(match)
    swap = [(0, 1), (1, 0)]
    mid = lax.all_gather(interior[None], ("z", "core"), axis=0, tiled=True)
    mid, lo, hi = lax.optimization_barrier((mid, lo, hi))
    own_mid, other_mid = gather_sum(mid, tables)
    theirs_mid = lax.ppermute(other_mid, "xl", swap)
    edges = edge_planes(aux, lo, hi, taper_y[:, None], consts)
    rim = lax.all_gather(edges[None], ("z", "core"), axis=0, tiled=True)
    own_rim, other_rim = gather_sum(rim, tables)
    theirs_rim = lax.ppermute(other_rim, "xl", swap)
    mid_sum = own_mid + theirs_mid
    rim_sum = own_rim + theirs_rim
    summed = jnp.concatenate([rim_sum[:, :1], mid_sum, rim_sum[:, 1:]], axis=1)
    return jnp.transpose(summed, (0, 2, 1, 3)).reshape(1, tile_dev, -1)


def select_kernel(es_ref, eb_ref, eq_ref, n_ref, g_hbm, own_ref, other_ref, buf, sem):
    n = n_ref[0]
    depth = buf.shape[0]
    half = own_ref.shape[0]
    own_ref[...] = jnp.zeros_like(own_ref)
    other_ref[...] = jnp.zeros_like(other_ref)

    def copy(e, slot):
        return pltpu.make_async_copy(g_hbm.at[es_ref[e], eb_ref[e]], buf.at[slot], sem.at[slot])

    for e in range(depth):
        @pl.when(e < n)
        def _():
            copy(e, e).start()

    def body(e, carry):
        slot = e % depth
        copy(e, slot).wait()
        q = eq_ref[e]

        @pl.when(q < half)
        def _():
            mine = jnp.minimum(q, half - 1)
            own_ref[mine] = own_ref[mine] + buf[slot]

        @pl.when(q >= half)
        def _():
            theirs = jnp.maximum(q - half, 0)
            other_ref[theirs] = other_ref[theirs] + buf[slot]

        @pl.when(e + depth < n)
        def _():
            copy(e + depth, slot).start()

        return carry

    lax.fori_loop(0, n, body, 0)


def contribution_tables(match):
    owners, shots, blocks = match.shape
    valid = jnp.any(match, axis=2).reshape(-1)
    which_block = jnp.sum(jnp.where(match, jnp.arange(blocks, dtype=jnp.int32), 0), axis=2).reshape(-1)
    shot_of = jnp.broadcast_to(jnp.arange(shots, dtype=jnp.int32)[None, :], (owners, shots)).reshape(-1)
    owner_of = jnp.broadcast_to(jnp.arange(owners, dtype=jnp.int32)[:, None], (owners, shots)).reshape(-1)
    count = owners * shots
    position = jnp.where(valid, jnp.cumsum(valid.astype(jnp.int32)) - 1, count)
    empty = jnp.zeros((count,), jnp.int32)
    es = empty.at[position].set(shot_of, mode="drop")
    eb = empty.at[position].set(which_block, mode="drop")
    eq = empty.at[position].set(owner_of, mode="drop")
    n = jnp.sum(valid.astype(jnp.int32)).reshape(1)
    return owners, (es, eb, eq, n)


def gather_sum(gathered, tables):
    owners, (es, eb, eq, n) = tables
    cell_shape = gathered.shape[2:]
    return pl.pallas_call(
        select_kernel,
        grid_spec=pltpu.PrefetchScalarGridSpec(
            num_scalar_prefetch=4,
            grid=(1,),
            in_specs=[pl.BlockSpec(memory_space=pl.ANY)],
            out_specs=[pl.BlockSpec((owners // 2,) + cell_shape, lambda i, *_: (0,) * (1 + len(cell_shape)))] * 2,
            scratch_shapes=[
                pltpu.VMEM((8,) + cell_shape, jnp.float32),
                pltpu.SemaphoreType.DMA((8,)),
            ],
        ),
        out_shape=[jax.ShapeDtypeStruct((owners // 2,) + cell_shape, jnp.float32)] * 2,
    )(es, eb, eq, n, gathered)


def solution(mesh):
    devices = mesh.devices
    shots, bricks = devices.shape
    split = jax.sharding.Mesh(devices.reshape(shots // 4, 2, 2, bricks), ("z", "xl", "core", "brick"))
    shot = ("z", "xl", "core")
    return jax.shard_map(
        per_device,
        mesh=split,
        in_specs=(
            P(shot, None, None, None, "brick", None),
            P(shot, None, "brick", None),
            P(),
            P(),
            P(),
        ),
        out_specs=P("brick", shot, None),
        check_vma=False,
    )
```

```python
import jax
import jax.numpy as jnp
from jax import lax
from jax.experimental import pallas as pl
from jax.experimental.pallas import tpu as pltpu
from jax.sharding import PartitionSpec as P

BLOCKS = 8


shift_beta = 0.5
relaxation = 0.8


def sine_taper(count, extent):
    positions = jnp.arange(count, dtype=jnp.int32).astype(jnp.float32)
    return jnp.sin(jnp.pi * (positions + 0.5) / extent)


def inverse_of(slow):
    real_d = 6.0 - slow
    imag_d = shift_beta * slow
    denominator = real_d * real_d + imag_d * imag_d
    scale = 1.0 / denominator
    return real_d * scale, imag_d * scale


def first_sweep(s0, s1, s2, s3, inv_re, inv_im, mask=None):
    f = (
        relaxation * (s0 * inv_re - s1 * inv_im),
        relaxation * (s0 * inv_im + s1 * inv_re),
        relaxation * (s2 * inv_re - s3 * inv_im),
        relaxation * (s2 * inv_im + s3 * inv_re),
    )
    if mask is None:
        return f
    return tuple(v * mask for v in f)


def gather_plane(rows8, plane, sub_ids):
    tile = jnp.broadcast_to(rows8[0][plane:plane + 1, :], rows8[0].shape)
    for i in range(1, len(rows8)):
        tile = jnp.where(sub_ids == i, jnp.broadcast_to(rows8[i][plane:plane + 1, :], tile.shape), tile)
    return tile


def boundary_kernel(mask_ref, src_hbm, sl_hbm, lo_ref, hi_ref, src_buf, sl_buf, sem):
    four = src_hbm.shape[0]
    planes = src_hbm.shape[2]
    copies = []
    for j, plane in enumerate((planes - 1, 0)):
        for k in range(four):
            copies.append(pltpu.make_async_copy(src_hbm.at[k, :, plane, :], src_buf.at[j, k], sem.at[j, k]))
        copies.append(pltpu.make_async_copy(sl_hbm.at[:, plane, :], sl_buf.at[j], sem.at[j, four]))
    for c in copies:
        c.start()
    for c in copies:
        c.wait()
    for j, (plane, out) in enumerate(((planes - 1, lo_ref), (0, hi_ref))):
        m = mask_ref[plane]
        inv_re, inv_im = inverse_of(sl_buf[j])
        f = first_sweep(src_buf[j, 0], src_buf[j, 1], src_buf[j, 2], src_buf[j, 3], inv_re, inv_im, m)
        for k in range(four):
            out[k] = f[k]


def boundary_planes(src4, slow, mask_col):
    four, wide_y, planes, wide_z = src4.shape
    face = jax.ShapeDtypeStruct((four, wide_y, wide_z), jnp.float32)
    vmem = pl.BlockSpec(memory_space=pltpu.VMEM)
    return pl.pallas_call(
        boundary_kernel,
        in_specs=[
            pl.BlockSpec(memory_space=pltpu.SMEM),
            pl.BlockSpec(memory_space=pl.ANY),
            pl.BlockSpec(memory_space=pl.ANY),
        ],
        out_specs=[vmem, vmem],
        out_shape=[face, face],
        scratch_shapes=[
            pltpu.VMEM((2, four, wide_y, wide_z), jnp.float32),
            pltpu.VMEM((2, wide_y, wide_z), jnp.float32),
            pltpu.SemaphoreType.DMA((2, four + 1)),
        ],
    )(mask_col, src4, slow)


def gradient_kernel(ty_ref, act_ref, src_ref, src_lo_ref, src_hi_ref, sl_ref, sl_lo_ref, sl_hi_ref, mask_ref, tx_ref,
                    tz_ref, out_ref, aux_ref, f1_s, inv_s, tp_s):
    active = act_ref[0] > 0

    @pl.when(jnp.logical_not(active))
    def _():
        out_ref[...] = jnp.zeros_like(out_ref)
        aux_ref[...] = jnp.zeros_like(aux_ref)

    @pl.when(active)
    def _():
        active_window(ty_ref, src_ref, src_lo_ref, src_hi_ref, sl_ref, sl_lo_ref, sl_hi_ref, mask_ref, tx_ref, tz_ref,
                      out_ref, aux_ref, f1_s, inv_s, tp_s)


def active_window(ty_ref, src_ref, src_lo_ref, src_hi_ref, sl_ref, sl_lo_ref, sl_hi_ref, mask_ref, tx_ref, tz_ref,
                  out_ref, aux_ref, f1_s, inv_s, tp_s):
    b = pl.program_id(0)
    nb = pl.num_programs(0)
    rows = src_ref.shape[1]
    mask = None

    def sweep_one(r, carry):
        inv_re, inv_im = inverse_of(sl_ref[r])
        inv_s[0, r] = inv_re
        inv_s[1, r] = inv_im
        f = first_sweep(src_ref[0, r], src_ref[1, r], src_ref[2, r], src_ref[3, r], inv_re, inv_im, mask)
        for k in range(4):
            f1_s[k, r + 1] = f[k]
        return carry

    lax.fori_loop(0, rows, sweep_one, 0, unroll=4)

    lo_keep = jnp.where(b > 0, 1.0, 0.0).astype(jnp.float32)
    hi_keep = jnp.where(b < nb - 1, 1.0, 0.0).astype(jnp.float32)
    for slot, s_ref, l_ref, keep in ((0, src_lo_ref, sl_lo_ref, lo_keep), (rows + 1, src_hi_ref, sl_hi_ref, hi_keep)):
        inv_re, inv_im = inverse_of(l_ref[0])
        f = first_sweep(s_ref[0, 0], s_ref[1, 0], s_ref[2, 0], s_ref[3, 0], inv_re, inv_im, mask)
        for k in range(4):
            f1_s[k, slot] = f[k] * keep

    shape = mask_ref.shape
    p_ids = lax.broadcasted_iota(jnp.int32, shape, 0)
    z_ids = lax.broadcasted_iota(jnp.int32, shape, 1)
    planes, width = shape
    tx = tx_ref[...]
    tz = tz_ref[...]

    def sweep_two(g, carry):
        base = pl.multiple_of(g * 8, 8)
        for i in range(8):
            r = base + i
            inv_re = inv_s[0, r]
            inv_im = inv_s[1, r]
            cur = []
            vals = []
            for k in range(4):
                c = f1_s[k, r + 1]
                acc = f1_s[k, r] + f1_s[k, r + 2]
                down = jnp.where(p_ids == 0, 0.0, pltpu.roll(c, 1, 0))
                acc = acc + down
                up = jnp.where(p_ids == planes - 1, 0.0, pltpu.roll(c, planes - 1, 0))
                acc = acc + up
                zm = jnp.where(z_ids == 0, 0.0, pltpu.roll(c, 1, 1))
                acc = acc + zm
                zp = jnp.where(z_ids == width - 1, 0.0, pltpu.roll(c, width - 1, 1))
                acc = acc + zp
                cur.append(c)
                vals.append(src_ref[k, r] + acc)
            upd = (
                vals[0] * inv_re - vals[1] * inv_im,
                vals[0] * inv_im + vals[1] * inv_re,
                vals[2] * inv_re - vals[3] * inv_im,
                vals[2] * inv_im + vals[3] * inv_re,
            )
            f2 = [(1.0 - relaxation) * cur[k] + relaxation * upd[k] for k in range(4)]
            imaging = f2[0] * f2[2] - f2[1] * f2[3] - shift_beta * (f2[0] * f2[3] + f2[1] * f2[2])
            taper = (ty_ref[b * rows + r] * tx) * tz
            for k, v in enumerate(f2 + [inv_re, inv_im, imaging * taper]):
                for h in range(2):
                    tp_s[k, h, i * planes:(i + 1) * planes, :] = v[:, h * 128:(h + 1) * 128]

        def plane_tile(k, plane):
            halves = [tp_s[k, h, pl.ds(plane, 8, stride=planes), :] for h in range(2)]
            return jnp.concatenate(halves, axis=1)

        for k in range(6):
            for j, plane in enumerate((0, planes - 1)):
                aux_ref[k, j, pl.ds(base, 8), :] = plane_tile(k, plane)
        for plane in range(1, planes - 1):
            out_ref[0, plane - 1, pl.ds(base, 8), :] = plane_tile(6, plane)
        return carry

    lax.fori_loop(0, rows // 8, sweep_two, 0)


def window_blocks(src4, slow, consts, ty, act):
    four, wide_y, planes, wide_z = src4.shape
    rows = wide_y // BLOCKS
    last = wide_y - 1

    def row_spec(pick):
        return pl.BlockSpec((four, 1, planes, wide_z), lambda b, t, a: (0, pick(b), 0, 0))

    def slow_row_spec(pick):
        return pl.BlockSpec((1, planes, wide_z), lambda b, t, a: (pick(b), 0, 0))

    below = lambda b: jnp.maximum(b * rows - 1, 0)
    above = lambda b: jnp.minimum(b * rows + rows, last)
    grid_spec = pltpu.PrefetchScalarGridSpec(
        num_scalar_prefetch=2,
        grid=(BLOCKS,),
        in_specs=[
            pl.BlockSpec((four, rows, planes, wide_z), lambda b, t, a: (0, b, 0, 0)),
            row_spec(below),
            row_spec(above),
            pl.BlockSpec((rows, planes, wide_z), lambda b, t, a: (b, 0, 0)),
            slow_row_spec(below),
            slow_row_spec(above),
            pl.BlockSpec((None, planes, wide_z), lambda b, t, a: (0, 0, 0)),
            pl.BlockSpec((None, planes, wide_z), lambda b, t, a: (1, 0, 0)),
            pl.BlockSpec((None, planes, wide_z), lambda b, t, a: (2, 0, 0)),
        ],
        out_specs=[
            pl.BlockSpec((1, planes - 2, rows, wide_z), lambda b, t, a: (b, 0, 0, 0)),
            pl.BlockSpec((6, 2, rows, wide_z), lambda b, t, a: (0, 0, b, 0)),
        ],
        scratch_shapes=[
            pltpu.VMEM((four, rows + 2, planes, wide_z), jnp.float32),
            pltpu.VMEM((2, rows, planes, wide_z), jnp.float32),
            pltpu.VMEM((7, 2, 8 * planes, wide_z // 2), jnp.float32),
        ],
    )
    return pl.pallas_call(
        gradient_kernel,
        grid_spec=grid_spec,
        out_shape=[
            jax.ShapeDtypeStruct((BLOCKS, planes - 2, rows, wide_z), jnp.float32),
            jax.ShapeDtypeStruct((6, 2, wide_y, wide_z), jnp.float32),
        ],
    )(ty, act, src4, src4, src4, slow, slow, slow, consts, consts, consts)


def halo_kernel(aux_ref, lo_ref, hi_ref, ty_ref, mask_ref, tx_ref, tz_ref, out_ref):
    rows = aux_ref.shape[2]
    planes = mask_ref.shape[0]
    tz = tz_ref[...]
    for g in range(rows // 8):
        span = pl.ds(g * 8, 8)
        ty = ty_ref[span, :]
        for j, plane, h_ref in ((0, 0, lo_ref), (1, planes - 1, hi_ref)):
            inv_re = aux_ref[4, j, span, :]
            inv_im = aux_ref[5, j, span, :]
            h = [h_ref[k, span, :] for k in range(4)]
            m = mask_ref[plane:plane + 1, :]
            d = (
                h[0] * inv_re - h[1] * inv_im,
                h[0] * inv_im + h[1] * inv_re,
                h[2] * inv_re - h[3] * inv_im,
                h[2] * inv_im + h[3] * inv_re,
            )
            f2 = [aux_ref[k, j, span, :] + relaxation * d[k] * m for k in range(4)]
            imaging = f2[0] * f2[2] - f2[1] * f2[3] - shift_beta * (f2[0] * f2[3] + f2[1] * f2[2])
            per_block = out_ref.shape[2]
            out_ref[(g * 8) // per_block, j, pl.ds((g * 8) % per_block, 8), :] = imaging * ((ty * tx_ref[plane:plane + 1, :]) * tz)


def edge_planes(aux, lo, hi, ty_col, consts):
    wide_y, wide_z = lo.shape[1:]
    rows = wide_y // 2
    four = lo.shape[0]
    planes = consts.shape[1]
    return pl.pallas_call(
        halo_kernel,
        grid=(2,),
        in_specs=[
            pl.BlockSpec((6, 2, rows, wide_z), lambda b: (0, 0, b, 0)),
            pl.BlockSpec((four, rows, wide_z), lambda b: (0, b, 0)),
            pl.BlockSpec((four, rows, wide_z), lambda b: (0, b, 0)),
            pl.BlockSpec((rows, 1), lambda b: (b, 0)),
            pl.BlockSpec((None, planes, wide_z), lambda b: (0, 0, 0)),
            pl.BlockSpec((None, planes, wide_z), lambda b: (1, 0, 0)),
            pl.BlockSpec((None, planes, wide_z), lambda b: (2, 0, 0)),
        ],
        out_specs=pl.BlockSpec((BLOCKS // 2, 2, wide_y // BLOCKS, wide_z), lambda b: (b, 0, 0, 0)),
        out_shape=jax.ShapeDtypeStruct((BLOCKS, 2, wide_y // BLOCKS, wide_z), jnp.float32),
    )(aux, lo, hi, ty_col, consts, consts, consts)


def per_device(sources, slowness, group_size, window_anchor, tile_slot):
    slowness_window = slowness[0]
    wide_y, planes, wide_z = slowness_window.shape
    brick_index = lax.axis_index("brick")
    z_index = lax.axis_index("z")
    x_index = lax.axis_index("xl")
    core_index = lax.axis_index("core")
    x_count = lax.axis_size("xl")
    core_count = lax.axis_size("core")
    shot_index = (z_index * x_count + x_index) * core_count + core_index
    brick_count = lax.axis_size("brick")
    shot_count_all = group_size.shape[0]
    extent = jnp.sum(jnp.where(jnp.arange(shot_count_all) == shot_index, group_size, 0)) * planes
    depth_ids = brick_index * planes + jnp.arange(planes, dtype=jnp.int32)
    active = depth_ids < extent
    mask_col = active.astype(jnp.float32)
    src4 = sources[0].reshape(4, wide_y, planes, wide_z)

    lo_send, hi_send = boundary_planes(src4, slowness_window, mask_col)
    up = [(i, i + 1) for i in range(brick_count - 1)]
    down = [(j, i) for i, j in up]
    lo = lax.ppermute(lo_send, "brick", up)
    hi = lax.ppermute(hi_send, "brick", down)

    extent_float = extent.astype(jnp.float32)
    depth_float = depth_ids.astype(jnp.float32)
    taper_x = jnp.where(active, jnp.sin(jnp.pi * (depth_float + 0.5) / extent_float), 0.0)
    taper_y = sine_taper(wide_y, float(wide_y))
    taper_z = sine_taper(wide_z, float(wide_z))
    consts = jnp.stack([
        jnp.broadcast_to(mask_col[:, None], (planes, wide_z)),
        jnp.broadcast_to(taper_x[:, None], (planes, wide_z)),
        jnp.broadcast_to(taper_z[None, :], (planes, wide_z)),
    ])
    whole_brick = (extent > brick_index * planes).astype(jnp.int32).reshape(1)
    interior, aux = window_blocks(src4, slowness_window, consts, taper_y, whole_brick)
    shot_count = lax.axis_size("z") * x_count * core_count
    tile_dev = tile_slot.shape[0] // shot_count
    partner = (z_index * x_count + (x_count - 1 - x_index)) * core_count + core_index
    slots = jnp.arange(tile_dev, dtype=jnp.int32)
    owners = jnp.concatenate([shot_index * tile_dev + slots, partner * tile_dev + slots])
    zs = jnp.arange(lax.axis_size("z"), dtype=jnp.int32)
    cs = jnp.arange(core_count, dtype=jnp.int32)
    held = ((zs[:, None] * x_count + x_index) * core_count + cs[None, :]).reshape(-1)
    piece_slots = tile_slot[window_anchor[held][:, None] + jnp.arange(BLOCKS, dtype=jnp.int32)[None, :]]
    match = owners[:, None, None] == piece_slots[None, :, :]
    tables = contribution_tables(match)
    swap = [(0, 1), (1, 0)]
    mid = lax.all_gather(interior[None], ("z", "core"), axis=0, tiled=True)
    mid, lo, hi = lax.optimization_barrier((mid, lo, hi))
    own_mid, other_mid = gather_sum(mid, tables)
    theirs_mid = lax.ppermute(other_mid, "xl", swap)
    edges = edge_planes(aux, lo, hi, taper_y[:, None], consts)
    rim = lax.all_gather(edges[None], ("z", "core"), axis=0, tiled=True)
    own_rim, other_rim = gather_sum(rim, tables)
    theirs_rim = lax.ppermute(other_rim, "xl", swap)
    mid_sum = own_mid + theirs_mid
    rim_sum = own_rim + theirs_rim
    summed = jnp.concatenate([rim_sum[:, :1], mid_sum, rim_sum[:, 1:]], axis=1)
    return jnp.transpose(summed, (0, 2, 1, 3)).reshape(1, tile_dev, -1)


def select_kernel(es_ref, eb_ref, eq_ref, n_ref, g_hbm, own_ref, other_ref, buf, sem):
    n = n_ref[0]
    depth = buf.shape[0]
    half = own_ref.shape[0]
    own_ref[...] = jnp.zeros_like(own_ref)
    other_ref[...] = jnp.zeros_like(other_ref)

    def copy(e, slot):
        return pltpu.make_async_copy(g_hbm.at[es_ref[e], eb_ref[e]], buf.at[slot], sem.at[slot])

    for e in range(depth):
        @pl.when(e < n)
        def _():
            copy(e, e).start()

    def body(e, carry):
        slot = e % depth
        copy(e, slot).wait()
        q = eq_ref[e]

        @pl.when(q < half)
        def _():
            mine = jnp.minimum(q, half - 1)
            own_ref[mine] = own_ref[mine] + buf[slot]

        @pl.when(q >= half)
        def _():
            theirs = jnp.maximum(q - half, 0)
            other_ref[theirs] = other_ref[theirs] + buf[slot]

        @pl.when(e + depth < n)
        def _():
            copy(e + depth, slot).start()

        return carry

    lax.fori_loop(0, n, body, 0)


def contribution_tables(match):
    owners, shots, blocks = match.shape
    valid = jnp.any(match, axis=2).reshape(-1)
    which_block = jnp.sum(jnp.where(match, jnp.arange(blocks, dtype=jnp.int32), 0), axis=2).reshape(-1)
    shot_of = jnp.broadcast_to(jnp.arange(shots, dtype=jnp.int32)[None, :], (owners, shots)).reshape(-1)
    owner_of = jnp.broadcast_to(jnp.arange(owners, dtype=jnp.int32)[:, None], (owners, shots)).reshape(-1)
    count = owners * shots
    position = jnp.where(valid, jnp.cumsum(valid.astype(jnp.int32)) - 1, count)
    empty = jnp.zeros((count,), jnp.int32)
    es = empty.at[position].set(shot_of, mode="drop")
    eb = empty.at[position].set(which_block, mode="drop")
    eq = empty.at[position].set(owner_of, mode="drop")
    n = jnp.sum(valid.astype(jnp.int32)).reshape(1)
    return owners, (es, eb, eq, n)


def gather_sum(gathered, tables):
    owners, (es, eb, eq, n) = tables
    cell_shape = gathered.shape[2:]
    return pl.pallas_call(
        select_kernel,
        grid_spec=pltpu.PrefetchScalarGridSpec(
            num_scalar_prefetch=4,
            grid=(1,),
            in_specs=[pl.BlockSpec(memory_space=pl.ANY)],
            out_specs=[pl.BlockSpec((owners // 2,) + cell_shape, lambda i, *_: (0,) * (1 + len(cell_shape)))] * 2,
            scratch_shapes=[
                pltpu.VMEM((8,) + cell_shape, jnp.float32),
                pltpu.SemaphoreType.DMA((8,)),
            ],
        ),
        out_shape=[jax.ShapeDtypeStruct((owners // 2,) + cell_shape, jnp.float32)] * 2,
    )(es, eb, eq, n, gathered)


def solution(mesh):
    devices = mesh.devices
    shots, bricks = devices.shape
    split = jax.sharding.Mesh(devices.reshape(shots // 4, 2, 2, bricks), ("z", "xl", "core", "brick"))
    shot = ("z", "xl", "core")
    return jax.shard_map(
        per_device,
        mesh=split,
        in_specs=(
            P(shot, None, None, None, "brick", None),
            P(shot, None, "brick", None),
            P(),
            P(),
            P(),
        ),
        out_specs=P("brick", shot, None),
        check_vma=False,
    )
```

```python
import jax
import jax.numpy as jnp
from jax import lax
from jax.experimental import pallas as pl
from jax.experimental.pallas import tpu as pltpu
from jax.sharding import PartitionSpec as P

BLOCKS = 8


shift_beta = 0.5
relaxation = 0.8


def sine_taper(count, extent):
    positions = jnp.arange(count, dtype=jnp.int32).astype(jnp.float32)
    return jnp.sin(jnp.pi * (positions + 0.5) / extent)


def inverse_of(slow):
    real_d = 6.0 - slow
    imag_d = shift_beta * slow
    denominator = real_d * real_d + imag_d * imag_d
    scale = 1.0 / denominator
    return real_d * scale, imag_d * scale


def first_sweep(s0, s1, s2, s3, inv_re, inv_im, mask=None):
    f = (
        relaxation * (s0 * inv_re - s1 * inv_im),
        relaxation * (s0 * inv_im + s1 * inv_re),
        relaxation * (s2 * inv_re - s3 * inv_im),
        relaxation * (s2 * inv_im + s3 * inv_re),
    )
    if mask is None:
        return f
    return tuple(v * mask for v in f)


def gather_plane(rows8, plane, sub_ids):
    tile = jnp.broadcast_to(rows8[0][plane:plane + 1, :], rows8[0].shape)
    for i in range(1, len(rows8)):
        tile = jnp.where(sub_ids == i, jnp.broadcast_to(rows8[i][plane:plane + 1, :], tile.shape), tile)
    return tile


def boundary_kernel(mask_ref, src_hbm, sl_hbm, lo_ref, hi_ref, src_buf, sl_buf, sem):
    four = src_hbm.shape[0]
    planes = src_hbm.shape[2]
    copies = []
    for j, plane in enumerate((planes - 1, 0)):
        for k in range(four):
            copies.append(pltpu.make_async_copy(src_hbm.at[k, :, plane, :], src_buf.at[j, k], sem.at[j, k]))
        copies.append(pltpu.make_async_copy(sl_hbm.at[:, plane, :], sl_buf.at[j], sem.at[j, four]))
    for c in copies:
        c.start()
    for c in copies:
        c.wait()
    for j, (plane, out) in enumerate(((planes - 1, lo_ref), (0, hi_ref))):
        m = mask_ref[plane]
        inv_re, inv_im = inverse_of(sl_buf[j])
        f = first_sweep(src_buf[j, 0], src_buf[j, 1], src_buf[j, 2], src_buf[j, 3], inv_re, inv_im, m)
        for k in range(four):
            out[k] = f[k]


def boundary_planes(src4, slow, mask_col):
    four, wide_y, planes, wide_z = src4.shape
    face = jax.ShapeDtypeStruct((four, wide_y, wide_z), jnp.float32)
    vmem = pl.BlockSpec(memory_space=pltpu.VMEM)
    return pl.pallas_call(
        boundary_kernel,
        in_specs=[
            pl.BlockSpec(memory_space=pltpu.SMEM),
            pl.BlockSpec(memory_space=pl.ANY),
            pl.BlockSpec(memory_space=pl.ANY),
        ],
        out_specs=[vmem, vmem],
        out_shape=[face, face],
        scratch_shapes=[
            pltpu.VMEM((2, four, wide_y, wide_z), jnp.float32),
            pltpu.VMEM((2, wide_y, wide_z), jnp.float32),
            pltpu.SemaphoreType.DMA((2, four + 1)),
        ],
    )(mask_col, src4, slow)


def gradient_kernel(ty_ref, act_ref, src_ref, src_lo_ref, src_hi_ref, sl_ref, sl_lo_ref, sl_hi_ref, mask_ref, tx_ref,
                    tz_ref, out_ref, aux_ref, f1_s, inv_s, tp_s):
    active = act_ref[0] > 0

    @pl.when(jnp.logical_not(active))
    def _():
        out_ref[...] = jnp.zeros_like(out_ref)
        aux_ref[...] = jnp.zeros_like(aux_ref)

    @pl.when(active)
    def _():
        active_window(ty_ref, src_ref, src_lo_ref, src_hi_ref, sl_ref, sl_lo_ref, sl_hi_ref, mask_ref, tx_ref, tz_ref,
                      out_ref, aux_ref, f1_s, inv_s, tp_s)


def active_window(ty_ref, src_ref, src_lo_ref, src_hi_ref, sl_ref, sl_lo_ref, sl_hi_ref, mask_ref, tx_ref, tz_ref,
                  out_ref, aux_ref, f1_s, inv_s, tp_s):
    b = pl.program_id(0)
    nb = pl.num_programs(0)
    rows = src_ref.shape[1]
    mask = None

    def sweep_one(r, carry):
        inv_re, inv_im = inverse_of(sl_ref[r])
        inv_s[0, r] = inv_re
        inv_s[1, r] = inv_im
        f = first_sweep(src_ref[0, r], src_ref[1, r], src_ref[2, r], src_ref[3, r], inv_re, inv_im, mask)
        for k in range(4):
            f1_s[k, r + 1] = f[k]
        return carry

    lax.fori_loop(0, rows, sweep_one, 0, unroll=4)

    lo_keep = jnp.where(b > 0, 1.0, 0.0).astype(jnp.float32)
    hi_keep = jnp.where(b < nb - 1, 1.0, 0.0).astype(jnp.float32)
    for slot, s_ref, l_ref, keep in ((0, src_lo_ref, sl_lo_ref, lo_keep), (rows + 1, src_hi_ref, sl_hi_ref, hi_keep)):
        inv_re, inv_im = inverse_of(l_ref[0])
        f = first_sweep(s_ref[0, 0], s_ref[1, 0], s_ref[2, 0], s_ref[3, 0], inv_re, inv_im, mask)
        for k in range(4):
            f1_s[k, slot] = f[k] * keep

    shape = mask_ref.shape
    p_ids = lax.broadcasted_iota(jnp.int32, shape, 0)
    z_ids = lax.broadcasted_iota(jnp.int32, shape, 1)
    planes, width = shape
    tx = tx_ref[...]
    tz = tz_ref[...]

    def sweep_two(g, carry):
        base = pl.multiple_of(g * 8, 8)
        for i in range(8):
            r = base + i
            inv_re = inv_s[0, r]
            inv_im = inv_s[1, r]
            cur = []
            vals = []
            for k in range(4):
                c = f1_s[k, r + 1]
                acc = f1_s[k, r] + f1_s[k, r + 2]
                down = jnp.where(p_ids == 0, 0.0, pltpu.roll(c, 1, 0))
                acc = acc + down
                up = jnp.where(p_ids == planes - 1, 0.0, pltpu.roll(c, planes - 1, 0))
                acc = acc + up
                zm = jnp.where(z_ids == 0, 0.0, pltpu.roll(c, 1, 1))
                acc = acc + zm
                zp = jnp.where(z_ids == width - 1, 0.0, pltpu.roll(c, width - 1, 1))
                acc = acc + zp
                cur.append(c)
                vals.append(src_ref[k, r] + acc)
            upd = (
                vals[0] * inv_re - vals[1] * inv_im,
                vals[0] * inv_im + vals[1] * inv_re,
                vals[2] * inv_re - vals[3] * inv_im,
                vals[2] * inv_im + vals[3] * inv_re,
            )
            f2 = [(1.0 - relaxation) * cur[k] + relaxation * upd[k] for k in range(4)]
            imaging = f2[0] * f2[2] - f2[1] * f2[3] - shift_beta * (f2[0] * f2[3] + f2[1] * f2[2])
            taper = (ty_ref[b * rows + r] * tx) * tz
            for k, v in enumerate(f2 + [inv_re, inv_im, imaging * taper]):
                for h in range(2):
                    tp_s[k, h, i * planes:(i + 1) * planes, :] = v[:, h * 128:(h + 1) * 128]

        def plane_tile(k, plane):
            halves = [tp_s[k, h, pl.ds(plane, 8, stride=planes), :] for h in range(2)]
            return jnp.concatenate(halves, axis=1)

        for k in range(6):
            for j, plane in enumerate((0, planes - 1)):
                aux_ref[k, j, pl.ds(base, 8), :] = plane_tile(k, plane)
        for plane in range(1, planes - 1):
            out_ref[0, plane - 1, pl.ds(base, 8), :] = plane_tile(6, plane)
        return carry

    lax.fori_loop(0, rows // 8, sweep_two, 0, unroll=2)


def window_blocks(src4, slow, consts, ty, act):
    four, wide_y, planes, wide_z = src4.shape
    rows = wide_y // BLOCKS
    last = wide_y - 1

    def row_spec(pick):
        return pl.BlockSpec((four, 1, planes, wide_z), lambda b, t, a: (0, pick(b), 0, 0))

    def slow_row_spec(pick):
        return pl.BlockSpec((1, planes, wide_z), lambda b, t, a: (pick(b), 0, 0))

    below = lambda b: jnp.maximum(b * rows - 1, 0)
    above = lambda b: jnp.minimum(b * rows + rows, last)
    grid_spec = pltpu.PrefetchScalarGridSpec(
        num_scalar_prefetch=2,
        grid=(BLOCKS,),
        in_specs=[
            pl.BlockSpec((four, rows, planes, wide_z), lambda b, t, a: (0, b, 0, 0)),
            row_spec(below),
            row_spec(above),
            pl.BlockSpec((rows, planes, wide_z), lambda b, t, a: (b, 0, 0)),
            slow_row_spec(below),
            slow_row_spec(above),
            pl.BlockSpec((None, planes, wide_z), lambda b, t, a: (0, 0, 0)),
            pl.BlockSpec((None, planes, wide_z), lambda b, t, a: (1, 0, 0)),
            pl.BlockSpec((None, planes, wide_z), lambda b, t, a: (2, 0, 0)),
        ],
        out_specs=[
            pl.BlockSpec((1, planes - 2, rows, wide_z), lambda b, t, a: (b, 0, 0, 0)),
            pl.BlockSpec((6, 2, rows, wide_z), lambda b, t, a: (0, 0, b, 0)),
        ],
        scratch_shapes=[
            pltpu.VMEM((four, rows + 2, planes, wide_z), jnp.float32),
            pltpu.VMEM((2, rows, planes, wide_z), jnp.float32),
            pltpu.VMEM((7, 2, 8 * planes, wide_z // 2), jnp.float32),
        ],
    )
    return pl.pallas_call(
        gradient_kernel,
        grid_spec=grid_spec,
        out_shape=[
            jax.ShapeDtypeStruct((BLOCKS, planes - 2, rows, wide_z), jnp.float32),
            jax.ShapeDtypeStruct((6, 2, wide_y, wide_z), jnp.float32),
        ],
    )(ty, act, src4, src4, src4, slow, slow, slow, consts, consts, consts)


def halo_kernel(aux_ref, lo_ref, hi_ref, ty_ref, mask_ref, tx_ref, tz_ref, out_ref):
    rows = aux_ref.shape[2]
    planes = mask_ref.shape[0]
    tz = tz_ref[...]
    for g in range(rows // 8):
        span = pl.ds(g * 8, 8)
        ty = ty_ref[span, :]
        for j, plane, h_ref in ((0, 0, lo_ref), (1, planes - 1, hi_ref)):
            inv_re = aux_ref[4, j, span, :]
            inv_im = aux_ref[5, j, span, :]
            h = [h_ref[k, span, :] for k in range(4)]
            m = mask_ref[plane:plane + 1, :]
            d = (
                h[0] * inv_re - h[1] * inv_im,
                h[0] * inv_im + h[1] * inv_re,
                h[2] * inv_re - h[3] * inv_im,
                h[2] * inv_im + h[3] * inv_re,
            )
            f2 = [aux_ref[k, j, span, :] + relaxation * d[k] * m for k in range(4)]
            imaging = f2[0] * f2[2] - f2[1] * f2[3] - shift_beta * (f2[0] * f2[3] + f2[1] * f2[2])
            per_block = out_ref.shape[2]
            out_ref[(g * 8) // per_block, j, pl.ds((g * 8) % per_block, 8), :] = imaging * ((ty * tx_ref[plane:plane + 1, :]) * tz)


def edge_planes(aux, lo, hi, ty_col, consts):
    wide_y, wide_z = lo.shape[1:]
    rows = wide_y // 2
    four = lo.shape[0]
    planes = consts.shape[1]
    return pl.pallas_call(
        halo_kernel,
        grid=(2,),
        in_specs=[
            pl.BlockSpec((6, 2, rows, wide_z), lambda b: (0, 0, b, 0)),
            pl.BlockSpec((four, rows, wide_z), lambda b: (0, b, 0)),
            pl.BlockSpec((four, rows, wide_z), lambda b: (0, b, 0)),
            pl.BlockSpec((rows, 1), lambda b: (b, 0)),
            pl.BlockSpec((None, planes, wide_z), lambda b: (0, 0, 0)),
            pl.BlockSpec((None, planes, wide_z), lambda b: (1, 0, 0)),
            pl.BlockSpec((None, planes, wide_z), lambda b: (2, 0, 0)),
        ],
        out_specs=pl.BlockSpec((BLOCKS // 2, 2, wide_y // BLOCKS, wide_z), lambda b: (b, 0, 0, 0)),
        out_shape=jax.ShapeDtypeStruct((BLOCKS, 2, wide_y // BLOCKS, wide_z), jnp.float32),
    )(aux, lo, hi, ty_col, consts, consts, consts)


def per_device(sources, slowness, group_size, window_anchor, tile_slot):
    slowness_window = slowness[0]
    wide_y, planes, wide_z = slowness_window.shape
    brick_index = lax.axis_index("brick")
    z_index = lax.axis_index("z")
    x_index = lax.axis_index("xl")
    core_index = lax.axis_index("core")
    x_count = lax.axis_size("xl")
    core_count = lax.axis_size("core")
    shot_index = (z_index * x_count + x_index) * core_count + core_index
    brick_count = lax.axis_size("brick")
    shot_count_all = group_size.shape[0]
    extent = jnp.sum(jnp.where(jnp.arange(shot_count_all) == shot_index, group_size, 0)) * planes
    depth_ids = brick_index * planes + jnp.arange(planes, dtype=jnp.int32)
    active = depth_ids < extent
    mask_col = active.astype(jnp.float32)
    src4 = sources[0].reshape(4, wide_y, planes, wide_z)

    lo_send, hi_send = boundary_planes(src4, slowness_window, mask_col)
    up = [(i, i + 1) for i in range(brick_count - 1)]
    down = [(j, i) for i, j in up]
    lo = lax.ppermute(lo_send, "brick", up)
    hi = lax.ppermute(hi_send, "brick", down)

    extent_float = extent.astype(jnp.float32)
    depth_float = depth_ids.astype(jnp.float32)
    taper_x = jnp.where(active, jnp.sin(jnp.pi * (depth_float + 0.5) / extent_float), 0.0)
    taper_y = sine_taper(wide_y, float(wide_y))
    taper_z = sine_taper(wide_z, float(wide_z))
    consts = jnp.stack([
        jnp.broadcast_to(mask_col[:, None], (planes, wide_z)),
        jnp.broadcast_to(taper_x[:, None], (planes, wide_z)),
        jnp.broadcast_to(taper_z[None, :], (planes, wide_z)),
    ])
    whole_brick = (extent > brick_index * planes).astype(jnp.int32).reshape(1)
    interior, aux = window_blocks(src4, slowness_window, consts, taper_y, whole_brick)
    shot_count = lax.axis_size("z") * x_count * core_count
    tile_dev = tile_slot.shape[0] // shot_count
    partner = (z_index * x_count + (x_count - 1 - x_index)) * core_count + core_index
    slots = jnp.arange(tile_dev, dtype=jnp.int32)
    owners = jnp.concatenate([shot_index * tile_dev + slots, partner * tile_dev + slots])
    zs = jnp.arange(lax.axis_size("z"), dtype=jnp.int32)
    cs = jnp.arange(core_count, dtype=jnp.int32)
    held = ((zs[:, None] * x_count + x_index) * core_count + cs[None, :]).reshape(-1)
    piece_slots = tile_slot[window_anchor[held][:, None] + jnp.arange(BLOCKS, dtype=jnp.int32)[None, :]]
    match = owners[:, None, None] == piece_slots[None, :, :]
    tables = contribution_tables(match)
    swap = [(0, 1), (1, 0)]
    mid = lax.all_gather(interior[None], ("z", "core"), axis=0, tiled=True)
    mid, lo, hi = lax.optimization_barrier((mid, lo, hi))
    own_mid, other_mid = gather_sum(mid, tables)
    theirs_mid = lax.ppermute(other_mid, "xl", swap)
    edges = edge_planes(aux, lo, hi, taper_y[:, None], consts)
    rim = lax.all_gather(edges[None], ("z", "core"), axis=0, tiled=True)
    own_rim, other_rim = gather_sum(rim, tables)
    theirs_rim = lax.ppermute(other_rim, "xl", swap)
    mid_sum = own_mid + theirs_mid
    rim_sum = own_rim + theirs_rim
    summed = jnp.concatenate([rim_sum[:, :1], mid_sum, rim_sum[:, 1:]], axis=1)
    return jnp.transpose(summed, (0, 2, 1, 3)).reshape(1, tile_dev, -1)


def select_kernel(es_ref, eb_ref, eq_ref, n_ref, g_hbm, own_ref, other_ref, buf, sem):
    n = n_ref[0]
    depth = buf.shape[0]
    half = own_ref.shape[0]
    own_ref[...] = jnp.zeros_like(own_ref)
    other_ref[...] = jnp.zeros_like(other_ref)

    def copy(e, slot):
        return pltpu.make_async_copy(g_hbm.at[es_ref[e], eb_ref[e]], buf.at[slot], sem.at[slot])

    for e in range(depth):
        @pl.when(e < n)
        def _():
            copy(e, e).start()

    def body(e, carry):
        slot = e % depth
        copy(e, slot).wait()
        q = eq_ref[e]

        @pl.when(q < half)
        def _():
            mine = jnp.minimum(q, half - 1)
            own_ref[mine] = own_ref[mine] + buf[slot]

        @pl.when(q >= half)
        def _():
            theirs = jnp.maximum(q - half, 0)
            other_ref[theirs] = other_ref[theirs] + buf[slot]

        @pl.when(e + depth < n)
        def _():
            copy(e + depth, slot).start()

        return carry

    lax.fori_loop(0, n, body, 0)


def contribution_tables(match):
    owners, shots, blocks = match.shape
    valid = jnp.any(match, axis=2).reshape(-1)
    which_block = jnp.sum(jnp.where(match, jnp.arange(blocks, dtype=jnp.int32), 0), axis=2).reshape(-1)
    shot_of = jnp.broadcast_to(jnp.arange(shots, dtype=jnp.int32)[None, :], (owners, shots)).reshape(-1)
    owner_of = jnp.broadcast_to(jnp.arange(owners, dtype=jnp.int32)[:, None], (owners, shots)).reshape(-1)
    count = owners * shots
    position = jnp.where(valid, jnp.cumsum(valid.astype(jnp.int32)) - 1, count)
    empty = jnp.zeros((count,), jnp.int32)
    es = empty.at[position].set(shot_of, mode="drop")
    eb = empty.at[position].set(which_block, mode="drop")
    eq = empty.at[position].set(owner_of, mode="drop")
    n = jnp.sum(valid.astype(jnp.int32)).reshape(1)
    return owners, (es, eb, eq, n)


def gather_sum(gathered, tables):
    owners, (es, eb, eq, n) = tables
    cell_shape = gathered.shape[2:]
    return pl.pallas_call(
        select_kernel,
        grid_spec=pltpu.PrefetchScalarGridSpec(
            num_scalar_prefetch=4,
            grid=(1,),
            in_specs=[pl.BlockSpec(memory_space=pl.ANY)],
            out_specs=[pl.BlockSpec((owners // 2,) + cell_shape, lambda i, *_: (0,) * (1 + len(cell_shape)))] * 2,
            scratch_shapes=[
                pltpu.VMEM((8,) + cell_shape, jnp.float32),
                pltpu.SemaphoreType.DMA((8,)),
            ],
        ),
        out_shape=[jax.ShapeDtypeStruct((owners // 2,) + cell_shape, jnp.float32)] * 2,
    )(es, eb, eq, n, gathered)


def solution(mesh):
    devices = mesh.devices
    shots, bricks = devices.shape
    split = jax.sharding.Mesh(devices.reshape(shots // 4, 2, 2, bricks), ("z", "xl", "core", "brick"))
    shot = ("z", "xl", "core")
    return jax.shard_map(
        per_device,
        mesh=split,
        in_specs=(
            P(shot, None, None, None, "brick", None),
            P(shot, None, "brick", None),
            P(),
            P(),
            P(),
        ),
        out_specs=P("brick", shot, None),
        check_vma=False,
    )
```

```python
import jax
import jax.numpy as jnp
from jax import lax
from jax.experimental import pallas as pl
from jax.experimental.pallas import tpu as pltpu
from jax.sharding import PartitionSpec as P

BLOCKS = 8


shift_beta = 0.5
relaxation = 0.8


def sine_taper(count, extent):
    positions = jnp.arange(count, dtype=jnp.int32).astype(jnp.float32)
    return jnp.sin(jnp.pi * (positions + 0.5) / extent)


def inverse_of(slow):
    real_d = 6.0 - slow
    imag_d = shift_beta * slow
    denominator = real_d * real_d + imag_d * imag_d
    scale = 1.0 / denominator
    return real_d * scale, imag_d * scale


def first_sweep(s0, s1, s2, s3, inv_re, inv_im, mask=None):
    f = (
        relaxation * (s0 * inv_re - s1 * inv_im),
        relaxation * (s0 * inv_im + s1 * inv_re),
        relaxation * (s2 * inv_re - s3 * inv_im),
        relaxation * (s2 * inv_im + s3 * inv_re),
    )
    if mask is None:
        return f
    return tuple(v * mask for v in f)


def gather_plane(rows8, plane, sub_ids):
    tile = jnp.broadcast_to(rows8[0][plane:plane + 1, :], rows8[0].shape)
    for i in range(1, len(rows8)):
        tile = jnp.where(sub_ids == i, jnp.broadcast_to(rows8[i][plane:plane + 1, :], tile.shape), tile)
    return tile


def boundary_kernel(mask_ref, src_hbm, sl_hbm, lo_ref, hi_ref, src_buf, sl_buf, sem):
    four = src_hbm.shape[0]
    planes = src_hbm.shape[2]
    copies = []
    for j, plane in enumerate((planes - 1, 0)):
        for k in range(four):
            copies.append(pltpu.make_async_copy(src_hbm.at[k, :, plane, :], src_buf.at[j, k], sem.at[j, k]))
        copies.append(pltpu.make_async_copy(sl_hbm.at[:, plane, :], sl_buf.at[j], sem.at[j, four]))
    for c in copies:
        c.start()
    for c in copies:
        c.wait()
    for j, (plane, out) in enumerate(((planes - 1, lo_ref), (0, hi_ref))):
        m = mask_ref[plane]
        inv_re, inv_im = inverse_of(sl_buf[j])
        f = first_sweep(src_buf[j, 0], src_buf[j, 1], src_buf[j, 2], src_buf[j, 3], inv_re, inv_im, m)
        for k in range(four):
            out[k] = f[k]


def boundary_planes(src4, slow, mask_col):
    four, wide_y, planes, wide_z = src4.shape
    face = jax.ShapeDtypeStruct((four, wide_y, wide_z), jnp.float32)
    vmem = pl.BlockSpec(memory_space=pltpu.VMEM)
    return pl.pallas_call(
        boundary_kernel,
        in_specs=[
            pl.BlockSpec(memory_space=pltpu.SMEM),
            pl.BlockSpec(memory_space=pl.ANY),
            pl.BlockSpec(memory_space=pl.ANY),
        ],
        out_specs=[vmem, vmem],
        out_shape=[face, face],
        scratch_shapes=[
            pltpu.VMEM((2, four, wide_y, wide_z), jnp.float32),
            pltpu.VMEM((2, wide_y, wide_z), jnp.float32),
            pltpu.SemaphoreType.DMA((2, four + 1)),
        ],
    )(mask_col, src4, slow)


def gradient_kernel(ty_ref, act_ref, src_ref, src_lo_ref, src_hi_ref, sl_ref, sl_lo_ref, sl_hi_ref, mask_ref, tx_ref,
                    tz_ref, out_ref, aux_ref, f1_s, inv_s, tp_s):
    active = act_ref[0] > 0

    @pl.when(jnp.logical_not(active))
    def _():
        out_ref[...] = jnp.zeros_like(out_ref)
        aux_ref[...] = jnp.zeros_like(aux_ref)

    @pl.when(active)
    def _():
        active_window(ty_ref, src_ref, src_lo_ref, src_hi_ref, sl_ref, sl_lo_ref, sl_hi_ref, mask_ref, tx_ref, tz_ref,
                      out_ref, aux_ref, f1_s, inv_s, tp_s)


def active_window(ty_ref, src_ref, src_lo_ref, src_hi_ref, sl_ref, sl_lo_ref, sl_hi_ref, mask_ref, tx_ref, tz_ref,
                  out_ref, aux_ref, f1_s, inv_s, tp_s):
    b = pl.program_id(0)
    nb = pl.num_programs(0)
    rows = src_ref.shape[1]
    mask = None

    def sweep_one(r, carry):
        inv_re, inv_im = inverse_of(sl_ref[r])
        inv_s[0, r] = inv_re
        inv_s[1, r] = inv_im
        f = first_sweep(src_ref[0, r], src_ref[1, r], src_ref[2, r], src_ref[3, r], inv_re, inv_im, mask)
        for k in range(4):
            f1_s[k, r + 1] = f[k]
        return carry

    lax.fori_loop(0, rows, sweep_one, 0, unroll=4)

    lo_keep = jnp.where(b > 0, 1.0, 0.0).astype(jnp.float32)
    hi_keep = jnp.where(b < nb - 1, 1.0, 0.0).astype(jnp.float32)
    for slot, s_ref, l_ref, keep in ((0, src_lo_ref, sl_lo_ref, lo_keep), (rows + 1, src_hi_ref, sl_hi_ref, hi_keep)):
        inv_re, inv_im = inverse_of(l_ref[0])
        f = first_sweep(s_ref[0, 0], s_ref[1, 0], s_ref[2, 0], s_ref[3, 0], inv_re, inv_im, mask)
        for k in range(4):
            f1_s[k, slot] = f[k] * keep

    shape = mask_ref.shape
    p_ids = lax.broadcasted_iota(jnp.int32, shape, 0)
    z_ids = lax.broadcasted_iota(jnp.int32, shape, 1)
    planes, width = shape
    tx = tx_ref[...]
    tz = tz_ref[...]

    def sweep_two(g, carry):
        base = pl.multiple_of(g * 8, 8)
        for i in range(8):
            r = base + i
            inv_re = inv_s[0, r]
            inv_im = inv_s[1, r]
            cur = []
            vals = []
            for k in range(4):
                c = f1_s[k, r + 1]
                acc = f1_s[k, r] + f1_s[k, r + 2]
                down = jnp.where(p_ids == 0, 0.0, pltpu.roll(c, 1, 0))
                acc = acc + down
                up = jnp.where(p_ids == planes - 1, 0.0, pltpu.roll(c, planes - 1, 0))
                acc = acc + up
                zm = jnp.where(z_ids == 0, 0.0, pltpu.roll(c, 1, 1))
                acc = acc + zm
                zp = jnp.where(z_ids == width - 1, 0.0, pltpu.roll(c, width - 1, 1))
                acc = acc + zp
                cur.append(c)
                vals.append(src_ref[k, r] + acc)
            upd = (
                vals[0] * inv_re - vals[1] * inv_im,
                vals[0] * inv_im + vals[1] * inv_re,
                vals[2] * inv_re - vals[3] * inv_im,
                vals[2] * inv_im + vals[3] * inv_re,
            )
            f2 = [(1.0 - relaxation) * cur[k] + relaxation * upd[k] for k in range(4)]
            imaging = f2[0] * f2[2] - f2[1] * f2[3] - shift_beta * (f2[0] * f2[3] + f2[1] * f2[2])
            taper = (ty_ref[b * rows + r] * tx) * tz
            for k, v in enumerate(f2 + [inv_re, inv_im, imaging * taper]):
                for h in range(2):
                    tp_s[k, h, i * planes:(i + 1) * planes, :] = v[:, h * 128:(h + 1) * 128]

        def plane_tile(k, plane):
            halves = [tp_s[k, h, pl.ds(plane, 8, stride=planes), :] for h in range(2)]
            return jnp.concatenate(halves, axis=1)

        for k in range(6):
            for j, plane in enumerate((0, planes - 1)):
                aux_ref[k, j, pl.ds(base, 8), :] = plane_tile(k, plane)
        for plane in range(1, planes - 1):
            out_ref[0, plane - 1, pl.ds(base, 8), :] = plane_tile(6, plane)
        return carry

    lax.fori_loop(0, rows // 8, sweep_two, 0, unroll=4)


def window_blocks(src4, slow, consts, ty, act):
    four, wide_y, planes, wide_z = src4.shape
    rows = wide_y // BLOCKS
    last = wide_y - 1

    def row_spec(pick):
        return pl.BlockSpec((four, 1, planes, wide_z), lambda b, t, a: (0, pick(b), 0, 0))

    def slow_row_spec(pick):
        return pl.BlockSpec((1, planes, wide_z), lambda b, t, a: (pick(b), 0, 0))

    below = lambda b: jnp.maximum(b * rows - 1, 0)
    above = lambda b: jnp.minimum(b * rows + rows, last)
    grid_spec = pltpu.PrefetchScalarGridSpec(
        num_scalar_prefetch=2,
        grid=(BLOCKS,),
        in_specs=[
            pl.BlockSpec((four, rows, planes, wide_z), lambda b, t, a: (0, b, 0, 0)),
            row_spec(below),
            row_spec(above),
            pl.BlockSpec((rows, planes, wide_z), lambda b, t, a: (b, 0, 0)),
            slow_row_spec(below),
            slow_row_spec(above),
            pl.BlockSpec((None, planes, wide_z), lambda b, t, a: (0, 0, 0)),
            pl.BlockSpec((None, planes, wide_z), lambda b, t, a: (1, 0, 0)),
            pl.BlockSpec((None, planes, wide_z), lambda b, t, a: (2, 0, 0)),
        ],
        out_specs=[
            pl.BlockSpec((1, planes - 2, rows, wide_z), lambda b, t, a: (b, 0, 0, 0)),
            pl.BlockSpec((6, 2, rows, wide_z), lambda b, t, a: (0, 0, b, 0)),
        ],
        scratch_shapes=[
            pltpu.VMEM((four, rows + 2, planes, wide_z), jnp.float32),
            pltpu.VMEM((2, rows, planes, wide_z), jnp.float32),
            pltpu.VMEM((7, 2, 8 * planes, wide_z // 2), jnp.float32),
        ],
    )
    return pl.pallas_call(
        gradient_kernel,
        grid_spec=grid_spec,
        out_shape=[
            jax.ShapeDtypeStruct((BLOCKS, planes - 2, rows, wide_z), jnp.float32),
            jax.ShapeDtypeStruct((6, 2, wide_y, wide_z), jnp.float32),
        ],
    )(ty, act, src4, src4, src4, slow, slow, slow, consts, consts, consts)


def halo_kernel(aux_ref, lo_ref, hi_ref, ty_ref, mask_ref, tx_ref, tz_ref, out_ref):
    rows = aux_ref.shape[2]
    planes = mask_ref.shape[0]
    tz = tz_ref[...]
    for g in range(rows // 8):
        span = pl.ds(g * 8, 8)
        ty = ty_ref[span, :]
        for j, plane, h_ref in ((0, 0, lo_ref), (1, planes - 1, hi_ref)):
            inv_re = aux_ref[4, j, span, :]
            inv_im = aux_ref[5, j, span, :]
            h = [h_ref[k, span, :] for k in range(4)]
            m = mask_ref[plane:plane + 1, :]
            d = (
                h[0] * inv_re - h[1] * inv_im,
                h[0] * inv_im + h[1] * inv_re,
                h[2] * inv_re - h[3] * inv_im,
                h[2] * inv_im + h[3] * inv_re,
            )
            f2 = [aux_ref[k, j, span, :] + relaxation * d[k] * m for k in range(4)]
            imaging = f2[0] * f2[2] - f2[1] * f2[3] - shift_beta * (f2[0] * f2[3] + f2[1] * f2[2])
            per_block = out_ref.shape[2]
            out_ref[(g * 8) // per_block, j, pl.ds((g * 8) % per_block, 8), :] = imaging * ((ty * tx_ref[plane:plane + 1, :]) * tz)


def edge_planes(aux, lo, hi, ty_col, consts):
    wide_y, wide_z = lo.shape[1:]
    rows = wide_y // 2
    four = lo.shape[0]
    planes = consts.shape[1]
    return pl.pallas_call(
        halo_kernel,
        grid=(2,),
        in_specs=[
            pl.BlockSpec((6, 2, rows, wide_z), lambda b: (0, 0, b, 0)),
            pl.BlockSpec((four, rows, wide_z), lambda b: (0, b, 0)),
            pl.BlockSpec((four, rows, wide_z), lambda b: (0, b, 0)),
            pl.BlockSpec((rows, 1), lambda b: (b, 0)),
            pl.BlockSpec((None, planes, wide_z), lambda b: (0, 0, 0)),
            pl.BlockSpec((None, planes, wide_z), lambda b: (1, 0, 0)),
            pl.BlockSpec((None, planes, wide_z), lambda b: (2, 0, 0)),
        ],
        out_specs=pl.BlockSpec((BLOCKS // 2, 2, wide_y // BLOCKS, wide_z), lambda b: (b, 0, 0, 0)),
        out_shape=jax.ShapeDtypeStruct((BLOCKS, 2, wide_y // BLOCKS, wide_z), jnp.float32),
    )(aux, lo, hi, ty_col, consts, consts, consts)


def per_device(sources, slowness, group_size, window_anchor, tile_slot):
    slowness_window = slowness[0]
    wide_y, planes, wide_z = slowness_window.shape
    brick_index = lax.axis_index("brick")
    z_index = lax.axis_index("z")
    x_index = lax.axis_index("xl")
    core_index = lax.axis_index("core")
    x_count = lax.axis_size("xl")
    core_count = lax.axis_size("core")
    shot_index = (z_index * x_count + x_index) * core_count + core_index
    brick_count = lax.axis_size("brick")
    shot_count_all = group_size.shape[0]
    extent = jnp.sum(jnp.where(jnp.arange(shot_count_all) == shot_index, group_size, 0)) * planes
    depth_ids = brick_index * planes + jnp.arange(planes, dtype=jnp.int32)
    active = depth_ids < extent
    mask_col = active.astype(jnp.float32)
    src4 = sources[0].reshape(4, wide_y, planes, wide_z)

    lo_send, hi_send = boundary_planes(src4, slowness_window, mask_col)
    up = [(i, i + 1) for i in range(brick_count - 1)]
    down = [(j, i) for i, j in up]
    lo = lax.ppermute(lo_send, "brick", up)
    hi = lax.ppermute(hi_send, "brick", down)

    extent_float = extent.astype(jnp.float32)
    depth_float = depth_ids.astype(jnp.float32)
    taper_x = jnp.where(active, jnp.sin(jnp.pi * (depth_float + 0.5) / extent_float), 0.0)
    taper_y = sine_taper(wide_y, float(wide_y))
    taper_z = sine_taper(wide_z, float(wide_z))
    consts = jnp.stack([
        jnp.broadcast_to(mask_col[:, None], (planes, wide_z)),
        jnp.broadcast_to(taper_x[:, None], (planes, wide_z)),
        jnp.broadcast_to(taper_z[None, :], (planes, wide_z)),
    ])
    whole_brick = (extent > brick_index * planes).astype(jnp.int32).reshape(1)
    interior, aux = window_blocks(src4, slowness_window, consts, taper_y, whole_brick)
    shot_count = lax.axis_size("z") * x_count * core_count
    tile_dev = tile_slot.shape[0] // shot_count
    partner = (z_index * x_count + (x_count - 1 - x_index)) * core_count + core_index
    slots = jnp.arange(tile_dev, dtype=jnp.int32)
    owners = jnp.concatenate([shot_index * tile_dev + slots, partner * tile_dev + slots])
    zs = jnp.arange(lax.axis_size("z"), dtype=jnp.int32)
    cs = jnp.arange(core_count, dtype=jnp.int32)
    held = ((zs[:, None] * x_count + x_index) * core_count + cs[None, :]).reshape(-1)
    piece_slots = tile_slot[window_anchor[held][:, None] + jnp.arange(BLOCKS, dtype=jnp.int32)[None, :]]
    match = owners[:, None, None] == piece_slots[None, :, :]
    tables = contribution_tables(match)
    swap = [(0, 1), (1, 0)]
    mid = lax.all_gather(interior[None], ("z", "core"), axis=0, tiled=True)
    mid, lo, hi = lax.optimization_barrier((mid, lo, hi))
    own_mid, other_mid = gather_sum(mid, tables)
    theirs_mid = lax.ppermute(other_mid, "xl", swap)
    edges = edge_planes(aux, lo, hi, taper_y[:, None], consts)
    rim = lax.all_gather(edges[None], ("z", "core"), axis=0, tiled=True)
    own_rim, other_rim = gather_sum(rim, tables)
    theirs_rim = lax.ppermute(other_rim, "xl", swap)
    mid_sum = own_mid + theirs_mid
    rim_sum = own_rim + theirs_rim
    summed = jnp.concatenate([rim_sum[:, :1], mid_sum, rim_sum[:, 1:]], axis=1)
    return jnp.transpose(summed, (0, 2, 1, 3)).reshape(1, tile_dev, -1)


def select_kernel(es_ref, eb_ref, eq_ref, n_ref, g_hbm, own_ref, other_ref, buf, sem):
    n = n_ref[0]
    depth = buf.shape[0]
    half = own_ref.shape[0]
    own_ref[...] = jnp.zeros_like(own_ref)
    other_ref[...] = jnp.zeros_like(other_ref)

    def copy(e, slot):
        return pltpu.make_async_copy(g_hbm.at[es_ref[e], eb_ref[e]], buf.at[slot], sem.at[slot])

    for e in range(depth):
        @pl.when(e < n)
        def _():
            copy(e, e).start()

    def body(e, carry):
        slot = e % depth
        copy(e, slot).wait()
        q = eq_ref[e]

        @pl.when(q < half)
        def _():
            mine = jnp.minimum(q, half - 1)
            own_ref[mine] = own_ref[mine] + buf[slot]

        @pl.when(q >= half)
        def _():
            theirs = jnp.maximum(q - half, 0)
            other_ref[theirs] = other_ref[theirs] + buf[slot]

        @pl.when(e + depth < n)
        def _():
            copy(e + depth, slot).start()

        return carry

    lax.fori_loop(0, n, body, 0)


def contribution_tables(match):
    owners, shots, blocks = match.shape
    valid = jnp.any(match, axis=2).reshape(-1)
    which_block = jnp.sum(jnp.where(match, jnp.arange(blocks, dtype=jnp.int32), 0), axis=2).reshape(-1)
    shot_of = jnp.broadcast_to(jnp.arange(shots, dtype=jnp.int32)[None, :], (owners, shots)).reshape(-1)
    owner_of = jnp.broadcast_to(jnp.arange(owners, dtype=jnp.int32)[:, None], (owners, shots)).reshape(-1)
    count = owners * shots
    position = jnp.where(valid, jnp.cumsum(valid.astype(jnp.int32)) - 1, count)
    empty = jnp.zeros((count,), jnp.int32)
    es = empty.at[position].set(shot_of, mode="drop")
    eb = empty.at[position].set(which_block, mode="drop")
    eq = empty.at[position].set(owner_of, mode="drop")
    n = jnp.sum(valid.astype(jnp.int32)).reshape(1)
    return owners, (es, eb, eq, n)


def gather_sum(gathered, tables):
    owners, (es, eb, eq, n) = tables
    cell_shape = gathered.shape[2:]
    return pl.pallas_call(
        select_kernel,
        grid_spec=pltpu.PrefetchScalarGridSpec(
            num_scalar_prefetch=4,
            grid=(1,),
            in_specs=[pl.BlockSpec(memory_space=pl.ANY)],
            out_specs=[pl.BlockSpec((owners // 2,) + cell_shape, lambda i, *_: (0,) * (1 + len(cell_shape)))] * 2,
            scratch_shapes=[
                pltpu.VMEM((8,) + cell_shape, jnp.float32),
                pltpu.SemaphoreType.DMA((8,)),
            ],
        ),
        out_shape=[jax.ShapeDtypeStruct((owners // 2,) + cell_shape, jnp.float32)] * 2,
    )(es, eb, eq, n, gathered)


def solution(mesh):
    devices = mesh.devices
    shots, bricks = devices.shape
    split = jax.sharding.Mesh(devices.reshape(shots // 4, 2, 2, bricks), ("z", "xl", "core", "brick"))
    shot = ("z", "xl", "core")
    return jax.shard_map(
        per_device,
        mesh=split,
        in_specs=(
            P(shot, None, None, None, "brick", None),
            P(shot, None, "brick", None),
            P(),
            P(),
            P(),
        ),
        out_specs=P("brick", shot, None),
        check_vma=False,
    )
```

```python
import jax
import jax.numpy as jnp
from jax import lax
from jax.experimental import pallas as pl
from jax.experimental.pallas import tpu as pltpu
from jax.sharding import PartitionSpec as P

BLOCKS = 8


shift_beta = 0.5
relaxation = 0.8


def sine_taper(count, extent):
    positions = jnp.arange(count, dtype=jnp.int32).astype(jnp.float32)
    return jnp.sin(jnp.pi * (positions + 0.5) / extent)


def inverse_of(slow):
    real_d = 6.0 - slow
    imag_d = shift_beta * slow
    denominator = real_d * real_d + imag_d * imag_d
    scale = 1.0 / denominator
    return real_d * scale, imag_d * scale


def first_sweep(s0, s1, s2, s3, inv_re, inv_im, mask=None):
    f = (
        relaxation * (s0 * inv_re - s1 * inv_im),
        relaxation * (s0 * inv_im + s1 * inv_re),
        relaxation * (s2 * inv_re - s3 * inv_im),
        relaxation * (s2 * inv_im + s3 * inv_re),
    )
    if mask is None:
        return f
    return tuple(v * mask for v in f)


def gather_plane(rows8, plane, sub_ids):
    tile = jnp.broadcast_to(rows8[0][plane:plane + 1, :], rows8[0].shape)
    for i in range(1, len(rows8)):
        tile = jnp.where(sub_ids == i, jnp.broadcast_to(rows8[i][plane:plane + 1, :], tile.shape), tile)
    return tile


def boundary_kernel(mask_ref, src_hbm, sl_hbm, lo_ref, hi_ref, src_buf, sl_buf, sem):
    four = src_hbm.shape[0]
    planes = src_hbm.shape[2]
    copies = []
    for j, plane in enumerate((planes - 1, 0)):
        for k in range(four):
            copies.append(pltpu.make_async_copy(src_hbm.at[k, :, plane, :], src_buf.at[j, k], sem.at[j, k]))
        copies.append(pltpu.make_async_copy(sl_hbm.at[:, plane, :], sl_buf.at[j], sem.at[j, four]))
    for c in copies:
        c.start()
    for c in copies:
        c.wait()
    for j, (plane, out) in enumerate(((planes - 1, lo_ref), (0, hi_ref))):
        m = mask_ref[plane]
        inv_re, inv_im = inverse_of(sl_buf[j])
        f = first_sweep(src_buf[j, 0], src_buf[j, 1], src_buf[j, 2], src_buf[j, 3], inv_re, inv_im, m)
        for k in range(four):
            out[k] = f[k]


def boundary_planes(src4, slow, mask_col):
    four, wide_y, planes, wide_z = src4.shape
    face = jax.ShapeDtypeStruct((four, wide_y, wide_z), jnp.float32)
    vmem = pl.BlockSpec(memory_space=pltpu.VMEM)
    return pl.pallas_call(
        boundary_kernel,
        in_specs=[
            pl.BlockSpec(memory_space=pltpu.SMEM),
            pl.BlockSpec(memory_space=pl.ANY),
            pl.BlockSpec(memory_space=pl.ANY),
        ],
        out_specs=[vmem, vmem],
        out_shape=[face, face],
        scratch_shapes=[
            pltpu.VMEM((2, four, wide_y, wide_z), jnp.float32),
            pltpu.VMEM((2, wide_y, wide_z), jnp.float32),
            pltpu.SemaphoreType.DMA((2, four + 1)),
        ],
    )(mask_col, src4, slow)


def gradient_kernel(ty_ref, act_ref, src_ref, src_lo_ref, src_hi_ref, sl_ref, sl_lo_ref, sl_hi_ref, mask_ref, tx_ref,
                    tz_ref, out_ref, aux_ref, f1_s, inv_s, tp_s):
    active = act_ref[0] > 0

    @pl.when(jnp.logical_not(active))
    def _():
        out_ref[...] = jnp.zeros_like(out_ref)
        aux_ref[...] = jnp.zeros_like(aux_ref)

    @pl.when(active)
    def _():
        active_window(ty_ref, src_ref, src_lo_ref, src_hi_ref, sl_ref, sl_lo_ref, sl_hi_ref, mask_ref, tx_ref, tz_ref,
                      out_ref, aux_ref, f1_s, inv_s, tp_s)


def active_window(ty_ref, src_ref, src_lo_ref, src_hi_ref, sl_ref, sl_lo_ref, sl_hi_ref, mask_ref, tx_ref, tz_ref,
                  out_ref, aux_ref, f1_s, inv_s, tp_s):
    b = pl.program_id(0)
    nb = pl.num_programs(0)
    rows = src_ref.shape[1]
    mask = None

    def sweep_one(r, carry):
        inv_re, inv_im = inverse_of(sl_ref[r])
        inv_s[0, r] = inv_re
        inv_s[1, r] = inv_im
        f = first_sweep(src_ref[0, r], src_ref[1, r], src_ref[2, r], src_ref[3, r], inv_re, inv_im, mask)
        for k in range(4):
            f1_s[k, r + 1] = f[k]
        return carry

    lax.fori_loop(0, rows, sweep_one, 0, unroll=8)

    lo_keep = jnp.where(b > 0, 1.0, 0.0).astype(jnp.float32)
    hi_keep = jnp.where(b < nb - 1, 1.0, 0.0).astype(jnp.float32)
    for slot, s_ref, l_ref, keep in ((0, src_lo_ref, sl_lo_ref, lo_keep), (rows + 1, src_hi_ref, sl_hi_ref, hi_keep)):
        inv_re, inv_im = inverse_of(l_ref[0])
        f = first_sweep(s_ref[0, 0], s_ref[1, 0], s_ref[2, 0], s_ref[3, 0], inv_re, inv_im, mask)
        for k in range(4):
            f1_s[k, slot] = f[k] * keep

    shape = mask_ref.shape
    p_ids = lax.broadcasted_iota(jnp.int32, shape, 0)
    z_ids = lax.broadcasted_iota(jnp.int32, shape, 1)
    planes, width = shape
    tx = tx_ref[...]
    tz = tz_ref[...]

    def sweep_two(g, carry):
        base = pl.multiple_of(g * 8, 8)
        for i in range(8):
            r = base + i
            inv_re = inv_s[0, r]
            inv_im = inv_s[1, r]
            cur = []
            vals = []
            for k in range(4):
                c = f1_s[k, r + 1]
                acc = f1_s[k, r] + f1_s[k, r + 2]
                down = jnp.where(p_ids == 0, 0.0, pltpu.roll(c, 1, 0))
                acc = acc + down
                up = jnp.where(p_ids == planes - 1, 0.0, pltpu.roll(c, planes - 1, 0))
                acc = acc + up
                zm = jnp.where(z_ids == 0, 0.0, pltpu.roll(c, 1, 1))
                acc = acc + zm
                zp = jnp.where(z_ids == width - 1, 0.0, pltpu.roll(c, width - 1, 1))
                acc = acc + zp
                cur.append(c)
                vals.append(src_ref[k, r] + acc)
            upd = (
                vals[0] * inv_re - vals[1] * inv_im,
                vals[0] * inv_im + vals[1] * inv_re,
                vals[2] * inv_re - vals[3] * inv_im,
                vals[2] * inv_im + vals[3] * inv_re,
            )
            f2 = [(1.0 - relaxation) * cur[k] + relaxation * upd[k] for k in range(4)]
            imaging = f2[0] * f2[2] - f2[1] * f2[3] - shift_beta * (f2[0] * f2[3] + f2[1] * f2[2])
            taper = (ty_ref[b * rows + r] * tx) * tz
            for k, v in enumerate(f2 + [inv_re, inv_im, imaging * taper]):
                for h in range(2):
                    tp_s[k, h, i * planes:(i + 1) * planes, :] = v[:, h * 128:(h + 1) * 128]

        def plane_tile(k, plane):
            halves = [tp_s[k, h, pl.ds(plane, 8, stride=planes), :] for h in range(2)]
            return jnp.concatenate(halves, axis=1)

        for k in range(6):
            for j, plane in enumerate((0, planes - 1)):
                aux_ref[k, j, pl.ds(base, 8), :] = plane_tile(k, plane)
        for plane in range(1, planes - 1):
            out_ref[0, plane - 1, pl.ds(base, 8), :] = plane_tile(6, plane)
        return carry

    lax.fori_loop(0, rows // 8, sweep_two, 0, unroll=2)


def window_blocks(src4, slow, consts, ty, act):
    four, wide_y, planes, wide_z = src4.shape
    rows = wide_y // BLOCKS
    last = wide_y - 1

    def row_spec(pick):
        return pl.BlockSpec((four, 1, planes, wide_z), lambda b, t, a: (0, pick(b), 0, 0))

    def slow_row_spec(pick):
        return pl.BlockSpec((1, planes, wide_z), lambda b, t, a: (pick(b), 0, 0))

    below = lambda b: jnp.maximum(b * rows - 1, 0)
    above = lambda b: jnp.minimum(b * rows + rows, last)
    grid_spec = pltpu.PrefetchScalarGridSpec(
        num_scalar_prefetch=2,
        grid=(BLOCKS,),
        in_specs=[
            pl.BlockSpec((four, rows, planes, wide_z), lambda b, t, a: (0, b, 0, 0)),
            row_spec(below),
            row_spec(above),
            pl.BlockSpec((rows, planes, wide_z), lambda b, t, a: (b, 0, 0)),
            slow_row_spec(below),
            slow_row_spec(above),
            pl.BlockSpec((None, planes, wide_z), lambda b, t, a: (0, 0, 0)),
            pl.BlockSpec((None, planes, wide_z), lambda b, t, a: (1, 0, 0)),
            pl.BlockSpec((None, planes, wide_z), lambda b, t, a: (2, 0, 0)),
        ],
        out_specs=[
            pl.BlockSpec((1, planes - 2, rows, wide_z), lambda b, t, a: (b, 0, 0, 0)),
            pl.BlockSpec((6, 2, rows, wide_z), lambda b, t, a: (0, 0, b, 0)),
        ],
        scratch_shapes=[
            pltpu.VMEM((four, rows + 2, planes, wide_z), jnp.float32),
            pltpu.VMEM((2, rows, planes, wide_z), jnp.float32),
            pltpu.VMEM((7, 2, 8 * planes, wide_z // 2), jnp.float32),
        ],
    )
    return pl.pallas_call(
        gradient_kernel,
        grid_spec=grid_spec,
        out_shape=[
            jax.ShapeDtypeStruct((BLOCKS, planes - 2, rows, wide_z), jnp.float32),
            jax.ShapeDtypeStruct((6, 2, wide_y, wide_z), jnp.float32),
        ],
    )(ty, act, src4, src4, src4, slow, slow, slow, consts, consts, consts)


def halo_kernel(aux_ref, lo_ref, hi_ref, ty_ref, mask_ref, tx_ref, tz_ref, out_ref):
    rows = aux_ref.shape[2]
    planes = mask_ref.shape[0]
    tz = tz_ref[...]
    for g in range(rows // 8):
        span = pl.ds(g * 8, 8)
        ty = ty_ref[span, :]
        for j, plane, h_ref in ((0, 0, lo_ref), (1, planes - 1, hi_ref)):
            inv_re = aux_ref[4, j, span, :]
            inv_im = aux_ref[5, j, span, :]
            h = [h_ref[k, span, :] for k in range(4)]
            m = mask_ref[plane:plane + 1, :]
            d = (
                h[0] * inv_re - h[1] * inv_im,
                h[0] * inv_im + h[1] * inv_re,
                h[2] * inv_re - h[3] * inv_im,
                h[2] * inv_im + h[3] * inv_re,
            )
            f2 = [aux_ref[k, j, span, :] + relaxation * d[k] * m for k in range(4)]
            imaging = f2[0] * f2[2] - f2[1] * f2[3] - shift_beta * (f2[0] * f2[3] + f2[1] * f2[2])
            per_block = out_ref.shape[2]
            out_ref[(g * 8) // per_block, j, pl.ds((g * 8) % per_block, 8), :] = imaging * ((ty * tx_ref[plane:plane + 1, :]) * tz)


def edge_planes(aux, lo, hi, ty_col, consts):
    wide_y, wide_z = lo.shape[1:]
    rows = wide_y // 2
    four = lo.shape[0]
    planes = consts.shape[1]
    return pl.pallas_call(
        halo_kernel,
        grid=(2,),
        in_specs=[
            pl.BlockSpec((6, 2, rows, wide_z), lambda b: (0, 0, b, 0)),
            pl.BlockSpec((four, rows, wide_z), lambda b: (0, b, 0)),
            pl.BlockSpec((four, rows, wide_z), lambda b: (0, b, 0)),
            pl.BlockSpec((rows, 1), lambda b: (b, 0)),
            pl.BlockSpec((None, planes, wide_z), lambda b: (0, 0, 0)),
            pl.BlockSpec((None, planes, wide_z), lambda b: (1, 0, 0)),
            pl.BlockSpec((None, planes, wide_z), lambda b: (2, 0, 0)),
        ],
        out_specs=pl.BlockSpec((BLOCKS // 2, 2, wide_y // BLOCKS, wide_z), lambda b: (b, 0, 0, 0)),
        out_shape=jax.ShapeDtypeStruct((BLOCKS, 2, wide_y // BLOCKS, wide_z), jnp.float32),
    )(aux, lo, hi, ty_col, consts, consts, consts)


def per_device(sources, slowness, group_size, window_anchor, tile_slot):
    slowness_window = slowness[0]
    wide_y, planes, wide_z = slowness_window.shape
    brick_index = lax.axis_index("brick")
    z_index = lax.axis_index("z")
    x_index = lax.axis_index("xl")
    core_index = lax.axis_index("core")
    x_count = lax.axis_size("xl")
    core_count = lax.axis_size("core")
    shot_index = (z_index * x_count + x_index) * core_count + core_index
    brick_count = lax.axis_size("brick")
    shot_count_all = group_size.shape[0]
    extent = jnp.sum(jnp.where(jnp.arange(shot_count_all) == shot_index, group_size, 0)) * planes
    depth_ids = brick_index * planes + jnp.arange(planes, dtype=jnp.int32)
    active = depth_ids < extent
    mask_col = active.astype(jnp.float32)
    src4 = sources[0].reshape(4, wide_y, planes, wide_z)

    lo_send, hi_send = boundary_planes(src4, slowness_window, mask_col)
    up = [(i, i + 1) for i in range(brick_count - 1)]
    down = [(j, i) for i, j in up]
    lo = lax.ppermute(lo_send, "brick", up)
    hi = lax.ppermute(hi_send, "brick", down)

    extent_float = extent.astype(jnp.float32)
    depth_float = depth_ids.astype(jnp.float32)
    taper_x = jnp.where(active, jnp.sin(jnp.pi * (depth_float + 0.5) / extent_float), 0.0)
    taper_y = sine_taper(wide_y, float(wide_y))
    taper_z = sine_taper(wide_z, float(wide_z))
    consts = jnp.stack([
        jnp.broadcast_to(mask_col[:, None], (planes, wide_z)),
        jnp.broadcast_to(taper_x[:, None], (planes, wide_z)),
        jnp.broadcast_to(taper_z[None, :], (planes, wide_z)),
    ])
    whole_brick = (extent > brick_index * planes).astype(jnp.int32).reshape(1)
    interior, aux = window_blocks(src4, slowness_window, consts, taper_y, whole_brick)
    shot_count = lax.axis_size("z") * x_count * core_count
    tile_dev = tile_slot.shape[0] // shot_count
    partner = (z_index * x_count + (x_count - 1 - x_index)) * core_count + core_index
    slots = jnp.arange(tile_dev, dtype=jnp.int32)
    owners = jnp.concatenate([shot_index * tile_dev + slots, partner * tile_dev + slots])
    zs = jnp.arange(lax.axis_size("z"), dtype=jnp.int32)
    cs = jnp.arange(core_count, dtype=jnp.int32)
    held = ((zs[:, None] * x_count + x_index) * core_count + cs[None, :]).reshape(-1)
    piece_slots = tile_slot[window_anchor[held][:, None] + jnp.arange(BLOCKS, dtype=jnp.int32)[None, :]]
    match = owners[:, None, None] == piece_slots[None, :, :]
    tables = contribution_tables(match)
    swap = [(0, 1), (1, 0)]
    mid = lax.all_gather(interior[None], ("z", "core"), axis=0, tiled=True)
    mid, lo, hi = lax.optimization_barrier((mid, lo, hi))
    own_mid, other_mid = gather_sum(mid, tables)
    theirs_mid = lax.ppermute(other_mid, "xl", swap)
    edges = edge_planes(aux, lo, hi, taper_y[:, None], consts)
    rim = lax.all_gather(edges[None], ("z", "core"), axis=0, tiled=True)
    own_rim, other_rim = gather_sum(rim, tables)
    theirs_rim = lax.ppermute(other_rim, "xl", swap)
    mid_sum = own_mid + theirs_mid
    rim_sum = own_rim + theirs_rim
    summed = jnp.concatenate([rim_sum[:, :1], mid_sum, rim_sum[:, 1:]], axis=1)
    return jnp.transpose(summed, (0, 2, 1, 3)).reshape(1, tile_dev, -1)


def select_kernel(es_ref, eb_ref, eq_ref, n_ref, g_hbm, own_ref, other_ref, buf, sem):
    n = n_ref[0]
    depth = buf.shape[0]
    half = own_ref.shape[0]
    own_ref[...] = jnp.zeros_like(own_ref)
    other_ref[...] = jnp.zeros_like(other_ref)

    def copy(e, slot):
        return pltpu.make_async_copy(g_hbm.at[es_ref[e], eb_ref[e]], buf.at[slot], sem.at[slot])

    for e in range(depth):
        @pl.when(e < n)
        def _():
            copy(e, e).start()

    def body(e, carry):
        slot = e % depth
        copy(e, slot).wait()
        q = eq_ref[e]

        @pl.when(q < half)
        def _():
            mine = jnp.minimum(q, half - 1)
            own_ref[mine] = own_ref[mine] + buf[slot]

        @pl.when(q >= half)
        def _():
            theirs = jnp.maximum(q - half, 0)
            other_ref[theirs] = other_ref[theirs] + buf[slot]

        @pl.when(e + depth < n)
        def _():
            copy(e + depth, slot).start()

        return carry

    lax.fori_loop(0, n, body, 0)


def contribution_tables(match):
    owners, shots, blocks = match.shape
    valid = jnp.any(match, axis=2).reshape(-1)
    which_block = jnp.sum(jnp.where(match, jnp.arange(blocks, dtype=jnp.int32), 0), axis=2).reshape(-1)
    shot_of = jnp.broadcast_to(jnp.arange(shots, dtype=jnp.int32)[None, :], (owners, shots)).reshape(-1)
    owner_of = jnp.broadcast_to(jnp.arange(owners, dtype=jnp.int32)[:, None], (owners, shots)).reshape(-1)
    count = owners * shots
    position = jnp.where(valid, jnp.cumsum(valid.astype(jnp.int32)) - 1, count)
    empty = jnp.zeros((count,), jnp.int32)
    es = empty.at[position].set(shot_of, mode="drop")
    eb = empty.at[position].set(which_block, mode="drop")
    eq = empty.at[position].set(owner_of, mode="drop")
    n = jnp.sum(valid.astype(jnp.int32)).reshape(1)
    return owners, (es, eb, eq, n)


def gather_sum(gathered, tables):
    owners, (es, eb, eq, n) = tables
    cell_shape = gathered.shape[2:]
    return pl.pallas_call(
        select_kernel,
        grid_spec=pltpu.PrefetchScalarGridSpec(
            num_scalar_prefetch=4,
            grid=(1,),
            in_specs=[pl.BlockSpec(memory_space=pl.ANY)],
            out_specs=[pl.BlockSpec((owners // 2,) + cell_shape, lambda i, *_: (0,) * (1 + len(cell_shape)))] * 2,
            scratch_shapes=[
                pltpu.VMEM((8,) + cell_shape, jnp.float32),
                pltpu.SemaphoreType.DMA((8,)),
            ],
        ),
        out_shape=[jax.ShapeDtypeStruct((owners // 2,) + cell_shape, jnp.float32)] * 2,
    )(es, eb, eq, n, gathered)


def solution(mesh):
    devices = mesh.devices
    shots, bricks = devices.shape
    split = jax.sharding.Mesh(devices.reshape(shots // 4, 2, 2, bricks), ("z", "xl", "core", "brick"))
    shot = ("z", "xl", "core")
    return jax.shard_map(
        per_device,
        mesh=split,
        in_specs=(
            P(shot, None, None, None, "brick", None),
            P(shot, None, "brick", None),
            P(),
            P(),
            P(),
        ),
        out_specs=P("brick", shot, None),
        check_vma=False,
    )
```

```python
import jax
import jax.numpy as jnp
from jax import lax
from jax.experimental import pallas as pl
from jax.experimental.pallas import tpu as pltpu
from jax.sharding import PartitionSpec as P

BLOCKS = 8


shift_beta = 0.5
relaxation = 0.8


def sine_taper(count, extent):
    positions = jnp.arange(count, dtype=jnp.int32).astype(jnp.float32)
    return jnp.sin(jnp.pi * (positions + 0.5) / extent)


def inverse_of(slow):
    real_d = 6.0 - slow
    imag_d = shift_beta * slow
    denominator = real_d * real_d + imag_d * imag_d
    scale = 1.0 / denominator
    return real_d * scale, imag_d * scale


def first_sweep(s0, s1, s2, s3, inv_re, inv_im, mask=None):
    f = (
        relaxation * (s0 * inv_re - s1 * inv_im),
        relaxation * (s0 * inv_im + s1 * inv_re),
        relaxation * (s2 * inv_re - s3 * inv_im),
        relaxation * (s2 * inv_im + s3 * inv_re),
    )
    if mask is None:
        return f
    return tuple(v * mask for v in f)


def gather_plane(rows8, plane, sub_ids):
    tile = jnp.broadcast_to(rows8[0][plane:plane + 1, :], rows8[0].shape)
    for i in range(1, len(rows8)):
        tile = jnp.where(sub_ids == i, jnp.broadcast_to(rows8[i][plane:plane + 1, :], tile.shape), tile)
    return tile


def boundary_kernel(mask_ref, src_hbm, sl_hbm, lo_ref, hi_ref, src_buf, sl_buf, sem):
    four = src_hbm.shape[0]
    planes = src_hbm.shape[2]
    copies = []
    for j, plane in enumerate((planes - 1, 0)):
        for k in range(four):
            copies.append(pltpu.make_async_copy(src_hbm.at[k, :, plane, :], src_buf.at[j, k], sem.at[j, k]))
        copies.append(pltpu.make_async_copy(sl_hbm.at[:, plane, :], sl_buf.at[j], sem.at[j, four]))
    for c in copies:
        c.start()
    for c in copies:
        c.wait()
    for j, (plane, out) in enumerate(((planes - 1, lo_ref), (0, hi_ref))):
        m = mask_ref[plane]
        inv_re, inv_im = inverse_of(sl_buf[j])
        f = first_sweep(src_buf[j, 0], src_buf[j, 1], src_buf[j, 2], src_buf[j, 3], inv_re, inv_im, m)
        for k in range(four):
            out[k] = f[k]


def boundary_planes(src4, slow, mask_col):
    four, wide_y, planes, wide_z = src4.shape
    face = jax.ShapeDtypeStruct((four, wide_y, wide_z), jnp.float32)
    vmem = pl.BlockSpec(memory_space=pltpu.VMEM)
    return pl.pallas_call(
        boundary_kernel,
        in_specs=[
            pl.BlockSpec(memory_space=pltpu.SMEM),
            pl.BlockSpec(memory_space=pl.ANY),
            pl.BlockSpec(memory_space=pl.ANY),
        ],
        out_specs=[vmem, vmem],
        out_shape=[face, face],
        scratch_shapes=[
            pltpu.VMEM((2, four, wide_y, wide_z), jnp.float32),
            pltpu.VMEM((2, wide_y, wide_z), jnp.float32),
            pltpu.SemaphoreType.DMA((2, four + 1)),
        ],
    )(mask_col, src4, slow)


def gradient_kernel(ty_ref, act_ref, src_ref, src_lo_ref, src_hi_ref, sl_ref, sl_lo_ref, sl_hi_ref, mask_ref, tx_ref,
                    tz_ref, out_ref, aux_ref, f1_s, inv_s, tp_s):
    active = act_ref[0] > 0

    @pl.when(jnp.logical_not(active))
    def _():
        out_ref[...] = jnp.zeros_like(out_ref)
        aux_ref[...] = jnp.zeros_like(aux_ref)

    @pl.when(active)
    def _():
        active_window(ty_ref, src_ref, src_lo_ref, src_hi_ref, sl_ref, sl_lo_ref, sl_hi_ref, mask_ref, tx_ref, tz_ref,
                      out_ref, aux_ref, f1_s, inv_s, tp_s)


def active_window(ty_ref, src_ref, src_lo_ref, src_hi_ref, sl_ref, sl_lo_ref, sl_hi_ref, mask_ref, tx_ref, tz_ref,
                  out_ref, aux_ref, f1_s, inv_s, tp_s):
    b = pl.program_id(0)
    nb = pl.num_programs(0)
    rows = src_ref.shape[1]
    mask = None

    def sweep_one(r, carry):
        inv_re, inv_im = inverse_of(sl_ref[r])
        inv_s[0, r] = inv_re
        inv_s[1, r] = inv_im
        f = first_sweep(src_ref[0, r], src_ref[1, r], src_ref[2, r], src_ref[3, r], inv_re, inv_im, mask)
        for k in range(4):
            f1_s[k, r + 1] = f[k]
        return carry

    lax.fori_loop(0, rows, sweep_one, 0, unroll=8)

    lo_keep = jnp.where(b > 0, 1.0, 0.0).astype(jnp.float32)
    hi_keep = jnp.where(b < nb - 1, 1.0, 0.0).astype(jnp.float32)
    for slot, s_ref, l_ref, keep in ((0, src_lo_ref, sl_lo_ref, lo_keep), (rows + 1, src_hi_ref, sl_hi_ref, hi_keep)):
        inv_re, inv_im = inverse_of(l_ref[0])
        f = first_sweep(s_ref[0, 0], s_ref[1, 0], s_ref[2, 0], s_ref[3, 0], inv_re, inv_im, mask)
        for k in range(4):
            f1_s[k, slot] = f[k] * keep

    shape = mask_ref.shape
    p_ids = lax.broadcasted_iota(jnp.int32, shape, 0)
    z_ids = lax.broadcasted_iota(jnp.int32, shape, 1)
    planes, width = shape
    tx = tx_ref[...]
    tz = tz_ref[...]

    def sweep_two(g, carry):
        base = pl.multiple_of(g * 8, 8)
        for i in range(8):
            r = base + i
            inv_re = inv_s[0, r]
            inv_im = inv_s[1, r]
            cur = []
            vals = []
            for k in range(4):
                c = f1_s[k, r + 1]
                acc = f1_s[k, r] + f1_s[k, r + 2]
                down = jnp.where(p_ids == 0, 0.0, pltpu.roll(c, 1, 0))
                acc = acc + down
                up = jnp.where(p_ids == planes - 1, 0.0, pltpu.roll(c, planes - 1, 0))
                acc = acc + up
                zm = jnp.where(z_ids == 0, 0.0, pltpu.roll(c, 1, 1))
                acc = acc + zm
                zp = jnp.where(z_ids == width - 1, 0.0, pltpu.roll(c, width - 1, 1))
                acc = acc + zp
                cur.append(c)
                vals.append(src_ref[k, r] + acc)
            upd = (
                vals[0] * inv_re - vals[1] * inv_im,
                vals[0] * inv_im + vals[1] * inv_re,
                vals[2] * inv_re - vals[3] * inv_im,
                vals[2] * inv_im + vals[3] * inv_re,
            )
            f2 = [(1.0 - relaxation) * cur[k] + relaxation * upd[k] for k in range(4)]
            imaging = f2[0] * f2[2] - f2[1] * f2[3] - shift_beta * (f2[0] * f2[3] + f2[1] * f2[2])
            taper = (ty_ref[b * rows + r] * tx) * tz
            for k, v in enumerate(f2 + [inv_re, inv_im, imaging * taper]):
                for h in range(2):
                    tp_s[k, h, i * planes:(i + 1) * planes, :] = v[:, h * 128:(h + 1) * 128]

        def plane_tile(k, plane):
            halves = [tp_s[k, h, pl.ds(plane, 8, stride=planes), :] for h in range(2)]
            return jnp.concatenate(halves, axis=1)

        for k in range(6):
            for j, plane in enumerate((0, planes - 1)):
                aux_ref[k, j, pl.ds(base, 8), :] = plane_tile(k, plane)
        for plane in range(1, planes - 1):
            out_ref[0, plane - 1, pl.ds(base, 8), :] = plane_tile(6, plane)
        return carry

    lax.fori_loop(0, rows // 8, sweep_two, 0, unroll=2)


def window_blocks(src4, slow, consts, ty, act):
    four, wide_y, planes, wide_z = src4.shape
    rows = wide_y // BLOCKS
    last = wide_y - 1

    def row_spec(pick):
        return pl.BlockSpec((four, 1, planes, wide_z), lambda b, t, a: (0, pick(b), 0, 0))

    def slow_row_spec(pick):
        return pl.BlockSpec((1, planes, wide_z), lambda b, t, a: (pick(b), 0, 0))

    below = lambda b: jnp.maximum(b * rows - 1, 0)
    above = lambda b: jnp.minimum(b * rows + rows, last)
    grid_spec = pltpu.PrefetchScalarGridSpec(
        num_scalar_prefetch=2,
        grid=(BLOCKS,),
        in_specs=[
            pl.BlockSpec((four, rows, planes, wide_z), lambda b, t, a: (0, b, 0, 0)),
            row_spec(below),
            row_spec(above),
            pl.BlockSpec((rows, planes, wide_z), lambda b, t, a: (b, 0, 0)),
            slow_row_spec(below),
            slow_row_spec(above),
            pl.BlockSpec((None, planes, wide_z), lambda b, t, a: (0, 0, 0)),
            pl.BlockSpec((None, planes, wide_z), lambda b, t, a: (1, 0, 0)),
            pl.BlockSpec((None, planes, wide_z), lambda b, t, a: (2, 0, 0)),
        ],
        out_specs=[
            pl.BlockSpec((1, planes - 2, rows, wide_z), lambda b, t, a: (b, 0, 0, 0)),
            pl.BlockSpec((6, 2, rows, wide_z), lambda b, t, a: (0, 0, b, 0)),
        ],
        scratch_shapes=[
            pltpu.VMEM((four, rows + 2, planes, wide_z), jnp.float32),
            pltpu.VMEM((2, rows, planes, wide_z), jnp.float32),
            pltpu.VMEM((7, 2, 8 * planes, wide_z // 2), jnp.float32),
        ],
    )
    return pl.pallas_call(
        gradient_kernel,
        grid_spec=grid_spec,
        out_shape=[
            jax.ShapeDtypeStruct((BLOCKS, planes - 2, rows, wide_z), jnp.float32),
            jax.ShapeDtypeStruct((6, 2, wide_y, wide_z), jnp.float32),
        ],
    )(ty, act, src4, src4, src4, slow, slow, slow, consts, consts, consts)


def halo_kernel(aux_ref, lo_ref, hi_ref, ty_ref, mask_ref, tx_ref, tz_ref, out_ref):
    rows = aux_ref.shape[2]
    planes = mask_ref.shape[0]
    tz = tz_ref[...]
    for g in range(rows // 8):
        span = pl.ds(g * 8, 8)
        ty = ty_ref[span, :]
        for j, plane, h_ref in ((0, 0, lo_ref), (1, planes - 1, hi_ref)):
            inv_re = aux_ref[4, j, span, :]
            inv_im = aux_ref[5, j, span, :]
            h = [h_ref[k, span, :] for k in range(4)]
            m = mask_ref[plane:plane + 1, :]
            d = (
                h[0] * inv_re - h[1] * inv_im,
                h[0] * inv_im + h[1] * inv_re,
                h[2] * inv_re - h[3] * inv_im,
                h[2] * inv_im + h[3] * inv_re,
            )
            f2 = [aux_ref[k, j, span, :] + relaxation * d[k] * m for k in range(4)]
            imaging = f2[0] * f2[2] - f2[1] * f2[3] - shift_beta * (f2[0] * f2[3] + f2[1] * f2[2])
            per_block = out_ref.shape[2]
            out_ref[(g * 8) // per_block, j, pl.ds((g * 8) % per_block, 8), :] = imaging * ((ty * tx_ref[plane:plane + 1, :]) * tz)


def edge_planes(aux, lo, hi, ty_col, consts):
    wide_y, wide_z = lo.shape[1:]
    rows = wide_y // 2
    four = lo.shape[0]
    planes = consts.shape[1]
    return pl.pallas_call(
        halo_kernel,
        grid=(2,),
        in_specs=[
            pl.BlockSpec((6, 2, rows, wide_z), lambda b: (0, 0, b, 0)),
            pl.BlockSpec((four, rows, wide_z), lambda b: (0, b, 0)),
            pl.BlockSpec((four, rows, wide_z), lambda b: (0, b, 0)),
            pl.BlockSpec((rows, 1), lambda b: (b, 0)),
            pl.BlockSpec((None, planes, wide_z), lambda b: (0, 0, 0)),
            pl.BlockSpec((None, planes, wide_z), lambda b: (1, 0, 0)),
            pl.BlockSpec((None, planes, wide_z), lambda b: (2, 0, 0)),
        ],
        out_specs=pl.BlockSpec((BLOCKS // 2, 2, wide_y // BLOCKS, wide_z), lambda b: (b, 0, 0, 0)),
        out_shape=jax.ShapeDtypeStruct((BLOCKS, 2, wide_y // BLOCKS, wide_z), jnp.float32),
    )(aux, lo, hi, ty_col, consts, consts, consts)


def per_device(sources, slowness, group_size, window_anchor, tile_slot):
    slowness_window = slowness[0]
    wide_y, planes, wide_z = slowness_window.shape
    brick_index = lax.axis_index("brick")
    z_index = lax.axis_index("z")
    x_index = lax.axis_index("xl")
    core_index = lax.axis_index("core")
    x_count = lax.axis_size("xl")
    core_count = lax.axis_size("core")
    shot_index = (z_index * x_count + x_index) * core_count + core_index
    brick_count = lax.axis_size("brick")
    shot_count_all = group_size.shape[0]
    extent = jnp.sum(jnp.where(jnp.arange(shot_count_all) == shot_index, group_size, 0)) * planes
    depth_ids = brick_index * planes + jnp.arange(planes, dtype=jnp.int32)
    active = depth_ids < extent
    mask_col = active.astype(jnp.float32)
    src4 = sources[0].reshape(4, wide_y, planes, wide_z)

    lo_send, hi_send = boundary_planes(src4, slowness_window, mask_col)
    up = [(i, i + 1) for i in range(brick_count - 1)]
    down = [(j, i) for i, j in up]
    lo = lax.ppermute(lo_send, "brick", up)
    hi = lax.ppermute(hi_send, "brick", down)

    extent_float = extent.astype(jnp.float32)
    depth_float = depth_ids.astype(jnp.float32)
    taper_x = jnp.where(active, jnp.sin(jnp.pi * (depth_float + 0.5) / extent_float), 0.0)
    taper_y = sine_taper(wide_y, float(wide_y))
    taper_z = sine_taper(wide_z, float(wide_z))
    consts = jnp.stack([
        jnp.broadcast_to(mask_col[:, None], (planes, wide_z)),
        jnp.broadcast_to(taper_x[:, None], (planes, wide_z)),
        jnp.broadcast_to(taper_z[None, :], (planes, wide_z)),
    ])
    whole_brick = (extent > brick_index * planes).astype(jnp.int32).reshape(1)
    interior, aux = window_blocks(src4, slowness_window, consts, taper_y, whole_brick)
    shot_count = lax.axis_size("z") * x_count * core_count
    tile_dev = tile_slot.shape[0] // shot_count
    partner = (z_index * x_count + (x_count - 1 - x_index)) * core_count + core_index
    slots = jnp.arange(tile_dev, dtype=jnp.int32)
    owners = jnp.concatenate([shot_index * tile_dev + slots, partner * tile_dev + slots])
    zs = jnp.arange(lax.axis_size("z"), dtype=jnp.int32)
    cs = jnp.arange(core_count, dtype=jnp.int32)
    held = ((zs[:, None] * x_count + x_index) * core_count + cs[None, :]).reshape(-1)
    piece_slots = tile_slot[window_anchor[held][:, None] + jnp.arange(BLOCKS, dtype=jnp.int32)[None, :]]
    match = owners[:, None, None] == piece_slots[None, :, :]
    tables = contribution_tables(match)
    swap = [(0, 1), (1, 0)]
    mid = lax.all_gather(interior[None], ("z", "core"), axis=0, tiled=True)
    mid, lo, hi = lax.optimization_barrier((mid, lo, hi))
    own_mid, other_mid = gather_sum(mid, tables)
    theirs_mid = lax.ppermute(other_mid, "xl", swap)
    edges = edge_planes(aux, lo, hi, taper_y[:, None], consts)
    rim = lax.all_gather(edges[None], ("z", "core"), axis=0, tiled=True)
    own_rim, other_rim = gather_sum(rim, tables)
    theirs_rim = lax.ppermute(other_rim, "xl", swap)
    mid_sum = own_mid + theirs_mid
    rim_sum = own_rim + theirs_rim
    summed = jnp.concatenate([rim_sum[:, :1], mid_sum, rim_sum[:, 1:]], axis=1)
    return jnp.transpose(summed, (0, 2, 1, 3)).reshape(1, tile_dev, -1)


def select_kernel(es_ref, eb_ref, eq_ref, n_ref, g_hbm, own_ref, other_ref, buf, sem):
    n = n_ref[0]
    depth = buf.shape[0]
    half = own_ref.shape[0]
    own_ref[...] = jnp.zeros_like(own_ref)
    other_ref[...] = jnp.zeros_like(other_ref)

    def copy(e, slot):
        return pltpu.make_async_copy(g_hbm.at[es_ref[e], eb_ref[e]], buf.at[slot], sem.at[slot])

    for e in range(depth):
        @pl.when(e < n)
        def _():
            copy(e, e).start()

    def body(e, carry):
        slot = e % depth
        copy(e, slot).wait()
        q = eq_ref[e]

        @pl.when(q < half)
        def _():
            mine = jnp.minimum(q, half - 1)
            own_ref[mine] = own_ref[mine] + buf[slot]

        @pl.when(q >= half)
        def _():
            theirs = jnp.maximum(q - half, 0)
            other_ref[theirs] = other_ref[theirs] + buf[slot]

        @pl.when(e + depth < n)
        def _():
            copy(e + depth, slot).start()

        return carry

    lax.fori_loop(0, n, body, 0)


def contribution_tables(match):
    owners, shots, blocks = match.shape
    valid = jnp.any(match, axis=2).reshape(-1)
    which_block = jnp.sum(jnp.where(match, jnp.arange(blocks, dtype=jnp.int32), 0), axis=2).reshape(-1)
    shot_of = jnp.broadcast_to(jnp.arange(shots, dtype=jnp.int32)[None, :], (owners, shots)).reshape(-1)
    owner_of = jnp.broadcast_to(jnp.arange(owners, dtype=jnp.int32)[:, None], (owners, shots)).reshape(-1)
    count = owners * shots
    position = jnp.where(valid, jnp.cumsum(valid.astype(jnp.int32)) - 1, count)
    empty = jnp.zeros((count,), jnp.int32)
    es = empty.at[position].set(shot_of, mode="drop")
    eb = empty.at[position].set(which_block, mode="drop")
    eq = empty.at[position].set(owner_of, mode="drop")
    n = jnp.sum(valid.astype(jnp.int32)).reshape(1)
    return owners, (es, eb, eq, n)


def gather_sum(gathered, tables):
    owners, (es, eb, eq, n) = tables
    cell_shape = gathered.shape[2:]
    return pl.pallas_call(
        select_kernel,
        grid_spec=pltpu.PrefetchScalarGridSpec(
            num_scalar_prefetch=4,
            grid=(1,),
            in_specs=[pl.BlockSpec(memory_space=pl.ANY)],
            out_specs=[pl.BlockSpec((owners // 2,) + cell_shape, lambda i, *_: (0,) * (1 + len(cell_shape)))] * 2,
            scratch_shapes=[
                pltpu.VMEM((16,) + cell_shape, jnp.float32),
                pltpu.SemaphoreType.DMA((16,)),
            ],
        ),
        out_shape=[jax.ShapeDtypeStruct((owners // 2,) + cell_shape, jnp.float32)] * 2,
    )(es, eb, eq, n, gathered)


def solution(mesh):
    devices = mesh.devices
    shots, bricks = devices.shape
    split = jax.sharding.Mesh(devices.reshape(shots // 4, 2, 2, bricks), ("z", "xl", "core", "brick"))
    shot = ("z", "xl", "core")
    return jax.shard_map(
        per_device,
        mesh=split,
        in_specs=(
            P(shot, None, None, None, "brick", None),
            P(shot, None, "brick", None),
            P(),
            P(),
            P(),
        ),
        out_specs=P("brick", shot, None),
        check_vma=False,
    )
```

```python
import jax
import jax.numpy as jnp
from jax import lax
from jax.experimental import pallas as pl
from jax.experimental.pallas import tpu as pltpu
from jax.sharding import PartitionSpec as P

BLOCKS = 8


shift_beta = 0.5
relaxation = 0.8


def sine_taper(count, extent):
    positions = jnp.arange(count, dtype=jnp.int32).astype(jnp.float32)
    return jnp.sin(jnp.pi * (positions + 0.5) / extent)


def inverse_of(slow):
    real_d = 6.0 - slow
    imag_d = shift_beta * slow
    denominator = real_d * real_d + imag_d * imag_d
    scale = 1.0 / denominator
    return real_d * scale, imag_d * scale


def first_sweep(s0, s1, s2, s3, inv_re, inv_im, mask=None):
    f = (
        relaxation * (s0 * inv_re - s1 * inv_im),
        relaxation * (s0 * inv_im + s1 * inv_re),
        relaxation * (s2 * inv_re - s3 * inv_im),
        relaxation * (s2 * inv_im + s3 * inv_re),
    )
    if mask is None:
        return f
    return tuple(v * mask for v in f)


def gather_plane(rows8, plane, sub_ids):
    tile = jnp.broadcast_to(rows8[0][plane:plane + 1, :], rows8[0].shape)
    for i in range(1, len(rows8)):
        tile = jnp.where(sub_ids == i, jnp.broadcast_to(rows8[i][plane:plane + 1, :], tile.shape), tile)
    return tile


def boundary_kernel(mask_ref, src_hbm, sl_hbm, lo_ref, hi_ref, src_buf, sl_buf, sem):
    four = src_hbm.shape[0]
    planes = src_hbm.shape[2]
    copies = []
    for j, plane in enumerate((planes - 1, 0)):
        for k in range(four):
            copies.append(pltpu.make_async_copy(src_hbm.at[k, :, plane, :], src_buf.at[j, k], sem.at[j, k]))
        copies.append(pltpu.make_async_copy(sl_hbm.at[:, plane, :], sl_buf.at[j], sem.at[j, four]))
    for c in copies:
        c.start()
    for c in copies:
        c.wait()
    for j, (plane, out) in enumerate(((planes - 1, lo_ref), (0, hi_ref))):
        m = mask_ref[plane]
        inv_re, inv_im = inverse_of(sl_buf[j])
        f = first_sweep(src_buf[j, 0], src_buf[j, 1], src_buf[j, 2], src_buf[j, 3], inv_re, inv_im, m)
        for k in range(four):
            out[k] = f[k]


def boundary_planes(src4, slow, mask_col):
    four, wide_y, planes, wide_z = src4.shape
    face = jax.ShapeDtypeStruct((four, wide_y, wide_z), jnp.float32)
    vmem = pl.BlockSpec(memory_space=pltpu.VMEM)
    return pl.pallas_call(
        boundary_kernel,
        in_specs=[
            pl.BlockSpec(memory_space=pltpu.SMEM),
            pl.BlockSpec(memory_space=pl.ANY),
            pl.BlockSpec(memory_space=pl.ANY),
        ],
        out_specs=[vmem, vmem],
        out_shape=[face, face],
        scratch_shapes=[
            pltpu.VMEM((2, four, wide_y, wide_z), jnp.float32),
            pltpu.VMEM((2, wide_y, wide_z), jnp.float32),
            pltpu.SemaphoreType.DMA((2, four + 1)),
        ],
    )(mask_col, src4, slow)


def gradient_kernel(ty_ref, act_ref, src_ref, src_lo_ref, src_hi_ref, sl_ref, sl_lo_ref, sl_hi_ref, mask_ref, tx_ref,
                    tz_ref, out_ref, aux_ref, f1_s, inv_s, tp_s):
    active = act_ref[0] > 0

    @pl.when(jnp.logical_not(active))
    def _():
        out_ref[...] = jnp.zeros_like(out_ref)
        aux_ref[...] = jnp.zeros_like(aux_ref)

    @pl.when(active)
    def _():
        active_window(ty_ref, src_ref, src_lo_ref, src_hi_ref, sl_ref, sl_lo_ref, sl_hi_ref, mask_ref, tx_ref, tz_ref,
                      out_ref, aux_ref, f1_s, inv_s, tp_s)


def active_window(ty_ref, src_ref, src_lo_ref, src_hi_ref, sl_ref, sl_lo_ref, sl_hi_ref, mask_ref, tx_ref, tz_ref,
                  out_ref, aux_ref, f1_s, inv_s, tp_s):
    b = pl.program_id(0)
    nb = pl.num_programs(0)
    rows = src_ref.shape[1]
    mask = None

    def sweep_one(r, carry):
        inv_re, inv_im = inverse_of(sl_ref[r])
        inv_s[0, r] = inv_re
        inv_s[1, r] = inv_im
        f = first_sweep(src_ref[0, r], src_ref[1, r], src_ref[2, r], src_ref[3, r], inv_re, inv_im, mask)
        for k in range(4):
            f1_s[k, r + 1] = f[k]
        return carry

    lax.fori_loop(0, rows, sweep_one, 0, unroll=16)

    lo_keep = jnp.where(b > 0, 1.0, 0.0).astype(jnp.float32)
    hi_keep = jnp.where(b < nb - 1, 1.0, 0.0).astype(jnp.float32)
    for slot, s_ref, l_ref, keep in ((0, src_lo_ref, sl_lo_ref, lo_keep), (rows + 1, src_hi_ref, sl_hi_ref, hi_keep)):
        inv_re, inv_im = inverse_of(l_ref[0])
        f = first_sweep(s_ref[0, 0], s_ref[1, 0], s_ref[2, 0], s_ref[3, 0], inv_re, inv_im, mask)
        for k in range(4):
            f1_s[k, slot] = f[k] * keep

    shape = mask_ref.shape
    p_ids = lax.broadcasted_iota(jnp.int32, shape, 0)
    z_ids = lax.broadcasted_iota(jnp.int32, shape, 1)
    planes, width = shape
    tx = tx_ref[...]
    tz = tz_ref[...]

    def sweep_two(g, carry):
        base = pl.multiple_of(g * 8, 8)
        for i in range(8):
            r = base + i
            inv_re = inv_s[0, r]
            inv_im = inv_s[1, r]
            cur = []
            vals = []
            for k in range(4):
                c = f1_s[k, r + 1]
                acc = f1_s[k, r] + f1_s[k, r + 2]
                down = jnp.where(p_ids == 0, 0.0, pltpu.roll(c, 1, 0))
                acc = acc + down
                up = jnp.where(p_ids == planes - 1, 0.0, pltpu.roll(c, planes - 1, 0))
                acc = acc + up
                zm = jnp.where(z_ids == 0, 0.0, pltpu.roll(c, 1, 1))
                acc = acc + zm
                zp = jnp.where(z_ids == width - 1, 0.0, pltpu.roll(c, width - 1, 1))
                acc = acc + zp
                cur.append(c)
                vals.append(src_ref[k, r] + acc)
            upd = (
                vals[0] * inv_re - vals[1] * inv_im,
                vals[0] * inv_im + vals[1] * inv_re,
                vals[2] * inv_re - vals[3] * inv_im,
                vals[2] * inv_im + vals[3] * inv_re,
            )
            f2 = [(1.0 - relaxation) * cur[k] + relaxation * upd[k] for k in range(4)]
            imaging = f2[0] * f2[2] - f2[1] * f2[3] - shift_beta * (f2[0] * f2[3] + f2[1] * f2[2])
            taper = (ty_ref[b * rows + r] * tx) * tz
            for k, v in enumerate(f2 + [inv_re, inv_im, imaging * taper]):
                for h in range(2):
                    tp_s[k, h, i * planes:(i + 1) * planes, :] = v[:, h * 128:(h + 1) * 128]

        def plane_tile(k, plane):
            halves = [tp_s[k, h, pl.ds(plane, 8, stride=planes), :] for h in range(2)]
            return jnp.concatenate(halves, axis=1)

        for k in range(6):
            for j, plane in enumerate((0, planes - 1)):
                aux_ref[k, j, pl.ds(base, 8), :] = plane_tile(k, plane)
        for plane in range(1, planes - 1):
            out_ref[0, plane - 1, pl.ds(base, 8), :] = plane_tile(6, plane)
        return carry

    lax.fori_loop(0, rows // 8, sweep_two, 0, unroll=2)


def window_blocks(src4, slow, consts, ty, act):
    four, wide_y, planes, wide_z = src4.shape
    rows = wide_y // BLOCKS
    last = wide_y - 1

    def row_spec(pick):
        return pl.BlockSpec((four, 1, planes, wide_z), lambda b, t, a: (0, pick(b), 0, 0))

    def slow_row_spec(pick):
        return pl.BlockSpec((1, planes, wide_z), lambda b, t, a: (pick(b), 0, 0))

    below = lambda b: jnp.maximum(b * rows - 1, 0)
    above = lambda b: jnp.minimum(b * rows + rows, last)
    grid_spec = pltpu.PrefetchScalarGridSpec(
        num_scalar_prefetch=2,
        grid=(BLOCKS,),
        in_specs=[
            pl.BlockSpec((four, rows, planes, wide_z), lambda b, t, a: (0, b, 0, 0)),
            row_spec(below),
            row_spec(above),
            pl.BlockSpec((rows, planes, wide_z), lambda b, t, a: (b, 0, 0)),
            slow_row_spec(below),
            slow_row_spec(above),
            pl.BlockSpec((None, planes, wide_z), lambda b, t, a: (0, 0, 0)),
            pl.BlockSpec((None, planes, wide_z), lambda b, t, a: (1, 0, 0)),
            pl.BlockSpec((None, planes, wide_z), lambda b, t, a: (2, 0, 0)),
        ],
        out_specs=[
            pl.BlockSpec((1, planes - 2, rows, wide_z), lambda b, t, a: (b, 0, 0, 0)),
            pl.BlockSpec((6, 2, rows, wide_z), lambda b, t, a: (0, 0, b, 0)),
        ],
        scratch_shapes=[
            pltpu.VMEM((four, rows + 2, planes, wide_z), jnp.float32),
            pltpu.VMEM((2, rows, planes, wide_z), jnp.float32),
            pltpu.VMEM((7, 2, 8 * planes, wide_z // 2), jnp.float32),
        ],
    )
    return pl.pallas_call(
        gradient_kernel,
        grid_spec=grid_spec,
        out_shape=[
            jax.ShapeDtypeStruct((BLOCKS, planes - 2, rows, wide_z), jnp.float32),
            jax.ShapeDtypeStruct((6, 2, wide_y, wide_z), jnp.float32),
        ],
    )(ty, act, src4, src4, src4, slow, slow, slow, consts, consts, consts)


def halo_kernel(aux_ref, lo_ref, hi_ref, ty_ref, mask_ref, tx_ref, tz_ref, out_ref):
    rows = aux_ref.shape[2]
    planes = mask_ref.shape[0]
    tz = tz_ref[...]
    for g in range(rows // 8):
        span = pl.ds(g * 8, 8)
        ty = ty_ref[span, :]
        for j, plane, h_ref in ((0, 0, lo_ref), (1, planes - 1, hi_ref)):
            inv_re = aux_ref[4, j, span, :]
            inv_im = aux_ref[5, j, span, :]
            h = [h_ref[k, span, :] for k in range(4)]
            m = mask_ref[plane:plane + 1, :]
            d = (
                h[0] * inv_re - h[1] * inv_im,
                h[0] * inv_im + h[1] * inv_re,
                h[2] * inv_re - h[3] * inv_im,
                h[2] * inv_im + h[3] * inv_re,
            )
            f2 = [aux_ref[k, j, span, :] + relaxation * d[k] * m for k in range(4)]
            imaging = f2[0] * f2[2] - f2[1] * f2[3] - shift_beta * (f2[0] * f2[3] + f2[1] * f2[2])
            per_block = out_ref.shape[2]
            out_ref[(g * 8) // per_block, j, pl.ds((g * 8) % per_block, 8), :] = imaging * ((ty * tx_ref[plane:plane + 1, :]) * tz)


def edge_planes(aux, lo, hi, ty_col, consts):
    wide_y, wide_z = lo.shape[1:]
    rows = wide_y // 2
    four = lo.shape[0]
    planes = consts.shape[1]
    return pl.pallas_call(
        halo_kernel,
        grid=(2,),
        in_specs=[
            pl.BlockSpec((6, 2, rows, wide_z), lambda b: (0, 0, b, 0)),
            pl.BlockSpec((four, rows, wide_z), lambda b: (0, b, 0)),
            pl.BlockSpec((four, rows, wide_z), lambda b: (0, b, 0)),
            pl.BlockSpec((rows, 1), lambda b: (b, 0)),
            pl.BlockSpec((None, planes, wide_z), lambda b: (0, 0, 0)),
            pl.BlockSpec((None, planes, wide_z), lambda b: (1, 0, 0)),
            pl.BlockSpec((None, planes, wide_z), lambda b: (2, 0, 0)),
        ],
        out_specs=pl.BlockSpec((BLOCKS // 2, 2, wide_y // BLOCKS, wide_z), lambda b: (b, 0, 0, 0)),
        out_shape=jax.ShapeDtypeStruct((BLOCKS, 2, wide_y // BLOCKS, wide_z), jnp.float32),
    )(aux, lo, hi, ty_col, consts, consts, consts)


def per_device(sources, slowness, group_size, window_anchor, tile_slot):
    slowness_window = slowness[0]
    wide_y, planes, wide_z = slowness_window.shape
    brick_index = lax.axis_index("brick")
    z_index = lax.axis_index("z")
    x_index = lax.axis_index("xl")
    core_index = lax.axis_index("core")
    x_count = lax.axis_size("xl")
    core_count = lax.axis_size("core")
    shot_index = (z_index * x_count + x_index) * core_count + core_index
    brick_count = lax.axis_size("brick")
    shot_count_all = group_size.shape[0]
    extent = jnp.sum(jnp.where(jnp.arange(shot_count_all) == shot_index, group_size, 0)) * planes
    depth_ids = brick_index * planes + jnp.arange(planes, dtype=jnp.int32)
    active = depth_ids < extent
    mask_col = active.astype(jnp.float32)
    src4 = sources[0].reshape(4, wide_y, planes, wide_z)

    lo_send, hi_send = boundary_planes(src4, slowness_window, mask_col)
    up = [(i, i + 1) for i in range(brick_count - 1)]
    down = [(j, i) for i, j in up]
    lo = lax.ppermute(lo_send, "brick", up)
    hi = lax.ppermute(hi_send, "brick", down)

    extent_float = extent.astype(jnp.float32)
    depth_float = depth_ids.astype(jnp.float32)
    taper_x = jnp.where(active, jnp.sin(jnp.pi * (depth_float + 0.5) / extent_float), 0.0)
    taper_y = sine_taper(wide_y, float(wide_y))
    taper_z = sine_taper(wide_z, float(wide_z))
    consts = jnp.stack([
        jnp.broadcast_to(mask_col[:, None], (planes, wide_z)),
        jnp.broadcast_to(taper_x[:, None], (planes, wide_z)),
        jnp.broadcast_to(taper_z[None, :], (planes, wide_z)),
    ])
    whole_brick = (extent > brick_index * planes).astype(jnp.int32).reshape(1)
    interior, aux = window_blocks(src4, slowness_window, consts, taper_y, whole_brick)
    shot_count = lax.axis_size("z") * x_count * core_count
    tile_dev = tile_slot.shape[0] // shot_count
    partner = (z_index * x_count + (x_count - 1 - x_index)) * core_count + core_index
    slots = jnp.arange(tile_dev, dtype=jnp.int32)
    owners = jnp.concatenate([shot_index * tile_dev + slots, partner * tile_dev + slots])
    zs = jnp.arange(lax.axis_size("z"), dtype=jnp.int32)
    cs = jnp.arange(core_count, dtype=jnp.int32)
    held = ((zs[:, None] * x_count + x_index) * core_count + cs[None, :]).reshape(-1)
    piece_slots = tile_slot[window_anchor[held][:, None] + jnp.arange(BLOCKS, dtype=jnp.int32)[None, :]]
    match = owners[:, None, None] == piece_slots[None, :, :]
    tables = contribution_tables(match)
    swap = [(0, 1), (1, 0)]
    mid = lax.all_gather(interior[None], ("z", "core"), axis=0, tiled=True)
    mid, lo, hi = lax.optimization_barrier((mid, lo, hi))
    own_mid, other_mid = gather_sum(mid, tables)
    theirs_mid = lax.ppermute(other_mid, "xl", swap)
    edges = edge_planes(aux, lo, hi, taper_y[:, None], consts)
    rim = lax.all_gather(edges[None], ("z", "core"), axis=0, tiled=True)
    own_rim, other_rim = gather_sum(rim, tables)
    theirs_rim = lax.ppermute(other_rim, "xl", swap)
    mid_sum = own_mid + theirs_mid
    rim_sum = own_rim + theirs_rim
    summed = jnp.concatenate([rim_sum[:, :1], mid_sum, rim_sum[:, 1:]], axis=1)
    return jnp.transpose(summed, (0, 2, 1, 3)).reshape(1, tile_dev, -1)


def select_kernel(es_ref, eb_ref, eq_ref, n_ref, g_hbm, own_ref, other_ref, buf, sem):
    n = n_ref[0]
    depth = buf.shape[0]
    half = own_ref.shape[0]
    own_ref[...] = jnp.zeros_like(own_ref)
    other_ref[...] = jnp.zeros_like(other_ref)

    def copy(e, slot):
        return pltpu.make_async_copy(g_hbm.at[es_ref[e], eb_ref[e]], buf.at[slot], sem.at[slot])

    for e in range(depth):
        @pl.when(e < n)
        def _():
            copy(e, e).start()

    def body(e, carry):
        slot = e % depth
        copy(e, slot).wait()
        q = eq_ref[e]

        @pl.when(q < half)
        def _():
            mine = jnp.minimum(q, half - 1)
            own_ref[mine] = own_ref[mine] + buf[slot]

        @pl.when(q >= half)
        def _():
            theirs = jnp.maximum(q - half, 0)
            other_ref[theirs] = other_ref[theirs] + buf[slot]

        @pl.when(e + depth < n)
        def _():
            copy(e + depth, slot).start()

        return carry

    lax.fori_loop(0, n, body, 0)


def contribution_tables(match):
    owners, shots, blocks = match.shape
    valid = jnp.any(match, axis=2).reshape(-1)
    which_block = jnp.sum(jnp.where(match, jnp.arange(blocks, dtype=jnp.int32), 0), axis=2).reshape(-1)
    shot_of = jnp.broadcast_to(jnp.arange(shots, dtype=jnp.int32)[None, :], (owners, shots)).reshape(-1)
    owner_of = jnp.broadcast_to(jnp.arange(owners, dtype=jnp.int32)[:, None], (owners, shots)).reshape(-1)
    count = owners * shots
    position = jnp.where(valid, jnp.cumsum(valid.astype(jnp.int32)) - 1, count)
    empty = jnp.zeros((count,), jnp.int32)
    es = empty.at[position].set(shot_of, mode="drop")
    eb = empty.at[position].set(which_block, mode="drop")
    eq = empty.at[position].set(owner_of, mode="drop")
    n = jnp.sum(valid.astype(jnp.int32)).reshape(1)
    return owners, (es, eb, eq, n)


def gather_sum(gathered, tables):
    owners, (es, eb, eq, n) = tables
    cell_shape = gathered.shape[2:]
    return pl.pallas_call(
        select_kernel,
        grid_spec=pltpu.PrefetchScalarGridSpec(
            num_scalar_prefetch=4,
            grid=(1,),
            in_specs=[pl.BlockSpec(memory_space=pl.ANY)],
            out_specs=[pl.BlockSpec((owners // 2,) + cell_shape, lambda i, *_: (0,) * (1 + len(cell_shape)))] * 2,
            scratch_shapes=[
                pltpu.VMEM((8,) + cell_shape, jnp.float32),
                pltpu.SemaphoreType.DMA((8,)),
            ],
        ),
        out_shape=[jax.ShapeDtypeStruct((owners // 2,) + cell_shape, jnp.float32)] * 2,
    )(es, eb, eq, n, gathered)


def solution(mesh):
    devices = mesh.devices
    shots, bricks = devices.shape
    split = jax.sharding.Mesh(devices.reshape(shots // 4, 2, 2, bricks), ("z", "xl", "core", "brick"))
    shot = ("z", "xl", "core")
    return jax.shard_map(
        per_device,
        mesh=split,
        in_specs=(
            P(shot, None, None, None, "brick", None),
            P(shot, None, "brick", None),
            P(),
            P(),
            P(),
        ),
        out_specs=P("brick", shot, None),
        check_vma=False,
    )
```
